32 devices in a mesh: slab: 2 (over x), curve: 16 (over z, y, core).
Axes of the slice: x: 2, y: 2, z: 4, core: 2. Of those that a mesh axis runs over, the one named last changes fastest.
Arguments:
- state: float32 [512, 8, 512], P(('slab', 'curve')), may hold values from -6 to 6
- velocity: bfloat16 [3, 64, 512], P(None, None, ('slab', 'curve')), may hold values from -4 to 4
- pre_exp: float32 [512], P(('slab', 'curve')), may hold values from 0.5 to 5
- stoich: float32 [8], replicated, may hold values from -3 to 3
- neighbours: int32 [512, 6], P(('slab', 'curve')), may hold values from 0 to 511, as said below
- switch: int32 [512], P(('slab', 'curve')), may hold values from 0 to 1
- new_owner: int32 [512], P(('slab', 'curve')), may hold values from 0 to 15, as said below
Outputs:
- state7_out: float32 [384, 8, 512], P(('slab', 'curve'))
- state3_out: float32 [512, 512], P(('slab', 'curve'))
The draws below stay inside these ranges and needn't reach their ends.
Inputs may be any that keep to these rules, and one draw needn't show every extreme that they name: Element g lives on device g // 16 of the mesh flattened slab first. The neighbour across face 0 (1) is on the same device or on the previous (next) curve index with wrap, same slab; across faces 2 and 3 on the same device; across face 4 (5) on the same device or the previous (next) slab with wrap, same curve index. The relation is symmetric: the neighbour of neighbours[g, s] across face s xor 1 is g, and face nodes match in the stated order. Each device has exactly 8 faces 0, 8 faces 1, 16 faces 4 and 16 faces 5 whose neighbour lies on another device. `new_owner`: the new owner is in the same slab: the element's own curve index or one next to it with wrap; elements with switch 1 keep their own. From one device at most 2 elements go to each of its two neighbours, and afterwards a device holds at most 12 elements with switch 0; both bounds are reached in every draw.
All inputs are finite; a program needn't handle non-finite values.
Results may differ from the reference program's by a relative error of at most 0.0005.
Values may be sent and summed in bfloat16 or wider, within the bound.
No kernel may reach another device: no remote copies, remote signals or barrier semaphores. Data moves between devices by JAX's collectives and lax.ppermute only.
A program may use at most 64 MiB of HBM per device.

```python
import math
import jax
import jax.numpy as jnp
import numpy as np
from jax import lax

P7 = 8
P3 = 4
FIELDS = 8
BX = 2
BY = 8
BZ = 1
NODES7 = 512
NODES3 = 64
E_DEV = 16
MOVE_CAP = 2
HOLD7 = 12
SLABS = 2
PIECES = 16
ELEMENTS = 512


def mesh_plan(key):
    plan_key = jax.random.fold_in(key, 417)
    local_count = BX * BY * BZ
    devices = SLABS * PIECES
    key_list = jax.random.split(plan_key, 8)
    labels = jax.vmap(lambda sub_key: jax.random.permutation(sub_key, local_count))(jax.random.split(key_list[0], devices)).astype(jnp.int32)
    places = jnp.argsort(labels, axis=1).astype(jnp.int32)
    device_grid = jnp.arange(devices, dtype=jnp.int32)[:, None]
    slab_of = device_grid // PIECES
    curve_of = device_grid % PIECES
    along_x = places // (BY * BZ)
    along_y = places // BZ % BY
    along_z = places % BZ
    flat_labels = labels.reshape(-1)

    def global_id(slab_new, curve_new, x_new, y_new, z_new):
        device_new = slab_new * PIECES + curve_new
        return device_new * local_count + flat_labels[device_new * local_count + x_new * BY * BZ + y_new * BZ + z_new]
    lower_x = along_x > 0
    upper_x = along_x < BX - 1
    lower_z = along_z > 0
    upper_z = along_z < BZ - 1
    sides = [global_id(slab_of, jnp.where(lower_x, curve_of, (curve_of + PIECES - 1) % PIECES), jnp.where(lower_x, along_x - 1, BX - 1), along_y, along_z), global_id(slab_of, jnp.where(upper_x, curve_of, (curve_of + 1) % PIECES), jnp.where(upper_x, along_x + 1, 0), along_y, along_z), global_id(slab_of, curve_of, along_x, (along_y + BY - 1) % BY, along_z), global_id(slab_of, curve_of, along_x, (along_y + 1) % BY, along_z), global_id(jnp.where(lower_z, slab_of, (slab_of + SLABS - 1) % SLABS), curve_of, along_x, along_y, jnp.where(lower_z, along_z - 1, BZ - 1)), global_id(jnp.where(upper_z, slab_of, (slab_of + 1) % SLABS), curve_of, along_x, along_y, jnp.where(upper_z, along_z + 1, 0))]
    neighbours = jnp.stack(sides, axis=-1).reshape(devices * local_count, 6).astype(jnp.int32)
    parity = jax.random.randint(key_list[1], (SLABS, 1), 0, 2)
    donor_mask = (curve_of + parity[slab_of[:, 0]]) % 2 == 0
    forced_pair = jax.random.randint(key_list[2], (SLABS, 1), 0, PIECES // 2)
    forced_curve = 2 * forced_pair + parity
    is_forced = curve_of == forced_curve[slab_of[:, 0]]
    donor_switch = jax.random.randint(key_list[3], (devices, 1), 0, 2 * MOVE_CAP + 1)
    taker_switch = jax.random.randint(key_list[4], (devices, 1), 4 * MOVE_CAP, 6 * MOVE_CAP + 1)
    switched_count = jnp.where(donor_mask, jnp.where(is_forced, 0, donor_switch), taker_switch)
    switch_order = jax.vmap(lambda sub_key: jax.random.permutation(sub_key, local_count))(jax.random.split(key_list[5], devices)).astype(jnp.int32)
    switched = switch_order < switched_count
    shed_count = jnp.where(donor_mask, 2 * MOVE_CAP - switched_count, 0)
    lower_bound = jnp.maximum(shed_count - MOVE_CAP, 0)
    upper_bound = jnp.minimum(shed_count, MOVE_CAP)
    left_count = jax.random.randint(key_list[6], (devices, 1), lower_bound, upper_bound + 1)
    right_count = shed_count - left_count
    mover_order = jax.vmap(lambda sub_key: jax.random.permutation(sub_key, local_count))(jax.random.split(key_list[7], devices)).astype(jnp.int32)
    mover_key = jnp.where(switched, local_count + mover_order, mover_order)
    mover_rank = jnp.argsort(jnp.argsort(mover_key, axis=1), axis=1).astype(jnp.int32)
    to_left = mover_rank < left_count
    to_right = (mover_rank >= left_count) & (mover_rank < left_count + right_count)
    owner_curve = jnp.where(to_left, (curve_of + PIECES - 1) % PIECES, jnp.where(to_right, (curve_of + 1) % PIECES, curve_of))
    return (neighbours, switched.astype(jnp.int32).reshape(-1), owner_curve.astype(jnp.int32).reshape(-1))


def draw_neighbours(key, part):
    return mesh_plan(key)[0]


def draw_switch(key, part):
    return mesh_plan(key)[1]


def draw_new_owner(key, part):
    return mesh_plan(key)[2]


def shard_levels(rng, shape, cuts, low, largest):
    def one(dim, parts):
        heights = jax.random.uniform(jax.random.fold_in(jax.random.fold_in(rng, 6), dim), (parts,), jnp.float32, low / len(cuts), largest / len(cuts))
        return jnp.repeat(jnp.exp(heights), shape[dim] // parts).reshape((-1,) + (1,) * (len(shape) - dim - 1))

    loudness = one(*cuts[0])
    for cut in cuts[1:]:
        loudness = loudness * one(*cut)
    return loudness


def normal_values(stream_key, shape, deviation, limit, cuts=(), held_as=jnp.bfloat16):
    values = deviation * jax.random.normal(stream_key, shape, jnp.float32)
    if cuts:
        values = values * shard_levels(stream_key, shape, cuts, -0.22, 0.18)
    return jnp.clip(values, -limit, limit).astype(held_as)


def setup_inputs(seed: int = 0) -> dict:
    streams_of = jax.random.split(jax.random.key(seed), 8)
    state = normal_values(streams_of[0], (ELEMENTS, FIELDS, NODES7), 1.0, 6.0, ((0, 32),), jnp.float32)
    velocity = normal_values(streams_of[1], (3, NODES3, ELEMENTS), 1.0, 4.0, ((2, 32),))
    pre_exp = jnp.clip(jnp.exp(math.log(5.0) - 2.3025851 * jax.random.uniform(streams_of[2], (ELEMENTS,), jnp.float32) ** shard_levels(streams_of[2], (ELEMENTS,), ((0, 32),), -0.2, 0.2)), 0.5, 5.0)
    stoich = normal_values(streams_of[3], (FIELDS,), 1.0, 3.0, (), jnp.float32)
    neighbours = draw_neighbours(jax.random.fold_in(streams_of[7], 71), 0)
    switch = draw_switch(jax.random.fold_in(streams_of[7], 71), 0)
    new_owner = draw_new_owner(jax.random.fold_in(streams_of[7], 71), 0)
    return {"state": state, "velocity": velocity, "pre_exp": pre_exp, "stoich": stoich, "neighbours": neighbours, "switch": switch, "new_owner": new_owner}


TIME_STEP = 0.002
ACTIVATION = 1.5
SIDE_SIGNS = (-1.0, 1.0, -1.0, 1.0, -1.0, 1.0)
OPPOSITE = (1, 0, 3, 2, 5, 4)


def lobatto_points(number):
    return -np.cos(np.pi * np.arange(number) / (number - 1))


def lagrange_weights(points):
    weights = np.ones(points.shape[0])
    for row_id in range(points.shape[0]):
        for col_id in range(points.shape[0]):
            if col_id != row_id:
                weights[row_id] = weights[row_id] / (points[row_id] - points[col_id])
    return weights


def derivative_matrix(points):
    weights = lagrange_weights(points)
    number = points.shape[0]
    matrix = np.zeros((number, number))
    for row_id in range(number):
        for col_id in range(number):
            if col_id != row_id:
                matrix[row_id, col_id] = weights[col_id] / weights[row_id] / (points[row_id] - points[col_id])
        matrix[row_id, row_id] = -np.sum(matrix[row_id])
    return matrix


def interpolation_matrix(source, target):
    matrix = np.ones((target.shape[0], source.shape[0]))
    for col_id in range(source.shape[0]):
        for other_id in range(source.shape[0]):
            if other_id != col_id:
                matrix[:, col_id] = matrix[:, col_id] * (target - source[other_id]) / (source[col_id] - source[other_id])
    return matrix


def spread_three(matrix, identity):
    return (np.kron(matrix, np.kron(identity, identity)), np.kron(identity, np.kron(matrix, identity)), np.kron(identity, np.kron(identity, matrix)))


def make_tables():
    fine_points = lobatto_points(P7)
    coarse_points = lobatto_points(P3)
    fine_derivs = spread_three(derivative_matrix(fine_points), np.eye(P7))
    coarse_derivs = spread_three(derivative_matrix(coarse_points), np.eye(P3))
    downward = interpolation_matrix(fine_points, coarse_points)
    upward = interpolation_matrix(coarse_points, fine_points)
    fine_stack = jnp.asarray(np.concatenate([matrix.T for matrix in fine_derivs], axis=0), jnp.float32).astype(jnp.bfloat16)
    coarse_stack = jnp.asarray(np.stack(coarse_derivs, axis=0), jnp.float32).astype(jnp.bfloat16)
    lift_table = jnp.asarray(np.kron(upward, np.kron(upward, upward)), jnp.float32).astype(jnp.bfloat16)
    projection = jnp.asarray(np.kron(downward, np.kron(downward, downward)), jnp.float32)
    mortar_up = jnp.asarray(np.kron(upward, upward), jnp.float32)
    mortar_down = jnp.asarray(np.kron(downward, downward), jnp.float32)
    return fine_stack, coarse_stack, lift_table, projection, mortar_up, mortar_down


def take_faces(volume):
    extent = volume.shape[-1]
    final_index = extent - 1
    pieces = (volume[:, :, 0], volume[:, :, final_index], volume[:, :, :, 0], volume[:, :, :, final_index], volume[:, :, :, :, 0], volume[:, :, :, :, final_index])
    return jnp.stack([face_part.reshape(volume.shape[0], volume.shape[1], extent * extent) for face_part in pieces], axis=1)


def add_faces(volume, face_terms):
    extent = volume.shape[-1]
    face_grids = face_terms.reshape(face_terms.shape[0], 6, face_terms.shape[2], extent, extent)
    total = volume
    for side_id in range(6):
        axis_id = 2 + side_id // 2
        piece = jnp.expand_dims(face_grids[:, side_id], axis_id)
        widths = [(0, 0)] * 5
        widths[axis_id] = (0, extent - 1) if side_id % 2 == 0 else (extent - 1, 0)
        total = total + jnp.pad(piece, widths)
    return total


def normal_speed(vel_faces):
    return jnp.stack([SIDE_SIGNS[side_id] * vel_faces[:, side_id, side_id // 2] for side_id in range(6)], axis=1)


def source_term(values, pre_exp, stoich):
    rate = pre_exp[:, None] * jnp.exp(-ACTIVATION * jnp.exp(-values[:, 0])) * values[:, 1] * values[:, 2]
    return stoich[None, :, None] * rate[:, None, :]


def fine_traces(values):
    elem_count, field_count, node_count = values.shape
    faces = take_faces(values.reshape(elem_count, field_count, P7, P7, P7)).astype(jnp.bfloat16)
    return faces.reshape(elem_count, 6, field_count * P7 * P7)


def coarse_traces(values, mortar_up):
    elem_count, field_count, node_count = values.shape
    faces = take_faces(values.reshape(elem_count, field_count, P3, P3, P3))
    mortar = jnp.einsum("mk,esfk->esfm", mortar_up, faces, precision=lax.Precision.HIGHEST)
    return mortar.astype(jnp.bfloat16).reshape(elem_count, 6, field_count * P7 * P7)


def fine_rate(values, fine_vel, pre_exp, stoich, own_tr, near_tr, fine_stack):
    elem_count, field_count, node_count = values.shape
    fluxes = (fine_vel.astype(jnp.float32)[:, None] * values[:, :, None]).astype(jnp.bfloat16)
    divergence = jnp.dot(fluxes.reshape(elem_count * field_count, 3 * node_count), fine_stack, preferred_element_type=jnp.float32).reshape(elem_count, field_count, node_count)
    result = source_term(values, pre_exp, stoich) - divergence
    normal_vel = normal_speed(take_faces(fine_vel.astype(jnp.float32).reshape(elem_count, 3, P7, P7, P7)))
    difference = (own_tr.astype(jnp.float32) - near_tr.astype(jnp.float32)).reshape(elem_count, 6, field_count, P7 * P7)
    jump_term = jnp.minimum(normal_vel, 0.0)[:, :, None] * difference
    lift_coef = P7 * (P7 - 1) / 2.0
    return add_faces(result.reshape(elem_count, field_count, P7, P7, P7), lift_coef * jump_term).reshape(elem_count, field_count, node_count)


def coarse_rate(values, coarse_vel, pre_exp, stoich, own_tr, near_tr, coarse_stack, mortar_up, mortar_down):
    elem_count, field_count, node_count = values.shape
    fluxes = (coarse_vel.astype(jnp.float32)[:, None] * values[:, :, None]).astype(jnp.bfloat16)
    divergence = jnp.einsum("dnm,efdm->efn", coarse_stack.astype(jnp.float32), fluxes.astype(jnp.float32))
    result = source_term(values, pre_exp, stoich) - divergence
    normal_vel = normal_speed(take_faces(coarse_vel.astype(jnp.float32).reshape(elem_count, 3, P3, P3, P3)))
    mortar_vel = jnp.einsum("mk,esk->esm", mortar_up, normal_vel, precision=lax.Precision.HIGHEST)
    difference = (own_tr.astype(jnp.float32) - near_tr.astype(jnp.float32)).reshape(elem_count, 6, field_count, P7 * P7)
    jump_term = jnp.minimum(mortar_vel, 0.0)[:, :, None] * difference
    coarse_jump = jnp.einsum("km,esfm->esfk", mortar_down, jump_term, precision=lax.Precision.HIGHEST)
    lift_coef = P3 * (P3 - 1) / 2.0
    return add_faces(result.reshape(elem_count, field_count, P3, P3, P3), lift_coef * coarse_jump).reshape(elem_count, field_count, node_count)


def blocked_fine(values, fine_vel, pre_exp, stoich, own_tr, near_tr, fine_stack):
    blocks = values.shape[0] // E_DEV

    def one_block(pieces):
        return fine_rate(pieces[0], pieces[1], pieces[2], stoich, pieces[3], pieces[4], fine_stack)

    packed = tuple(member.reshape((blocks, E_DEV) + member.shape[1:]) for member in (values, fine_vel, pre_exp, own_tr, near_tr))
    return lax.map(one_block, packed).reshape(values.shape)


def reference(state, velocity, pre_exp, stoich, neighbours, switch, new_owner):
    fine_stack, coarse_stack, lift_table, projection, mortar_up, mortar_down = make_tables()
    total_count = state.shape[0]
    trace_width = FIELDS * P7 * P7
    coarse_vel = jnp.transpose(velocity, (2, 0, 1))
    fine_vel = jnp.einsum("nm,edm->edn", lift_table.astype(jnp.float32), coarse_vel.astype(jnp.float32)).astype(jnp.bfloat16)
    gather_index = (neighbours * 6 + jnp.asarray(OPPOSITE, jnp.int32)[None, :]).astype(jnp.int32)

    def near_of(own_tr):
        return own_tr.reshape(total_count * 6, trace_width)[gather_index]

    def fine_only(current):
        own_tr = fine_traces(current)
        return blocked_fine(current, fine_vel, pre_exp, stoich, own_tr, near_of(own_tr), fine_stack)

    first_section = state + TIME_STEP * fine_only(state)
    after_one = 0.5 * (state + first_section + TIME_STEP * fine_only(first_section))
    coarse = jnp.einsum("mn,efn->efm", projection, after_one, precision=lax.Precision.HIGHEST)
    switched = (switch == 1)[:, None, None]

    def mixed(fine_now, coarse_now):
        own_fine = fine_traces(fine_now)
        own_coarse = coarse_traces(coarse_now, mortar_up)
        near_tr = near_of(jnp.where(switched, own_coarse, own_fine))
        fine_part = blocked_fine(fine_now, fine_vel, pre_exp, stoich, own_fine, near_tr, fine_stack)
        coarse_part = coarse_rate(coarse_now, coarse_vel, pre_exp, stoich, own_coarse, near_tr, coarse_stack, mortar_up, mortar_down)
        return fine_part, coarse_part

    fine_step, coarse_step = mixed(after_one, coarse)
    first_fine = after_one + TIME_STEP * fine_step
    first_coarse = coarse + TIME_STEP * coarse_step
    fine_again, coarse_again = mixed(first_fine, first_coarse)
    final_fine = 0.5 * (after_one + first_fine + TIME_STEP * fine_again)
    final_coarse = 0.5 * (coarse + first_coarse + TIME_STEP * coarse_again)

    element_ids = jnp.arange(total_count, dtype=jnp.int32)
    home_device = element_ids // E_DEV
    owner_dev = ((home_device // PIECES) * PIECES + new_owner).astype(jnp.int32)
    held_mask = switch == 0
    device_total = SLABS * PIECES
    sort_key = jnp.where(held_mask, owner_dev * total_count + element_ids, device_total * total_count + element_ids).astype(jnp.int32)
    ordering = jnp.argsort(sort_key).astype(jnp.int32)
    counts = jax.ops.segment_sum(held_mask.astype(jnp.int32), owner_dev, num_segments=device_total).astype(jnp.int32)
    starts = (jnp.cumsum(counts) - counts).astype(jnp.int32)
    sorted_owner = owner_dev[ordering]
    sorted_held = held_mask[ordering]
    slot_index = (element_ids - starts[sorted_owner]).astype(jnp.int32)
    target_rows = jnp.where(sorted_held, sorted_owner * HOLD7 + slot_index, device_total * HOLD7).astype(jnp.int32)
    state7_out = jnp.zeros((device_total * HOLD7, FIELDS, NODES7), jnp.float32).at[target_rows].set(final_fine[ordering], mode="drop")
    state3_out = jnp.where(switched, final_coarse, 0.0).reshape(total_count, FIELDS * NODES3)
    return state7_out, state3_out
```

```python
import functools

import jax
import jax.numpy as jnp
import ml_dtypes
import numpy as np
from jax import lax
from jax.experimental import pallas as pl
from jax.experimental.pallas import tpu as pltpu
from jax.sharding import PartitionSpec as P

P7 = 8
P3 = 4
MOVE_CAP = 2
HOLD7 = 12
LANE = 128

TIME_STEP = 0.002
ACTIVATION = 1.5
SIDE_SIGNS = (-1.0, 1.0, -1.0, 1.0, -1.0, 1.0)
OPPOSITE = (1, 0, 3, 2, 5, 4)
SEND_FACES = (0, 1, 4, 5)
missing_id = 1 << 30

f32 = jnp.float32
bf16 = jnp.bfloat16


def shifted(value, axis, steps):
    count = lax.axis_size(axis)
    pairs = [(source, (source + steps) % count) for source in range(count)]
    return lax.ppermute(value, axis, pairs)


def lobatto_points(number):
    return -np.cos(np.pi * np.arange(number) / (number - 1))


def lagrange_weights(points):
    weights = np.ones(points.shape[0])
    for row_id in range(points.shape[0]):
        for col_id in range(points.shape[0]):
            if col_id != row_id:
                weights[row_id] = weights[row_id] / (points[row_id] - points[col_id])
    return weights


def derivative_matrix(points):
    weights = lagrange_weights(points)
    number = points.shape[0]
    matrix = np.zeros((number, number))
    for row_id in range(number):
        for col_id in range(number):
            if col_id != row_id:
                matrix[row_id, col_id] = (
                    weights[col_id] / weights[row_id] / (points[row_id] - points[col_id])
                )
        matrix[row_id, row_id] = -np.sum(matrix[row_id])
    return matrix


def interpolation_matrix(source, target):
    matrix = np.ones((target.shape[0], source.shape[0]))
    for col_id in range(source.shape[0]):
        for other_id in range(source.shape[0]):
            if other_id != col_id:
                matrix[:, col_id] = (
                    matrix[:, col_id]
                    * (target - source[other_id])
                    / (source[col_id] - source[other_id])
                )
    return matrix


def spread_three(matrix, identity):
    return (
        np.kron(matrix, np.kron(identity, identity)),
        np.kron(identity, np.kron(matrix, identity)),
        np.kron(identity, np.kron(identity, matrix)),
    )


def face_nodes(extent):
    grid = np.arange(extent**3).reshape(extent, extent, extent)
    last = extent - 1
    pieces = (grid[0], grid[last], grid[:, 0], grid[:, last], grid[:, :, 0], grid[:, :, last])
    return [piece.reshape(-1) for piece in pieces]


def to_bf16(x):
    return np.asarray(np.asarray(x, np.float32).astype(ml_dtypes.bfloat16))


def split_parts(x):
    x = np.asarray(x, np.float32)
    hi = x.astype(ml_dtypes.bfloat16)
    rest = x - hi.astype(np.float32)
    mid = rest.astype(ml_dtypes.bfloat16)
    lo = (rest - mid.astype(np.float32)).astype(ml_dtypes.bfloat16)
    return np.stack([hi, mid, lo])


def make_tables():
    fine_points = lobatto_points(P7)
    coarse_points = lobatto_points(P3)
    fine_derivs = spread_three(derivative_matrix(fine_points), np.eye(P7))
    coarse_derivs = spread_three(derivative_matrix(coarse_points), np.eye(P3))
    downward = interpolation_matrix(fine_points, coarse_points)
    upward = interpolation_matrix(coarse_points, fine_points)
    d7t = np.stack([to_bf16(m.T) for m in fine_derivs])
    d3t = np.stack([to_bf16(m).T for m in coarse_derivs])
    lift_table = to_bf16(np.kron(upward, np.kron(upward, upward)))
    projection = np.asarray(np.kron(downward, np.kron(downward, downward)), np.float32)
    mortar_up = np.asarray(np.kron(upward, upward), np.float32)
    mortar_down = np.asarray(np.kron(downward, downward), np.float32)
    nodes7 = face_nodes(P7)
    nodes3 = face_nodes(P3)
    n7 = P7**3
    n3 = P3**3
    g7 = np.zeros((n7, 6 * LANE), np.float32)
    tm = np.zeros((n3, 6 * LANE), np.float32)
    mds = np.zeros((6 * LANE, n3), np.float32)
    for side in range(6):
        for q, node in enumerate(nodes7[side]):
            g7[node, side * LANE + q] = 1.0
        for k, node in enumerate(nodes3[side]):
            tm[node, side * LANE : side * LANE + P7 * P7] = mortar_up[:, k]
            mds[side * LANE : side * LANE + P7 * P7, node] = mortar_down[k, :]
    send_cols = np.concatenate([np.arange(s * LANE, (s + 1) * LANE) for s in SEND_FACES])
    tables = {
        "d7t": to_bf16(d7t),
        "d3t": to_bf16(d3t),
        "lift": lift_table,
        "mortar_up": mortar_up,
        "g7": to_bf16(g7),
        "s7": to_bf16(g7.T),
        "g7s": to_bf16(g7[:, send_cols]),
        "tm": split_parts(tm),
        "tms": split_parts(tm[:, send_cols]),
        "mds": split_parts(mds),
        "pjt": split_parts(projection.T),
        "nodes7": nodes7,
        "nodes3": nodes3,
    }
    return tables


def _dot(a, b):
    return jnp.dot(a, b, preferred_element_type=f32)


def _split(x):
    hi = x.astype(bf16)
    rest = x - hi.astype(f32)
    mid = rest.astype(bf16)
    lo = (rest - mid.astype(f32)).astype(bf16)
    return hi, mid, lo


def _exact_left(x, table):
    hi, mid, lo = _split(x)
    return (_dot(hi, table) + _dot(mid, table)) + _dot(lo, table)


def _exact_right(table, x):
    hi, mid, lo = _split(x)
    return (_dot(table, hi) + _dot(table, mid)) + _dot(table, lo)


def _full(x, parts_ref):
    xh, xm, xl = _split(x)
    bh = parts_ref[0]
    bm = parts_ref[1]
    bl = parts_ref[2]
    return _dot(xh, bh) + (_dot(xh, bm) + _dot(xm, bh)) + (
        _dot(xh, bl) + _dot(xm, bm) + _dot(xl, bh)
    )


def _rate_source(values, pre, stc, bc, sel, local):
    picked = _exact_right(sel, values)
    v0 = picked[0:local]
    v1 = picked[local : 2 * local]
    v2 = picked[2 * local : 3 * local]
    rate = pre * jnp.exp(-ACTIVATION * jnp.exp(-v0)) * v1 * v2
    return stc * _exact_right(bc, rate)


def stage_kernel(coarse, second, project, sends, local, *refs):
    refs = list(refs)

    def take():
        return refs.pop(0)

    u_ref = take()
    c_ref = take() if coarse else None
    bu_ref = take() if second else None
    bc_ref = take() if (second and coarse) else None
    recv = {s: take() for s in SEND_FACES}
    pl_ref = take()
    pr_ref = take()
    v7_ref = take()
    m7_ref = take()
    pre_ref = take()
    stc_ref = take()
    bc_tab = take()
    sel_tab = take()
    d7_ref = take()
    g7_ref = take()
    s7_ref = take()
    if coarse:
        v3_ref = take()
        m3_ref = take()
        d3_ref = take()
        mds_ref = take()
    if coarse or project:
        tm_ref = take()
        sw_ref = take()
    if sends:
        g7s_ref = take()
        if coarse or project:
            tms_ref = take()
    if project:
        pj_ref = take()
    out_u = take()
    out_c = take() if (coarse or project) else None
    out_send = [take() for _ in SEND_FACES] if sends else None

    pre = pre_ref[...]
    stc = stc_ref[...]
    bcast = bc_tab[...]
    sel = sel_tab[...]
    u = u_ref[...]
    trace7 = _dot(u.astype(bf16), g7_ref[...])
    if coarse:
        c = c_ref[...]
        trace3 = _full(c, tm_ref).astype(bf16).astype(f32)
        switched = sw_ref[...] > 0.5
        own = jnp.where(switched, trace3, trace7)
    else:
        own = trace7
    own_b = own.astype(bf16)
    near_blocks = []
    for side in range(6):
        other = OPPOSITE[side]
        block = own_b[:, other * LANE : (other + 1) * LANE]
        near = _dot(pl_ref[side], block)
        if side in SEND_FACES:
            k = SEND_FACES.index(side)
            near = near + _dot(pr_ref[k], recv[side][...])
        near_blocks.append(near)
    near = jnp.concatenate(near_blocks, axis=1)

    divergence = None
    for d in range(3):
        flux = (v7_ref[d].astype(f32) * u).astype(bf16)
        term = _dot(flux, d7_ref[d])
        divergence = term if divergence is None else divergence + term
    result = _rate_source(u, pre, stc, bcast, sel, local) - divergence
    jump = (P7 * (P7 - 1) / 2.0) * (m7_ref[...] * (trace7 - near))
    rate7 = result + _exact_left(jump, s7_ref[...])

    if coarse:
        div3 = None
        for d in range(3):
            flux3 = (v3_ref[d] * c).astype(bf16)
            term = _dot(flux3, d3_ref[d])
            div3 = term if div3 is None else div3 + term
        result3 = _rate_source(c, pre, stc, bcast, sel, local) - div3
        jump3 = m3_ref[...] * (trace3 - near)
        rate3 = result3 + (P3 * (P3 - 1) / 2.0) * _full(jump3, mds_ref)

    if second:
        new_u = 0.5 * (bu_ref[...] + u + TIME_STEP * rate7)
    else:
        new_u = u + TIME_STEP * rate7
    out_u[...] = new_u
    new_c = None
    if coarse:
        if second:
            new_c = 0.5 * (bc_ref[...] + c + TIME_STEP * rate3)
        else:
            new_c = c + TIME_STEP * rate3
        out_c[...] = new_c
    if project:
        new_c = _full(new_u, pj_ref)
        out_c[...] = new_c
    if sends:
        send7 = _dot(new_u.astype(bf16), g7s_ref[...])
        if new_c is not None:
            send3 = _full(new_c, tms_ref).astype(bf16).astype(f32)
            send = jnp.where(sw_ref[...] > 0.5, send3, send7)
        else:
            send = send7
        send = send.astype(bf16)
        for k in range(len(SEND_FACES)):
            out_send[k][...] = send[:, k * LANE : (k + 1) * LANE]


def _vmem():
    return pl.BlockSpec(memory_space=pltpu.VMEM)


def run_stage(flags, inputs, out_shapes):
    coarse, second, project, sends, local = flags
    kernel = functools.partial(stage_kernel, coarse, second, project, sends, local)
    return pl.pallas_call(
        kernel,
        out_shape=out_shapes,
        in_specs=[_vmem() for _ in inputs],
        out_specs=[_vmem() for _ in out_shapes],
        compiler_params=pltpu.CompilerParams(vmem_limit_bytes=48 * 1024 * 1024),
    )(*inputs)


def trace_kernel(u_ref, g7s_ref, *out_refs):
    send = _dot(u_ref[...].astype(bf16), g7s_ref[...]).astype(bf16)
    for k in range(len(SEND_FACES)):
        out_refs[k][...] = send[:, k * LANE : (k + 1) * LANE]


def per_device(state, velocity, pre_exp, stoich, neighbours, switch, new_owner):
    tab = make_tables()
    local_count = state.shape[0]
    field_count = state.shape[1]
    rows = local_count * field_count
    curve_count = lax.axis_size("curve")
    curve_pos = lax.axis_index("curve")
    device_id = lax.axis_index("slab") * curve_count + curve_pos
    first_global = device_id * local_count
    positions = jnp.arange(local_count, dtype=jnp.int32)

    lift = jnp.asarray(tab["lift"])
    fine_vel = jnp.einsum("nm,dme->edn", lift, velocity, preferred_element_type=f32).astype(bf16)
    v7 = jnp.broadcast_to(
        jnp.transpose(fine_vel, (1, 0, 2))[:, :, None, :], (3, local_count, field_count, P7**3)
    ).reshape(3, rows, P7**3)
    fvf = fine_vel.astype(f32)
    m7_parts = []
    for side in range(6):
        vals = SIDE_SIGNS[side] * fvf[:, side // 2, tab["nodes7"][side]]
        m7_parts.append(jnp.pad(jnp.minimum(vals, 0.0), ((0, 0), (0, LANE - P7 * P7))))
    m7 = jnp.repeat(jnp.concatenate(m7_parts, axis=1), field_count, axis=0)
    coarse_vel = jnp.transpose(velocity, (0, 2, 1)).astype(f32)
    v3 = jnp.broadcast_to(
        coarse_vel[:, :, None, :], (3, local_count, field_count, P3**3)
    ).reshape(3, rows, P3**3)
    normal3 = jnp.stack(
        [SIDE_SIGNS[s] * coarse_vel[s // 2][:, tab["nodes3"][s]] for s in range(6)], axis=1
    )
    mortar_vel = jnp.einsum(
        "mk,esk->esm", jnp.asarray(tab["mortar_up"]), normal3, precision=lax.Precision.HIGHEST
    )
    m3 = jnp.pad(jnp.minimum(mortar_vel, 0.0), ((0, 0), (0, 0), (0, LANE - P7 * P7)))
    m3 = jnp.repeat(m3.reshape(local_count, 6 * LANE), field_count, axis=0)

    near_device = neighbours // local_count
    near_local = neighbours - near_device * local_count
    remote = near_device != device_id
    row_elem = jnp.arange(rows, dtype=jnp.int32) // field_count
    row_field = jnp.arange(rows, dtype=jnp.int32) % field_count
    col = jnp.arange(rows, dtype=jnp.int32)
    src_row = near_local[row_elem] * field_count + row_field[:, None]
    hit = src_row[:, :, None] == col[None, None, :]
    rem = remote[row_elem]
    p_local = jnp.transpose(hit & ~rem[:, :, None], (1, 0, 2)).astype(bf16)
    p_remote = jnp.transpose(hit & rem[:, :, None], (1, 0, 2))[np.array(SEND_FACES)].astype(bf16)

    pre = pre_exp.reshape(local_count, 1)
    stc = jnp.tile(stoich, local_count).reshape(rows, 1)
    bcast = (row_elem[:, None] == positions[None, :]).astype(bf16)
    pick_rows = (jnp.arange(3, dtype=jnp.int32)[:, None] + field_count * positions[None, :]).reshape(-1)
    sel = (pick_rows[:, None] == col[None, :]).astype(bf16)
    sw = jnp.repeat(switch.astype(f32), field_count).reshape(rows, 1)

    d7t = jnp.asarray(tab["d7t"])
    g7 = jnp.asarray(tab["g7"])
    s7 = jnp.asarray(tab["s7"])
    g7s = jnp.asarray(tab["g7s"])
    d3t = jnp.asarray(tab["d3t"])
    tm = jnp.asarray(tab["tm"])
    tms = jnp.asarray(tab["tms"])
    mds = jnp.asarray(tab["mds"])
    pjt = jnp.asarray(tab["pjt"])

    send_shape = jax.ShapeDtypeStruct((rows, LANE), bf16)
    u_shape = jax.ShapeDtypeStruct((rows, P7**3), f32)
    c_shape = jax.ShapeDtypeStruct((rows, P3**3), f32)

    def exchange(sends):
        out = dict(zip(SEND_FACES, sends))
        return [
            shifted(out[1], "curve", 1),
            shifted(out[0], "curve", -1),
            shifted(out[5], "slab", 1),
            shifted(out[4], "slab", -1),
        ]

    common = [p_local, p_remote, v7, m7, pre, stc, bcast, sel, d7t, g7, s7]
    u0 = state.reshape(rows, P7**3)
    sends = pl.pallas_call(
        trace_kernel,
        out_shape=[send_shape] * 4,
        in_specs=[_vmem(), _vmem()],
        out_specs=[_vmem()] * 4,
    )(u0, g7s)
    recv = exchange(sends)
    res = run_stage(
        (False, False, False, True, local_count),
        [u0] + recv + common + [g7s],
        [u_shape] + [send_shape] * 4,
    )
    first, sends = res[0], res[1:]
    recv = exchange(sends)
    res = run_stage(
        (False, True, True, True, local_count),
        [first, u0] + recv + common + [tm, sw, g7s, tms, pjt],
        [u_shape, c_shape] + [send_shape] * 4,
    )
    after, coarse, sends = res[0], res[1], res[2:]
    recv = exchange(sends)
    mixed_tail = [v3, m3, d3t, mds, tm, sw]
    res = run_stage(
        (True, False, False, True, local_count),
        [after, coarse] + recv + common + mixed_tail + [g7s, tms],
        [u_shape, c_shape] + [send_shape] * 4,
    )
    first7, first3, sends = res[0], res[1], res[2:]
    recv = exchange(sends)
    res = run_stage(
        (True, True, False, False, local_count),
        [first7, first3, after, coarse] + recv + common + mixed_tail,
        [u_shape, c_shape],
    )
    final7 = res[0].reshape(local_count, field_count, P7**3)
    final3 = res[1].reshape(local_count, field_count * P3**3)

    switched = switch == 1
    left_pos = (curve_pos + curve_count - 1) % curve_count
    right_pos = (curve_pos + 1) % curve_count
    to_left = (new_owner == left_pos) & ~switched
    to_right = (new_owner == right_pos) & ~switched
    stays_home = ~switched & ~to_left & ~to_right

    def first_rows(mask):
        rank = jnp.cumsum(mask.astype(jnp.int32)) - 1
        slot = jnp.arange(MOVE_CAP, dtype=jnp.int32)
        chosen = mask[None, :] & (rank[None, :] == slot[:, None])
        live = jnp.any(chosen, axis=1)
        row = jnp.sum(jnp.where(chosen, positions[None, :], 0), axis=1)
        return row, live

    left_rows, left_live = first_rows(to_left)
    right_rows, right_live = first_rows(to_right)
    left_ids = jnp.where(left_live, first_global + left_rows, missing_id)
    right_ids = jnp.where(right_live, first_global + right_rows, missing_id)
    home_ids = jnp.where(stays_home, first_global + positions, missing_id)
    from_right_ids = shifted(left_ids, "curve", -1)
    from_left_ids = shifted(right_ids, "curve", 1)
    from_right = shifted(final7[left_rows], "curve", -1)
    from_left = shifted(final7[right_rows], "curve", 1)
    cand_ids = jnp.concatenate([home_ids, from_left_ids, from_right_ids])
    cand_count = cand_ids.shape[0]
    rank = jnp.sum((cand_ids[None, :] < cand_ids[:, None]).astype(jnp.int32), axis=1)
    slot = jnp.arange(HOLD7, dtype=jnp.int32)
    pick = (rank[None, :] == slot[:, None]) & (cand_ids[None, :] < missing_id)
    order = jnp.sum(jnp.where(pick, jnp.arange(cand_count, dtype=jnp.int32)[None, :], 0), axis=1)
    slot_live = jnp.any(pick, axis=1)
    held = jnp.concatenate([final7, from_left, from_right], axis=0)[order]
    state7_out = jnp.where(slot_live[:, None, None], held, 0.0)
    state3_out = jnp.where(switched[:, None], final3, 0.0)
    return (state7_out, state3_out)


def solution(mesh):
    return jax.shard_map(
        per_device,
        mesh=mesh,
        in_specs=(
            P(("slab", "curve"), None, None),
            P(None, None, ("slab", "curve")),
            P(("slab", "curve")),
            P(),
            P(("slab", "curve"), None),
            P(("slab", "curve")),
            P(("slab", "curve")),
        ),
        out_specs=(P(("slab", "curve"), None, None), P(("slab", "curve"), None)),
        check_vma=False,
    )
```

```python
import functools

import jax
import jax.numpy as jnp
import ml_dtypes
import numpy as np
from jax import lax
from jax.experimental import pallas as pl
from jax.experimental.pallas import tpu as pltpu
from jax.sharding import PartitionSpec as P

P7 = 8
P3 = 4
MOVE_CAP = 2
HOLD7 = 12
LANE = 128

TIME_STEP = 0.002
ACTIVATION = 1.5
SIDE_SIGNS = (-1.0, 1.0, -1.0, 1.0, -1.0, 1.0)
OPPOSITE = (1, 0, 3, 2, 5, 4)
SEND_FACES = (0, 1, 4, 5)
missing_id = 1 << 30

f32 = jnp.float32
bf16 = jnp.bfloat16


def shifted(value, axis, steps):
    count = lax.axis_size(axis)
    pairs = [(source, (source + steps) % count) for source in range(count)]
    return lax.ppermute(value, axis, pairs)


def lobatto_points(number):
    return -np.cos(np.pi * np.arange(number) / (number - 1))


def lagrange_weights(points):
    weights = np.ones(points.shape[0])
    for row_id in range(points.shape[0]):
        for col_id in range(points.shape[0]):
            if col_id != row_id:
                weights[row_id] = weights[row_id] / (points[row_id] - points[col_id])
    return weights


def derivative_matrix(points):
    weights = lagrange_weights(points)
    number = points.shape[0]
    matrix = np.zeros((number, number))
    for row_id in range(number):
        for col_id in range(number):
            if col_id != row_id:
                matrix[row_id, col_id] = (
                    weights[col_id] / weights[row_id] / (points[row_id] - points[col_id])
                )
        matrix[row_id, row_id] = -np.sum(matrix[row_id])
    return matrix


def interpolation_matrix(source, target):
    matrix = np.ones((target.shape[0], source.shape[0]))
    for col_id in range(source.shape[0]):
        for other_id in range(source.shape[0]):
            if other_id != col_id:
                matrix[:, col_id] = (
                    matrix[:, col_id]
                    * (target - source[other_id])
                    / (source[col_id] - source[other_id])
                )
    return matrix


def spread_three(matrix, identity):
    return (
        np.kron(matrix, np.kron(identity, identity)),
        np.kron(identity, np.kron(matrix, identity)),
        np.kron(identity, np.kron(identity, matrix)),
    )


def face_nodes(extent):
    grid = np.arange(extent**3).reshape(extent, extent, extent)
    last = extent - 1
    pieces = (grid[0], grid[last], grid[:, 0], grid[:, last], grid[:, :, 0], grid[:, :, last])
    return [piece.reshape(-1) for piece in pieces]


def to_bf16(x):
    return np.asarray(np.asarray(x, np.float32).astype(ml_dtypes.bfloat16))


def split_parts(x):
    x = np.asarray(x, np.float32)
    hi = x.astype(ml_dtypes.bfloat16)
    rest = x - hi.astype(np.float32)
    mid = rest.astype(ml_dtypes.bfloat16)
    lo = (rest - mid.astype(np.float32)).astype(ml_dtypes.bfloat16)
    return np.stack([hi, mid, lo])


def make_tables():
    fine_points = lobatto_points(P7)
    coarse_points = lobatto_points(P3)
    fine_derivs = spread_three(derivative_matrix(fine_points), np.eye(P7))
    coarse_derivs = spread_three(derivative_matrix(coarse_points), np.eye(P3))
    downward = interpolation_matrix(fine_points, coarse_points)
    upward = interpolation_matrix(coarse_points, fine_points)
    d7t = np.stack([to_bf16(m.T) for m in fine_derivs])
    d3t = np.stack([to_bf16(m).T for m in coarse_derivs])
    lift_table = to_bf16(np.kron(upward, np.kron(upward, upward)))
    projection = np.asarray(np.kron(downward, np.kron(downward, downward)), np.float32)
    mortar_up = np.asarray(np.kron(upward, upward), np.float32)
    mortar_down = np.asarray(np.kron(downward, downward), np.float32)
    nodes7 = face_nodes(P7)
    nodes3 = face_nodes(P3)
    n7 = P7**3
    n3 = P3**3
    g7 = np.zeros((n7, 6 * LANE), np.float32)
    tm = np.zeros((n3, 6 * LANE), np.float32)
    mds = np.zeros((6 * LANE, n3), np.float32)
    for side in range(6):
        for q, node in enumerate(nodes7[side]):
            g7[node, side * LANE + q] = 1.0
        for k, node in enumerate(nodes3[side]):
            tm[node, side * LANE : side * LANE + P7 * P7] = mortar_up[:, k]
            mds[side * LANE : side * LANE + P7 * P7, node] = mortar_down[k, :]
    send_cols = np.concatenate([np.arange(s * LANE, (s + 1) * LANE) for s in SEND_FACES])
    tables = {
        "d7t": to_bf16(d7t),
        "d3t": to_bf16(d3t),
        "lift": lift_table,
        "mortar_up": mortar_up,
        "g7": to_bf16(g7),
        "s7": to_bf16(g7.T),
        "g7s": to_bf16(g7[:, send_cols]),
        "tm": split_parts(tm),
        "tms": split_parts(tm[:, send_cols]),
        "mds": split_parts(mds),
        "pjt": split_parts(projection.T),
        "nodes7": nodes7,
        "nodes3": nodes3,
    }
    return tables


def _dot(a, b):
    return jnp.dot(a, b, preferred_element_type=f32)


def _split(x):
    hi = x.astype(bf16)
    rest = x - hi.astype(f32)
    mid = rest.astype(bf16)
    lo = (rest - mid.astype(f32)).astype(bf16)
    return hi, mid, lo


def _exact_left(x, table):
    hi, mid, lo = _split(x)
    return (_dot(hi, table) + _dot(mid, table)) + _dot(lo, table)


def _exact_right(table, x):
    hi, mid, lo = _split(x)
    return (_dot(table, hi) + _dot(table, mid)) + _dot(table, lo)


def _full(x, parts_ref):
    xh, xm, xl = _split(x)
    bh = parts_ref[0]
    bm = parts_ref[1]
    bl = parts_ref[2]
    return _dot(xh, bh) + (_dot(xh, bm) + _dot(xm, bh)) + (
        _dot(xh, bl) + _dot(xm, bm) + _dot(xl, bh)
    )


def _rate_source(values, pre, stc, bc, sel, local):
    picked = _exact_right(sel, values)
    v0 = picked[0:local]
    v1 = picked[local : 2 * local]
    v2 = picked[2 * local : 3 * local]
    rate = pre * jnp.exp(-ACTIVATION * jnp.exp(-v0)) * v1 * v2
    return stc * _exact_right(bc, rate)


def stage_kernel(coarse, second, project, sends, local, *refs):
    refs = list(refs)

    def take():
        return refs.pop(0)

    u_ref = take()
    c_ref = take() if coarse else None
    bu_ref = take() if second else None
    bc_ref = take() if (second and coarse) else None
    recv = {s: take() for s in SEND_FACES}
    pl_ref = take()
    pr_ref = take()
    v7_ref = take()
    m7_ref = take()
    pre_ref = take()
    stc_ref = take()
    bc_tab = take()
    sel_tab = take()
    d7_ref = take()
    g7_ref = take()
    s7_ref = take()
    if coarse:
        v3_ref = take()
        m3_ref = take()
        d3_ref = take()
        mds_ref = take()
    if coarse or project:
        tm_ref = take()
        sw_ref = take()
    if sends:
        g7s_ref = take()
        if coarse or project:
            tms_ref = take()
    if project:
        pj_ref = take()
    out_u = take()
    out_c = take() if (coarse or project) else None
    out_send = [take() for _ in SEND_FACES] if sends else None

    pre = pre_ref[...]
    stc = stc_ref[...]
    bcast = bc_tab[...]
    sel = sel_tab[...]
    u = u_ref[...]
    trace7 = _dot(u.astype(bf16), g7_ref[...])
    if coarse:
        c = c_ref[...]
        trace3 = _full(c, tm_ref).astype(bf16).astype(f32)
        switched = sw_ref[...] > 0.5
        own = jnp.where(switched, trace3, trace7)
    else:
        own = trace7
    own_b = own.astype(bf16)
    near_blocks = []
    for side in range(6):
        other = OPPOSITE[side]
        block = own_b[:, other * LANE : (other + 1) * LANE]
        near = _dot(pl_ref[side], block)
        if side in SEND_FACES:
            k = SEND_FACES.index(side)
            near = near + _dot(pr_ref[k], recv[side][...])
        near_blocks.append(near)
    near = jnp.concatenate(near_blocks, axis=1)

    divergence = None
    for d in range(3):
        flux = (v7_ref[d].astype(f32) * u).astype(bf16)
        term = _dot(flux, d7_ref[d])
        divergence = term if divergence is None else divergence + term
    result = _rate_source(u, pre, stc, bcast, sel, local) - divergence
    jump = (P7 * (P7 - 1) / 2.0) * (m7_ref[...] * (trace7 - near))
    rate7 = result + _exact_left(jump, s7_ref[...])

    if coarse:
        div3 = None
        for d in range(3):
            flux3 = (v3_ref[d] * c).astype(bf16)
            term = _dot(flux3, d3_ref[d])
            div3 = term if div3 is None else div3 + term
        result3 = _rate_source(c, pre, stc, bcast, sel, local) - div3
        jump3 = m3_ref[...] * (trace3 - near)
        rate3 = result3 + (P3 * (P3 - 1) / 2.0) * _full(jump3, mds_ref)

    if second:
        new_u = 0.5 * (bu_ref[...] + u + TIME_STEP * rate7)
    else:
        new_u = u + TIME_STEP * rate7
    out_u[...] = new_u
    new_c = None
    if coarse:
        if second:
            new_c = 0.5 * (bc_ref[...] + c + TIME_STEP * rate3)
        else:
            new_c = c + TIME_STEP * rate3
        out_c[...] = new_c
    if project:
        new_c = _full(new_u, pj_ref)
        out_c[...] = new_c
    if sends:
        send7 = _dot(new_u.astype(bf16), g7s_ref[...])
        if new_c is not None:
            send3 = _full(new_c, tms_ref).astype(bf16).astype(f32)
            send = jnp.where(sw_ref[...] > 0.5, send3, send7)
        else:
            send = send7
        send = send.astype(bf16)
        for k in range(len(SEND_FACES)):
            out_send[k][...] = send[:, k * LANE : (k + 1) * LANE]


def _vmem():
    return pl.BlockSpec(memory_space=pltpu.VMEM)


def run_stage(flags, inputs, out_shapes):
    coarse, second, project, sends, local = flags
    kernel = functools.partial(stage_kernel, coarse, second, project, sends, local)
    return pl.pallas_call(
        kernel,
        out_shape=out_shapes,
        in_specs=[_vmem() for _ in inputs],
        out_specs=[_vmem() for _ in out_shapes],
        compiler_params=pltpu.CompilerParams(vmem_limit_bytes=48 * 1024 * 1024),
    )(*inputs)


def trace_kernel(u_ref, g7s_ref, *out_refs):
    send = _dot(u_ref[...].astype(bf16), g7s_ref[...]).astype(bf16)
    for k in range(len(SEND_FACES)):
        out_refs[k][...] = send[:, k * LANE : (k + 1) * LANE]


def setup_kernel(local, fields, u_ref, vt_ref, packed_ref, lift_ref, g7_ref, tm_ref, bc_ref,
                 g7s_ref, pre_ref, sto_ref, v7_out, m7_out, v3_out, m3_out, pl_out, pr_out,
                 pre_out, stc_out, sw_out, *send_refs):
    rows = local * fields
    bcast = bc_ref[...]
    lanes = lax.broadcasted_iota(jnp.int32, (local, 6 * LANE), 1) // LANE
    sign = jnp.where(lanes % 2 == 0, -1.0, 1.0)
    fvg = []
    mvg = []
    for d in range(3):
        vt = vt_ref[d]
        fv = _dot(vt, lift_ref[...]).astype(bf16)
        v7_out[d] = _dot(bcast, fv).astype(bf16)
        v3_out[d] = _dot(bcast, vt)
        fvg.append(_dot(fv, g7_ref[...]))
        mvg.append((_dot(vt, tm_ref[0]) + _dot(vt, tm_ref[1])) + _dot(vt, tm_ref[2]))

    def by_block(parts):
        return jnp.where(lanes < 2, parts[0], jnp.where(lanes < 4, parts[1], parts[2]))

    m7 = jnp.minimum(sign * by_block(fvg), 0.0)
    m7_out[...] = _dot(bcast, m7.astype(bf16))
    m3 = jnp.minimum(sign * by_block(mvg), 0.0)
    m3_out[...] = _exact_right(bcast, m3)
    rep = _dot(bcast, packed_ref[...].astype(bf16))
    row_f = (lax.broadcasted_iota(jnp.int32, (rows, 1), 0) % fields).astype(f32)
    cols = lax.broadcasted_iota(jnp.int32, (rows, rows), 1).astype(f32)
    for side in range(6):
        code = rep[:, side : side + 1]
        far = code >= local
        target = (code - jnp.where(far, float(local), 0.0)) * fields + row_f
        hit = cols == target
        pl_out[side] = jnp.where(hit & ~far, 1.0, 0.0).astype(bf16)
        if side in SEND_FACES:
            pr_out[SEND_FACES.index(side)] = jnp.where(hit & far, 1.0, 0.0).astype(bf16)
    sw_out[...] = rep[:, 6:7]
    elem = lax.broadcasted_iota(jnp.int32, (local, 1), 0)
    pre = jnp.zeros((local, 1), f32)
    for e in range(local):
        pre = jnp.where(elem == e, pre_ref[e], pre)
    pre_out[...] = pre
    row_fi = lax.broadcasted_iota(jnp.int32, (rows, 1), 0) % fields
    stc = jnp.zeros((rows, 1), f32)
    for f in range(fields):
        stc = jnp.where(row_fi == f, sto_ref[f], stc)
    stc_out[...] = stc
    send = _dot(u_ref[...].astype(bf16), g7s_ref[...]).astype(bf16)
    for k in range(len(SEND_FACES)):
        send_refs[k][...] = send[:, k * LANE : (k + 1) * LANE]


def per_device(state, velocity, pre_exp, stoich, neighbours, switch, new_owner):
    tab = make_tables()
    local_count = state.shape[0]
    field_count = state.shape[1]
    rows = local_count * field_count
    curve_count = lax.axis_size("curve")
    curve_pos = lax.axis_index("curve")
    device_id = lax.axis_index("slab") * curve_count + curve_pos
    first_global = device_id * local_count
    positions = jnp.arange(local_count, dtype=jnp.int32)

    near_device = neighbours // local_count
    near_local = neighbours - near_device * local_count
    remote = near_device != device_id
    codes = (near_local + local_count * remote.astype(jnp.int32)).astype(f32)
    packed = jnp.concatenate(
        [codes, switch.astype(f32)[:, None], jnp.zeros((local_count, LANE - 7), f32)], axis=1
    )
    vt = jnp.transpose(velocity, (0, 2, 1))
    row_elem = np.arange(rows) // field_count
    bcast = jnp.asarray(to_bf16(row_elem[:, None] == np.arange(local_count)[None, :]))
    pick_rows = (np.arange(3)[:, None] + field_count * np.arange(local_count)[None, :]).reshape(-1)
    sel = jnp.asarray(to_bf16(pick_rows[:, None] == np.arange(rows)[None, :]))
    lift_t = jnp.asarray(to_bf16(tab["lift"].astype(np.float32).T))
    d7t = jnp.asarray(tab["d7t"])
    g7 = jnp.asarray(tab["g7"])
    s7 = jnp.asarray(tab["s7"])
    g7s = jnp.asarray(tab["g7s"])
    d3t = jnp.asarray(tab["d3t"])
    tm = jnp.asarray(tab["tm"])
    tms = jnp.asarray(tab["tms"])
    mds = jnp.asarray(tab["mds"])
    pjt = jnp.asarray(tab["pjt"])

    send_shape = jax.ShapeDtypeStruct((rows, LANE), bf16)
    u_shape = jax.ShapeDtypeStruct((rows, P7**3), f32)
    c_shape = jax.ShapeDtypeStruct((rows, P3**3), f32)

    def exchange(sends):
        out = dict(zip(SEND_FACES, sends))
        return [
            shifted(out[1], "curve", 1),
            shifted(out[0], "curve", -1),
            shifted(out[5], "slab", 1),
            shifted(out[4], "slab", -1),
        ]

    setup_out = [
        jax.ShapeDtypeStruct((3, rows, P7**3), bf16),
        jax.ShapeDtypeStruct((rows, 6 * LANE), f32),
        jax.ShapeDtypeStruct((3, rows, P3**3), f32),
        jax.ShapeDtypeStruct((rows, 6 * LANE), f32),
        jax.ShapeDtypeStruct((6, rows, rows), bf16),
        jax.ShapeDtypeStruct((len(SEND_FACES), rows, rows), bf16),
        jax.ShapeDtypeStruct((local_count, 1), f32),
        jax.ShapeDtypeStruct((rows, 1), f32),
        jax.ShapeDtypeStruct((rows, 1), f32),
    ] + [send_shape] * 4
    u0 = state.reshape(rows, P7**3)
    smem = pl.BlockSpec(memory_space=pltpu.SMEM)
    res = pl.pallas_call(
        functools.partial(setup_kernel, local_count, field_count),
        out_shape=setup_out,
        in_specs=[_vmem()] * 8 + [smem, smem],
        out_specs=[_vmem() for _ in setup_out],
        compiler_params=pltpu.CompilerParams(vmem_limit_bytes=48 * 1024 * 1024),
    )(u0, vt, packed, lift_t, g7, tm, bcast, g7s, pre_exp, stoich)
    v7, m7, v3, m3, p_local, p_remote, pre, stc, sw = res[:9]
    sends = res[9:]
    common = [p_local, p_remote, v7, m7, pre, stc, bcast, sel, d7t, g7, s7]
    recv = exchange(sends)
    res = run_stage(
        (False, False, False, True, local_count),
        [u0] + recv + common + [g7s],
        [u_shape] + [send_shape] * 4,
    )
    first, sends = res[0], res[1:]
    recv = exchange(sends)
    res = run_stage(
        (False, True, True, True, local_count),
        [first, u0] + recv + common + [tm, sw, g7s, tms, pjt],
        [u_shape, c_shape] + [send_shape] * 4,
    )
    after, coarse, sends = res[0], res[1], res[2:]
    recv = exchange(sends)
    mixed_tail = [v3, m3, d3t, mds, tm, sw]
    res = run_stage(
        (True, False, False, True, local_count),
        [after, coarse] + recv + common + mixed_tail + [g7s, tms],
        [u_shape, c_shape] + [send_shape] * 4,
    )
    first7, first3, sends = res[0], res[1], res[2:]
    recv = exchange(sends)
    res = run_stage(
        (True, True, False, False, local_count),
        [first7, first3, after, coarse] + recv + common + mixed_tail,
        [u_shape, c_shape],
    )
    final7 = res[0].reshape(local_count, field_count, P7**3)
    final3 = res[1].reshape(local_count, field_count * P3**3)

    switched = switch == 1
    left_pos = (curve_pos + curve_count - 1) % curve_count
    right_pos = (curve_pos + 1) % curve_count
    to_left = (new_owner == left_pos) & ~switched
    to_right = (new_owner == right_pos) & ~switched
    stays_home = ~switched & ~to_left & ~to_right

    def first_rows(mask):
        rank = jnp.cumsum(mask.astype(jnp.int32)) - 1
        slot = jnp.arange(MOVE_CAP, dtype=jnp.int32)
        chosen = mask[None, :] & (rank[None, :] == slot[:, None])
        live = jnp.any(chosen, axis=1)
        row = jnp.sum(jnp.where(chosen, positions[None, :], 0), axis=1)
        return row, live

    left_rows, left_live = first_rows(to_left)
    right_rows, right_live = first_rows(to_right)
    left_ids = jnp.where(left_live, first_global + left_rows, missing_id)
    right_ids = jnp.where(right_live, first_global + right_rows, missing_id)
    home_ids = jnp.where(stays_home, first_global + positions, missing_id)
    from_right_ids = shifted(left_ids, "curve", -1)
    from_left_ids = shifted(right_ids, "curve", 1)
    from_right = shifted(final7[left_rows], "curve", -1)
    from_left = shifted(final7[right_rows], "curve", 1)
    cand_ids = jnp.concatenate([home_ids, from_left_ids, from_right_ids])
    cand_count = cand_ids.shape[0]
    rank = jnp.sum((cand_ids[None, :] < cand_ids[:, None]).astype(jnp.int32), axis=1)
    slot = jnp.arange(HOLD7, dtype=jnp.int32)
    pick = (rank[None, :] == slot[:, None]) & (cand_ids[None, :] < missing_id)
    order = jnp.sum(jnp.where(pick, jnp.arange(cand_count, dtype=jnp.int32)[None, :], 0), axis=1)
    slot_live = jnp.any(pick, axis=1)
    held = jnp.concatenate([final7, from_left, from_right], axis=0)[order]
    state7_out = jnp.where(slot_live[:, None, None], held, 0.0)
    state3_out = jnp.where(switched[:, None], final3, 0.0)
    return (state7_out, state3_out)


def solution(mesh):
    return jax.shard_map(
        per_device,
        mesh=mesh,
        in_specs=(
            P(("slab", "curve"), None, None),
            P(None, None, ("slab", "curve")),
            P(("slab", "curve")),
            P(),
            P(("slab", "curve"), None),
            P(("slab", "curve")),
            P(("slab", "curve")),
        ),
        out_specs=(P(("slab", "curve"), None, None), P(("slab", "curve"), None)),
        check_vma=False,
    )
```

```python
import functools

import jax
import jax.numpy as jnp
import ml_dtypes
import numpy as np
from jax import lax
from jax.experimental import pallas as pl
from jax.experimental.pallas import tpu as pltpu
from jax.sharding import PartitionSpec as P

P7 = 8
P3 = 4
MOVE_CAP = 2
HOLD7 = 12
LANE = 128

TIME_STEP = 0.002
ACTIVATION = 1.5
SIDE_SIGNS = (-1.0, 1.0, -1.0, 1.0, -1.0, 1.0)
OPPOSITE = (1, 0, 3, 2, 5, 4)
SEND_FACES = (0, 1, 4, 5)
missing_id = 1 << 30

f32 = jnp.float32
bf16 = jnp.bfloat16


def shifted(value, axis, steps):
    count = lax.axis_size(axis)
    pairs = [(source, (source + steps) % count) for source in range(count)]
    return lax.ppermute(value, axis, pairs)


def lobatto_points(number):
    return -np.cos(np.pi * np.arange(number) / (number - 1))


def lagrange_weights(points):
    weights = np.ones(points.shape[0])
    for row_id in range(points.shape[0]):
        for col_id in range(points.shape[0]):
            if col_id != row_id:
                weights[row_id] = weights[row_id] / (points[row_id] - points[col_id])
    return weights


def derivative_matrix(points):
    weights = lagrange_weights(points)
    number = points.shape[0]
    matrix = np.zeros((number, number))
    for row_id in range(number):
        for col_id in range(number):
            if col_id != row_id:
                matrix[row_id, col_id] = (
                    weights[col_id] / weights[row_id] / (points[row_id] - points[col_id])
                )
        matrix[row_id, row_id] = -np.sum(matrix[row_id])
    return matrix


def interpolation_matrix(source, target):
    matrix = np.ones((target.shape[0], source.shape[0]))
    for col_id in range(source.shape[0]):
        for other_id in range(source.shape[0]):
            if other_id != col_id:
                matrix[:, col_id] = (
                    matrix[:, col_id]
                    * (target - source[other_id])
                    / (source[col_id] - source[other_id])
                )
    return matrix


def spread_three(matrix, identity):
    return (
        np.kron(matrix, np.kron(identity, identity)),
        np.kron(identity, np.kron(matrix, identity)),
        np.kron(identity, np.kron(identity, matrix)),
    )


def face_nodes(extent):
    grid = np.arange(extent**3).reshape(extent, extent, extent)
    last = extent - 1
    pieces = (grid[0], grid[last], grid[:, 0], grid[:, last], grid[:, :, 0], grid[:, :, last])
    return [piece.reshape(-1) for piece in pieces]


def to_bf16(x):
    return np.asarray(np.asarray(x, np.float32).astype(ml_dtypes.bfloat16))


def split_parts(x):
    x = np.asarray(x, np.float32)
    hi = x.astype(ml_dtypes.bfloat16)
    rest = x - hi.astype(np.float32)
    mid = rest.astype(ml_dtypes.bfloat16)
    lo = (rest - mid.astype(np.float32)).astype(ml_dtypes.bfloat16)
    return np.stack([hi, mid, lo])


def make_tables():
    fine_points = lobatto_points(P7)
    coarse_points = lobatto_points(P3)
    fine_derivs = spread_three(derivative_matrix(fine_points), np.eye(P7))
    coarse_derivs = spread_three(derivative_matrix(coarse_points), np.eye(P3))
    downward = interpolation_matrix(fine_points, coarse_points)
    upward = interpolation_matrix(coarse_points, fine_points)
    d7t = np.stack([to_bf16(m.T) for m in fine_derivs])
    d3t = np.stack([to_bf16(m).T for m in coarse_derivs])
    lift_table = to_bf16(np.kron(upward, np.kron(upward, upward)))
    projection = np.asarray(np.kron(downward, np.kron(downward, downward)), np.float32)
    mortar_up = np.asarray(np.kron(upward, upward), np.float32)
    mortar_down = np.asarray(np.kron(downward, downward), np.float32)
    nodes7 = face_nodes(P7)
    nodes3 = face_nodes(P3)
    n7 = P7**3
    n3 = P3**3
    g7 = np.zeros((n7, 6 * LANE), np.float32)
    tm = np.zeros((n3, 6 * LANE), np.float32)
    mds = np.zeros((6 * LANE, n3), np.float32)
    for side in range(6):
        for q, node in enumerate(nodes7[side]):
            g7[node, side * LANE + q] = 1.0
        for k, node in enumerate(nodes3[side]):
            tm[node, side * LANE : side * LANE + P7 * P7] = mortar_up[:, k]
            mds[side * LANE : side * LANE + P7 * P7, node] = mortar_down[k, :]
    tables = {
        "d7t": to_bf16(d7t),
        "d3t": to_bf16(d3t),
        "lift": lift_table,
        "mortar_up": mortar_up,
        "g7": to_bf16(g7),
        "tm": split_parts(tm),
        "mds": split_parts(mds),
        "pjt": split_parts(projection.T),
        "nodes7": nodes7,
        "nodes3": nodes3,
    }
    return tables


def _dot(a, b):
    return jnp.dot(a, b, preferred_element_type=f32)


def _split(x):
    hi = x.astype(bf16)
    rest = x - hi.astype(f32)
    mid = rest.astype(bf16)
    lo = (rest - mid.astype(f32)).astype(bf16)
    return hi, mid, lo


def _exact_left(x, table):
    hi, mid, lo = _split(x)
    return (_dot(hi, table) + _dot(mid, table)) + _dot(lo, table)


def _dot_t(a, b):
    return lax.dot_general(a, b, (((1,), (1,)), ((), ())), preferred_element_type=f32)


def _exact_left_t(x, table):
    hi, mid, lo = _split(x)
    return (_dot_t(hi, table) + _dot_t(mid, table)) + _dot_t(lo, table)


def _exact_right(table, x):
    hi, mid, lo = _split(x)
    return (_dot(table, hi) + _dot(table, mid)) + _dot(table, lo)


def _full(x, parts_ref):
    xh, xm, xl = _split(x)
    bh = parts_ref[0]
    bm = parts_ref[1]
    bl = parts_ref[2]
    return _dot(xh, bh) + (_dot(xh, bm) + _dot(xm, bh)) + (
        _dot(xh, bl) + _dot(xm, bm) + _dot(xl, bh)
    )


def _rate_source(values, pre, stc, bc, sel, local):
    picked = _exact_right(sel, values)
    v0 = picked[0:local]
    v1 = picked[local : 2 * local]
    v2 = picked[2 * local : 3 * local]
    rate = pre * jnp.exp(-ACTIVATION * jnp.exp(-v0)) * v1 * v2
    return stc * _exact_right(bc, rate)


def stage_kernel(coarse, second, project, sends, local, *refs):
    refs = list(refs)

    def take():
        return refs.pop(0)

    u_ref = take()
    c_ref = take() if coarse else None
    bu_ref = take() if second else None
    bc_ref = take() if (second and coarse) else None
    recv = {s: take() for s in SEND_FACES}
    pl_ref = take()
    pr_ref = take()
    v7_ref = take()
    m7_ref = take()
    pre_ref = take()
    stc_ref = take()
    bc_tab = take()
    sel_tab = take()
    d7_ref = take()
    g7_ref = take()
    if coarse:
        v3_ref = take()
        m3_ref = take()
        d3_ref = take()
        mds_ref = take()
    if coarse or project:
        tm_ref = take()
        sw_ref = take()
    if project:
        pj_ref = take()
    out_u = take()
    out_c = take() if (coarse or project) else None
    out_send = [take() for _ in SEND_FACES] if sends else None

    pre = pre_ref[...]
    stc = stc_ref[...]
    bcast = bc_tab[...]
    sel = sel_tab[...]
    u = u_ref[...]
    trace7 = _dot(u.astype(bf16), g7_ref[...])
    if coarse:
        c = c_ref[...]
        trace3 = _full(c, tm_ref).astype(bf16).astype(f32)
        switched = sw_ref[...] > 0.5
        own = jnp.where(switched, trace3, trace7)
    else:
        own = trace7
    own_b = own.astype(bf16)
    near_blocks = []
    for side in range(6):
        other = OPPOSITE[side]
        block = own_b[:, other * LANE : (other + 1) * LANE]
        near = _dot(pl_ref[side], block)
        if side in SEND_FACES:
            k = SEND_FACES.index(side)
            near = near + _dot(pr_ref[k], recv[side][...])
        near_blocks.append(near)
    near = jnp.concatenate(near_blocks, axis=1)

    divergence = None
    for d in range(3):
        flux = (v7_ref[d].astype(f32) * u).astype(bf16)
        term = _dot(flux, d7_ref[d])
        divergence = term if divergence is None else divergence + term
    result = _rate_source(u, pre, stc, bcast, sel, local) - divergence
    jump = (P7 * (P7 - 1) / 2.0) * (m7_ref[...] * (trace7 - near))
    rate7 = result + _exact_left_t(jump, g7_ref[...])

    if coarse:
        div3 = None
        for d in range(3):
            flux3 = (v3_ref[d] * c).astype(bf16)
            term = _dot(flux3, d3_ref[d])
            div3 = term if div3 is None else div3 + term
        result3 = _rate_source(c, pre, stc, bcast, sel, local) - div3
        jump3 = m3_ref[...] * (trace3 - near)
        rate3 = result3 + (P3 * (P3 - 1) / 2.0) * _full(jump3, mds_ref)

    if second:
        new_u = 0.5 * (bu_ref[...] + u + TIME_STEP * rate7)
    else:
        new_u = u + TIME_STEP * rate7
    out_u[...] = new_u
    new_c = None
    if coarse:
        if second:
            new_c = 0.5 * (bc_ref[...] + c + TIME_STEP * rate3)
        else:
            new_c = c + TIME_STEP * rate3
        out_c[...] = new_c
    if project:
        new_c = _full(new_u, pj_ref)
        out_c[...] = new_c
    if sends:
        send7 = _dot(new_u.astype(bf16), g7_ref[...])
        if new_c is not None:
            send3 = _full(new_c, tm_ref).astype(bf16).astype(f32)
            send = jnp.where(sw_ref[...] > 0.5, send3, send7)
        else:
            send = send7
        send = send.astype(bf16)
        for k, side in enumerate(SEND_FACES):
            out_send[k][...] = send[:, side * LANE : (side + 1) * LANE]


def _vmem():
    return pl.BlockSpec(memory_space=pltpu.VMEM)


def run_stage(flags, inputs, out_shapes):
    coarse, second, project, sends, local = flags
    kernel = functools.partial(stage_kernel, coarse, second, project, sends, local)
    return pl.pallas_call(
        kernel,
        out_shape=out_shapes,
        in_specs=[_vmem() for _ in inputs],
        out_specs=[_vmem() for _ in out_shapes],
        compiler_params=pltpu.CompilerParams(vmem_limit_bytes=48 * 1024 * 1024),
    )(*inputs)


def setup_kernel(local, fields, u_ref, vt_ref, packed_ref, lift_ref, g7_ref, tm_ref, bc_ref,
                 fsel_ref, v7_out, m7_out, v3_out, m3_out, pl_out, pr_out,
                 pre_out, stc_out, sw_out, *send_refs):
    rows = local * fields
    bcast = bc_ref[...]
    lanes = lax.broadcasted_iota(jnp.int32, (local, 6 * LANE), 1) // LANE
    sign = jnp.where(lanes % 2 == 0, -1.0, 1.0)
    fvg = []
    mvg = []
    for d in range(3):
        vt = vt_ref[d]
        fv = _dot(vt, lift_ref[...]).astype(bf16)
        v7_out[d] = _dot(bcast, fv).astype(bf16)
        v3_out[d] = _dot(bcast, vt)
        fvg.append(_dot(fv, g7_ref[...]))
        mvg.append((_dot(vt, tm_ref[0]) + _dot(vt, tm_ref[1])) + _dot(vt, tm_ref[2]))

    def by_block(parts):
        return jnp.where(lanes < 2, parts[0], jnp.where(lanes < 4, parts[1], parts[2]))

    m7 = jnp.minimum(sign * by_block(fvg), 0.0)
    m7_out[...] = _dot(bcast, m7.astype(bf16))
    m3 = jnp.minimum(sign * by_block(mvg), 0.0)
    m3_out[...] = _exact_right(bcast, m3)
    rep = _dot(bcast, packed_ref[...].astype(bf16))
    row_f = (lax.broadcasted_iota(jnp.int32, (rows, 1), 0) % fields).astype(f32)
    cols = lax.broadcasted_iota(jnp.int32, (rows, rows), 1).astype(f32)
    for side in range(6):
        code = rep[:, side : side + 1]
        far = code >= local
        target = (code - jnp.where(far, float(local), 0.0)) * fields + row_f
        hit = cols == target
        pl_out[side] = jnp.where(hit & ~far, 1.0, 0.0).astype(bf16)
        if side in SEND_FACES:
            pr_out[SEND_FACES.index(side)] = jnp.where(hit & far, 1.0, 0.0).astype(bf16)
    sw_out[...] = rep[:, 6:7]
    pre_out[...] = packed_ref[:, 7:8]
    stc_out[...] = _exact_right(fsel_ref[...], packed_ref[...])[:, 8:9]
    send = _dot(u_ref[...].astype(bf16), g7_ref[...]).astype(bf16)
    for k, side in enumerate(SEND_FACES):
        send_refs[k][...] = send[:, side * LANE : (side + 1) * LANE]


def setup_entry(local, fields, n_in, n_out, *refs):
    sources = refs[:n_in]
    outs = refs[n_in : n_in + n_out]
    buffers = refs[n_in + n_out : 2 * n_in + n_out]
    sems = refs[2 * n_in + n_out]
    copies = [
        pltpu.make_async_copy(sources[i], buffers[i], sems.at[i]) for i in range(n_in)
    ]
    for copy in copies:
        copy.start()
    for copy in copies:
        copy.wait()
    setup_kernel(local, fields, *buffers, *outs)


def per_device(state, velocity, pre_exp, stoich, neighbours, switch, new_owner):
    tab = make_tables()
    local_count = state.shape[0]
    field_count = state.shape[1]
    rows = local_count * field_count
    curve_count = lax.axis_size("curve")
    curve_pos = lax.axis_index("curve")
    device_id = lax.axis_index("slab") * curve_count + curve_pos
    first_global = device_id * local_count
    positions = jnp.arange(local_count, dtype=jnp.int32)

    near_device = neighbours // local_count
    near_local = neighbours - near_device * local_count
    remote = near_device != device_id
    codes = (near_local + local_count * remote.astype(jnp.int32)).astype(f32)
    sto_col = jnp.zeros((local_count,), f32).at[:field_count].set(stoich)
    packed = jnp.concatenate(
        [
            codes,
            switch.astype(f32)[:, None],
            pre_exp[:, None],
            sto_col[:, None],
            jnp.zeros((local_count, LANE - 9), f32),
        ],
        axis=1,
    )
    fsel = jnp.asarray(to_bf16(np.arange(rows)[:, None] % field_count == np.arange(local_count)[None, :]))
    vt = jnp.transpose(velocity, (0, 2, 1))
    row_elem = np.arange(rows) // field_count
    bcast = jnp.asarray(to_bf16(row_elem[:, None] == np.arange(local_count)[None, :]))
    pick_rows = (np.arange(3)[:, None] + field_count * np.arange(local_count)[None, :]).reshape(-1)
    sel = jnp.asarray(to_bf16(pick_rows[:, None] == np.arange(rows)[None, :]))
    lift_t = jnp.asarray(to_bf16(tab["lift"].astype(np.float32).T))
    d7t = jnp.asarray(tab["d7t"])
    g7 = jnp.asarray(tab["g7"])
    d3t = jnp.asarray(tab["d3t"])
    tm = jnp.asarray(tab["tm"])
    mds = jnp.asarray(tab["mds"])
    pjt = jnp.asarray(tab["pjt"])

    send_shape = jax.ShapeDtypeStruct((rows, LANE), bf16)
    u_shape = jax.ShapeDtypeStruct((rows, P7**3), f32)
    c_shape = jax.ShapeDtypeStruct((rows, P3**3), f32)

    def exchange(sends):
        out = dict(zip(SEND_FACES, sends))
        return [
            shifted(out[1], "curve", 1),
            shifted(out[0], "curve", -1),
            shifted(out[5], "slab", 1),
            shifted(out[4], "slab", -1),
        ]

    setup_out = [
        jax.ShapeDtypeStruct((3, rows, P7**3), bf16),
        jax.ShapeDtypeStruct((rows, 6 * LANE), f32),
        jax.ShapeDtypeStruct((3, rows, P3**3), f32),
        jax.ShapeDtypeStruct((rows, 6 * LANE), f32),
        jax.ShapeDtypeStruct((6, rows, rows), bf16),
        jax.ShapeDtypeStruct((len(SEND_FACES), rows, rows), bf16),
        jax.ShapeDtypeStruct((local_count, 1), f32),
        jax.ShapeDtypeStruct((rows, 1), f32),
        jax.ShapeDtypeStruct((rows, 1), f32),
    ] + [send_shape] * 4
    u0 = state.reshape(rows, P7**3)
    setup_in = [u0, vt, packed, lift_t, g7, tm, bcast, fsel]
    res = pl.pallas_call(
        functools.partial(setup_entry, local_count, field_count, len(setup_in), len(setup_out)),
        out_shape=setup_out,
        in_specs=[pl.BlockSpec(memory_space=pl.ANY) for _ in setup_in],
        out_specs=[_vmem() for _ in setup_out],
        scratch_shapes=[pltpu.VMEM(x.shape, x.dtype) for x in setup_in]
        + [pltpu.SemaphoreType.DMA((len(setup_in),))],
        compiler_params=pltpu.CompilerParams(vmem_limit_bytes=48 * 1024 * 1024),
    )(*setup_in)
    v7, m7, v3, m3, p_local, p_remote, pre, stc, sw = res[:9]
    sends = res[9:]
    common = [p_local, p_remote, v7, m7, pre, stc, bcast, sel, d7t, g7]
    recv = exchange(sends)
    res = run_stage(
        (False, False, False, True, local_count),
        [u0] + recv + common,
        [u_shape] + [send_shape] * 4,
    )
    first, sends = res[0], res[1:]
    recv = exchange(sends)
    res = run_stage(
        (False, True, True, True, local_count),
        [first, u0] + recv + common + [tm, sw, pjt],
        [u_shape, c_shape] + [send_shape] * 4,
    )
    after, coarse, sends = res[0], res[1], res[2:]
    recv = exchange(sends)
    mixed_tail = [v3, m3, d3t, mds, tm, sw]
    res = run_stage(
        (True, False, False, True, local_count),
        [after, coarse] + recv + common + mixed_tail,
        [u_shape, c_shape] + [send_shape] * 4,
    )
    first7, first3, sends = res[0], res[1], res[2:]
    recv = exchange(sends)
    res = run_stage(
        (True, True, False, False, local_count),
        [first7, first3, after, coarse] + recv + common + mixed_tail,
        [u_shape, c_shape],
    )
    final7 = res[0].reshape(local_count, field_count, P7**3)
    final3 = res[1].reshape(local_count, field_count * P3**3)

    switched = switch == 1
    left_pos = (curve_pos + curve_count - 1) % curve_count
    right_pos = (curve_pos + 1) % curve_count
    to_left = (new_owner == left_pos) & ~switched
    to_right = (new_owner == right_pos) & ~switched
    stays_home = ~switched & ~to_left & ~to_right

    def first_rows(mask):
        rank = jnp.cumsum(mask.astype(jnp.int32)) - 1
        slot = jnp.arange(MOVE_CAP, dtype=jnp.int32)
        chosen = mask[None, :] & (rank[None, :] == slot[:, None])
        live = jnp.any(chosen, axis=1)
        row = jnp.sum(jnp.where(chosen, positions[None, :], 0), axis=1)
        return row, live

    left_rows, left_live = first_rows(to_left)
    right_rows, right_live = first_rows(to_right)
    left_ids = jnp.where(left_live, first_global + left_rows, missing_id)
    right_ids = jnp.where(right_live, first_global + right_rows, missing_id)
    home_ids = jnp.where(stays_home, first_global + positions, missing_id)
    from_right_ids = shifted(left_ids, "curve", -1)
    from_left_ids = shifted(right_ids, "curve", 1)
    from_right = shifted(final7[left_rows], "curve", -1)
    from_left = shifted(final7[right_rows], "curve", 1)
    cand_ids = jnp.concatenate([home_ids, from_left_ids, from_right_ids])
    cand_count = cand_ids.shape[0]
    rank = jnp.sum((cand_ids[None, :] < cand_ids[:, None]).astype(jnp.int32), axis=1)
    slot = jnp.arange(HOLD7, dtype=jnp.int32)
    pick = (rank[None, :] == slot[:, None]) & (cand_ids[None, :] < missing_id)
    order = jnp.sum(jnp.where(pick, jnp.arange(cand_count, dtype=jnp.int32)[None, :], 0), axis=1)
    slot_live = jnp.any(pick, axis=1)
    held = jnp.concatenate([final7, from_left, from_right], axis=0)[order]
    state7_out = jnp.where(slot_live[:, None, None], held, 0.0)
    state3_out = jnp.where(switched[:, None], final3, 0.0)
    return (state7_out, state3_out)


def solution(mesh):
    return jax.shard_map(
        per_device,
        mesh=mesh,
        in_specs=(
            P(("slab", "curve"), None, None),
            P(None, None, ("slab", "curve")),
            P(("slab", "curve")),
            P(),
            P(("slab", "curve"), None),
            P(("slab", "curve")),
            P(("slab", "curve")),
        ),
        out_specs=(P(("slab", "curve"), None, None), P(("slab", "curve"), None)),
        check_vma=False,
    )
```

```python
import functools

import jax
import jax.numpy as jnp
import ml_dtypes
import numpy as np
from jax import lax
from jax.experimental import pallas as pl
from jax.experimental.pallas import tpu as pltpu
from jax.sharding import PartitionSpec as P

P7 = 8
P3 = 4
MOVE_CAP = 2
HOLD7 = 12
LANE = 128

TIME_STEP = 0.002
ACTIVATION = 1.5
SIDE_SIGNS = (-1.0, 1.0, -1.0, 1.0, -1.0, 1.0)
OPPOSITE = (1, 0, 3, 2, 5, 4)
SEND_FACES = (0, 1, 4, 5)
missing_id = 1 << 30

f32 = jnp.float32
bf16 = jnp.bfloat16


def shifted(value, axis, steps):
    count = lax.axis_size(axis)
    pairs = [(source, (source + steps) % count) for source in range(count)]
    return lax.ppermute(value, axis, pairs)


def lobatto_points(number):
    return -np.cos(np.pi * np.arange(number) / (number - 1))


def lagrange_weights(points):
    weights = np.ones(points.shape[0])
    for row_id in range(points.shape[0]):
        for col_id in range(points.shape[0]):
            if col_id != row_id:
                weights[row_id] = weights[row_id] / (points[row_id] - points[col_id])
    return weights


def derivative_matrix(points):
    weights = lagrange_weights(points)
    number = points.shape[0]
    matrix = np.zeros((number, number))
    for row_id in range(number):
        for col_id in range(number):
            if col_id != row_id:
                matrix[row_id, col_id] = (
                    weights[col_id] / weights[row_id] / (points[row_id] - points[col_id])
                )
        matrix[row_id, row_id] = -np.sum(matrix[row_id])
    return matrix


def interpolation_matrix(source, target):
    matrix = np.ones((target.shape[0], source.shape[0]))
    for col_id in range(source.shape[0]):
        for other_id in range(source.shape[0]):
            if other_id != col_id:
                matrix[:, col_id] = (
                    matrix[:, col_id]
                    * (target - source[other_id])
                    / (source[col_id] - source[other_id])
                )
    return matrix


def spread_three(matrix, identity):
    return (
        np.kron(matrix, np.kron(identity, identity)),
        np.kron(identity, np.kron(matrix, identity)),
        np.kron(identity, np.kron(identity, matrix)),
    )


def face_nodes(extent):
    grid = np.arange(extent**3).reshape(extent, extent, extent)
    last = extent - 1
    pieces = (grid[0], grid[last], grid[:, 0], grid[:, last], grid[:, :, 0], grid[:, :, last])
    return [piece.reshape(-1) for piece in pieces]


def to_bf16(x):
    return np.asarray(np.asarray(x, np.float32).astype(ml_dtypes.bfloat16))


def split_parts(x):
    x = np.asarray(x, np.float32)
    hi = x.astype(ml_dtypes.bfloat16)
    rest = x - hi.astype(np.float32)
    mid = rest.astype(ml_dtypes.bfloat16)
    lo = (rest - mid.astype(np.float32)).astype(ml_dtypes.bfloat16)
    return np.stack([hi, mid, lo])


def make_tables():
    fine_points = lobatto_points(P7)
    coarse_points = lobatto_points(P3)
    fine_derivs = spread_three(derivative_matrix(fine_points), np.eye(P7))
    coarse_derivs = spread_three(derivative_matrix(coarse_points), np.eye(P3))
    downward = interpolation_matrix(fine_points, coarse_points)
    upward = interpolation_matrix(coarse_points, fine_points)
    d7t = np.stack([to_bf16(m.T) for m in fine_derivs])
    d3t = np.stack([to_bf16(m).T for m in coarse_derivs])
    lift_table = to_bf16(np.kron(upward, np.kron(upward, upward)))
    projection = np.asarray(np.kron(downward, np.kron(downward, downward)), np.float32)
    mortar_up = np.asarray(np.kron(upward, upward), np.float32)
    mortar_down = np.asarray(np.kron(downward, downward), np.float32)
    nodes7 = face_nodes(P7)
    nodes3 = face_nodes(P3)
    n7 = P7**3
    n3 = P3**3
    g7 = np.zeros((n7, 6 * LANE), np.float32)
    tm = np.zeros((n3, 6 * LANE), np.float32)
    mds = np.zeros((6 * LANE, n3), np.float32)
    for side in range(6):
        for q, node in enumerate(nodes7[side]):
            g7[node, side * LANE + q] = 1.0
        for k, node in enumerate(nodes3[side]):
            tm[node, side * LANE : side * LANE + P7 * P7] = mortar_up[:, k]
            mds[side * LANE : side * LANE + P7 * P7, node] = mortar_down[k, :]
    tables = {
        "d7t": to_bf16(d7t),
        "d3t": to_bf16(d3t),
        "lift": lift_table,
        "mortar_up": mortar_up,
        "g7": to_bf16(g7),
        "tm": split_parts(tm),
        "mds": split_parts(mds),
        "pjt": split_parts(projection.T),
        "nodes7": nodes7,
        "nodes3": nodes3,
    }
    return tables


def _dot(a, b):
    return jnp.dot(a, b, preferred_element_type=f32)


def _split(x):
    hi = x.astype(bf16)
    rest = x - hi.astype(f32)
    mid = rest.astype(bf16)
    lo = (rest - mid.astype(f32)).astype(bf16)
    return hi, mid, lo


def _exact_left(x, table):
    hi, mid, lo = _split(x)
    return (_dot(hi, table) + _dot(mid, table)) + _dot(lo, table)


def _dot_t(a, b):
    return lax.dot_general(a, b, (((1,), (1,)), ((), ())), preferred_element_type=f32)


def _exact_left_t(x, table):
    hi, mid, lo = _split(x)
    return (_dot_t(hi, table) + _dot_t(mid, table)) + _dot_t(lo, table)


def _exact_right(table, x):
    hi, mid, lo = _split(x)
    return (_dot(table, hi) + _dot(table, mid)) + _dot(table, lo)


def _full(x, parts_ref):
    xh, xm, xl = _split(x)
    bh = parts_ref[0]
    bm = parts_ref[1]
    bl = parts_ref[2]
    return _dot(xh, bh) + (_dot(xh, bm) + _dot(xm, bh)) + (
        _dot(xh, bl) + _dot(xm, bm) + _dot(xl, bh)
    )


def _rate_source(values, pre, stc, bc, sel, local):
    picked = _exact_right(sel, values)
    v0 = picked[0:local]
    v1 = picked[local : 2 * local]
    v2 = picked[2 * local : 3 * local]
    rate = pre * jnp.exp(-ACTIVATION * jnp.exp(-v0)) * v1 * v2
    return stc * _exact_right(bc, rate)


def stage_kernel(coarse, second, project, sends, local, *refs):
    refs = list(refs)

    def take():
        return refs.pop(0)

    u_ref = take()
    c_ref = take() if coarse else None
    bu_ref = take() if second else None
    bc_ref = take() if (second and coarse) else None
    recv = {s: take() for s in SEND_FACES}
    pl_ref = take()
    pr_ref = take()
    v7_ref = take()
    m7_ref = take()
    pre_ref = take()
    stc_ref = take()
    bc_tab = take()
    sel_tab = take()
    d7_ref = take()
    g7_ref = take()
    if coarse:
        v3_ref = take()
        m3_ref = take()
        d3_ref = take()
        mds_ref = take()
    if coarse or project:
        tm_ref = take()
        sw_ref = take()
    if project:
        pj_ref = take()
    last = coarse and not sends
    if last:
        sel_l_ref = take()
        sel_r_ref = take()
    out_u = take()
    out_c = take() if (coarse or project) else None
    out_send = [take() for _ in SEND_FACES] if sends else None
    if last:
        pay_l_ref = take()
        pay_r_ref = take()

    pre = pre_ref[...]
    stc = stc_ref[...]
    bcast = bc_tab[...]
    sel = sel_tab[...]
    u = u_ref[...]
    trace7 = _dot(u.astype(bf16), g7_ref[...])
    if coarse:
        c = c_ref[...]
        trace3 = _full(c, tm_ref).astype(bf16).astype(f32)
        switched = sw_ref[...] > 0.5
        own = jnp.where(switched, trace3, trace7)
    else:
        own = trace7
    own_b = own.astype(bf16)
    near_blocks = []
    for side in range(6):
        other = OPPOSITE[side]
        block = own_b[:, other * LANE : (other + 1) * LANE]
        near = _dot(pl_ref[side], block)
        if side in SEND_FACES:
            k = SEND_FACES.index(side)
            near = near + _dot(pr_ref[k], recv[side][...])
        near_blocks.append(near)
    near = jnp.concatenate(near_blocks, axis=1)

    divergence = None
    for d in range(3):
        flux = (v7_ref[d].astype(f32) * u).astype(bf16)
        term = _dot(flux, d7_ref[d])
        divergence = term if divergence is None else divergence + term
    result = _rate_source(u, pre, stc, bcast, sel, local) - divergence
    jump = (P7 * (P7 - 1) / 2.0) * (m7_ref[...] * (trace7 - near))
    rate7 = result + _exact_left_t(jump, g7_ref[...])

    if coarse:
        div3 = None
        for d in range(3):
            flux3 = (v3_ref[d] * c).astype(bf16)
            term = _dot(flux3, d3_ref[d])
            div3 = term if div3 is None else div3 + term
        result3 = _rate_source(c, pre, stc, bcast, sel, local) - div3
        jump3 = m3_ref[...] * (trace3 - near)
        rate3 = result3 + (P3 * (P3 - 1) / 2.0) * _full(jump3, mds_ref)

    if second:
        new_u = 0.5 * (bu_ref[...] + u + TIME_STEP * rate7)
    else:
        new_u = u + TIME_STEP * rate7
    out_u[...] = new_u
    new_c = None
    if coarse:
        if second:
            new_c = 0.5 * (bc_ref[...] + c + TIME_STEP * rate3)
        else:
            new_c = c + TIME_STEP * rate3
        if last:
            out_c[...] = jnp.where(sw_ref[...] > 0.5, new_c, 0.0)
            pay_l_ref[...] = _exact_right(sel_l_ref[...], new_u)
            pay_r_ref[...] = _exact_right(sel_r_ref[...], new_u)
        else:
            out_c[...] = new_c
    if project:
        new_c = _full(new_u, pj_ref)
        out_c[...] = new_c
    if sends:
        send7 = _dot(new_u.astype(bf16), g7_ref[...])
        if new_c is not None:
            send3 = _full(new_c, tm_ref).astype(bf16).astype(f32)
            send = jnp.where(sw_ref[...] > 0.5, send3, send7)
        else:
            send = send7
        send = send.astype(bf16)
        for k, side in enumerate(SEND_FACES):
            out_send[k][...] = send[:, side * LANE : (side + 1) * LANE]


def _vmem():
    return pl.BlockSpec(memory_space=pltpu.VMEM)


def run_stage(flags, inputs, out_shapes):
    coarse, second, project, sends, local = flags
    kernel = functools.partial(stage_kernel, coarse, second, project, sends, local)
    return pl.pallas_call(
        kernel,
        out_shape=out_shapes,
        in_specs=[_vmem() for _ in inputs],
        out_specs=[_vmem() for _ in out_shapes],
        compiler_params=pltpu.CompilerParams(vmem_limit_bytes=48 * 1024 * 1024),
    )(*inputs)


def setup_kernel(local, fields, u_ref, vt_ref, packed_ref, lift_ref, g7_ref, tm_ref, bc_ref,
                 fsel_ref, v7_out, m7_out, v3_out, m3_out, pl_out, pr_out,
                 pre_out, stc_out, sw_out, hinfo_out, cnt_l_out, cnt_r_out, sel_l_out,
                 sel_r_out, *send_refs):
    rows = local * fields
    bcast = bc_ref[...]
    lanes = lax.broadcasted_iota(jnp.int32, (local, 6 * LANE), 1) // LANE
    sign = jnp.where(lanes % 2 == 0, -1.0, 1.0)
    fvg = []
    mvg = []
    for d in range(3):
        vt = vt_ref[d]
        fv = _dot(vt, lift_ref[...]).astype(bf16)
        v7_out[d] = _dot(bcast, fv).astype(bf16)
        v3_out[d] = _dot(bcast, vt)
        fvg.append(_dot(fv, g7_ref[...]))
        mvg.append((_dot(vt, tm_ref[0]) + _dot(vt, tm_ref[1])) + _dot(vt, tm_ref[2]))

    def by_block(parts):
        return jnp.where(lanes < 2, parts[0], jnp.where(lanes < 4, parts[1], parts[2]))

    m7 = jnp.minimum(sign * by_block(fvg), 0.0)
    m7_out[...] = _dot(bcast, m7.astype(bf16))
    m3 = jnp.minimum(sign * by_block(mvg), 0.0)
    m3_out[...] = _exact_right(bcast, m3)
    rep = _dot(bcast, packed_ref[...].astype(bf16))
    row_f = (lax.broadcasted_iota(jnp.int32, (rows, 1), 0) % fields).astype(f32)
    cols = lax.broadcasted_iota(jnp.int32, (rows, rows), 1).astype(f32)
    for side in range(6):
        code = rep[:, side : side + 1]
        far = code >= local
        target = (code - jnp.where(far, float(local), 0.0)) * fields + row_f
        hit = cols == target
        pl_out[side] = jnp.where(hit & ~far, 1.0, 0.0).astype(bf16)
        if side in SEND_FACES:
            pr_out[SEND_FACES.index(side)] = jnp.where(hit & far, 1.0, 0.0).astype(bf16)
    sw_out[...] = rep[:, 6:7]
    packed = packed_ref[...]
    stay_sw = packed[:, 6:7] < 0.5
    go_left = (packed[:, 9:10] == packed[:, 10:11]) & stay_sw
    go_right = (packed[:, 9:10] == packed[:, 11:12]) & stay_sw
    stays = stay_sw & ~go_left & ~go_right
    lane16 = lax.broadcasted_iota(jnp.int32, (local, LANE), 1)
    marks = jnp.where(
        lane16 == 0, go_left.astype(f32),
        jnp.where(lane16 == 1, go_right.astype(f32), jnp.where(lane16 == 2, stays.astype(f32), 0.0)),
    ).astype(bf16)
    er = lax.broadcasted_iota(jnp.int32, (local, local), 0)
    ec = lax.broadcasted_iota(jnp.int32, (local, local), 1)
    before = _dot(jnp.where(ec < er, 1.0, 0.0).astype(bf16), marks)
    totals = _dot(jnp.ones((local, local), bf16), marks)
    info = jnp.where(lane16 < 3, marks.astype(f32), 0.0)
    for k in range(3):
        info = jnp.where(lane16 == 3 + k, before[:, k : k + 1], info)
    info = jnp.where(lane16 == 6, totals[:, 2:3], info)
    info = jnp.where(lane16 == 7, packed[:, 12:13], info)
    info = jnp.where(lane16 == 8, packed[:, 13:14], info)
    hinfo = _dot(bcast, info.astype(bf16))
    hinfo_out[...] = hinfo
    cnt_l_out[...] = jnp.broadcast_to(totals[0:1, 0:1], cnt_l_out.shape)
    cnt_r_out[...] = jnp.broadcast_to(totals[0:1, 1:2], cnt_r_out.shape)
    rf = lax.broadcasted_iota(jnp.int32, (rows, LANE), 0) % fields
    cc = lax.broadcasted_iota(jnp.int32, (rows, LANE), 1)
    eye = jnp.where(
        lax.broadcasted_iota(jnp.int32, (MOVE_CAP * fields, LANE), 0)
        == lax.broadcasted_iota(jnp.int32, (MOVE_CAP * fields, LANE), 1), 1.0, 0.0
    ).astype(bf16)
    for mark_lane, rank_lane, out in ((0, 3, sel_l_out), (1, 4, sel_r_out)):
        hit = (
            (hinfo[:, mark_lane : mark_lane + 1] > 0.5)
            & (hinfo[:, rank_lane : rank_lane + 1] == (cc // fields).astype(f32))
            & (rf == cc % fields)
            & (cc < MOVE_CAP * fields)
        )
        out[...] = _dot_t(eye, jnp.where(hit, 1.0, 0.0).astype(bf16)).astype(bf16)
    pre_out[...] = packed_ref[:, 7:8]
    stc_out[...] = _exact_right(fsel_ref[...], packed_ref[...])[:, 8:9]
    send = _dot(u_ref[...].astype(bf16), g7_ref[...]).astype(bf16)
    for k, side in enumerate(SEND_FACES):
        send_refs[k][...] = send[:, side * LANE : (side + 1) * LANE]


def final_kernel(fields, hold, home_ref, from_l_ref, from_r_ref, n_l_ref, n_r_ref, hinfo_ref,
                 out_ref):
    hinfo = hinfo_ref[...]
    n_l = n_l_ref[0:1, 0:1]
    n_r = n_r_ref[0:1, 0:1]
    n_h = hinfo[0:1, 6:7]
    first = hinfo[0:1, 7:8] > 0.5
    final = hinfo[0:1, 8:9] > 0.5
    off_l = jnp.where(first, n_h + n_r, jnp.where(final, n_r, 0.0))
    off_h = jnp.where(first, 0.0, jnp.where(final, n_r + n_l, n_l))
    off_r = jnp.where(first, n_h, jnp.where(final, 0.0, n_l + n_h))
    width = hold * fields
    eye = jnp.where(
        lax.broadcasted_iota(jnp.int32, (width, LANE), 0)
        == lax.broadcasted_iota(jnp.int32, (width, LANE), 1), 1.0, 0.0
    ).astype(bf16)

    def gather(values, valid, pos):
        count = values.shape[0]
        rf = lax.broadcasted_iota(jnp.int32, (count, LANE), 0) % fields
        cc = lax.broadcasted_iota(jnp.int32, (count, LANE), 1)
        hit = valid & (pos == (cc // fields).astype(f32)) & (rf == cc % fields) & (cc < width)
        pick = _dot_t(eye, jnp.where(hit, 1.0, 0.0).astype(bf16)).astype(bf16)
        return _exact_right(pick, values)

    total = gather(home_ref[...], hinfo[:, 2:3] > 0.5, off_h + hinfo[:, 5:6])
    moved = from_l_ref.shape[0]
    slot = (lax.broadcasted_iota(jnp.int32, (moved, 1), 0) // fields).astype(f32)
    total = total + gather(from_l_ref[...], slot < n_l, off_l + slot)
    total = total + gather(from_r_ref[...], slot < n_r, off_r + slot)
    out_ref[...] = total


def setup_entry(local, fields, n_in, n_out, *refs):
    sources = refs[:n_in]
    outs = refs[n_in : n_in + n_out]
    buffers = refs[n_in + n_out : 2 * n_in + n_out]
    sems = refs[2 * n_in + n_out]
    copies = [
        pltpu.make_async_copy(sources[i], buffers[i], sems.at[i]) for i in range(n_in)
    ]
    for copy in copies:
        copy.start()
    for copy in copies:
        copy.wait()
    setup_kernel(local, fields, *buffers, *outs)


def per_device(state, velocity, pre_exp, stoich, neighbours, switch, new_owner):
    tab = make_tables()
    local_count = state.shape[0]
    field_count = state.shape[1]
    rows = local_count * field_count
    curve_count = lax.axis_size("curve")
    curve_pos = lax.axis_index("curve")
    device_id = lax.axis_index("slab") * curve_count + curve_pos
    first_global = device_id * local_count
    positions = jnp.arange(local_count, dtype=jnp.int32)

    near_device = neighbours // local_count
    near_local = neighbours - near_device * local_count
    remote = near_device != device_id
    codes = (near_local + local_count * remote.astype(jnp.int32)).astype(f32)
    sto_col = jnp.zeros((local_count,), f32).at[:field_count].set(stoich)
    left_pos = (curve_pos + curve_count - 1) % curve_count
    right_pos = (curve_pos + 1) % curve_count
    ones = jnp.ones((local_count, 1), f32)
    packed = jnp.concatenate(
        [
            codes,
            switch.astype(f32)[:, None],
            pre_exp[:, None],
            sto_col[:, None],
            new_owner.astype(f32)[:, None],
            ones * left_pos.astype(f32),
            ones * right_pos.astype(f32),
            ones * (curve_pos == 0).astype(f32),
            ones * (curve_pos == curve_count - 1).astype(f32),
            jnp.zeros((local_count, LANE - 14), f32),
        ],
        axis=1,
    )
    fsel = jnp.asarray(to_bf16(np.arange(rows)[:, None] % field_count == np.arange(local_count)[None, :]))
    vt = jnp.transpose(velocity, (0, 2, 1))
    row_elem = np.arange(rows) // field_count
    bcast = jnp.asarray(to_bf16(row_elem[:, None] == np.arange(local_count)[None, :]))
    pick_rows = (np.arange(3)[:, None] + field_count * np.arange(local_count)[None, :]).reshape(-1)
    sel = jnp.asarray(to_bf16(pick_rows[:, None] == np.arange(rows)[None, :]))
    lift_t = jnp.asarray(to_bf16(tab["lift"].astype(np.float32).T))
    d7t = jnp.asarray(tab["d7t"])
    g7 = jnp.asarray(tab["g7"])
    d3t = jnp.asarray(tab["d3t"])
    tm = jnp.asarray(tab["tm"])
    mds = jnp.asarray(tab["mds"])
    pjt = jnp.asarray(tab["pjt"])

    send_shape = jax.ShapeDtypeStruct((rows, LANE), bf16)
    u_shape = jax.ShapeDtypeStruct((rows, P7**3), f32)
    c_shape = jax.ShapeDtypeStruct((rows, P3**3), f32)

    def exchange(sends):
        out = dict(zip(SEND_FACES, sends))
        return [
            shifted(out[1], "curve", 1),
            shifted(out[0], "curve", -1),
            shifted(out[5], "slab", 1),
            shifted(out[4], "slab", -1),
        ]

    setup_out = [
        jax.ShapeDtypeStruct((3, rows, P7**3), bf16),
        jax.ShapeDtypeStruct((rows, 6 * LANE), f32),
        jax.ShapeDtypeStruct((3, rows, P3**3), f32),
        jax.ShapeDtypeStruct((rows, 6 * LANE), f32),
        jax.ShapeDtypeStruct((6, rows, rows), bf16),
        jax.ShapeDtypeStruct((len(SEND_FACES), rows, rows), bf16),
        jax.ShapeDtypeStruct((local_count, 1), f32),
        jax.ShapeDtypeStruct((rows, 1), f32),
        jax.ShapeDtypeStruct((rows, 1), f32),
        jax.ShapeDtypeStruct((rows, LANE), f32),
        jax.ShapeDtypeStruct((8, LANE), f32),
        jax.ShapeDtypeStruct((8, LANE), f32),
        jax.ShapeDtypeStruct((MOVE_CAP * field_count, rows), bf16),
        jax.ShapeDtypeStruct((MOVE_CAP * field_count, rows), bf16),
    ] + [send_shape] * 4
    u0 = state.reshape(rows, P7**3)
    setup_in = [u0, vt, packed, lift_t, g7, tm, bcast, fsel]
    res = pl.pallas_call(
        functools.partial(setup_entry, local_count, field_count, len(setup_in), len(setup_out)),
        out_shape=setup_out,
        in_specs=[pl.BlockSpec(memory_space=pltpu.HBM) for _ in setup_in],
        out_specs=[_vmem() for _ in setup_out],
        scratch_shapes=[pltpu.VMEM(x.shape, x.dtype) for x in setup_in]
        + [pltpu.SemaphoreType.DMA((len(setup_in),))],
        compiler_params=pltpu.CompilerParams(vmem_limit_bytes=63 * 1024 * 1024),
    )(*setup_in)
    v7, m7, v3, m3, p_local, p_remote, pre, stc, sw = res[:9]
    hinfo, cnt_l, cnt_r, sel_l, sel_r = res[9:14]
    sends = res[14:]
    n_from_right = shifted(cnt_l, "curve", -1)
    n_from_left = shifted(cnt_r, "curve", 1)
    common = [p_local, p_remote, v7, m7, pre, stc, bcast, sel, d7t, g7]
    recv = exchange(sends)
    res = run_stage(
        (False, False, False, True, local_count),
        [u0] + recv + common,
        [u_shape] + [send_shape] * 4,
    )
    first, sends = res[0], res[1:]
    recv = exchange(sends)
    res = run_stage(
        (False, True, True, True, local_count),
        [first, u0] + recv + common + [tm, sw, pjt],
        [u_shape, c_shape] + [send_shape] * 4,
    )
    after, coarse, sends = res[0], res[1], res[2:]
    recv = exchange(sends)
    mixed_tail = [v3, m3, d3t, mds, tm, sw]
    res = run_stage(
        (True, False, False, True, local_count),
        [after, coarse] + recv + common + mixed_tail,
        [u_shape, c_shape] + [send_shape] * 4,
    )
    first7, first3, sends = res[0], res[1], res[2:]
    recv = exchange(sends)
    pay_shape = jax.ShapeDtypeStruct((MOVE_CAP * field_count, P7**3), f32)
    res = run_stage(
        (True, True, False, False, local_count),
        [first7, first3, after, coarse] + recv + common + mixed_tail + [sel_l, sel_r],
        [u_shape, c_shape, pay_shape, pay_shape],
    )
    final7, final3, pay_l, pay_r = res
    from_right = shifted(pay_l, "curve", -1)
    from_left = shifted(pay_r, "curve", 1)
    held = pl.pallas_call(
        functools.partial(final_kernel, field_count, HOLD7),
        out_shape=jax.ShapeDtypeStruct((HOLD7 * field_count, P7**3), f32),
        in_specs=[_vmem() for _ in range(6)],
        out_specs=_vmem(),
    )(final7, from_left, from_right, n_from_left, n_from_right, hinfo)
    state7_out = held.reshape(HOLD7, field_count, P7**3)
    state3_out = final3.reshape(local_count, field_count * P3**3)
    return (state7_out, state3_out)


def solution(mesh):
    return jax.shard_map(
        per_device,
        mesh=mesh,
        in_specs=(
            P(("slab", "curve"), None, None),
            P(None, None, ("slab", "curve")),
            P(("slab", "curve")),
            P(),
            P(("slab", "curve"), None),
            P(("slab", "curve")),
            P(("slab", "curve")),
        ),
        out_specs=(P(("slab", "curve"), None, None), P(("slab", "curve"), None)),
        check_vma=False,
    )
```

```python
import functools

import jax
import jax.numpy as jnp
import ml_dtypes
import numpy as np
from jax import lax
from jax.experimental import pallas as pl
from jax.experimental.pallas import tpu as pltpu
from jax.sharding import PartitionSpec as P

P7 = 8
P3 = 4
MOVE_CAP = 2
HOLD7 = 12
LANE = 128

TIME_STEP = 0.002
ACTIVATION = 1.5
SIDE_SIGNS = (-1.0, 1.0, -1.0, 1.0, -1.0, 1.0)
OPPOSITE = (1, 0, 3, 2, 5, 4)
SEND_FACES = (0, 1, 4, 5)
missing_id = 1 << 30

f32 = jnp.float32
bf16 = jnp.bfloat16


def shifted(value, axis, steps):
    count = lax.axis_size(axis)
    pairs = [(source, (source + steps) % count) for source in range(count)]
    return lax.ppermute(value, axis, pairs)


def lobatto_points(number):
    return -np.cos(np.pi * np.arange(number) / (number - 1))


def lagrange_weights(points):
    weights = np.ones(points.shape[0])
    for row_id in range(points.shape[0]):
        for col_id in range(points.shape[0]):
            if col_id != row_id:
                weights[row_id] = weights[row_id] / (points[row_id] - points[col_id])
    return weights


def derivative_matrix(points):
    weights = lagrange_weights(points)
    number = points.shape[0]
    matrix = np.zeros((number, number))
    for row_id in range(number):
        for col_id in range(number):
            if col_id != row_id:
                matrix[row_id, col_id] = (
                    weights[col_id] / weights[row_id] / (points[row_id] - points[col_id])
                )
        matrix[row_id, row_id] = -np.sum(matrix[row_id])
    return matrix


def interpolation_matrix(source, target):
    matrix = np.ones((target.shape[0], source.shape[0]))
    for col_id in range(source.shape[0]):
        for other_id in range(source.shape[0]):
            if other_id != col_id:
                matrix[:, col_id] = (
                    matrix[:, col_id]
                    * (target - source[other_id])
                    / (source[col_id] - source[other_id])
                )
    return matrix


def spread_three(matrix, identity):
    return (
        np.kron(matrix, np.kron(identity, identity)),
        np.kron(identity, np.kron(matrix, identity)),
        np.kron(identity, np.kron(identity, matrix)),
    )


def face_nodes(extent):
    grid = np.arange(extent**3).reshape(extent, extent, extent)
    last = extent - 1
    pieces = (grid[0], grid[last], grid[:, 0], grid[:, last], grid[:, :, 0], grid[:, :, last])
    return [piece.reshape(-1) for piece in pieces]


def to_bf16(x):
    return np.asarray(np.asarray(x, np.float32).astype(ml_dtypes.bfloat16))


def split_parts(x):
    x = np.asarray(x, np.float32)
    hi = x.astype(ml_dtypes.bfloat16)
    rest = x - hi.astype(np.float32)
    mid = rest.astype(ml_dtypes.bfloat16)
    lo = (rest - mid.astype(np.float32)).astype(ml_dtypes.bfloat16)
    return np.stack([hi, mid, lo])


def make_tables():
    fine_points = lobatto_points(P7)
    coarse_points = lobatto_points(P3)
    fine_derivs = spread_three(derivative_matrix(fine_points), np.eye(P7))
    coarse_derivs = spread_three(derivative_matrix(coarse_points), np.eye(P3))
    downward = interpolation_matrix(fine_points, coarse_points)
    upward = interpolation_matrix(coarse_points, fine_points)
    d7t = np.stack([to_bf16(m.T) for m in fine_derivs])
    d3t = np.stack([to_bf16(m).T for m in coarse_derivs])
    lift_table = to_bf16(np.kron(upward, np.kron(upward, upward)))
    projection = np.asarray(np.kron(downward, np.kron(downward, downward)), np.float32)
    mortar_up = np.asarray(np.kron(upward, upward), np.float32)
    mortar_down = np.asarray(np.kron(downward, downward), np.float32)
    nodes7 = face_nodes(P7)
    nodes3 = face_nodes(P3)
    n7 = P7**3
    n3 = P3**3
    g7 = np.zeros((n7, 6 * LANE), np.float32)
    tm = np.zeros((n3, 6 * LANE), np.float32)
    mds = np.zeros((6 * LANE, n3), np.float32)
    for side in range(6):
        for q, node in enumerate(nodes7[side]):
            g7[node, side * LANE + q] = 1.0
        for k, node in enumerate(nodes3[side]):
            tm[node, side * LANE : side * LANE + P7 * P7] = mortar_up[:, k]
            mds[side * LANE : side * LANE + P7 * P7, node] = mortar_down[k, :]
    tables = {
        "d7t": to_bf16(d7t),
        "d3t": to_bf16(d3t),
        "lift": lift_table,
        "mortar_up": mortar_up,
        "g7": to_bf16(g7),
        "tm": split_parts(tm),
        "mds": split_parts(mds),
        "pjt": split_parts(projection.T),
        "nodes7": nodes7,
        "nodes3": nodes3,
    }
    return tables


def _dot(a, b):
    return jnp.dot(a, b, preferred_element_type=f32)


def _split(x):
    hi = x.astype(bf16)
    rest = x - hi.astype(f32)
    mid = rest.astype(bf16)
    lo = (rest - mid.astype(f32)).astype(bf16)
    return hi, mid, lo


def _exact_left(x, table):
    hi, mid, lo = _split(x)
    return (_dot(hi, table) + _dot(mid, table)) + _dot(lo, table)


def _dot_t(a, b):
    return lax.dot_general(a, b, (((1,), (1,)), ((), ())), preferred_element_type=f32)


def _exact_left_t(x, table):
    hi, mid, lo = _split(x)
    return (_dot_t(hi, table) + _dot_t(mid, table)) + _dot_t(lo, table)


def _exact_right(table, x):
    hi, mid, lo = _split(x)
    return (_dot(table, hi) + _dot(table, mid)) + _dot(table, lo)


def _full_t(x, parts_ref):
    xh, xm, xl = _split(x)
    bh = parts_ref[0]
    bm = parts_ref[1]
    bl = parts_ref[2]
    return _dot_t(xh, bh) + (_dot_t(xh, bm) + _dot_t(xm, bh)) + (
        _dot_t(xh, bl) + _dot_t(xm, bm) + _dot_t(xl, bh)
    )


class View:
    def __init__(self, ref, start, rows, width):
        self.ref = ref
        self.start = start
        self.rows = rows
        self.width = width

    def __getitem__(self, k):
        if k is Ellipsis:
            k = 0
        top = self.start + k * self.rows
        return self.ref[top : top + self.rows, 0 : self.width]


def table_layout(rows, local):
    n7 = P7**3
    n3 = P3**3
    wide = {"g7": (0, n7, 6 * LANE), "tm": (n7, n3, 6 * LANE), "mdst": (n7 + 3 * n3, n3, 6 * LANE)}
    mid = {"d7t": (0, n7, n7), "lift_t": (3 * n7, n3, n7), "pj": (3 * n7 + n3, n3, n7)}
    narrow = {
        "bcast": (0, rows, local),
        "sel": (rows, 3 * local, rows),
        "fsel": (rows + 3 * local, rows, local),
        "d3t": (2 * rows + 3 * local, n3, n3),
    }
    return wide, mid, narrow


def table_views(wide_ref, mid_ref, narrow_ref, local):
    rows = narrow_ref.shape[1]
    layouts = table_layout(rows, local)
    views = {}
    for ref, layout in zip((wide_ref, mid_ref, narrow_ref), layouts):
        for name, (start, count, width) in layout.items():
            views[name] = View(ref, start, count, width)
    return views


def _full(x, parts_ref):
    xh, xm, xl = _split(x)
    bh = parts_ref[0]
    bm = parts_ref[1]
    bl = parts_ref[2]
    return _dot(xh, bh) + (_dot(xh, bm) + _dot(xm, bh)) + (
        _dot(xh, bl) + _dot(xm, bm) + _dot(xl, bh)
    )


def _rate_source(values, pre, stc, bc, sel, local):
    picked = _exact_right(sel, values)
    v0 = picked[0:local]
    v1 = picked[local : 2 * local]
    v2 = picked[2 * local : 3 * local]
    rate = pre * jnp.exp(-ACTIVATION * jnp.exp(-v0)) * v1 * v2
    return stc * _exact_right(bc, rate)


def stage_kernel(coarse, second, project, sends, local, *refs):
    refs = list(refs)

    def take():
        return refs.pop(0)

    u_ref = take()
    c_ref = take() if coarse else None
    bu_ref = take() if second else None
    bc_ref = take() if (second and coarse) else None
    recv = {s: take() for s in SEND_FACES}
    pl_ref = take()
    pr_ref = take()
    v7_ref = take()
    m7_ref = take()
    pre_ref = take()
    stc_ref = take()
    views = table_views(take(), take(), take(), local)
    bc_tab = views["bcast"]
    sel_tab = views["sel"]
    d7_ref = views["d7t"]
    g7_ref = views["g7"]
    d3_ref = views["d3t"]
    mds_ref = views["mdst"]
    tm_ref = views["tm"]
    pj_ref = views["pj"]
    if coarse:
        v3_ref = take()
        m3_ref = take()
    if coarse or project:
        sw_ref = take()
    last = coarse and not sends
    if last:
        sel_l_ref = take()
        sel_r_ref = take()
        cnt_l_ref = take()
        cnt_r_ref = take()
    out_u = take()
    out_c = take() if (coarse or project) else None
    out_send = [take() for _ in SEND_FACES] if sends else None
    if last:
        pay_l_ref = take()
        pay_r_ref = take()

    pre = pre_ref[...]
    stc = stc_ref[...]
    bcast = bc_tab[...]
    sel = sel_tab[...]
    u = u_ref[...]
    trace7 = _dot(u.astype(bf16), g7_ref[...])
    if coarse:
        c = c_ref[...]
        trace3 = _full(c, tm_ref).astype(bf16).astype(f32)
        switched = sw_ref[...] > 0.5
        own = jnp.where(switched, trace3, trace7)
    else:
        own = trace7
    own_b = own.astype(bf16)
    near_blocks = []
    for side in range(6):
        other = OPPOSITE[side]
        block = own_b[:, other * LANE : (other + 1) * LANE]
        near = _dot(pl_ref[side], block)
        if side in SEND_FACES:
            k = SEND_FACES.index(side)
            near = near + _dot(pr_ref[k], recv[side][...])
        near_blocks.append(near)
    near = jnp.concatenate(near_blocks, axis=1)

    divergence = None
    for d in range(3):
        flux = (v7_ref[d].astype(f32) * u).astype(bf16)
        term = _dot(flux, d7_ref[d])
        divergence = term if divergence is None else divergence + term
    result = _rate_source(u, pre, stc, bcast, sel, local) - divergence
    jump = (P7 * (P7 - 1) / 2.0) * (m7_ref[...] * (trace7 - near))
    rate7 = result + _exact_left_t(jump, g7_ref[...])

    if coarse:
        div3 = None
        for d in range(3):
            flux3 = (v3_ref[d] * c).astype(bf16)
            term = _dot(flux3, d3_ref[d])
            div3 = term if div3 is None else div3 + term
        result3 = _rate_source(c, pre, stc, bcast, sel, local) - div3
        jump3 = m3_ref[...] * (trace3 - near)
        rate3 = result3 + (P3 * (P3 - 1) / 2.0) * _full_t(jump3, mds_ref)

    if second:
        new_u = 0.5 * (bu_ref[...] + u + TIME_STEP * rate7)
    else:
        new_u = u + TIME_STEP * rate7
    out_u[...] = new_u
    new_c = None
    if coarse:
        if second:
            new_c = 0.5 * (bc_ref[...] + c + TIME_STEP * rate3)
        else:
            new_c = c + TIME_STEP * rate3
        if last:
            out_c[...] = jnp.where(sw_ref[...] > 0.5, new_c, 0.0)
            moved = sel_l_ref.shape[0]
            pay_l_ref[0:moved, :] = _exact_right(sel_l_ref[...], new_u)
            pay_r_ref[0:moved, :] = _exact_right(sel_r_ref[...], new_u)
            tail = (pay_l_ref.shape[0] - moved, pay_l_ref.shape[1])
            pay_l_ref[moved:, :] = jnp.broadcast_to(cnt_l_ref[0:1, 0:1], tail)
            pay_r_ref[moved:, :] = jnp.broadcast_to(cnt_r_ref[0:1, 0:1], tail)
        else:
            out_c[...] = new_c
    if project:
        new_c = _full_t(new_u, pj_ref)
        out_c[...] = new_c
    if sends:
        send7 = _dot(new_u.astype(bf16), g7_ref[...])
        if new_c is not None:
            send3 = _full(new_c, tm_ref).astype(bf16).astype(f32)
            send = jnp.where(sw_ref[...] > 0.5, send3, send7)
        else:
            send = send7
        send = send.astype(bf16)
        for k, side in enumerate(SEND_FACES):
            out_send[k][...] = send[:, side * LANE : (side + 1) * LANE]


def _vmem():
    return pl.BlockSpec(memory_space=pltpu.VMEM)


def run_stage(flags, inputs, out_shapes):
    coarse, second, project, sends, local = flags
    kernel = functools.partial(stage_kernel, coarse, second, project, sends, local)
    return pl.pallas_call(
        kernel,
        out_shape=out_shapes,
        in_specs=[_vmem() for _ in inputs],
        out_specs=[_vmem() for _ in out_shapes],
        compiler_params=pltpu.CompilerParams(vmem_limit_bytes=48 * 1024 * 1024),
    )(*inputs)


def setup_kernel(local, fields, u_ref, vt_ref, packed_ref, wide_ref, mid_ref, narrow_ref, v7_out, m7_out, v3_out, m3_out, pl_out, pr_out,
                 pre_out, stc_out, sw_out, hinfo_out, cnt_l_out, cnt_r_out, sel_l_out,
                 sel_r_out, *send_refs):
    rows = local * fields
    views = table_views(wide_ref, mid_ref, narrow_ref, local)
    lift_ref = views["lift_t"]
    g7_ref = views["g7"]
    tm_ref = views["tm"]
    fsel_ref = views["fsel"]
    bcast = views["bcast"][...]
    lanes = lax.broadcasted_iota(jnp.int32, (local, 6 * LANE), 1) // LANE
    sign = jnp.where(lanes % 2 == 0, -1.0, 1.0)
    fvg = []
    mvg = []
    for d in range(3):
        vt = vt_ref[d]
        fv = _dot(vt, lift_ref[...]).astype(bf16)
        v7_out[d] = _dot(bcast, fv).astype(bf16)
        v3_out[d] = _dot(bcast, vt)
        fvg.append(_dot(fv, g7_ref[...]))
        mvg.append((_dot(vt, tm_ref[0]) + _dot(vt, tm_ref[1])) + _dot(vt, tm_ref[2]))

    def by_block(parts):
        return jnp.where(lanes < 2, parts[0], jnp.where(lanes < 4, parts[1], parts[2]))

    m7 = jnp.minimum(sign * by_block(fvg), 0.0)
    m7_out[...] = _dot(bcast, m7.astype(bf16))
    m3 = jnp.minimum(sign * by_block(mvg), 0.0)
    m3_out[...] = _exact_right(bcast, m3)
    rep = _dot(bcast, packed_ref[...].astype(bf16))
    row_f = (lax.broadcasted_iota(jnp.int32, (rows, 1), 0) % fields).astype(f32)
    cols = lax.broadcasted_iota(jnp.int32, (rows, rows), 1).astype(f32)
    for side in range(6):
        code = rep[:, side : side + 1]
        far = code >= local
        target = (code - jnp.where(far, float(local), 0.0)) * fields + row_f
        hit = cols == target
        pl_out[side] = jnp.where(hit & ~far, 1.0, 0.0).astype(bf16)
        if side in SEND_FACES:
            pr_out[SEND_FACES.index(side)] = jnp.where(hit & far, 1.0, 0.0).astype(bf16)
    sw_out[...] = rep[:, 6:7]
    packed = packed_ref[...]
    stay_sw = packed[:, 6:7] < 0.5
    go_left = (packed[:, 9:10] == packed[:, 10:11]) & stay_sw
    go_right = (packed[:, 9:10] == packed[:, 11:12]) & stay_sw
    stays = stay_sw & ~go_left & ~go_right
    lane16 = lax.broadcasted_iota(jnp.int32, (local, LANE), 1)
    marks = jnp.where(
        lane16 == 0, go_left.astype(f32),
        jnp.where(lane16 == 1, go_right.astype(f32), jnp.where(lane16 == 2, stays.astype(f32), 0.0)),
    ).astype(bf16)
    er = lax.broadcasted_iota(jnp.int32, (local, local), 0)
    ec = lax.broadcasted_iota(jnp.int32, (local, local), 1)
    before = _dot(jnp.where(ec < er, 1.0, 0.0).astype(bf16), marks)
    totals = _dot(jnp.ones((local, local), bf16), marks)
    info = jnp.where(lane16 < 3, marks.astype(f32), 0.0)
    for k in range(3):
        info = jnp.where(lane16 == 3 + k, before[:, k : k + 1], info)
    info = jnp.where(lane16 == 6, totals[:, 2:3], info)
    info = jnp.where(lane16 == 7, packed[:, 12:13], info)
    info = jnp.where(lane16 == 8, packed[:, 13:14], info)
    hinfo = _dot(bcast, info.astype(bf16))
    hinfo_out[...] = hinfo
    cnt_l_out[...] = jnp.broadcast_to(totals[0:1, 0:1], cnt_l_out.shape)
    cnt_r_out[...] = jnp.broadcast_to(totals[0:1, 1:2], cnt_r_out.shape)
    rf = lax.broadcasted_iota(jnp.int32, (rows, LANE), 0) % fields
    cc = lax.broadcasted_iota(jnp.int32, (rows, LANE), 1)
    eye = jnp.where(
        lax.broadcasted_iota(jnp.int32, (MOVE_CAP * fields, LANE), 0)
        == lax.broadcasted_iota(jnp.int32, (MOVE_CAP * fields, LANE), 1), 1.0, 0.0
    ).astype(bf16)
    for mark_lane, rank_lane, out in ((0, 3, sel_l_out), (1, 4, sel_r_out)):
        hit = (
            (hinfo[:, mark_lane : mark_lane + 1] > 0.5)
            & (hinfo[:, rank_lane : rank_lane + 1] == (cc // fields).astype(f32))
            & (rf == cc % fields)
            & (cc < MOVE_CAP * fields)
        )
        out[...] = _dot_t(eye, jnp.where(hit, 1.0, 0.0).astype(bf16)).astype(bf16)
    pre_out[...] = packed_ref[:, 7:8]
    stc_out[...] = _exact_right(fsel_ref[...], packed_ref[...])[:, 8:9]
    send = _dot(u_ref[...].astype(bf16), g7_ref[...]).astype(bf16)
    for k, side in enumerate(SEND_FACES):
        send_refs[k][...] = send[:, side * LANE : (side + 1) * LANE]


def final_kernel(fields, hold, home_ref, from_l_ref, from_r_ref, hinfo_ref, out_ref):
    hinfo = hinfo_ref[...]
    moved = MOVE_CAP * fields
    n_l = from_l_ref[moved : moved + 1, 0:1]
    n_r = from_r_ref[moved : moved + 1, 0:1]
    n_h = hinfo[0:1, 6:7]
    first = hinfo[0:1, 7:8] > 0.5
    final = hinfo[0:1, 8:9] > 0.5
    off_l = jnp.where(first, n_h + n_r, jnp.where(final, n_r, 0.0))
    off_h = jnp.where(first, 0.0, jnp.where(final, n_r + n_l, n_l))
    off_r = jnp.where(first, n_h, jnp.where(final, 0.0, n_l + n_h))
    width = hold * fields
    eye = jnp.where(
        lax.broadcasted_iota(jnp.int32, (width, LANE), 0)
        == lax.broadcasted_iota(jnp.int32, (width, LANE), 1), 1.0, 0.0
    ).astype(bf16)

    def gather(values, valid, pos):
        count = values.shape[0]
        rf = lax.broadcasted_iota(jnp.int32, (count, LANE), 0) % fields
        cc = lax.broadcasted_iota(jnp.int32, (count, LANE), 1)
        hit = valid & (pos == (cc // fields).astype(f32)) & (rf == cc % fields) & (cc < width)
        pick = _dot_t(eye, jnp.where(hit, 1.0, 0.0).astype(bf16)).astype(bf16)
        return _exact_right(pick, values)

    total = gather(home_ref[...], hinfo[:, 2:3] > 0.5, off_h + hinfo[:, 5:6])
    slot = (lax.broadcasted_iota(jnp.int32, (moved, 1), 0) // fields).astype(f32)
    total = total + gather(from_l_ref[0:moved, :], slot < n_l, off_l + slot)
    total = total + gather(from_r_ref[0:moved, :], slot < n_r, off_r + slot)
    out_ref[...] = total


def setup_entry(local, fields, n_in, n_out, *refs):
    sources = refs[:n_in]
    outs = refs[n_in : n_in + n_out]
    n_tab = 3
    n_own = n_in - n_tab
    buffers = refs[n_in + n_out : n_in + n_out + n_own]
    sems = refs[n_in + n_out + n_own]
    targets = list(buffers) + list(outs[n_out - n_tab :])
    copies = [
        pltpu.make_async_copy(sources[i], targets[i], sems.at[i]) for i in range(n_in)
    ]
    for copy in copies:
        copy.start()
    for copy in copies:
        copy.wait()
    setup_kernel(local, fields, *targets, *outs[: n_out - n_tab])


def per_device(state, velocity, pre_exp, stoich, neighbours, switch, new_owner):
    tab = make_tables()
    local_count = state.shape[0]
    field_count = state.shape[1]
    rows = local_count * field_count
    curve_count = lax.axis_size("curve")
    curve_pos = lax.axis_index("curve")
    device_id = lax.axis_index("slab") * curve_count + curve_pos
    first_global = device_id * local_count
    positions = jnp.arange(local_count, dtype=jnp.int32)

    near_device = neighbours // local_count
    near_local = neighbours - near_device * local_count
    remote = near_device != device_id
    codes = (near_local + local_count * remote.astype(jnp.int32)).astype(f32)
    sto_col = jnp.zeros((local_count,), f32).at[:field_count].set(stoich)
    left_pos = (curve_pos + curve_count - 1) % curve_count
    right_pos = (curve_pos + 1) % curve_count
    ones = jnp.ones((local_count, 1), f32)
    packed = jnp.concatenate(
        [
            codes,
            switch.astype(f32)[:, None],
            pre_exp[:, None],
            sto_col[:, None],
            new_owner.astype(f32)[:, None],
            ones * left_pos.astype(f32),
            ones * right_pos.astype(f32),
            ones * (curve_pos == 0).astype(f32),
            ones * (curve_pos == curve_count - 1).astype(f32),
            jnp.zeros((local_count, LANE - 14), f32),
        ],
        axis=1,
    )
    fsel_np = np.arange(rows)[:, None] % field_count == np.arange(local_count)[None, :]
    vt = jnp.transpose(velocity, (0, 2, 1))
    row_elem = np.arange(rows) // field_count
    bcast_np = row_elem[:, None] == np.arange(local_count)[None, :]
    pick_rows = (np.arange(3)[:, None] + field_count * np.arange(local_count)[None, :]).reshape(-1)
    sel_np = pick_rows[:, None] == np.arange(rows)[None, :]
    n7 = P7**3
    n3 = P3**3
    layouts = table_layout(rows, local_count)
    wide_np = np.zeros((n7 + 6 * n3, 6 * LANE), np.float32)
    mid_np = np.zeros((3 * n7 + 4 * n3, n7), np.float32)
    narrow_np = np.zeros((2 * rows + 3 * local_count + 3 * n3, rows), np.float32)
    pieces = {
        "g7": tab["g7"][None],
        "tm": tab["tm"],
        "mdst": np.transpose(tab["mds"], (0, 2, 1)),
        "d7t": tab["d7t"],
        "lift_t": tab["lift"].T[None],
        "pj": np.transpose(tab["pjt"], (0, 2, 1)),
        "bcast": bcast_np[None],
        "sel": sel_np[None],
        "fsel": fsel_np[None],
        "d3t": tab["d3t"],
    }
    for target, layout in zip((wide_np, mid_np, narrow_np), layouts):
        for name, (start, count, width) in layout.items():
            parts = np.asarray(pieces[name], np.float32)
            for k in range(parts.shape[0]):
                target[start + k * count : start + (k + 1) * count, :width] = parts[k]
    wide = jnp.asarray(to_bf16(wide_np))
    mid = jnp.asarray(to_bf16(mid_np))
    narrow = jnp.asarray(to_bf16(narrow_np))

    send_shape = jax.ShapeDtypeStruct((rows, LANE), bf16)
    u_shape = jax.ShapeDtypeStruct((rows, P7**3), f32)
    c_shape = jax.ShapeDtypeStruct((rows, P3**3), f32)

    def exchange(sends):
        out = dict(zip(SEND_FACES, sends))
        return [
            shifted(out[1], "curve", 1),
            shifted(out[0], "curve", -1),
            shifted(out[5], "slab", 1),
            shifted(out[4], "slab", -1),
        ]

    setup_out = [
        jax.ShapeDtypeStruct((3, rows, P7**3), bf16),
        jax.ShapeDtypeStruct((rows, 6 * LANE), f32),
        jax.ShapeDtypeStruct((3, rows, P3**3), f32),
        jax.ShapeDtypeStruct((rows, 6 * LANE), f32),
        jax.ShapeDtypeStruct((6, rows, rows), bf16),
        jax.ShapeDtypeStruct((len(SEND_FACES), rows, rows), bf16),
        jax.ShapeDtypeStruct((local_count, 1), f32),
        jax.ShapeDtypeStruct((rows, 1), f32),
        jax.ShapeDtypeStruct((rows, 1), f32),
        jax.ShapeDtypeStruct((rows, LANE), f32),
        jax.ShapeDtypeStruct((8, LANE), f32),
        jax.ShapeDtypeStruct((8, LANE), f32),
        jax.ShapeDtypeStruct((MOVE_CAP * field_count, rows), bf16),
        jax.ShapeDtypeStruct((MOVE_CAP * field_count, rows), bf16),
    ] + [send_shape] * 4
    setup_out = setup_out + [jax.ShapeDtypeStruct(x.shape, x.dtype) for x in (wide, mid, narrow)]
    u0 = state.reshape(rows, P7**3)
    setup_in = [u0, vt, packed, wide, mid, narrow]
    res = pl.pallas_call(
        functools.partial(setup_entry, local_count, field_count, len(setup_in), len(setup_out)),
        out_shape=setup_out,
        in_specs=[pl.BlockSpec(memory_space=pltpu.HBM) for _ in setup_in],
        out_specs=[_vmem() for _ in setup_out],
        scratch_shapes=[pltpu.VMEM(x.shape, x.dtype) for x in setup_in[:3]]
        + [pltpu.SemaphoreType.DMA((len(setup_in),))],
        compiler_params=pltpu.CompilerParams(vmem_limit_bytes=24 * 1024 * 1024),
    )(*setup_in)
    v7, m7, v3, m3, p_local, p_remote, pre, stc, sw = res[:9]
    hinfo, cnt_l, cnt_r, sel_l, sel_r = res[9:14]
    sends = res[14:18]
    wide, mid, narrow = res[18:21]
    common = [p_local, p_remote, v7, m7, pre, stc, wide, mid, narrow]
    recv = exchange(sends)
    res = run_stage(
        (False, False, False, True, local_count),
        [u0] + recv + common,
        [u_shape] + [send_shape] * 4,
    )
    first, sends = res[0], res[1:]
    recv = exchange(sends)
    res = run_stage(
        (False, True, True, True, local_count),
        [first, u0] + recv + common + [sw],
        [u_shape, c_shape] + [send_shape] * 4,
    )
    after, coarse, sends = res[0], res[1], res[2:]
    recv = exchange(sends)
    mixed_tail = [v3, m3, sw]
    res = run_stage(
        (True, False, False, True, local_count),
        [after, coarse] + recv + common + mixed_tail,
        [u_shape, c_shape] + [send_shape] * 4,
    )
    first7, first3, sends = res[0], res[1], res[2:]
    recv = exchange(sends)
    pay_shape = jax.ShapeDtypeStruct((MOVE_CAP * field_count + 8, P7**3), f32)
    res = run_stage(
        (True, True, False, False, local_count),
        [first7, first3, after, coarse] + recv + common + mixed_tail + [sel_l, sel_r, cnt_l, cnt_r],
        [u_shape, c_shape, pay_shape, pay_shape],
    )
    final7, final3, pay_l, pay_r = res
    from_right = shifted(pay_l, "curve", -1)
    from_left = shifted(pay_r, "curve", 1)
    held = pl.pallas_call(
        functools.partial(final_kernel, field_count, HOLD7),
        out_shape=jax.ShapeDtypeStruct((HOLD7 * field_count, P7**3), f32),
        in_specs=[_vmem() for _ in range(4)],
        out_specs=_vmem(),
    )(final7, from_left, from_right, hinfo)
    state7_out = held.reshape(HOLD7, field_count, P7**3)
    state3_out = final3.reshape(local_count, field_count * P3**3)
    return (state7_out, state3_out)


def solution(mesh):
    return jax.shard_map(
        per_device,
        mesh=mesh,
        in_specs=(
            P(("slab", "curve"), None, None),
            P(None, None, ("slab", "curve")),
            P(("slab", "curve")),
            P(),
            P(("slab", "curve"), None),
            P(("slab", "curve")),
            P(("slab", "curve")),
        ),
        out_specs=(P(("slab", "curve"), None, None), P(("slab", "curve"), None)),
        check_vma=False,
    )
```

```python
import functools

import jax
import jax.numpy as jnp
import ml_dtypes
import numpy as np
from jax import lax
from jax.experimental import pallas as pl
from jax.experimental.pallas import tpu as pltpu
from jax.sharding import PartitionSpec as P

P7 = 8
P3 = 4
MOVE_CAP = 2
HOLD7 = 12
LANE = 128

TIME_STEP = 0.002
ACTIVATION = 1.5
SIDE_SIGNS = (-1.0, 1.0, -1.0, 1.0, -1.0, 1.0)
OPPOSITE = (1, 0, 3, 2, 5, 4)
SEND_FACES = (0, 1, 4, 5)
missing_id = 1 << 30

f32 = jnp.float32
bf16 = jnp.bfloat16


def shifted(value, axis, steps):
    count = lax.axis_size(axis)
    pairs = [(source, (source + steps) % count) for source in range(count)]
    return lax.ppermute(value, axis, pairs)


def lobatto_points(number):
    return -np.cos(np.pi * np.arange(number) / (number - 1))


def lagrange_weights(points):
    weights = np.ones(points.shape[0])
    for row_id in range(points.shape[0]):
        for col_id in range(points.shape[0]):
            if col_id != row_id:
                weights[row_id] = weights[row_id] / (points[row_id] - points[col_id])
    return weights


def derivative_matrix(points):
    weights = lagrange_weights(points)
    number = points.shape[0]
    matrix = np.zeros((number, number))
    for row_id in range(number):
        for col_id in range(number):
            if col_id != row_id:
                matrix[row_id, col_id] = (
                    weights[col_id] / weights[row_id] / (points[row_id] - points[col_id])
                )
        matrix[row_id, row_id] = -np.sum(matrix[row_id])
    return matrix


def interpolation_matrix(source, target):
    matrix = np.ones((target.shape[0], source.shape[0]))
    for col_id in range(source.shape[0]):
        for other_id in range(source.shape[0]):
            if other_id != col_id:
                matrix[:, col_id] = (
                    matrix[:, col_id]
                    * (target - source[other_id])
                    / (source[col_id] - source[other_id])
                )
    return matrix


def spread_three(matrix, identity):
    return (
        np.kron(matrix, np.kron(identity, identity)),
        np.kron(identity, np.kron(matrix, identity)),
        np.kron(identity, np.kron(identity, matrix)),
    )


def face_nodes(extent):
    grid = np.arange(extent**3).reshape(extent, extent, extent)
    last = extent - 1
    pieces = (grid[0], grid[last], grid[:, 0], grid[:, last], grid[:, :, 0], grid[:, :, last])
    return [piece.reshape(-1) for piece in pieces]


def to_bf16(x):
    return np.asarray(np.asarray(x, np.float32).astype(ml_dtypes.bfloat16))


def split_parts(x):
    x = np.asarray(x, np.float32)
    hi = x.astype(ml_dtypes.bfloat16)
    rest = x - hi.astype(np.float32)
    mid = rest.astype(ml_dtypes.bfloat16)
    lo = (rest - mid.astype(np.float32)).astype(ml_dtypes.bfloat16)
    return np.stack([hi, mid, lo])


def make_tables():
    fine_points = lobatto_points(P7)
    coarse_points = lobatto_points(P3)
    fine_derivs = spread_three(derivative_matrix(fine_points), np.eye(P7))
    coarse_derivs = spread_three(derivative_matrix(coarse_points), np.eye(P3))
    downward = interpolation_matrix(fine_points, coarse_points)
    upward = interpolation_matrix(coarse_points, fine_points)
    d7t = np.stack([to_bf16(m.T) for m in fine_derivs])
    d3t = np.stack([to_bf16(m).T for m in coarse_derivs])
    lift_table = to_bf16(np.kron(upward, np.kron(upward, upward)))
    projection = np.asarray(np.kron(downward, np.kron(downward, downward)), np.float32)
    mortar_up = np.asarray(np.kron(upward, upward), np.float32)
    mortar_down = np.asarray(np.kron(downward, downward), np.float32)
    nodes7 = face_nodes(P7)
    nodes3 = face_nodes(P3)
    n7 = P7**3
    n3 = P3**3
    g7 = np.zeros((n7, 6 * LANE), np.float32)
    tm = np.zeros((n3, 6 * LANE), np.float32)
    mds = np.zeros((6 * LANE, n3), np.float32)
    for side in range(6):
        for q, node in enumerate(nodes7[side]):
            g7[node, side * LANE + q] = 1.0
        for k, node in enumerate(nodes3[side]):
            tm[node, side * LANE : side * LANE + P7 * P7] = mortar_up[:, k]
            mds[side * LANE : side * LANE + P7 * P7, node] = mortar_down[k, :]
    tables = {
        "d7t": to_bf16(d7t),
        "d3t": to_bf16(d3t),
        "lift": lift_table,
        "mortar_up": mortar_up,
        "g7": to_bf16(g7),
        "tm": split_parts(tm),
        "mds": split_parts(mds),
        "pjt": split_parts(projection.T),
        "nodes7": nodes7,
        "nodes3": nodes3,
    }
    return tables


def _dot(a, b):
    return jnp.dot(a, b, preferred_element_type=f32)


def _split(x):
    hi = x.astype(bf16)
    rest = x - hi.astype(f32)
    mid = rest.astype(bf16)
    lo = (rest - mid.astype(f32)).astype(bf16)
    return hi, mid, lo


def _exact_left(x, table):
    hi, mid, lo = _split(x)
    return (_dot(hi, table) + _dot(mid, table)) + _dot(lo, table)


def _dot_t(a, b):
    return lax.dot_general(a, b, (((1,), (1,)), ((), ())), preferred_element_type=f32)


def _exact_left_t(x, table):
    hi, mid, lo = _split(x)
    return (_dot_t(hi, table) + _dot_t(mid, table)) + _dot_t(lo, table)


def _exact_right(table, x):
    hi, mid, lo = _split(x)
    return (_dot(table, hi) + _dot(table, mid)) + _dot(table, lo)


def _full_t(x, parts_ref):
    xh, xm, xl = _split(x)
    bh = parts_ref[0]
    bm = parts_ref[1]
    bl = parts_ref[2]
    return _dot_t(xh, bh) + (_dot_t(xh, bm) + _dot_t(xm, bh)) + (
        _dot_t(xh, bl) + _dot_t(xm, bm) + _dot_t(xl, bh)
    )


class View:
    def __init__(self, ref, start, rows, width):
        self.ref = ref
        self.start = start
        self.rows = rows
        self.width = width

    def __getitem__(self, k):
        if k is Ellipsis:
            k = 0
        top = self.start + k * self.rows
        return self.ref[top : top + self.rows, 0 : self.width]


def table_layout(rows, local):
    n7 = P7**3
    n3 = P3**3
    wide = {"g7": (0, n7, 6 * LANE), "tm": (n7, n3, 6 * LANE), "mdst": (n7 + 3 * n3, n3, 6 * LANE)}
    mid = {"d7t": (0, n7, n7), "lift_t": (3 * n7, n3, n7), "pj": (3 * n7 + n3, n3, n7)}
    narrow = {
        "bcast": (0, rows, local),
        "sel": (rows, 3 * local, rows),
        "fsel": (rows + 3 * local, rows, local),
        "d3t": (2 * rows + 3 * local, n3, n3),
    }
    return wide, mid, narrow


def table_views(wide_ref, mid_ref, narrow_ref, local):
    rows = narrow_ref.shape[1]
    layouts = table_layout(rows, local)
    views = {}
    for ref, layout in zip((wide_ref, mid_ref, narrow_ref), layouts):
        for name, (start, count, width) in layout.items():
            views[name] = View(ref, start, count, width)
    return views


def _full(x, parts_ref):
    xh, xm, xl = _split(x)
    bh = parts_ref[0]
    bm = parts_ref[1]
    bl = parts_ref[2]
    return _dot(xh, bh) + (_dot(xh, bm) + _dot(xm, bh)) + (
        _dot(xh, bl) + _dot(xm, bm) + _dot(xl, bh)
    )


def _rate_source(values, pre, stc, bc, sel, local):
    picked = _exact_right(sel, values)
    v0 = picked[0:local]
    v1 = picked[local : 2 * local]
    v2 = picked[2 * local : 3 * local]
    rate = pre * jnp.exp(-ACTIVATION * jnp.exp(-v0)) * v1 * v2
    return stc * _exact_right(bc, rate)


def recv_block(recv, side):
    ref = recv[side]
    if side in (4, 5):
        rows = ref.shape[0] // 2
        top = 0 if side == 4 else rows
        return ref[top : top + rows, :]
    return ref[...]


def write_sends(out_refs, send):
    rows = send.shape[0]
    out_refs[0][...] = send[:, 0:LANE]
    out_refs[1][...] = send[:, LANE : 2 * LANE]
    out_refs[2][0:rows, :] = send[:, 5 * LANE : 6 * LANE]
    out_refs[2][rows : 2 * rows, :] = send[:, 4 * LANE : 5 * LANE]


def stage_kernel(coarse, second, project, sends, local, *refs):
    refs = list(refs)

    def take():
        return refs.pop(0)

    u_ref = take()
    c_ref = take() if coarse else None
    bu_ref = take() if second else None
    bc_ref = take() if (second and coarse) else None
    recv = {s: take() for s in SEND_FACES}
    pl_ref = take()
    pr_ref = take()
    v7_ref = take()
    m7_ref = take()
    pre_ref = take()
    stc_ref = take()
    views = table_views(take(), take(), take(), local)
    bc_tab = views["bcast"]
    sel_tab = views["sel"]
    d7_ref = views["d7t"]
    g7_ref = views["g7"]
    d3_ref = views["d3t"]
    mds_ref = views["mdst"]
    tm_ref = views["tm"]
    pj_ref = views["pj"]
    if coarse:
        v3_ref = take()
        m3_ref = take()
    if coarse or project:
        sw_ref = take()
    last = coarse and not sends
    if last:
        sel_l_ref = take()
        sel_r_ref = take()
        cnt_l_ref = take()
        cnt_r_ref = take()
    out_u = take()
    out_c = take() if (coarse or project) else None
    out_send = [take() for _ in range(3)] if sends else None
    if last:
        pay_l_ref = take()
        pay_r_ref = take()

    pre = pre_ref[...]
    stc = stc_ref[...]
    bcast = bc_tab[...]
    sel = sel_tab[...]
    u = u_ref[...]
    trace7 = _dot(u.astype(bf16), g7_ref[...])
    if coarse:
        c = c_ref[...]
        trace3 = _full(c, tm_ref).astype(bf16).astype(f32)
        switched = sw_ref[...] > 0.5
        own = jnp.where(switched, trace3, trace7)
    else:
        own = trace7
    own_b = own.astype(bf16)
    near_blocks = []
    for side in range(6):
        other = OPPOSITE[side]
        block = own_b[:, other * LANE : (other + 1) * LANE]
        near = _dot(pl_ref[side], block)
        if side in SEND_FACES:
            k = SEND_FACES.index(side)
            near = near + _dot(pr_ref[k], recv_block(recv, side))
        near_blocks.append(near)
    near = jnp.concatenate(near_blocks, axis=1)

    divergence = None
    for d in range(3):
        flux = (v7_ref[d].astype(f32) * u).astype(bf16)
        term = _dot(flux, d7_ref[d])
        divergence = term if divergence is None else divergence + term
    result = _rate_source(u, pre, stc, bcast, sel, local) - divergence
    jump = (P7 * (P7 - 1) / 2.0) * (m7_ref[...] * (trace7 - near))
    rate7 = result + _exact_left_t(jump, g7_ref[...])

    if coarse:
        div3 = None
        for d in range(3):
            flux3 = (v3_ref[d] * c).astype(bf16)
            term = _dot(flux3, d3_ref[d])
            div3 = term if div3 is None else div3 + term
        result3 = _rate_source(c, pre, stc, bcast, sel, local) - div3
        jump3 = m3_ref[...] * (trace3 - near)
        rate3 = result3 + (P3 * (P3 - 1) / 2.0) * _full_t(jump3, mds_ref)

    if second:
        new_u = 0.5 * (bu_ref[...] + u + TIME_STEP * rate7)
    else:
        new_u = u + TIME_STEP * rate7
    out_u[...] = new_u
    new_c = None
    if coarse:
        if second:
            new_c = 0.5 * (bc_ref[...] + c + TIME_STEP * rate3)
        else:
            new_c = c + TIME_STEP * rate3
        if last:
            out_c[...] = jnp.where(sw_ref[...] > 0.5, new_c, 0.0)
            moved = sel_l_ref.shape[0]
            pay_l_ref[0:moved, :] = _exact_right(sel_l_ref[...], new_u)
            pay_r_ref[0:moved, :] = _exact_right(sel_r_ref[...], new_u)
            tail = (pay_l_ref.shape[0] - moved, pay_l_ref.shape[1])
            pay_l_ref[moved:, :] = jnp.broadcast_to(cnt_l_ref[0:1, 0:1], tail)
            pay_r_ref[moved:, :] = jnp.broadcast_to(cnt_r_ref[0:1, 0:1], tail)
        else:
            out_c[...] = new_c
    if project:
        new_c = _full_t(new_u, pj_ref)
        out_c[...] = new_c
    if sends:
        send7 = _dot(new_u.astype(bf16), g7_ref[...])
        if new_c is not None:
            send3 = _full(new_c, tm_ref).astype(bf16).astype(f32)
            send = jnp.where(sw_ref[...] > 0.5, send3, send7)
        else:
            send = send7
        write_sends(out_send, send.astype(bf16))


def _vmem():
    return pl.BlockSpec(memory_space=pltpu.VMEM)


def run_stage(flags, inputs, out_shapes):
    coarse, second, project, sends, local = flags
    kernel = functools.partial(stage_kernel, coarse, second, project, sends, local)
    return pl.pallas_call(
        kernel,
        out_shape=out_shapes,
        in_specs=[_vmem() for _ in inputs],
        out_specs=[_vmem() for _ in out_shapes],
        compiler_params=pltpu.CompilerParams(vmem_limit_bytes=48 * 1024 * 1024),
    )(*inputs)


def setup_kernel(local, fields, u_ref, vt_ref, packed_ref, wide_ref, mid_ref, narrow_ref, v7_out, m7_out, v3_out, m3_out, pl_out, pr_out,
                 pre_out, stc_out, sw_out, hinfo_out, cnt_l_out, cnt_r_out, sel_l_out,
                 sel_r_out, *send_refs):
    rows = local * fields
    views = table_views(wide_ref, mid_ref, narrow_ref, local)
    lift_ref = views["lift_t"]
    g7_ref = views["g7"]
    tm_ref = views["tm"]
    fsel_ref = views["fsel"]
    bcast = views["bcast"][...]
    lanes = lax.broadcasted_iota(jnp.int32, (local, 6 * LANE), 1) // LANE
    sign = jnp.where(lanes % 2 == 0, -1.0, 1.0)
    fvg = []
    mvg = []
    for d in range(3):
        vt = vt_ref[d]
        fv = _dot(vt, lift_ref[...]).astype(bf16)
        v7_out[d] = _dot(bcast, fv).astype(bf16)
        v3_out[d] = _dot(bcast, vt)
        fvg.append(_dot(fv, g7_ref[...]))
        mvg.append((_dot(vt, tm_ref[0]) + _dot(vt, tm_ref[1])) + _dot(vt, tm_ref[2]))

    def by_block(parts):
        return jnp.where(lanes < 2, parts[0], jnp.where(lanes < 4, parts[1], parts[2]))

    m7 = jnp.minimum(sign * by_block(fvg), 0.0)
    m7_out[...] = _dot(bcast, m7.astype(bf16))
    m3 = jnp.minimum(sign * by_block(mvg), 0.0)
    m3_out[...] = _exact_right(bcast, m3)
    rep = _dot(bcast, packed_ref[...].astype(bf16))
    row_f = (lax.broadcasted_iota(jnp.int32, (rows, 1), 0) % fields).astype(f32)
    cols = lax.broadcasted_iota(jnp.int32, (rows, rows), 1).astype(f32)
    for side in range(6):
        code = rep[:, side : side + 1]
        far = code >= local
        target = (code - jnp.where(far, float(local), 0.0)) * fields + row_f
        hit = cols == target
        pl_out[side] = jnp.where(hit & ~far, 1.0, 0.0).astype(bf16)
        if side in SEND_FACES:
            pr_out[SEND_FACES.index(side)] = jnp.where(hit & far, 1.0, 0.0).astype(bf16)
    sw_out[...] = rep[:, 6:7]
    packed = packed_ref[...]
    stay_sw = packed[:, 6:7] < 0.5
    go_left = (packed[:, 9:10] == packed[:, 10:11]) & stay_sw
    go_right = (packed[:, 9:10] == packed[:, 11:12]) & stay_sw
    stays = stay_sw & ~go_left & ~go_right
    lane16 = lax.broadcasted_iota(jnp.int32, (local, LANE), 1)
    marks = jnp.where(
        lane16 == 0, go_left.astype(f32),
        jnp.where(lane16 == 1, go_right.astype(f32), jnp.where(lane16 == 2, stays.astype(f32), 0.0)),
    ).astype(bf16)
    er = lax.broadcasted_iota(jnp.int32, (local, local), 0)
    ec = lax.broadcasted_iota(jnp.int32, (local, local), 1)
    before = _dot(jnp.where(ec < er, 1.0, 0.0).astype(bf16), marks)
    totals = _dot(jnp.ones((local, local), bf16), marks)
    info = jnp.where(lane16 < 3, marks.astype(f32), 0.0)
    for k in range(3):
        info = jnp.where(lane16 == 3 + k, before[:, k : k + 1], info)
    info = jnp.where(lane16 == 6, totals[:, 2:3], info)
    info = jnp.where(lane16 == 7, packed[:, 12:13], info)
    info = jnp.where(lane16 == 8, packed[:, 13:14], info)
    hinfo = _dot(bcast, info.astype(bf16))
    hinfo_out[...] = hinfo
    cnt_l_out[...] = jnp.broadcast_to(totals[0:1, 0:1], cnt_l_out.shape)
    cnt_r_out[...] = jnp.broadcast_to(totals[0:1, 1:2], cnt_r_out.shape)
    rf = lax.broadcasted_iota(jnp.int32, (rows, LANE), 0) % fields
    cc = lax.broadcasted_iota(jnp.int32, (rows, LANE), 1)
    eye = jnp.where(
        lax.broadcasted_iota(jnp.int32, (MOVE_CAP * fields, LANE), 0)
        == lax.broadcasted_iota(jnp.int32, (MOVE_CAP * fields, LANE), 1), 1.0, 0.0
    ).astype(bf16)
    for mark_lane, rank_lane, out in ((0, 3, sel_l_out), (1, 4, sel_r_out)):
        hit = (
            (hinfo[:, mark_lane : mark_lane + 1] > 0.5)
            & (hinfo[:, rank_lane : rank_lane + 1] == (cc // fields).astype(f32))
            & (rf == cc % fields)
            & (cc < MOVE_CAP * fields)
        )
        out[...] = _dot_t(eye, jnp.where(hit, 1.0, 0.0).astype(bf16)).astype(bf16)
    pre_out[...] = packed_ref[:, 7:8]
    stc_out[...] = _exact_right(fsel_ref[...], packed_ref[...])[:, 8:9]
    write_sends(send_refs, _dot(u_ref[...].astype(bf16), g7_ref[...]).astype(bf16))


def final_kernel(fields, hold, home_ref, from_l_ref, from_r_ref, hinfo_ref, out_ref):
    hinfo = hinfo_ref[...]
    moved = MOVE_CAP * fields
    n_l = from_l_ref[moved : moved + 1, 0:1]
    n_r = from_r_ref[moved : moved + 1, 0:1]
    n_h = hinfo[0:1, 6:7]
    first = hinfo[0:1, 7:8] > 0.5
    final = hinfo[0:1, 8:9] > 0.5
    off_l = jnp.where(first, n_h + n_r, jnp.where(final, n_r, 0.0))
    off_h = jnp.where(first, 0.0, jnp.where(final, n_r + n_l, n_l))
    off_r = jnp.where(first, n_h, jnp.where(final, 0.0, n_l + n_h))
    width = hold * fields
    eye = jnp.where(
        lax.broadcasted_iota(jnp.int32, (width, LANE), 0)
        == lax.broadcasted_iota(jnp.int32, (width, LANE), 1), 1.0, 0.0
    ).astype(bf16)

    def gather(values, valid, pos):
        count = values.shape[0]
        rf = lax.broadcasted_iota(jnp.int32, (count, LANE), 0) % fields
        cc = lax.broadcasted_iota(jnp.int32, (count, LANE), 1)
        hit = valid & (pos == (cc // fields).astype(f32)) & (rf == cc % fields) & (cc < width)
        pick = _dot_t(eye, jnp.where(hit, 1.0, 0.0).astype(bf16)).astype(bf16)
        return _exact_right(pick, values)

    total = gather(home_ref[...], hinfo[:, 2:3] > 0.5, off_h + hinfo[:, 5:6])
    slot = (lax.broadcasted_iota(jnp.int32, (moved, 1), 0) // fields).astype(f32)
    total = total + gather(from_l_ref[0:moved, :], slot < n_l, off_l + slot)
    total = total + gather(from_r_ref[0:moved, :], slot < n_r, off_r + slot)
    out_ref[...] = total


def setup_entry(local, fields, n_in, n_out, *refs):
    sources = refs[:n_in]
    outs = refs[n_in : n_in + n_out]
    n_tab = 3
    n_own = n_in - n_tab
    buffers = refs[n_in + n_out : n_in + n_out + n_own]
    sems = refs[n_in + n_out + n_own]
    targets = list(buffers) + list(outs[n_out - n_tab :])
    copies = [
        pltpu.make_async_copy(sources[i], targets[i], sems.at[i]) for i in range(n_in)
    ]
    for copy in copies:
        copy.start()
    for copy in copies:
        copy.wait()
    setup_kernel(local, fields, *targets, *outs[: n_out - n_tab])


def per_device(state, velocity, pre_exp, stoich, neighbours, switch, new_owner):
    tab = make_tables()
    local_count = state.shape[0]
    field_count = state.shape[1]
    rows = local_count * field_count
    curve_count = lax.axis_size("curve")
    curve_pos = lax.axis_index("curve")
    device_id = lax.axis_index("slab") * curve_count + curve_pos
    first_global = device_id * local_count
    positions = jnp.arange(local_count, dtype=jnp.int32)

    near_device = neighbours // local_count
    near_local = neighbours - near_device * local_count
    remote = near_device != device_id
    codes = (near_local + local_count * remote.astype(jnp.int32)).astype(f32)
    sto_col = jnp.zeros((local_count,), f32).at[:field_count].set(stoich)
    left_pos = (curve_pos + curve_count - 1) % curve_count
    right_pos = (curve_pos + 1) % curve_count
    ones = jnp.ones((local_count, 1), f32)
    packed = jnp.concatenate(
        [
            codes,
            switch.astype(f32)[:, None],
            pre_exp[:, None],
            sto_col[:, None],
            new_owner.astype(f32)[:, None],
            ones * left_pos.astype(f32),
            ones * right_pos.astype(f32),
            ones * (curve_pos == 0).astype(f32),
            ones * (curve_pos == curve_count - 1).astype(f32),
            jnp.zeros((local_count, LANE - 14), f32),
        ],
        axis=1,
    )
    fsel_np = np.arange(rows)[:, None] % field_count == np.arange(local_count)[None, :]
    vt = jnp.transpose(velocity, (0, 2, 1))
    row_elem = np.arange(rows) // field_count
    bcast_np = row_elem[:, None] == np.arange(local_count)[None, :]
    pick_rows = (np.arange(3)[:, None] + field_count * np.arange(local_count)[None, :]).reshape(-1)
    sel_np = pick_rows[:, None] == np.arange(rows)[None, :]
    n7 = P7**3
    n3 = P3**3
    layouts = table_layout(rows, local_count)
    wide_np = np.zeros((n7 + 6 * n3, 6 * LANE), np.float32)
    mid_np = np.zeros((3 * n7 + 4 * n3, n7), np.float32)
    narrow_np = np.zeros((2 * rows + 3 * local_count + 3 * n3, rows), np.float32)
    pieces = {
        "g7": tab["g7"][None],
        "tm": tab["tm"],
        "mdst": np.transpose(tab["mds"], (0, 2, 1)),
        "d7t": tab["d7t"],
        "lift_t": tab["lift"].T[None],
        "pj": np.transpose(tab["pjt"], (0, 2, 1)),
        "bcast": bcast_np[None],
        "sel": sel_np[None],
        "fsel": fsel_np[None],
        "d3t": tab["d3t"],
    }
    for target, layout in zip((wide_np, mid_np, narrow_np), layouts):
        for name, (start, count, width) in layout.items():
            parts = np.asarray(pieces[name], np.float32)
            for k in range(parts.shape[0]):
                target[start + k * count : start + (k + 1) * count, :width] = parts[k]
    wide = jnp.asarray(to_bf16(wide_np))
    mid = jnp.asarray(to_bf16(mid_np))
    narrow = jnp.asarray(to_bf16(narrow_np))

    send_shape = jax.ShapeDtypeStruct((rows, LANE), bf16)
    sends_shape = [send_shape, send_shape, jax.ShapeDtypeStruct((2 * rows, LANE), bf16)]
    u_shape = jax.ShapeDtypeStruct((rows, P7**3), f32)
    c_shape = jax.ShapeDtypeStruct((rows, P3**3), f32)

    def exchange(sends):
        face0, face1, faces_z = sends
        from_prev = shifted(faces_z, "slab", 1)
        if lax.axis_size("slab") == 2:
            from_next = from_prev
        else:
            from_next = shifted(faces_z, "slab", -1)
        return [shifted(face1, "curve", 1), shifted(face0, "curve", -1), from_prev, from_next]

    setup_out = [
        jax.ShapeDtypeStruct((3, rows, P7**3), bf16),
        jax.ShapeDtypeStruct((rows, 6 * LANE), f32),
        jax.ShapeDtypeStruct((3, rows, P3**3), f32),
        jax.ShapeDtypeStruct((rows, 6 * LANE), f32),
        jax.ShapeDtypeStruct((6, rows, rows), bf16),
        jax.ShapeDtypeStruct((len(SEND_FACES), rows, rows), bf16),
        jax.ShapeDtypeStruct((local_count, 1), f32),
        jax.ShapeDtypeStruct((rows, 1), f32),
        jax.ShapeDtypeStruct((rows, 1), f32),
        jax.ShapeDtypeStruct((rows, LANE), f32),
        jax.ShapeDtypeStruct((8, LANE), f32),
        jax.ShapeDtypeStruct((8, LANE), f32),
        jax.ShapeDtypeStruct((MOVE_CAP * field_count, rows), bf16),
        jax.ShapeDtypeStruct((MOVE_CAP * field_count, rows), bf16),
    ] + sends_shape
    setup_out = setup_out + [jax.ShapeDtypeStruct(x.shape, x.dtype) for x in (wide, mid, narrow)]
    u0 = state.reshape(rows, P7**3)
    setup_in = [u0, vt, packed, wide, mid, narrow]
    res = pl.pallas_call(
        functools.partial(setup_entry, local_count, field_count, len(setup_in), len(setup_out)),
        out_shape=setup_out,
        in_specs=[pl.BlockSpec(memory_space=pltpu.HBM) for _ in setup_in],
        out_specs=[_vmem() for _ in setup_out],
        scratch_shapes=[pltpu.VMEM(x.shape, x.dtype) for x in setup_in[:3]]
        + [pltpu.SemaphoreType.DMA((len(setup_in),))],
        compiler_params=pltpu.CompilerParams(vmem_limit_bytes=24 * 1024 * 1024),
    )(*setup_in)
    v7, m7, v3, m3, p_local, p_remote, pre, stc, sw = res[:9]
    hinfo, cnt_l, cnt_r, sel_l, sel_r = res[9:14]
    sends = res[14:17]
    wide, mid, narrow = res[17:20]
    common = [p_local, p_remote, v7, m7, pre, stc, wide, mid, narrow]
    recv = exchange(sends)
    res = run_stage(
        (False, False, False, True, local_count),
        [u0] + recv + common,
        [u_shape] + sends_shape,
    )
    first, sends = res[0], res[1:]
    recv = exchange(sends)
    res = run_stage(
        (False, True, True, True, local_count),
        [first, u0] + recv + common + [sw],
        [u_shape, c_shape] + sends_shape,
    )
    after, coarse, sends = res[0], res[1], res[2:]
    recv = exchange(sends)
    mixed_tail = [v3, m3, sw]
    res = run_stage(
        (True, False, False, True, local_count),
        [after, coarse] + recv + common + mixed_tail,
        [u_shape, c_shape] + sends_shape,
    )
    first7, first3, sends = res[0], res[1], res[2:]
    recv = exchange(sends)
    pay_shape = jax.ShapeDtypeStruct((MOVE_CAP * field_count + 8, P7**3), f32)
    res = run_stage(
        (True, True, False, False, local_count),
        [first7, first3, after, coarse] + recv + common + mixed_tail + [sel_l, sel_r, cnt_l, cnt_r],
        [u_shape, c_shape, pay_shape, pay_shape],
    )
    final7, final3, pay_l, pay_r = res
    from_right = shifted(pay_l, "curve", -1)
    from_left = shifted(pay_r, "curve", 1)
    held = pl.pallas_call(
        functools.partial(final_kernel, field_count, HOLD7),
        out_shape=jax.ShapeDtypeStruct((HOLD7 * field_count, P7**3), f32),
        in_specs=[_vmem() for _ in range(4)],
        out_specs=_vmem(),
    )(final7, from_left, from_right, hinfo)
    state7_out = held.reshape(HOLD7, field_count, P7**3)
    state3_out = final3.reshape(local_count, field_count * P3**3)
    return (state7_out, state3_out)


def solution(mesh):
    return jax.shard_map(
        per_device,
        mesh=mesh,
        in_specs=(
            P(("slab", "curve"), None, None),
            P(None, None, ("slab", "curve")),
            P(("slab", "curve")),
            P(),
            P(("slab", "curve"), None),
            P(("slab", "curve")),
            P(("slab", "curve")),
        ),
        out_specs=(P(("slab", "curve"), None, None), P(("slab", "curve"), None)),
        check_vma=False,
    )
```

```python
import functools

import jax
import jax.numpy as jnp
import ml_dtypes
import numpy as np
from jax import lax
from jax.experimental import pallas as pl
from jax.experimental.pallas import tpu as pltpu
from jax.sharding import PartitionSpec as P

P7 = 8
P3 = 4
MOVE_CAP = 2
HOLD7 = 12
LANE = 128

TIME_STEP = 0.002
ACTIVATION = 1.5
SIDE_SIGNS = (-1.0, 1.0, -1.0, 1.0, -1.0, 1.0)
OPPOSITE = (1, 0, 3, 2, 5, 4)
SEND_FACES = (0, 1, 4, 5)
missing_id = 1 << 30

f32 = jnp.float32
bf16 = jnp.bfloat16


def shifted(value, axis, steps):
    count = lax.axis_size(axis)
    pairs = [(source, (source + steps) % count) for source in range(count)]
    return lax.ppermute(value, axis, pairs)


def lobatto_points(number):
    return -np.cos(np.pi * np.arange(number) / (number - 1))


def lagrange_weights(points):
    weights = np.ones(points.shape[0])
    for row_id in range(points.shape[0]):
        for col_id in range(points.shape[0]):
            if col_id != row_id:
                weights[row_id] = weights[row_id] / (points[row_id] - points[col_id])
    return weights


def derivative_matrix(points):
    weights = lagrange_weights(points)
    number = points.shape[0]
    matrix = np.zeros((number, number))
    for row_id in range(number):
        for col_id in range(number):
            if col_id != row_id:
                matrix[row_id, col_id] = (
                    weights[col_id] / weights[row_id] / (points[row_id] - points[col_id])
                )
        matrix[row_id, row_id] = -np.sum(matrix[row_id])
    return matrix


def interpolation_matrix(source, target):
    matrix = np.ones((target.shape[0], source.shape[0]))
    for col_id in range(source.shape[0]):
        for other_id in range(source.shape[0]):
            if other_id != col_id:
                matrix[:, col_id] = (
                    matrix[:, col_id]
                    * (target - source[other_id])
                    / (source[col_id] - source[other_id])
                )
    return matrix


def spread_three(matrix, identity):
    return (
        np.kron(matrix, np.kron(identity, identity)),
        np.kron(identity, np.kron(matrix, identity)),
        np.kron(identity, np.kron(identity, matrix)),
    )


def face_nodes(extent):
    grid = np.arange(extent**3).reshape(extent, extent, extent)
    last = extent - 1
    pieces = (grid[0], grid[last], grid[:, 0], grid[:, last], grid[:, :, 0], grid[:, :, last])
    return [piece.reshape(-1) for piece in pieces]


def to_bf16(x):
    return np.asarray(np.asarray(x, np.float32).astype(ml_dtypes.bfloat16))


def split_parts(x):
    x = np.asarray(x, np.float32)
    hi = x.astype(ml_dtypes.bfloat16)
    rest = x - hi.astype(np.float32)
    mid = rest.astype(ml_dtypes.bfloat16)
    lo = (rest - mid.astype(np.float32)).astype(ml_dtypes.bfloat16)
    return np.stack([hi, mid, lo])


def make_tables():
    fine_points = lobatto_points(P7)
    coarse_points = lobatto_points(P3)
    fine_derivs = spread_three(derivative_matrix(fine_points), np.eye(P7))
    coarse_derivs = spread_three(derivative_matrix(coarse_points), np.eye(P3))
    downward = interpolation_matrix(fine_points, coarse_points)
    upward = interpolation_matrix(coarse_points, fine_points)
    d7t = np.stack([to_bf16(m.T) for m in fine_derivs])
    d3t = np.stack([to_bf16(m).T for m in coarse_derivs])
    lift_table = to_bf16(np.kron(upward, np.kron(upward, upward)))
    projection = np.asarray(np.kron(downward, np.kron(downward, downward)), np.float32)
    mortar_up = np.asarray(np.kron(upward, upward), np.float32)
    mortar_down = np.asarray(np.kron(downward, downward), np.float32)
    nodes7 = face_nodes(P7)
    nodes3 = face_nodes(P3)
    n7 = P7**3
    n3 = P3**3
    g7 = np.zeros((n7, 6 * LANE), np.float32)
    tm = np.zeros((n3, 6 * LANE), np.float32)
    mds = np.zeros((6 * LANE, n3), np.float32)
    for side in range(6):
        for q, node in enumerate(nodes7[side]):
            g7[node, side * LANE + q] = 1.0
        for k, node in enumerate(nodes3[side]):
            tm[node, side * LANE : side * LANE + P7 * P7] = mortar_up[:, k]
            mds[side * LANE : side * LANE + P7 * P7, node] = mortar_down[k, :]
    tables = {
        "d7t": to_bf16(d7t),
        "d3t": to_bf16(d3t),
        "lift": lift_table,
        "mortar_up": mortar_up,
        "g7": to_bf16(g7),
        "tm": split_parts(tm),
        "mds": split_parts(mds),
        "pjt": split_parts(projection.T),
        "nodes7": nodes7,
        "nodes3": nodes3,
    }
    return tables


def _dot(a, b):
    return jnp.dot(a, b, preferred_element_type=f32)


def _split(x):
    hi = x.astype(bf16)
    rest = x - hi.astype(f32)
    mid = rest.astype(bf16)
    lo = (rest - mid.astype(f32)).astype(bf16)
    return hi, mid, lo


def _exact_left(x, table):
    hi, mid, lo = _split(x)
    return (_dot(hi, table) + _dot(mid, table)) + _dot(lo, table)


def _dot_t(a, b):
    return lax.dot_general(a, b, (((1,), (1,)), ((), ())), preferred_element_type=f32)


def _exact_left_t(x, table):
    hi, mid, lo = _split(x)
    return (_dot_t(hi, table) + _dot_t(mid, table)) + _dot_t(lo, table)


def _exact_right(table, x):
    hi, mid, lo = _split(x)
    return (_dot(table, hi) + _dot(table, mid)) + _dot(table, lo)


def _full_t(x, parts_ref):
    xh, xm, xl = _split(x)
    bh = parts_ref[0]
    bm = parts_ref[1]
    bl = parts_ref[2]
    return _dot_t(xh, bh) + (_dot_t(xh, bm) + _dot_t(xm, bh)) + (
        _dot_t(xh, bl) + _dot_t(xm, bm) + _dot_t(xl, bh)
    )


class View:
    def __init__(self, ref, start, rows, width):
        self.ref = ref
        self.start = start
        self.rows = rows
        self.width = width

    def __getitem__(self, k):
        if k is Ellipsis:
            k = 0
        top = self.start + k * self.rows
        return self.ref[top : top + self.rows, 0 : self.width]


def table_layout(rows, local):
    n7 = P7**3
    n3 = P3**3
    wide = {"g7": (0, n7, 6 * LANE), "tm": (n7, n3, 6 * LANE), "mdst": (n7 + 3 * n3, n3, 6 * LANE)}
    mid = {"d7t": (0, n7, n7), "lift_t": (3 * n7, n3, n7), "pj": (3 * n7 + n3, n3, n7)}
    narrow = {
        "bcast": (0, rows, local),
        "sel": (rows, 3 * local, rows),
        "fsel": (rows + 3 * local, rows, local),
        "d3t": (2 * rows + 3 * local, n3, n3),
    }
    return wide, mid, narrow


def table_views(wide_ref, mid_ref, narrow_ref, local):
    rows = narrow_ref.shape[1]
    layouts = table_layout(rows, local)
    views = {}
    for ref, layout in zip((wide_ref, mid_ref, narrow_ref), layouts):
        for name, (start, count, width) in layout.items():
            views[name] = View(ref, start, count, width)
    return views


def _full(x, parts_ref):
    xh, xm, xl = _split(x)
    bh = parts_ref[0]
    bm = parts_ref[1]
    bl = parts_ref[2]
    return _dot(xh, bh) + (_dot(xh, bm) + _dot(xm, bh)) + (
        _dot(xh, bl) + _dot(xm, bm) + _dot(xl, bh)
    )


def _rate_source(values, pre, stc, bc, sel, local):
    picked = _exact_right(sel, values)
    v0 = picked[0:local]
    v1 = picked[local : 2 * local]
    v2 = picked[2 * local : 3 * local]
    rate = pre * jnp.exp(-ACTIVATION * jnp.exp(-v0)) * v1 * v2
    return stc * _exact_right(bc, rate)


def recv_block(recv, side):
    ref = recv[side]
    if side in (4, 5):
        rows = ref.shape[0] // 2
        top = 0 if side == 4 else rows
        return ref[top : top + rows, :]
    return ref[...]


def write_sends(out_refs, send):
    rows = send.shape[0]
    out_refs[0][...] = send[:, 0:LANE]
    out_refs[1][...] = send[:, LANE : 2 * LANE]
    out_refs[2][0:rows, :] = send[:, 5 * LANE : 6 * LANE]
    out_refs[2][rows : 2 * rows, :] = send[:, 4 * LANE : 5 * LANE]


def stage_kernel(coarse, second, project, sends, local, *refs):
    refs = list(refs)

    def take():
        return refs.pop(0)

    u_ref = take()
    c_ref = take() if coarse else None
    bu_ref = take() if second else None
    bc_ref = take() if (second and coarse) else None
    recv = {s: take() for s in SEND_FACES}
    pl_ref = take()
    pr_ref = take()
    v7_ref = take()
    m7_ref = take()
    pre_ref = take()
    stc_ref = take()
    views = table_views(take(), take(), take(), local)
    bc_tab = views["bcast"]
    sel_tab = views["sel"]
    d7_ref = views["d7t"]
    g7_ref = views["g7"]
    d3_ref = views["d3t"]
    mds_ref = views["mdst"]
    tm_ref = views["tm"]
    pj_ref = views["pj"]
    if coarse:
        v3_ref = take()
        m3_ref = take()
    if coarse or project:
        sw_ref = take()
    last = coarse and not sends
    if last:
        sel_l_ref = take()
        sel_r_ref = take()
        cnt_l_ref = take()
        cnt_r_ref = take()
    res7_ref = take()
    res3_ref = take() if coarse else None
    out_u = take()
    out_c = take() if (coarse or project) else None
    out_send = [take() for _ in range(3)] if sends else None
    if last:
        pay_l_ref = take()
        pay_r_ref = take()

    pre = pre_ref[...]
    stc = stc_ref[...]
    bcast = bc_tab[...]
    sel = sel_tab[...]
    u = u_ref[...]
    trace7 = _dot(u.astype(bf16), g7_ref[...])
    if coarse:
        c = c_ref[...]
        trace3 = _full(c, tm_ref).astype(bf16).astype(f32)
        switched = sw_ref[...] > 0.5
        own = jnp.where(switched, trace3, trace7)
    else:
        own = trace7
    own_b = own.astype(bf16)
    near_blocks = []
    for side in range(6):
        other = OPPOSITE[side]
        block = own_b[:, other * LANE : (other + 1) * LANE]
        near = _dot(pl_ref[side], block)
        if side in SEND_FACES:
            k = SEND_FACES.index(side)
            near = near + _dot(pr_ref[k], recv_block(recv, side))
        near_blocks.append(near)
    near = jnp.concatenate(near_blocks, axis=1)

    result = res7_ref[...]
    jump = (P7 * (P7 - 1) / 2.0) * (m7_ref[...] * (trace7 - near))
    rate7 = result + _exact_left_t(jump, g7_ref[...])

    if coarse:
        result3 = res3_ref[...]
        jump3 = m3_ref[...] * (trace3 - near)
        rate3 = result3 + (P3 * (P3 - 1) / 2.0) * _full_t(jump3, mds_ref)

    if second:
        new_u = 0.5 * (bu_ref[...] + u + TIME_STEP * rate7)
    else:
        new_u = u + TIME_STEP * rate7
    out_u[...] = new_u
    new_c = None
    if coarse:
        if second:
            new_c = 0.5 * (bc_ref[...] + c + TIME_STEP * rate3)
        else:
            new_c = c + TIME_STEP * rate3
        if last:
            out_c[...] = jnp.where(sw_ref[...] > 0.5, new_c, 0.0)
            moved = sel_l_ref.shape[0]
            pay_l_ref[0:moved, :] = _exact_right(sel_l_ref[...], new_u)
            pay_r_ref[0:moved, :] = _exact_right(sel_r_ref[...], new_u)
            tail = (pay_l_ref.shape[0] - moved, pay_l_ref.shape[1])
            pay_l_ref[moved:, :] = jnp.broadcast_to(cnt_l_ref[0:1, 0:1], tail)
            pay_r_ref[moved:, :] = jnp.broadcast_to(cnt_r_ref[0:1, 0:1], tail)
        else:
            out_c[...] = new_c
    if project:
        new_c = _full_t(new_u, pj_ref)
        out_c[...] = new_c
    if sends:
        send7 = _dot(new_u.astype(bf16), g7_ref[...])
        if new_c is not None:
            send3 = _full(new_c, tm_ref).astype(bf16).astype(f32)
            send = jnp.where(sw_ref[...] > 0.5, send3, send7)
        else:
            send = send7
        write_sends(out_send, send.astype(bf16))


def _vmem():
    return pl.BlockSpec(memory_space=pltpu.VMEM)


def bulk_kernel(coarse, local, *refs):
    refs = list(refs)
    u_ref = refs.pop(0)
    c_ref = refs.pop(0) if coarse else None
    v7_ref, pre_ref, stc_ref = refs.pop(0), refs.pop(0), refs.pop(0)
    views = table_views(refs.pop(0), refs.pop(0), refs.pop(0), local)
    v3_ref = refs.pop(0) if coarse else None
    out7 = refs.pop(0)
    out3 = refs.pop(0) if coarse else None
    pre = pre_ref[...]
    stc = stc_ref[...]
    bcast = views["bcast"][...]
    sel = views["sel"][...]
    u = u_ref[...]
    divergence = None
    for d in range(3):
        flux = (v7_ref[d].astype(f32) * u).astype(bf16)
        term = _dot(flux, views["d7t"][d])
        divergence = term if divergence is None else divergence + term
    out7[...] = _rate_source(u, pre, stc, bcast, sel, local) - divergence
    if coarse:
        c = c_ref[...]
        div3 = None
        for d in range(3):
            flux3 = (v3_ref[d] * c).astype(bf16)
            term = _dot(flux3, views["d3t"][d])
            div3 = term if div3 is None else div3 + term
        out3[...] = _rate_source(c, pre, stc, bcast, sel, local) - div3


def run_bulk(coarse, local, inputs, out_shapes):
    return pl.pallas_call(
        functools.partial(bulk_kernel, coarse, local),
        out_shape=out_shapes,
        in_specs=[_vmem() for _ in inputs],
        out_specs=[_vmem() for _ in out_shapes],
        compiler_params=pltpu.CompilerParams(vmem_limit_bytes=24 * 1024 * 1024),
    )(*inputs)


def run_stage(flags, inputs, out_shapes):
    coarse, second, project, sends, local = flags
    kernel = functools.partial(stage_kernel, coarse, second, project, sends, local)
    return pl.pallas_call(
        kernel,
        out_shape=out_shapes,
        in_specs=[_vmem() for _ in inputs],
        out_specs=[_vmem() for _ in out_shapes],
        compiler_params=pltpu.CompilerParams(vmem_limit_bytes=48 * 1024 * 1024),
    )(*inputs)


def setup_kernel(local, fields, u_ref, vt_ref, packed_ref, wide_ref, mid_ref, narrow_ref, v7_out, m7_out, v3_out, m3_out, pl_out, pr_out,
                 pre_out, stc_out, sw_out, hinfo_out, cnt_l_out, cnt_r_out, sel_l_out,
                 sel_r_out, *send_refs):
    rows = local * fields
    views = table_views(wide_ref, mid_ref, narrow_ref, local)
    lift_ref = views["lift_t"]
    g7_ref = views["g7"]
    tm_ref = views["tm"]
    fsel_ref = views["fsel"]
    bcast = views["bcast"][...]
    lanes = lax.broadcasted_iota(jnp.int32, (local, 6 * LANE), 1) // LANE
    sign = jnp.where(lanes % 2 == 0, -1.0, 1.0)
    fvg = []
    mvg = []
    for d in range(3):
        vt = vt_ref[d]
        fv = _dot(vt, lift_ref[...]).astype(bf16)
        v7_out[d] = _dot(bcast, fv).astype(bf16)
        v3_out[d] = _dot(bcast, vt)
        fvg.append(_dot(fv, g7_ref[...]))
        mvg.append((_dot(vt, tm_ref[0]) + _dot(vt, tm_ref[1])) + _dot(vt, tm_ref[2]))

    def by_block(parts):
        return jnp.where(lanes < 2, parts[0], jnp.where(lanes < 4, parts[1], parts[2]))

    m7 = jnp.minimum(sign * by_block(fvg), 0.0)
    m7_out[...] = _dot(bcast, m7.astype(bf16))
    m3 = jnp.minimum(sign * by_block(mvg), 0.0)
    m3_out[...] = _exact_right(bcast, m3)
    rep = _dot(bcast, packed_ref[...].astype(bf16))
    row_f = (lax.broadcasted_iota(jnp.int32, (rows, 1), 0) % fields).astype(f32)
    cols = lax.broadcasted_iota(jnp.int32, (rows, rows), 1).astype(f32)
    for side in range(6):
        code = rep[:, side : side + 1]
        far = code >= local
        target = (code - jnp.where(far, float(local), 0.0)) * fields + row_f
        hit = cols == target
        pl_out[side] = jnp.where(hit & ~far, 1.0, 0.0).astype(bf16)
        if side in SEND_FACES:
            pr_out[SEND_FACES.index(side)] = jnp.where(hit & far, 1.0, 0.0).astype(bf16)
    sw_out[...] = rep[:, 6:7]
    packed = packed_ref[...]
    stay_sw = packed[:, 6:7] < 0.5
    go_left = (packed[:, 9:10] == packed[:, 10:11]) & stay_sw
    go_right = (packed[:, 9:10] == packed[:, 11:12]) & stay_sw
    stays = stay_sw & ~go_left & ~go_right
    lane16 = lax.broadcasted_iota(jnp.int32, (local, LANE), 1)
    marks = jnp.where(
        lane16 == 0, go_left.astype(f32),
        jnp.where(lane16 == 1, go_right.astype(f32), jnp.where(lane16 == 2, stays.astype(f32), 0.0)),
    ).astype(bf16)
    er = lax.broadcasted_iota(jnp.int32, (local, local), 0)
    ec = lax.broadcasted_iota(jnp.int32, (local, local), 1)
    before = _dot(jnp.where(ec < er, 1.0, 0.0).astype(bf16), marks)
    totals = _dot(jnp.ones((local, local), bf16), marks)
    info = jnp.where(lane16 < 3, marks.astype(f32), 0.0)
    for k in range(3):
        info = jnp.where(lane16 == 3 + k, before[:, k : k + 1], info)
    info = jnp.where(lane16 == 6, totals[:, 2:3], info)
    info = jnp.where(lane16 == 7, packed[:, 12:13], info)
    info = jnp.where(lane16 == 8, packed[:, 13:14], info)
    hinfo = _dot(bcast, info.astype(bf16))
    hinfo_out[...] = hinfo
    cnt_l_out[...] = jnp.broadcast_to(totals[0:1, 0:1], cnt_l_out.shape)
    cnt_r_out[...] = jnp.broadcast_to(totals[0:1, 1:2], cnt_r_out.shape)
    rf = lax.broadcasted_iota(jnp.int32, (rows, LANE), 0) % fields
    cc = lax.broadcasted_iota(jnp.int32, (rows, LANE), 1)
    eye = jnp.where(
        lax.broadcasted_iota(jnp.int32, (MOVE_CAP * fields, LANE), 0)
        == lax.broadcasted_iota(jnp.int32, (MOVE_CAP * fields, LANE), 1), 1.0, 0.0
    ).astype(bf16)
    for mark_lane, rank_lane, out in ((0, 3, sel_l_out), (1, 4, sel_r_out)):
        hit = (
            (hinfo[:, mark_lane : mark_lane + 1] > 0.5)
            & (hinfo[:, rank_lane : rank_lane + 1] == (cc // fields).astype(f32))
            & (rf == cc % fields)
            & (cc < MOVE_CAP * fields)
        )
        out[...] = _dot_t(eye, jnp.where(hit, 1.0, 0.0).astype(bf16)).astype(bf16)
    pre_out[...] = packed_ref[:, 7:8]
    stc_out[...] = _exact_right(fsel_ref[...], packed_ref[...])[:, 8:9]
    write_sends(send_refs, _dot(u_ref[...].astype(bf16), g7_ref[...]).astype(bf16))


def final_kernel(fields, hold, home_ref, from_l_ref, from_r_ref, hinfo_ref, out_ref):
    hinfo = hinfo_ref[...]
    moved = MOVE_CAP * fields
    n_l = from_l_ref[moved : moved + 1, 0:1]
    n_r = from_r_ref[moved : moved + 1, 0:1]
    n_h = hinfo[0:1, 6:7]
    first = hinfo[0:1, 7:8] > 0.5
    final = hinfo[0:1, 8:9] > 0.5
    off_l = jnp.where(first, n_h + n_r, jnp.where(final, n_r, 0.0))
    off_h = jnp.where(first, 0.0, jnp.where(final, n_r + n_l, n_l))
    off_r = jnp.where(first, n_h, jnp.where(final, 0.0, n_l + n_h))
    width = hold * fields
    eye = jnp.where(
        lax.broadcasted_iota(jnp.int32, (width, LANE), 0)
        == lax.broadcasted_iota(jnp.int32, (width, LANE), 1), 1.0, 0.0
    ).astype(bf16)

    def gather(values, valid, pos):
        count = values.shape[0]
        rf = lax.broadcasted_iota(jnp.int32, (count, LANE), 0) % fields
        cc = lax.broadcasted_iota(jnp.int32, (count, LANE), 1)
        hit = valid & (pos == (cc // fields).astype(f32)) & (rf == cc % fields) & (cc < width)
        pick = _dot_t(eye, jnp.where(hit, 1.0, 0.0).astype(bf16)).astype(bf16)
        return _exact_right(pick, values)

    total = gather(home_ref[...], hinfo[:, 2:3] > 0.5, off_h + hinfo[:, 5:6])
    slot = (lax.broadcasted_iota(jnp.int32, (moved, 1), 0) // fields).astype(f32)
    total = total + gather(from_l_ref[0:moved, :], slot < n_l, off_l + slot)
    total = total + gather(from_r_ref[0:moved, :], slot < n_r, off_r + slot)
    out_ref[...] = total


def setup_entry(local, fields, n_in, n_out, *refs):
    sources = refs[:n_in]
    outs = refs[n_in : n_in + n_out]
    n_tab = 3
    n_own = n_in - n_tab
    buffers = refs[n_in + n_out : n_in + n_out + n_own]
    sems = refs[n_in + n_out + n_own]
    targets = list(buffers) + list(outs[n_out - n_tab :])
    copies = [
        pltpu.make_async_copy(sources[i], targets[i], sems.at[i]) for i in range(n_in)
    ]
    for copy in copies:
        copy.start()
    for copy in copies:
        copy.wait()
    setup_kernel(local, fields, *targets, *outs[: n_out - n_tab])


def per_device(state, velocity, pre_exp, stoich, neighbours, switch, new_owner):
    tab = make_tables()
    local_count = state.shape[0]
    field_count = state.shape[1]
    rows = local_count * field_count
    curve_count = lax.axis_size("curve")
    curve_pos = lax.axis_index("curve")
    device_id = lax.axis_index("slab") * curve_count + curve_pos
    first_global = device_id * local_count
    positions = jnp.arange(local_count, dtype=jnp.int32)

    near_device = neighbours // local_count
    near_local = neighbours - near_device * local_count
    remote = near_device != device_id
    codes = (near_local + local_count * remote.astype(jnp.int32)).astype(f32)
    sto_col = jnp.zeros((local_count,), f32).at[:field_count].set(stoich)
    left_pos = (curve_pos + curve_count - 1) % curve_count
    right_pos = (curve_pos + 1) % curve_count
    ones = jnp.ones((local_count, 1), f32)
    packed = jnp.concatenate(
        [
            codes,
            switch.astype(f32)[:, None],
            pre_exp[:, None],
            sto_col[:, None],
            new_owner.astype(f32)[:, None],
            ones * left_pos.astype(f32),
            ones * right_pos.astype(f32),
            ones * (curve_pos == 0).astype(f32),
            ones * (curve_pos == curve_count - 1).astype(f32),
            jnp.zeros((local_count, LANE - 14), f32),
        ],
        axis=1,
    )
    fsel_np = np.arange(rows)[:, None] % field_count == np.arange(local_count)[None, :]
    vt = jnp.transpose(velocity, (0, 2, 1))
    row_elem = np.arange(rows) // field_count
    bcast_np = row_elem[:, None] == np.arange(local_count)[None, :]
    pick_rows = (np.arange(3)[:, None] + field_count * np.arange(local_count)[None, :]).reshape(-1)
    sel_np = pick_rows[:, None] == np.arange(rows)[None, :]
    n7 = P7**3
    n3 = P3**3
    layouts = table_layout(rows, local_count)
    wide_np = np.zeros((n7 + 6 * n3, 6 * LANE), np.float32)
    mid_np = np.zeros((3 * n7 + 4 * n3, n7), np.float32)
    narrow_np = np.zeros((2 * rows + 3 * local_count + 3 * n3, rows), np.float32)
    pieces = {
        "g7": tab["g7"][None],
        "tm": tab["tm"],
        "mdst": np.transpose(tab["mds"], (0, 2, 1)),
        "d7t": tab["d7t"],
        "lift_t": tab["lift"].T[None],
        "pj": np.transpose(tab["pjt"], (0, 2, 1)),
        "bcast": bcast_np[None],
        "sel": sel_np[None],
        "fsel": fsel_np[None],
        "d3t": tab["d3t"],
    }
    for target, layout in zip((wide_np, mid_np, narrow_np), layouts):
        for name, (start, count, width) in layout.items():
            parts = np.asarray(pieces[name], np.float32)
            for k in range(parts.shape[0]):
                target[start + k * count : start + (k + 1) * count, :width] = parts[k]
    wide = jnp.asarray(to_bf16(wide_np))
    mid = jnp.asarray(to_bf16(mid_np))
    narrow = jnp.asarray(to_bf16(narrow_np))

    send_shape = jax.ShapeDtypeStruct((rows, LANE), bf16)
    sends_shape = [send_shape, send_shape, jax.ShapeDtypeStruct((2 * rows, LANE), bf16)]
    u_shape = jax.ShapeDtypeStruct((rows, P7**3), f32)
    c_shape = jax.ShapeDtypeStruct((rows, P3**3), f32)

    def exchange(sends):
        face0, face1, faces_z = sends
        from_prev = shifted(faces_z, "slab", 1)
        if lax.axis_size("slab") == 2:
            from_next = from_prev
        else:
            from_next = shifted(faces_z, "slab", -1)
        return [shifted(face1, "curve", 1), shifted(face0, "curve", -1), from_prev, from_next]

    setup_out = [
        jax.ShapeDtypeStruct((3, rows, P7**3), bf16),
        jax.ShapeDtypeStruct((rows, 6 * LANE), f32),
        jax.ShapeDtypeStruct((3, rows, P3**3), f32),
        jax.ShapeDtypeStruct((rows, 6 * LANE), f32),
        jax.ShapeDtypeStruct((6, rows, rows), bf16),
        jax.ShapeDtypeStruct((len(SEND_FACES), rows, rows), bf16),
        jax.ShapeDtypeStruct((local_count, 1), f32),
        jax.ShapeDtypeStruct((rows, 1), f32),
        jax.ShapeDtypeStruct((rows, 1), f32),
        jax.ShapeDtypeStruct((rows, LANE), f32),
        jax.ShapeDtypeStruct((8, LANE), f32),
        jax.ShapeDtypeStruct((8, LANE), f32),
        jax.ShapeDtypeStruct((MOVE_CAP * field_count, rows), bf16),
        jax.ShapeDtypeStruct((MOVE_CAP * field_count, rows), bf16),
    ] + sends_shape
    setup_out = setup_out + [jax.ShapeDtypeStruct(x.shape, x.dtype) for x in (wide, mid, narrow)]
    u0 = state.reshape(rows, P7**3)
    setup_in = [u0, vt, packed, wide, mid, narrow]
    res = pl.pallas_call(
        functools.partial(setup_entry, local_count, field_count, len(setup_in), len(setup_out)),
        out_shape=setup_out,
        in_specs=[pl.BlockSpec(memory_space=pltpu.HBM) for _ in setup_in],
        out_specs=[_vmem() for _ in setup_out],
        scratch_shapes=[pltpu.VMEM(x.shape, x.dtype) for x in setup_in[:3]]
        + [pltpu.SemaphoreType.DMA((len(setup_in),))],
        compiler_params=pltpu.CompilerParams(vmem_limit_bytes=24 * 1024 * 1024),
    )(*setup_in)
    v7, m7, v3, m3, p_local, p_remote, pre, stc, sw = res[:9]
    hinfo, cnt_l, cnt_r, sel_l, sel_r = res[9:14]
    sends = res[14:17]
    wide, mid, narrow = res[17:20]
    common = [p_local, p_remote, v7, m7, pre, stc, wide, mid, narrow]
    recv = exchange(sends)
    bulk_tabs = [v7, pre, stc, wide, mid, narrow]
    (bulk7,) = run_bulk(False, local_count, [u0] + bulk_tabs, [u_shape])
    res = run_stage(
        (False, False, False, True, local_count),
        [u0] + recv + common + [bulk7],
        [u_shape] + sends_shape,
    )
    first, sends = res[0], res[1:]
    recv = exchange(sends)
    (bulk7,) = run_bulk(False, local_count, [first] + bulk_tabs, [u_shape])
    res = run_stage(
        (False, True, True, True, local_count),
        [first, u0] + recv + common + [sw, bulk7],
        [u_shape, c_shape] + sends_shape,
    )
    after, coarse, sends = res[0], res[1], res[2:]
    recv = exchange(sends)
    mixed_tail = [v3, m3, sw]
    bulk7, bulk3 = run_bulk(True, local_count, [after, coarse] + bulk_tabs + [v3], [u_shape, c_shape])
    res = run_stage(
        (True, False, False, True, local_count),
        [after, coarse] + recv + common + mixed_tail + [bulk7, bulk3],
        [u_shape, c_shape] + sends_shape,
    )
    first7, first3, sends = res[0], res[1], res[2:]
    recv = exchange(sends)
    pay_shape = jax.ShapeDtypeStruct((MOVE_CAP * field_count + 8, P7**3), f32)
    bulk7, bulk3 = run_bulk(True, local_count, [first7, first3] + bulk_tabs + [v3], [u_shape, c_shape])
    res = run_stage(
        (True, True, False, False, local_count),
        [first7, first3, after, coarse] + recv + common + mixed_tail
        + [sel_l, sel_r, cnt_l, cnt_r, bulk7, bulk3],
        [u_shape, c_shape, pay_shape, pay_shape],
    )
    final7, final3, pay_l, pay_r = res
    from_right = shifted(pay_l, "curve", -1)
    from_left = shifted(pay_r, "curve", 1)
    held = pl.pallas_call(
        functools.partial(final_kernel, field_count, HOLD7),
        out_shape=jax.ShapeDtypeStruct((HOLD7 * field_count, P7**3), f32),
        in_specs=[_vmem() for _ in range(4)],
        out_specs=_vmem(),
    )(final7, from_left, from_right, hinfo)
    state7_out = held.reshape(HOLD7, field_count, P7**3)
    state3_out = final3.reshape(local_count, field_count * P3**3)
    return (state7_out, state3_out)


def solution(mesh):
    return jax.shard_map(
        per_device,
        mesh=mesh,
        in_specs=(
            P(("slab", "curve"), None, None),
            P(None, None, ("slab", "curve")),
            P(("slab", "curve")),
            P(),
            P(("slab", "curve"), None),
            P(("slab", "curve")),
            P(("slab", "curve")),
        ),
        out_specs=(P(("slab", "curve"), None, None), P(("slab", "curve"), None)),
        check_vma=False,
    )
```

```python
import functools

import jax
import jax.numpy as jnp
import ml_dtypes
import numpy as np
from jax import lax
from jax.experimental import pallas as pl
from jax.experimental.pallas import tpu as pltpu
from jax.sharding import PartitionSpec as P

P7 = 8
P3 = 4
MOVE_CAP = 2
HOLD7 = 12
LANE = 128

TIME_STEP = 0.002
ACTIVATION = 1.5
SIDE_SIGNS = (-1.0, 1.0, -1.0, 1.0, -1.0, 1.0)
OPPOSITE = (1, 0, 3, 2, 5, 4)
SEND_FACES = (0, 1, 4, 5)
missing_id = 1 << 30

f32 = jnp.float32
bf16 = jnp.bfloat16


def shifted(value, axis, steps):
    count = lax.axis_size(axis)
    pairs = [(source, (source + steps) % count) for source in range(count)]
    return lax.ppermute(value, axis, pairs)


def lobatto_points(number):
    return -np.cos(np.pi * np.arange(number) / (number - 1))


def lagrange_weights(points):
    weights = np.ones(points.shape[0])
    for row_id in range(points.shape[0]):
        for col_id in range(points.shape[0]):
            if col_id != row_id:
                weights[row_id] = weights[row_id] / (points[row_id] - points[col_id])
    return weights


def derivative_matrix(points):
    weights = lagrange_weights(points)
    number = points.shape[0]
    matrix = np.zeros((number, number))
    for row_id in range(number):
        for col_id in range(number):
            if col_id != row_id:
                matrix[row_id, col_id] = (
                    weights[col_id] / weights[row_id] / (points[row_id] - points[col_id])
                )
        matrix[row_id, row_id] = -np.sum(matrix[row_id])
    return matrix


def interpolation_matrix(source, target):
    matrix = np.ones((target.shape[0], source.shape[0]))
    for col_id in range(source.shape[0]):
        for other_id in range(source.shape[0]):
            if other_id != col_id:
                matrix[:, col_id] = (
                    matrix[:, col_id]
                    * (target - source[other_id])
                    / (source[col_id] - source[other_id])
                )
    return matrix


def spread_three(matrix, identity):
    return (
        np.kron(matrix, np.kron(identity, identity)),
        np.kron(identity, np.kron(matrix, identity)),
        np.kron(identity, np.kron(identity, matrix)),
    )


def face_nodes(extent):
    grid = np.arange(extent**3).reshape(extent, extent, extent)
    last = extent - 1
    pieces = (grid[0], grid[last], grid[:, 0], grid[:, last], grid[:, :, 0], grid[:, :, last])
    return [piece.reshape(-1) for piece in pieces]


def to_bf16(x):
    return np.asarray(np.asarray(x, np.float32).astype(ml_dtypes.bfloat16))


def split_parts(x):
    x = np.asarray(x, np.float32)
    hi = x.astype(ml_dtypes.bfloat16)
    rest = x - hi.astype(np.float32)
    mid = rest.astype(ml_dtypes.bfloat16)
    lo = (rest - mid.astype(np.float32)).astype(ml_dtypes.bfloat16)
    return np.stack([hi, mid, lo])


def make_tables():
    fine_points = lobatto_points(P7)
    coarse_points = lobatto_points(P3)
    fine_derivs = spread_three(derivative_matrix(fine_points), np.eye(P7))
    coarse_derivs = spread_three(derivative_matrix(coarse_points), np.eye(P3))
    downward = interpolation_matrix(fine_points, coarse_points)
    upward = interpolation_matrix(coarse_points, fine_points)
    d7t = np.stack([to_bf16(m.T) for m in fine_derivs])
    d3t = np.stack([to_bf16(m).T for m in coarse_derivs])
    lift_table = to_bf16(np.kron(upward, np.kron(upward, upward)))
    projection = np.asarray(np.kron(downward, np.kron(downward, downward)), np.float32)
    mortar_up = np.asarray(np.kron(upward, upward), np.float32)
    mortar_down = np.asarray(np.kron(downward, downward), np.float32)
    nodes7 = face_nodes(P7)
    nodes3 = face_nodes(P3)
    n7 = P7**3
    n3 = P3**3
    g7 = np.zeros((n7, 6 * LANE), np.float32)
    tm = np.zeros((n3, 6 * LANE), np.float32)
    mds = np.zeros((6 * LANE, n3), np.float32)
    for side in range(6):
        for q, node in enumerate(nodes7[side]):
            g7[node, side * LANE + q] = 1.0
        for k, node in enumerate(nodes3[side]):
            tm[node, side * LANE : side * LANE + P7 * P7] = mortar_up[:, k]
            mds[side * LANE : side * LANE + P7 * P7, node] = mortar_down[k, :]
    tables = {
        "d7t": to_bf16(d7t),
        "d3t": to_bf16(d3t),
        "lift": lift_table,
        "mortar_up": mortar_up,
        "g7": to_bf16(g7),
        "tm": split_parts(tm),
        "mds": split_parts(mds),
        "pjt": split_parts(projection.T),
        "nodes7": nodes7,
        "nodes3": nodes3,
    }
    return tables


def _dot(a, b):
    return jnp.dot(a, b, preferred_element_type=f32)


def _split(x):
    hi = x.astype(bf16)
    rest = x - hi.astype(f32)
    mid = rest.astype(bf16)
    lo = (rest - mid.astype(f32)).astype(bf16)
    return hi, mid, lo


def _exact_left(x, table):
    hi, mid, lo = _split(x)
    return (_dot(hi, table) + _dot(mid, table)) + _dot(lo, table)


def _dot_t(a, b):
    return lax.dot_general(a, b, (((1,), (1,)), ((), ())), preferred_element_type=f32)


def _exact_left_t(x, table):
    hi, mid, lo = _split(x)
    return (_dot_t(hi, table) + _dot_t(mid, table)) + _dot_t(lo, table)


def _exact_right(table, x):
    hi, mid, lo = _split(x)
    return (_dot(table, hi) + _dot(table, mid)) + _dot(table, lo)


def _full_t(x, parts_ref):
    xh, xm, xl = _split(x)
    bh = parts_ref[0]
    bm = parts_ref[1]
    bl = parts_ref[2]
    return _dot_t(xh, bh) + (_dot_t(xh, bm) + _dot_t(xm, bh)) + (
        _dot_t(xh, bl) + _dot_t(xm, bm) + _dot_t(xl, bh)
    )


class View:
    def __init__(self, ref, start, rows, width):
        self.ref = ref
        self.start = start
        self.rows = rows
        self.width = width

    def __getitem__(self, k):
        if k is Ellipsis:
            k = 0
        top = self.start + k * self.rows
        return self.ref[top : top + self.rows, 0 : self.width]


def table_layout(rows, local):
    n7 = P7**3
    n3 = P3**3
    wide = {"g7": (0, n7, 6 * LANE), "tm": (n7, n3, 6 * LANE), "mdst": (n7 + 3 * n3, n3, 6 * LANE)}
    mid = {"d7t": (0, n7, n7), "lift_t": (3 * n7, n3, n7), "pj": (3 * n7 + n3, n3, n7)}
    narrow = {
        "bcast": (0, rows, local),
        "sel": (rows, 3 * local, rows),
        "fsel": (rows + 3 * local, rows, local),
        "d3t": (2 * rows + 3 * local, n3, n3),
    }
    return wide, mid, narrow


def table_views(wide_ref, mid_ref, narrow_ref, local):
    rows = narrow_ref.shape[1]
    layouts = table_layout(rows, local)
    views = {}
    for ref, layout in zip((wide_ref, mid_ref, narrow_ref), layouts):
        for name, (start, count, width) in layout.items():
            views[name] = View(ref, start, count, width)
    return views


def _full(x, parts_ref):
    xh, xm, xl = _split(x)
    bh = parts_ref[0]
    bm = parts_ref[1]
    bl = parts_ref[2]
    return _dot(xh, bh) + (_dot(xh, bm) + _dot(xm, bh)) + (
        _dot(xh, bl) + _dot(xm, bm) + _dot(xl, bh)
    )


def _rate_source(values, pre, stc, bc, sel, local):
    picked = _exact_right(sel, values)
    v0 = picked[0:local]
    v1 = picked[local : 2 * local]
    v2 = picked[2 * local : 3 * local]
    rate = pre * jnp.exp(-ACTIVATION * jnp.exp(-v0)) * v1 * v2
    return stc * _exact_right(bc, rate)


def recv_block(recv, side):
    ref = recv[side]
    if side in (4, 5):
        rows = ref.shape[0] // 2
        top = 0 if side == 4 else rows
        return ref[top : top + rows, :]
    return ref[...]


def write_sends(out_refs, send):
    rows = send.shape[0]
    out_refs[0][...] = send[:, 0:LANE]
    out_refs[1][...] = send[:, LANE : 2 * LANE]
    out_refs[2][0:rows, :] = send[:, 5 * LANE : 6 * LANE]
    out_refs[2][rows : 2 * rows, :] = send[:, 4 * LANE : 5 * LANE]


def stage_kernel(coarse, second, project, sends, local, *refs):
    refs = list(refs)

    def take():
        return refs.pop(0)

    u_ref = take()
    c_ref = take() if coarse else None
    bu_ref = take() if second else None
    bc_ref = take() if (second and coarse) else None
    recv = {s: take() for s in SEND_FACES}
    pl_ref = take()
    pr_ref = take()
    v7_ref = take()
    m7_ref = take()
    pre_ref = take()
    stc_ref = take()
    views = table_views(take(), take(), take(), local)
    bc_tab = views["bcast"]
    sel_tab = views["sel"]
    d7_ref = views["d7t"]
    g7_ref = views["g7"]
    d3_ref = views["d3t"]
    mds_ref = views["mdst"]
    tm_ref = views["tm"]
    pj_ref = views["pj"]
    if coarse:
        v3_ref = take()
        m3_ref = take()
    if coarse or project:
        sw_ref = take()
    last = coarse and not sends
    if last:
        sel_l_ref = take()
        sel_r_ref = take()
        cnt_l_ref = take()
        cnt_r_ref = take()
    res7_ref = take()
    res3_ref = take() if coarse else None
    out_u = take()
    out_c = take() if (coarse or project) else None
    out_send = [take() for _ in range(3)] if sends else None
    if last:
        pay_l_ref = take()
        pay_r_ref = take()

    pre = pre_ref[...]
    stc = stc_ref[...]
    bcast = bc_tab[...]
    sel = sel_tab[...]
    u = u_ref[...]
    trace7 = _dot(u.astype(bf16), g7_ref[...])
    if coarse:
        c = c_ref[...]
        trace3 = _full(c, tm_ref).astype(bf16).astype(f32)
        switched = sw_ref[...] > 0.5
        own = jnp.where(switched, trace3, trace7)
    else:
        own = trace7
    own_b = own.astype(bf16)
    near_blocks = []
    for side in range(6):
        other = OPPOSITE[side]
        block = own_b[:, other * LANE : (other + 1) * LANE]
        near = _dot(pl_ref[side], block)
        if side in SEND_FACES:
            k = SEND_FACES.index(side)
            near = near + _dot(pr_ref[k], recv_block(recv, side))
        near_blocks.append(near)
    near = jnp.concatenate(near_blocks, axis=1)

    result = res7_ref[...]
    jump = (P7 * (P7 - 1) / 2.0) * (m7_ref[...] * (trace7 - near))
    rate7 = result + _exact_left_t(jump, g7_ref[...])

    if coarse:
        result3 = res3_ref[...]
        jump3 = m3_ref[...] * (trace3 - near)
        rate3 = result3 + (P3 * (P3 - 1) / 2.0) * _full_t(jump3, mds_ref)

    if second:
        new_u = 0.5 * (bu_ref[...] + u + TIME_STEP * rate7)
    else:
        new_u = u + TIME_STEP * rate7
    out_u[...] = new_u
    new_c = None
    if coarse:
        if second:
            new_c = 0.5 * (bc_ref[...] + c + TIME_STEP * rate3)
        else:
            new_c = c + TIME_STEP * rate3
        if last:
            out_c[...] = jnp.where(sw_ref[...] > 0.5, new_c, 0.0)
            moved = sel_l_ref.shape[0]
            pay_l_ref[0:moved, :] = _exact_right(sel_l_ref[...], new_u)
            pay_r_ref[0:moved, :] = _exact_right(sel_r_ref[...], new_u)
            tail = (pay_l_ref.shape[0] - moved, pay_l_ref.shape[1])
            pay_l_ref[moved:, :] = jnp.broadcast_to(cnt_l_ref[0:1, 0:1], tail)
            pay_r_ref[moved:, :] = jnp.broadcast_to(cnt_r_ref[0:1, 0:1], tail)
        else:
            out_c[...] = new_c
    if project:
        new_c = _full_t(new_u, pj_ref)
        out_c[...] = new_c
    if sends:
        send7 = _dot(new_u.astype(bf16), g7_ref[...])
        if new_c is not None:
            send3 = _full(new_c, tm_ref).astype(bf16).astype(f32)
            send = jnp.where(sw_ref[...] > 0.5, send3, send7)
        else:
            send = send7
        write_sends(out_send, send.astype(bf16))


def _vmem():
    return pl.BlockSpec(memory_space=pltpu.VMEM)


def bulk_kernel(coarse, local, *refs):
    refs = list(refs)
    u_ref = refs.pop(0)
    c_ref = refs.pop(0) if coarse else None
    v7_ref, pre_ref, stc_ref = refs.pop(0), refs.pop(0), refs.pop(0)
    views = table_views(refs.pop(0), refs.pop(0), refs.pop(0), local)
    v3_ref = refs.pop(0) if coarse else None
    out7 = refs.pop(0)
    out3 = refs.pop(0) if coarse else None
    pre = pre_ref[...]
    stc = stc_ref[...]
    bcast = views["bcast"][...]
    sel = views["sel"][...]
    u = u_ref[...]
    divergence = None
    for d in range(3):
        flux = (v7_ref[d].astype(f32) * u).astype(bf16)
        term = _dot(flux, views["d7t"][d])
        divergence = term if divergence is None else divergence + term
    out7[...] = _rate_source(u, pre, stc, bcast, sel, local) - divergence
    if coarse:
        c = c_ref[...]
        div3 = None
        for d in range(3):
            flux3 = (v3_ref[d] * c).astype(bf16)
            term = _dot(flux3, views["d3t"][d])
            div3 = term if div3 is None else div3 + term
        out3[...] = _rate_source(c, pre, stc, bcast, sel, local) - div3


def run_bulk(coarse, local, inputs, out_shapes):
    return pl.pallas_call(
        functools.partial(bulk_kernel, coarse, local),
        out_shape=out_shapes,
        in_specs=[_vmem() for _ in inputs],
        out_specs=[_vmem() for _ in out_shapes],
        compiler_params=pltpu.CompilerParams(vmem_limit_bytes=24 * 1024 * 1024),
    )(*inputs)


def run_stage(flags, inputs, out_shapes):
    coarse, second, project, sends, local = flags
    kernel = functools.partial(stage_kernel, coarse, second, project, sends, local)
    return pl.pallas_call(
        kernel,
        out_shape=out_shapes,
        in_specs=[_vmem() for _ in inputs],
        out_specs=[_vmem() for _ in out_shapes],
        compiler_params=pltpu.CompilerParams(vmem_limit_bytes=48 * 1024 * 1024),
    )(*inputs)


def setup_kernel(local, fields, u_ref, vt_ref, packed_ref, wide_ref, mid_ref, narrow_ref, v7_out, m7_out, v3_out, m3_out, pl_out, pr_out,
                 pre_out, stc_out, sw_out, hinfo_out, cnt_l_out, cnt_r_out, sel_l_out,
                 sel_r_out, *send_refs):
    rows = local * fields
    views = table_views(wide_ref, mid_ref, narrow_ref, local)
    lift_ref = views["lift_t"]
    g7_ref = views["g7"]
    tm_ref = views["tm"]
    fsel_ref = views["fsel"]
    bcast = views["bcast"][...]
    lanes = lax.broadcasted_iota(jnp.int32, (local, 6 * LANE), 1) // LANE
    sign = jnp.where(lanes % 2 == 0, -1.0, 1.0)
    fvg = []
    mvg = []
    for d in range(3):
        vt = vt_ref[d]
        fv = _dot(vt, lift_ref[...]).astype(bf16)
        v7_out[d] = _dot(bcast, fv).astype(bf16)
        v3_out[d] = _dot(bcast, vt)
        fvg.append(_dot(fv, g7_ref[...]))
        mvg.append((_dot(vt, tm_ref[0]) + _dot(vt, tm_ref[1])) + _dot(vt, tm_ref[2]))

    def by_block(parts):
        return jnp.where(lanes < 2, parts[0], jnp.where(lanes < 4, parts[1], parts[2]))

    m7 = jnp.minimum(sign * by_block(fvg), 0.0)
    m7_out[...] = _dot(bcast, m7.astype(bf16))
    m3 = jnp.minimum(sign * by_block(mvg), 0.0)
    m3_out[...] = _exact_right(bcast, m3)
    eye16 = jnp.where(
        lax.broadcasted_iota(jnp.int32, (local, LANE), 0)
        == lax.broadcasted_iota(jnp.int32, (local, LANE), 1), 1.0, 0.0
    ).astype(bf16)
    p_hi, p_mid, p_lo = _split(packed_ref[...])
    packed = (_dot_t(eye16, p_hi) + _dot_t(eye16, p_mid)) + _dot_t(eye16, p_lo)
    rep = _dot(bcast, packed.astype(bf16))
    row_f = (lax.broadcasted_iota(jnp.int32, (rows, 1), 0) % fields).astype(f32)
    cols = lax.broadcasted_iota(jnp.int32, (rows, rows), 1).astype(f32)
    for side in range(6):
        code = rep[:, side : side + 1]
        far = code >= local
        target = (code - jnp.where(far, float(local), 0.0)) * fields + row_f
        hit = cols == target
        pl_out[side] = jnp.where(hit & ~far, 1.0, 0.0).astype(bf16)
        if side in SEND_FACES:
            pr_out[SEND_FACES.index(side)] = jnp.where(hit & far, 1.0, 0.0).astype(bf16)
    sw_out[...] = rep[:, 6:7]
    curve_count = lax.axis_size("curve")
    curve_pos = lax.axis_index("curve")
    left_f = ((curve_pos + curve_count - 1) % curve_count).astype(f32)
    right_f = ((curve_pos + 1) % curve_count).astype(f32)
    first_f = jnp.where(curve_pos == 0, 1.0, 0.0)
    last_f = jnp.where(curve_pos == curve_count - 1, 1.0, 0.0)
    stay_sw = packed[:, 6:7] < 0.5
    go_left = (packed[:, 9:10] == left_f) & stay_sw
    go_right = (packed[:, 9:10] == right_f) & stay_sw
    stays = stay_sw & ~go_left & ~go_right
    lane16 = lax.broadcasted_iota(jnp.int32, (local, LANE), 1)
    marks = jnp.where(
        lane16 == 0, go_left.astype(f32),
        jnp.where(lane16 == 1, go_right.astype(f32), jnp.where(lane16 == 2, stays.astype(f32), 0.0)),
    ).astype(bf16)
    er = lax.broadcasted_iota(jnp.int32, (local, local), 0)
    ec = lax.broadcasted_iota(jnp.int32, (local, local), 1)
    before = _dot(jnp.where(ec < er, 1.0, 0.0).astype(bf16), marks)
    totals = _dot(jnp.ones((local, local), bf16), marks)
    info = jnp.where(lane16 < 3, marks.astype(f32), 0.0)
    for k in range(3):
        info = jnp.where(lane16 == 3 + k, before[:, k : k + 1], info)
    info = jnp.where(lane16 == 6, totals[:, 2:3], info)
    info = jnp.where(lane16 == 7, first_f, info)
    info = jnp.where(lane16 == 8, last_f, info)
    hinfo = _dot(bcast, info.astype(bf16))
    hinfo_out[...] = hinfo
    cnt_l_out[...] = jnp.broadcast_to(totals[0:1, 0:1], cnt_l_out.shape)
    cnt_r_out[...] = jnp.broadcast_to(totals[0:1, 1:2], cnt_r_out.shape)
    rf = lax.broadcasted_iota(jnp.int32, (rows, LANE), 0) % fields
    cc = lax.broadcasted_iota(jnp.int32, (rows, LANE), 1)
    eye = jnp.where(
        lax.broadcasted_iota(jnp.int32, (MOVE_CAP * fields, LANE), 0)
        == lax.broadcasted_iota(jnp.int32, (MOVE_CAP * fields, LANE), 1), 1.0, 0.0
    ).astype(bf16)
    for mark_lane, rank_lane, out in ((0, 3, sel_l_out), (1, 4, sel_r_out)):
        hit = (
            (hinfo[:, mark_lane : mark_lane + 1] > 0.5)
            & (hinfo[:, rank_lane : rank_lane + 1] == (cc // fields).astype(f32))
            & (rf == cc % fields)
            & (cc < MOVE_CAP * fields)
        )
        out[...] = _dot_t(eye, jnp.where(hit, 1.0, 0.0).astype(bf16)).astype(bf16)
    pre_out[...] = packed[:, 7:8]
    stc_out[...] = _exact_right(fsel_ref[...], packed)[:, 8:9]
    write_sends(send_refs, _dot(u_ref[...].astype(bf16), g7_ref[...]).astype(bf16))


def final_kernel(fields, hold, home_ref, from_l_ref, from_r_ref, hinfo_ref, out_ref):
    hinfo = hinfo_ref[...]
    moved = MOVE_CAP * fields
    n_l = from_l_ref[moved : moved + 1, 0:1]
    n_r = from_r_ref[moved : moved + 1, 0:1]
    n_h = hinfo[0:1, 6:7]
    first = hinfo[0:1, 7:8] > 0.5
    final = hinfo[0:1, 8:9] > 0.5
    off_l = jnp.where(first, n_h + n_r, jnp.where(final, n_r, 0.0))
    off_h = jnp.where(first, 0.0, jnp.where(final, n_r + n_l, n_l))
    off_r = jnp.where(first, n_h, jnp.where(final, 0.0, n_l + n_h))
    width = hold * fields
    eye = jnp.where(
        lax.broadcasted_iota(jnp.int32, (width, LANE), 0)
        == lax.broadcasted_iota(jnp.int32, (width, LANE), 1), 1.0, 0.0
    ).astype(bf16)

    def gather(values, valid, pos):
        count = values.shape[0]
        rf = lax.broadcasted_iota(jnp.int32, (count, LANE), 0) % fields
        cc = lax.broadcasted_iota(jnp.int32, (count, LANE), 1)
        hit = valid & (pos == (cc // fields).astype(f32)) & (rf == cc % fields) & (cc < width)
        pick = _dot_t(eye, jnp.where(hit, 1.0, 0.0).astype(bf16)).astype(bf16)
        return _exact_right(pick, values)

    total = gather(home_ref[...], hinfo[:, 2:3] > 0.5, off_h + hinfo[:, 5:6])
    slot = (lax.broadcasted_iota(jnp.int32, (moved, 1), 0) // fields).astype(f32)
    total = total + gather(from_l_ref[0:moved, :], slot < n_l, off_l + slot)
    total = total + gather(from_r_ref[0:moved, :], slot < n_r, off_r + slot)
    out_ref[...] = total


def setup_entry(local, fields, n_in, n_out, *refs):
    sources = refs[:n_in]
    outs = refs[n_in : n_in + n_out]
    n_tab = 3
    n_own = n_in - n_tab
    buffers = refs[n_in + n_out : n_in + n_out + n_own]
    sems = refs[n_in + n_out + n_own]
    targets = list(buffers) + list(outs[n_out - n_tab :])
    copies = [
        pltpu.make_async_copy(sources[i], targets[i], sems.at[i]) for i in range(n_in)
    ]
    for copy in copies:
        copy.start()
    for copy in copies:
        copy.wait()
    setup_kernel(local, fields, *targets, *outs[: n_out - n_tab])


def per_device(state, velocity, pre_exp, stoich, neighbours, switch, new_owner):
    tab = make_tables()
    local_count = state.shape[0]
    field_count = state.shape[1]
    rows = local_count * field_count
    curve_count = lax.axis_size("curve")
    curve_pos = lax.axis_index("curve")
    device_id = lax.axis_index("slab") * curve_count + curve_pos
    first_global = device_id * local_count
    positions = jnp.arange(local_count, dtype=jnp.int32)

    near_device = neighbours // local_count
    near_local = neighbours - near_device * local_count
    remote = near_device != device_id
    codes = (near_local + local_count * remote.astype(jnp.int32)).astype(f32)
    left_pos = (curve_pos + curve_count - 1) % curve_count
    right_pos = (curve_pos + 1) % curve_count
    sto_col = jnp.pad(stoich, (0, local_count - field_count))
    packed_t = jnp.concatenate(
        [
            jnp.transpose(codes),
            jnp.stack([switch.astype(f32), pre_exp, sto_col, new_owner.astype(f32)]),
        ]
    )
    packed = jnp.pad(packed_t, ((0, local_count - 10), (0, LANE - local_count)))
    fsel_np = np.arange(rows)[:, None] % field_count == np.arange(local_count)[None, :]
    vt = jnp.transpose(velocity, (0, 2, 1))
    row_elem = np.arange(rows) // field_count
    bcast_np = row_elem[:, None] == np.arange(local_count)[None, :]
    pick_rows = (np.arange(3)[:, None] + field_count * np.arange(local_count)[None, :]).reshape(-1)
    sel_np = pick_rows[:, None] == np.arange(rows)[None, :]
    n7 = P7**3
    n3 = P3**3
    layouts = table_layout(rows, local_count)
    wide_np = np.zeros((n7 + 6 * n3, 6 * LANE), np.float32)
    mid_np = np.zeros((3 * n7 + 4 * n3, n7), np.float32)
    narrow_np = np.zeros((2 * rows + 3 * local_count + 3 * n3, rows), np.float32)
    pieces = {
        "g7": tab["g7"][None],
        "tm": tab["tm"],
        "mdst": np.transpose(tab["mds"], (0, 2, 1)),
        "d7t": tab["d7t"],
        "lift_t": tab["lift"].T[None],
        "pj": np.transpose(tab["pjt"], (0, 2, 1)),
        "bcast": bcast_np[None],
        "sel": sel_np[None],
        "fsel": fsel_np[None],
        "d3t": tab["d3t"],
    }
    for target, layout in zip((wide_np, mid_np, narrow_np), layouts):
        for name, (start, count, width) in layout.items():
            parts = np.asarray(pieces[name], np.float32)
            for k in range(parts.shape[0]):
                target[start + k * count : start + (k + 1) * count, :width] = parts[k]
    wide = jnp.asarray(to_bf16(wide_np))
    mid = jnp.asarray(to_bf16(mid_np))
    narrow = jnp.asarray(to_bf16(narrow_np))

    send_shape = jax.ShapeDtypeStruct((rows, LANE), bf16)
    sends_shape = [send_shape, send_shape, jax.ShapeDtypeStruct((2 * rows, LANE), bf16)]
    u_shape = jax.ShapeDtypeStruct((rows, P7**3), f32)
    c_shape = jax.ShapeDtypeStruct((rows, P3**3), f32)

    def exchange(sends):
        face0, face1, faces_z = sends
        from_prev = shifted(faces_z, "slab", 1)
        if lax.axis_size("slab") == 2:
            from_next = from_prev
        else:
            from_next = shifted(faces_z, "slab", -1)
        return [shifted(face1, "curve", 1), shifted(face0, "curve", -1), from_prev, from_next]

    setup_out = [
        jax.ShapeDtypeStruct((3, rows, P7**3), bf16),
        jax.ShapeDtypeStruct((rows, 6 * LANE), f32),
        jax.ShapeDtypeStruct((3, rows, P3**3), f32),
        jax.ShapeDtypeStruct((rows, 6 * LANE), f32),
        jax.ShapeDtypeStruct((6, rows, rows), bf16),
        jax.ShapeDtypeStruct((len(SEND_FACES), rows, rows), bf16),
        jax.ShapeDtypeStruct((local_count, 1), f32),
        jax.ShapeDtypeStruct((rows, 1), f32),
        jax.ShapeDtypeStruct((rows, 1), f32),
        jax.ShapeDtypeStruct((rows, LANE), f32),
        jax.ShapeDtypeStruct((8, LANE), f32),
        jax.ShapeDtypeStruct((8, LANE), f32),
        jax.ShapeDtypeStruct((MOVE_CAP * field_count, rows), bf16),
        jax.ShapeDtypeStruct((MOVE_CAP * field_count, rows), bf16),
    ] + sends_shape
    setup_out = setup_out + [jax.ShapeDtypeStruct(x.shape, x.dtype) for x in (wide, mid, narrow)]
    u0 = state.reshape(rows, P7**3)
    setup_in = [u0, vt, packed, wide, mid, narrow]
    res = pl.pallas_call(
        functools.partial(setup_entry, local_count, field_count, len(setup_in), len(setup_out)),
        out_shape=setup_out,
        in_specs=[pl.BlockSpec(memory_space=pltpu.HBM) for _ in setup_in],
        out_specs=[_vmem() for _ in setup_out],
        scratch_shapes=[pltpu.VMEM(x.shape, x.dtype) for x in setup_in[:3]]
        + [pltpu.SemaphoreType.DMA((len(setup_in),))],
        compiler_params=pltpu.CompilerParams(vmem_limit_bytes=24 * 1024 * 1024),
    )(*setup_in)
    v7, m7, v3, m3, p_local, p_remote, pre, stc, sw = res[:9]
    hinfo, cnt_l, cnt_r, sel_l, sel_r = res[9:14]
    sends = res[14:17]
    wide, mid, narrow = res[17:20]
    common = [p_local, p_remote, v7, m7, pre, stc, wide, mid, narrow]
    recv = exchange(sends)
    bulk_tabs = [v7, pre, stc, wide, mid, narrow]
    (bulk7,) = run_bulk(False, local_count, [u0] + bulk_tabs, [u_shape])
    res = run_stage(
        (False, False, False, True, local_count),
        [u0] + recv + common + [bulk7],
        [u_shape] + sends_shape,
    )
    first, sends = res[0], res[1:]
    recv = exchange(sends)
    (bulk7,) = run_bulk(False, local_count, [first] + bulk_tabs, [u_shape])
    res = run_stage(
        (False, True, True, True, local_count),
        [first, u0] + recv + common + [sw, bulk7],
        [u_shape, c_shape] + sends_shape,
    )
    after, coarse, sends = res[0], res[1], res[2:]
    recv = exchange(sends)
    mixed_tail = [v3, m3, sw]
    bulk7, bulk3 = run_bulk(True, local_count, [after, coarse] + bulk_tabs + [v3], [u_shape, c_shape])
    res = run_stage(
        (True, False, False, True, local_count),
        [after, coarse] + recv + common + mixed_tail + [bulk7, bulk3],
        [u_shape, c_shape] + sends_shape,
    )
    first7, first3, sends = res[0], res[1], res[2:]
    recv = exchange(sends)
    pay_shape = jax.ShapeDtypeStruct((MOVE_CAP * field_count + 8, P7**3), f32)
    bulk7, bulk3 = run_bulk(True, local_count, [first7, first3] + bulk_tabs + [v3], [u_shape, c_shape])
    res = run_stage(
        (True, True, False, False, local_count),
        [first7, first3, after, coarse] + recv + common + mixed_tail
        + [sel_l, sel_r, cnt_l, cnt_r, bulk7, bulk3],
        [u_shape, c_shape, pay_shape, pay_shape],
    )
    final7, final3, pay_l, pay_r = res
    from_right = shifted(pay_l, "curve", -1)
    from_left = shifted(pay_r, "curve", 1)
    held = pl.pallas_call(
        functools.partial(final_kernel, field_count, HOLD7),
        out_shape=jax.ShapeDtypeStruct((HOLD7 * field_count, P7**3), f32),
        in_specs=[_vmem() for _ in range(4)],
        out_specs=_vmem(),
    )(final7, from_left, from_right, hinfo)
    state7_out = held.reshape(HOLD7, field_count, P7**3)
    state3_out = final3.reshape(local_count, field_count * P3**3)
    return (state7_out, state3_out)


def solution(mesh):
    return jax.shard_map(
        per_device,
        mesh=mesh,
        in_specs=(
            P(("slab", "curve"), None, None),
            P(None, None, ("slab", "curve")),
            P(("slab", "curve")),
            P(),
            P(("slab", "curve"), None),
            P(("slab", "curve")),
            P(("slab", "curve")),
        ),
        out_specs=(P(("slab", "curve"), None, None), P(("slab", "curve"), None)),
        check_vma=False,
    )
```

```python
import functools

import jax
import jax.numpy as jnp
import ml_dtypes
import numpy as np
from jax import lax
from jax.experimental import pallas as pl
from jax.experimental.pallas import tpu as pltpu
from jax.sharding import PartitionSpec as P

P7 = 8
P3 = 4
MOVE_CAP = 2
HOLD7 = 12
LANE = 128

TIME_STEP = 0.002
ACTIVATION = 1.5
SIDE_SIGNS = (-1.0, 1.0, -1.0, 1.0, -1.0, 1.0)
OPPOSITE = (1, 0, 3, 2, 5, 4)
SEND_FACES = (0, 1, 4, 5)
missing_id = 1 << 30

f32 = jnp.float32
bf16 = jnp.bfloat16


def shifted(value, axis, steps):
    count = lax.axis_size(axis)
    pairs = [(source, (source + steps) % count) for source in range(count)]
    return lax.ppermute(value, axis, pairs)


def lobatto_points(number):
    return -np.cos(np.pi * np.arange(number) / (number - 1))


def lagrange_weights(points):
    weights = np.ones(points.shape[0])
    for row_id in range(points.shape[0]):
        for col_id in range(points.shape[0]):
            if col_id != row_id:
                weights[row_id] = weights[row_id] / (points[row_id] - points[col_id])
    return weights


def derivative_matrix(points):
    weights = lagrange_weights(points)
    number = points.shape[0]
    matrix = np.zeros((number, number))
    for row_id in range(number):
        for col_id in range(number):
            if col_id != row_id:
                matrix[row_id, col_id] = (
                    weights[col_id] / weights[row_id] / (points[row_id] - points[col_id])
                )
        matrix[row_id, row_id] = -np.sum(matrix[row_id])
    return matrix


def interpolation_matrix(source, target):
    matrix = np.ones((target.shape[0], source.shape[0]))
    for col_id in range(source.shape[0]):
        for other_id in range(source.shape[0]):
            if other_id != col_id:
                matrix[:, col_id] = (
                    matrix[:, col_id]
                    * (target - source[other_id])
                    / (source[col_id] - source[other_id])
                )
    return matrix


def spread_three(matrix, identity):
    return (
        np.kron(matrix, np.kron(identity, identity)),
        np.kron(identity, np.kron(matrix, identity)),
        np.kron(identity, np.kron(identity, matrix)),
    )


def face_nodes(extent):
    grid = np.arange(extent**3).reshape(extent, extent, extent)
    last = extent - 1
    pieces = (grid[0], grid[last], grid[:, 0], grid[:, last], grid[:, :, 0], grid[:, :, last])
    return [piece.reshape(-1) for piece in pieces]


def to_bf16(x):
    return np.asarray(np.asarray(x, np.float32).astype(ml_dtypes.bfloat16))


def split_parts(x):
    x = np.asarray(x, np.float32)
    hi = x.astype(ml_dtypes.bfloat16)
    rest = x - hi.astype(np.float32)
    mid = rest.astype(ml_dtypes.bfloat16)
    lo = (rest - mid.astype(np.float32)).astype(ml_dtypes.bfloat16)
    return np.stack([hi, mid, lo])


def make_tables():
    fine_points = lobatto_points(P7)
    coarse_points = lobatto_points(P3)
    fine_derivs = spread_three(derivative_matrix(fine_points), np.eye(P7))
    coarse_derivs = spread_three(derivative_matrix(coarse_points), np.eye(P3))
    downward = interpolation_matrix(fine_points, coarse_points)
    upward = interpolation_matrix(coarse_points, fine_points)
    d7t = np.stack([to_bf16(m.T) for m in fine_derivs])
    d3t = np.stack([to_bf16(m).T for m in coarse_derivs])
    lift_table = to_bf16(np.kron(upward, np.kron(upward, upward)))
    projection = np.asarray(np.kron(downward, np.kron(downward, downward)), np.float32)
    mortar_up = np.asarray(np.kron(upward, upward), np.float32)
    mortar_down = np.asarray(np.kron(downward, downward), np.float32)
    nodes7 = face_nodes(P7)
    nodes3 = face_nodes(P3)
    n7 = P7**3
    n3 = P3**3
    g7 = np.zeros((n7, 6 * LANE), np.float32)
    tm = np.zeros((n3, 6 * LANE), np.float32)
    mds = np.zeros((6 * LANE, n3), np.float32)
    for side in range(6):
        for q, node in enumerate(nodes7[side]):
            g7[node, side * LANE + q] = 1.0
        for k, node in enumerate(nodes3[side]):
            tm[node, side * LANE : side * LANE + P7 * P7] = mortar_up[:, k]
            mds[side * LANE : side * LANE + P7 * P7, node] = mortar_down[k, :]
    tables = {
        "d7t": to_bf16(d7t),
        "d3t": to_bf16(d3t),
        "lift": lift_table,
        "mortar_up": mortar_up,
        "g7": to_bf16(g7),
        "tm": split_parts(tm),
        "mds": split_parts(mds),
        "pjt": split_parts(projection.T),
        "nodes7": nodes7,
        "nodes3": nodes3,
    }
    return tables


def _dot(a, b):
    return jnp.dot(a, b, preferred_element_type=f32)


def _split(x):
    hi = x.astype(bf16)
    rest = x - hi.astype(f32)
    mid = rest.astype(bf16)
    lo = (rest - mid.astype(f32)).astype(bf16)
    return hi, mid, lo


def _exact_left(x, table):
    hi, mid, lo = _split(x)
    return (_dot(hi, table) + _dot(mid, table)) + _dot(lo, table)


def _dot_t(a, b):
    return lax.dot_general(a, b, (((1,), (1,)), ((), ())), preferred_element_type=f32)


def _exact_left_t(x, table):
    hi, mid, lo = _split(x)
    return (_dot_t(hi, table) + _dot_t(mid, table)) + _dot_t(lo, table)


def _exact_right(table, x):
    hi, mid, lo = _split(x)
    return (_dot(table, hi) + _dot(table, mid)) + _dot(table, lo)


def _full_t(x, parts_ref):
    xh, xm, xl = _split(x)
    bh = parts_ref[0]
    bm = parts_ref[1]
    bl = parts_ref[2]
    return _dot_t(xh, bh) + (_dot_t(xh, bm) + _dot_t(xm, bh)) + (
        _dot_t(xh, bl) + _dot_t(xm, bm) + _dot_t(xl, bh)
    )


class View:
    def __init__(self, ref, start, rows, width):
        self.ref = ref
        self.start = start
        self.rows = rows
        self.width = width

    def __getitem__(self, k):
        if k is Ellipsis:
            k = 0
        top = self.start + k * self.rows
        return self.ref[top : top + self.rows, 0 : self.width]


def table_layout(rows, local):
    n7 = P7**3
    n3 = P3**3
    wide = {"g7": (0, n7, 6 * LANE), "tm": (n7, n3, 6 * LANE), "mdst": (n7 + 3 * n3, n3, 6 * LANE)}
    mid = {
        "dx": (0, n7, n7),
        "lift_t": (n7, n3, n7),
        "pj": (n7 + n3, n3, n7),
        "byz": (n7 + 4 * n3, LANE, LANE),
    }
    narrow = {
        "bcast": (0, rows, local),
        "sel": (rows, 3 * local, rows),
        "fsel": (rows + 3 * local, rows, local),
        "d3t": (2 * rows + 3 * local, n3, n3),
    }
    return wide, mid, narrow


def table_views(wide_ref, mid_ref, narrow_ref, local):
    rows = narrow_ref.shape[1]
    layouts = table_layout(rows, local)
    views = {}
    for ref, layout in zip((wide_ref, mid_ref, narrow_ref), layouts):
        for name, (start, count, width) in layout.items():
            views[name] = View(ref, start, count, width)
    return views


def _full(x, parts_ref):
    xh, xm, xl = _split(x)
    bh = parts_ref[0]
    bm = parts_ref[1]
    bl = parts_ref[2]
    return _dot(xh, bh) + (_dot(xh, bm) + _dot(xm, bh)) + (
        _dot(xh, bl) + _dot(xm, bm) + _dot(xl, bh)
    )


def _rate_source(values, pre, stc, bc, sel, local):
    picked = _exact_right(sel, values)
    v0 = picked[0:local]
    v1 = picked[local : 2 * local]
    v2 = picked[2 * local : 3 * local]
    rate = pre * jnp.exp(-ACTIVATION * jnp.exp(-v0)) * v1 * v2
    return stc * _exact_right(bc, rate)


def recv_block(recv, side):
    ref = recv[side]
    if side in (4, 5):
        rows = ref.shape[0] // 2
        top = 0 if side == 4 else rows
        return ref[top : top + rows, :]
    return ref[...]


def write_sends(out_refs, send):
    rows = send.shape[0]
    out_refs[0][...] = send[:, 0:LANE]
    out_refs[1][...] = send[:, LANE : 2 * LANE]
    out_refs[2][0:rows, :] = send[:, 5 * LANE : 6 * LANE]
    out_refs[2][rows : 2 * rows, :] = send[:, 4 * LANE : 5 * LANE]


def stage_kernel(coarse, second, project, sends, local, *refs):
    refs = list(refs)

    def take():
        return refs.pop(0)

    u_ref = take()
    c_ref = take() if coarse else None
    bu_ref = take() if second else None
    bc_ref = take() if (second and coarse) else None
    recv = {s: take() for s in SEND_FACES}
    pl_ref = take()
    pr_ref = take()
    v7_ref = take()
    m7_ref = take()
    pre_ref = take()
    stc_ref = take()
    views = table_views(take(), take(), take(), local)
    bc_tab = views["bcast"]
    sel_tab = views["sel"]
    g7_ref = views["g7"]
    d3_ref = views["d3t"]
    mds_ref = views["mdst"]
    tm_ref = views["tm"]
    pj_ref = views["pj"]
    if coarse:
        v3_ref = take()
        m3_ref = take()
    if coarse or project:
        sw_ref = take()
    last = coarse and not sends
    if last:
        sel_l_ref = take()
        sel_r_ref = take()
        cnt_l_ref = take()
        cnt_r_ref = take()
    res7_ref = take()
    res3_ref = take() if coarse else None
    out_u = take()
    out_c = take() if (coarse or project) else None
    out_send = [take() for _ in range(3)] if sends else None
    if last:
        pay_l_ref = take()
        pay_r_ref = take()

    pre = pre_ref[...]
    stc = stc_ref[...]
    bcast = bc_tab[...]
    sel = sel_tab[...]
    u = u_ref[...]
    trace7 = _dot(u.astype(bf16), g7_ref[...])
    if coarse:
        c = c_ref[...]
        trace3 = _full(c, tm_ref).astype(bf16).astype(f32)
        switched = sw_ref[...] > 0.5
        own = jnp.where(switched, trace3, trace7)
    else:
        own = trace7
    own_b = own.astype(bf16)
    near_blocks = []
    for side in range(6):
        other = OPPOSITE[side]
        block = own_b[:, other * LANE : (other + 1) * LANE]
        near = _dot(pl_ref[side], block)
        if side in SEND_FACES:
            k = SEND_FACES.index(side)
            near = near + _dot(pr_ref[k], recv_block(recv, side))
        near_blocks.append(near)
    near = jnp.concatenate(near_blocks, axis=1)

    result = res7_ref[...]
    jump = (P7 * (P7 - 1) / 2.0) * (m7_ref[...] * (trace7 - near))
    rate7 = result + _exact_left_t(jump, g7_ref[...])

    if coarse:
        result3 = res3_ref[...]
        jump3 = m3_ref[...] * (trace3 - near)
        rate3 = result3 + (P3 * (P3 - 1) / 2.0) * _full_t(jump3, mds_ref)

    if second:
        new_u = 0.5 * (bu_ref[...] + u + TIME_STEP * rate7)
    else:
        new_u = u + TIME_STEP * rate7
    out_u[...] = new_u
    new_c = None
    if coarse:
        if second:
            new_c = 0.5 * (bc_ref[...] + c + TIME_STEP * rate3)
        else:
            new_c = c + TIME_STEP * rate3
        if last:
            out_c[...] = jnp.where(sw_ref[...] > 0.5, new_c, 0.0)
            moved = sel_l_ref.shape[0]
            pay_l_ref[0:moved, :] = _exact_right(sel_l_ref[...], new_u)
            pay_r_ref[0:moved, :] = _exact_right(sel_r_ref[...], new_u)
            tail = (pay_l_ref.shape[0] - moved, pay_l_ref.shape[1])
            pay_l_ref[moved:, :] = jnp.broadcast_to(cnt_l_ref[0:1, 0:1], tail)
            pay_r_ref[moved:, :] = jnp.broadcast_to(cnt_r_ref[0:1, 0:1], tail)
        else:
            out_c[...] = new_c
    if project:
        new_c = _full_t(new_u, pj_ref)
        out_c[...] = new_c
    if sends:
        send7 = _dot(new_u.astype(bf16), g7_ref[...])
        if new_c is not None:
            send3 = _full(new_c, tm_ref).astype(bf16).astype(f32)
            send = jnp.where(sw_ref[...] > 0.5, send3, send7)
        else:
            send = send7
        write_sends(out_send, send.astype(bf16))


def _vmem():
    return pl.BlockSpec(memory_space=pltpu.VMEM)


def bulk_kernel(coarse, local, *refs):
    refs = list(refs)
    u_ref = refs.pop(0)
    c_ref = refs.pop(0) if coarse else None
    v7_ref, pre_ref, stc_ref = refs.pop(0), refs.pop(0), refs.pop(0)
    views = table_views(refs.pop(0), refs.pop(0), refs.pop(0), local)
    v3_ref = refs.pop(0) if coarse else None
    out7 = refs.pop(0)
    out3 = refs.pop(0) if coarse else None
    pre = pre_ref[...]
    stc = stc_ref[...]
    bcast = views["bcast"][...]
    sel = views["sel"][...]
    u = u_ref[...]
    fluxes = [(v7_ref[d].astype(f32) * u).astype(bf16) for d in range(3)]
    divergence = _dot(fluxes[0], views["dx"][0])
    by = views["byz"][0]
    bz = views["byz"][1]
    chunks = []
    for k in range(u.shape[1] // LANE):
        part = slice(k * LANE, (k + 1) * LANE)
        chunks.append(_dot(fluxes[1][:, part], by) + _dot(fluxes[2][:, part], bz))
    divergence = divergence + jnp.concatenate(chunks, axis=1)
    out7[...] = _rate_source(u, pre, stc, bcast, sel, local) - divergence
    if coarse:
        c = c_ref[...]
        div3 = None
        for d in range(3):
            flux3 = (v3_ref[d] * c).astype(bf16)
            term = _dot(flux3, views["d3t"][d])
            div3 = term if div3 is None else div3 + term
        out3[...] = _rate_source(c, pre, stc, bcast, sel, local) - div3


def run_bulk(coarse, local, inputs, out_shapes):
    return pl.pallas_call(
        functools.partial(bulk_kernel, coarse, local),
        out_shape=out_shapes,
        in_specs=[_vmem() for _ in inputs],
        out_specs=[_vmem() for _ in out_shapes],
        compiler_params=pltpu.CompilerParams(vmem_limit_bytes=24 * 1024 * 1024),
    )(*inputs)


def run_stage(flags, inputs, out_shapes):
    coarse, second, project, sends, local = flags
    kernel = functools.partial(stage_kernel, coarse, second, project, sends, local)
    return pl.pallas_call(
        kernel,
        out_shape=out_shapes,
        in_specs=[_vmem() for _ in inputs],
        out_specs=[_vmem() for _ in out_shapes],
        compiler_params=pltpu.CompilerParams(vmem_limit_bytes=48 * 1024 * 1024),
    )(*inputs)


def setup_kernel(local, fields, u_ref, vt_ref, packed_ref, wide_ref, mid_ref, narrow_ref, v7_out, m7_out, v3_out, m3_out, pl_out, pr_out,
                 pre_out, stc_out, sw_out, hinfo_out, cnt_l_out, cnt_r_out, sel_l_out,
                 sel_r_out, *send_refs):
    rows = local * fields
    views = table_views(wide_ref, mid_ref, narrow_ref, local)
    lift_ref = views["lift_t"]
    g7_ref = views["g7"]
    tm_ref = views["tm"]
    fsel_ref = views["fsel"]
    bcast = views["bcast"][...]
    lanes = lax.broadcasted_iota(jnp.int32, (local, 6 * LANE), 1) // LANE
    sign = jnp.where(lanes % 2 == 0, -1.0, 1.0)
    fvg = []
    mvg = []
    for d in range(3):
        vt = vt_ref[d]
        fv = _dot(vt, lift_ref[...]).astype(bf16)
        v7_out[d] = _dot(bcast, fv).astype(bf16)
        v3_out[d] = _dot(bcast, vt)
        fvg.append(_dot(fv, g7_ref[...]))
        mvg.append((_dot(vt, tm_ref[0]) + _dot(vt, tm_ref[1])) + _dot(vt, tm_ref[2]))

    def by_block(parts):
        return jnp.where(lanes < 2, parts[0], jnp.where(lanes < 4, parts[1], parts[2]))

    m7 = jnp.minimum(sign * by_block(fvg), 0.0)
    m7_out[...] = _dot(bcast, m7.astype(bf16))
    m3 = jnp.minimum(sign * by_block(mvg), 0.0)
    m3_out[...] = _exact_right(bcast, m3)
    eye16 = jnp.where(
        lax.broadcasted_iota(jnp.int32, (local, LANE), 0)
        == lax.broadcasted_iota(jnp.int32, (local, LANE), 1), 1.0, 0.0
    ).astype(bf16)
    p_hi, p_mid, p_lo = _split(packed_ref[...])
    packed = (_dot_t(eye16, p_hi) + _dot_t(eye16, p_mid)) + _dot_t(eye16, p_lo)
    rep = _dot(bcast, packed.astype(bf16))
    row_f = (lax.broadcasted_iota(jnp.int32, (rows, 1), 0) % fields).astype(f32)
    cols = lax.broadcasted_iota(jnp.int32, (rows, rows), 1).astype(f32)
    for side in range(6):
        code = rep[:, side : side + 1]
        far = code >= local
        target = (code - jnp.where(far, float(local), 0.0)) * fields + row_f
        hit = cols == target
        pl_out[side] = jnp.where(hit & ~far, 1.0, 0.0).astype(bf16)
        if side in SEND_FACES:
            pr_out[SEND_FACES.index(side)] = jnp.where(hit & far, 1.0, 0.0).astype(bf16)
    sw_out[...] = rep[:, 6:7]
    curve_count = lax.axis_size("curve")
    curve_pos = lax.axis_index("curve")
    left_f = ((curve_pos + curve_count - 1) % curve_count).astype(f32)
    right_f = ((curve_pos + 1) % curve_count).astype(f32)
    first_f = jnp.where(curve_pos == 0, 1.0, 0.0)
    last_f = jnp.where(curve_pos == curve_count - 1, 1.0, 0.0)
    stay_sw = packed[:, 6:7] < 0.5
    go_left = (packed[:, 9:10] == left_f) & stay_sw
    go_right = (packed[:, 9:10] == right_f) & stay_sw
    stays = stay_sw & ~go_left & ~go_right
    lane16 = lax.broadcasted_iota(jnp.int32, (local, LANE), 1)
    marks = jnp.where(
        lane16 == 0, go_left.astype(f32),
        jnp.where(lane16 == 1, go_right.astype(f32), jnp.where(lane16 == 2, stays.astype(f32), 0.0)),
    ).astype(bf16)
    er = lax.broadcasted_iota(jnp.int32, (local, local), 0)
    ec = lax.broadcasted_iota(jnp.int32, (local, local), 1)
    before = _dot(jnp.where(ec < er, 1.0, 0.0).astype(bf16), marks)
    totals = _dot(jnp.ones((local, local), bf16), marks)
    info = jnp.where(lane16 < 3, marks.astype(f32), 0.0)
    for k in range(3):
        info = jnp.where(lane16 == 3 + k, before[:, k : k + 1], info)
    info = jnp.where(lane16 == 6, totals[:, 2:3], info)
    info = jnp.where(lane16 == 7, first_f, info)
    info = jnp.where(lane16 == 8, last_f, info)
    hinfo = _dot(bcast, info.astype(bf16))
    hinfo_out[...] = hinfo
    cnt_l_out[...] = jnp.broadcast_to(totals[0:1, 0:1], cnt_l_out.shape)
    cnt_r_out[...] = jnp.broadcast_to(totals[0:1, 1:2], cnt_r_out.shape)
    rf = lax.broadcasted_iota(jnp.int32, (rows, LANE), 0) % fields
    cc = lax.broadcasted_iota(jnp.int32, (rows, LANE), 1)
    eye = jnp.where(
        lax.broadcasted_iota(jnp.int32, (MOVE_CAP * fields, LANE), 0)
        == lax.broadcasted_iota(jnp.int32, (MOVE_CAP * fields, LANE), 1), 1.0, 0.0
    ).astype(bf16)
    for mark_lane, rank_lane, out in ((0, 3, sel_l_out), (1, 4, sel_r_out)):
        hit = (
            (hinfo[:, mark_lane : mark_lane + 1] > 0.5)
            & (hinfo[:, rank_lane : rank_lane + 1] == (cc // fields).astype(f32))
            & (rf == cc % fields)
            & (cc < MOVE_CAP * fields)
        )
        out[...] = _dot_t(eye, jnp.where(hit, 1.0, 0.0).astype(bf16)).astype(bf16)
    pre_out[...] = packed[:, 7:8]
    stc_out[...] = _exact_right(fsel_ref[...], packed)[:, 8:9]
    write_sends(send_refs, _dot(u_ref[...].astype(bf16), g7_ref[...]).astype(bf16))


def final_kernel(fields, hold, home_ref, from_l_ref, from_r_ref, hinfo_ref, out_ref):
    hinfo = hinfo_ref[...]
    moved = MOVE_CAP * fields
    n_l = from_l_ref[moved : moved + 1, 0:1]
    n_r = from_r_ref[moved : moved + 1, 0:1]
    n_h = hinfo[0:1, 6:7]
    first = hinfo[0:1, 7:8] > 0.5
    final = hinfo[0:1, 8:9] > 0.5
    off_l = jnp.where(first, n_h + n_r, jnp.where(final, n_r, 0.0))
    off_h = jnp.where(first, 0.0, jnp.where(final, n_r + n_l, n_l))
    off_r = jnp.where(first, n_h, jnp.where(final, 0.0, n_l + n_h))
    width = hold * fields
    eye = jnp.where(
        lax.broadcasted_iota(jnp.int32, (width, LANE), 0)
        == lax.broadcasted_iota(jnp.int32, (width, LANE), 1), 1.0, 0.0
    ).astype(bf16)

    def gather(values, valid, pos):
        count = values.shape[0]
        rf = lax.broadcasted_iota(jnp.int32, (count, LANE), 0) % fields
        cc = lax.broadcasted_iota(jnp.int32, (count, LANE), 1)
        hit = valid & (pos == (cc // fields).astype(f32)) & (rf == cc % fields) & (cc < width)
        pick = _dot_t(eye, jnp.where(hit, 1.0, 0.0).astype(bf16)).astype(bf16)
        return _exact_right(pick, values)

    total = gather(home_ref[...], hinfo[:, 2:3] > 0.5, off_h + hinfo[:, 5:6])
    slot = (lax.broadcasted_iota(jnp.int32, (moved, 1), 0) // fields).astype(f32)
    total = total + gather(from_l_ref[0:moved, :], slot < n_l, off_l + slot)
    total = total + gather(from_r_ref[0:moved, :], slot < n_r, off_r + slot)
    out_ref[...] = total


def setup_entry(local, fields, n_in, n_out, *refs):
    sources = refs[:n_in]
    outs = refs[n_in : n_in + n_out]
    n_tab = 3
    n_own = n_in - n_tab
    buffers = refs[n_in + n_out : n_in + n_out + n_own]
    sems = refs[n_in + n_out + n_own]
    targets = list(buffers) + list(outs[n_out - n_tab :])
    copies = [
        pltpu.make_async_copy(sources[i], targets[i], sems.at[i]) for i in range(n_in)
    ]
    for copy in copies:
        copy.start()
    for copy in copies:
        copy.wait()
    setup_kernel(local, fields, *targets, *outs[: n_out - n_tab])


def per_device(state, velocity, pre_exp, stoich, neighbours, switch, new_owner):
    tab = make_tables()
    local_count = state.shape[0]
    field_count = state.shape[1]
    rows = local_count * field_count
    curve_count = lax.axis_size("curve")
    curve_pos = lax.axis_index("curve")
    device_id = lax.axis_index("slab") * curve_count + curve_pos
    first_global = device_id * local_count
    positions = jnp.arange(local_count, dtype=jnp.int32)

    near_device = neighbours // local_count
    near_local = neighbours - near_device * local_count
    remote = near_device != device_id
    codes = (near_local + local_count * remote.astype(jnp.int32)).astype(f32)
    left_pos = (curve_pos + curve_count - 1) % curve_count
    right_pos = (curve_pos + 1) % curve_count
    sto_col = jnp.pad(stoich, (0, local_count - field_count))
    packed_t = jnp.concatenate(
        [
            jnp.transpose(codes),
            jnp.stack([switch.astype(f32), pre_exp, sto_col, new_owner.astype(f32)]),
        ]
    )
    packed = jnp.pad(packed_t, ((0, local_count - 10), (0, LANE - local_count)))
    fsel_np = np.arange(rows)[:, None] % field_count == np.arange(local_count)[None, :]
    vt = jnp.transpose(velocity, (0, 2, 1))
    row_elem = np.arange(rows) // field_count
    bcast_np = row_elem[:, None] == np.arange(local_count)[None, :]
    pick_rows = (np.arange(3)[:, None] + field_count * np.arange(local_count)[None, :]).reshape(-1)
    sel_np = pick_rows[:, None] == np.arange(rows)[None, :]
    n7 = P7**3
    n3 = P3**3
    layouts = table_layout(rows, local_count)
    wide_np = np.zeros((n7 + 6 * n3, 6 * LANE), np.float32)
    mid_np = np.zeros((n7 + 4 * n3 + 2 * LANE, n7), np.float32)
    for d in (1, 2):
        block = tab["d7t"][d][:LANE, :LANE].astype(np.float32)
        assert np.array_equal(
            tab["d7t"][d].astype(np.float32), np.kron(np.eye(n7 // LANE), block)
        )
    narrow_np = np.zeros((2 * rows + 3 * local_count + 3 * n3, rows), np.float32)
    pieces = {
        "g7": tab["g7"][None],
        "tm": tab["tm"],
        "mdst": np.transpose(tab["mds"], (0, 2, 1)),
        "dx": tab["d7t"][0:1],
        "byz": np.stack([tab["d7t"][1][:LANE, :LANE], tab["d7t"][2][:LANE, :LANE]]),
        "lift_t": tab["lift"].T[None],
        "pj": np.transpose(tab["pjt"], (0, 2, 1)),
        "bcast": bcast_np[None],
        "sel": sel_np[None],
        "fsel": fsel_np[None],
        "d3t": tab["d3t"],
    }
    for target, layout in zip((wide_np, mid_np, narrow_np), layouts):
        for name, (start, count, width) in layout.items():
            parts = np.asarray(pieces[name], np.float32)
            for k in range(parts.shape[0]):
                target[start + k * count : start + (k + 1) * count, :width] = parts[k]
    wide = jnp.asarray(to_bf16(wide_np))
    mid = jnp.asarray(to_bf16(mid_np))
    narrow = jnp.asarray(to_bf16(narrow_np))

    send_shape = jax.ShapeDtypeStruct((rows, LANE), bf16)
    sends_shape = [send_shape, send_shape, jax.ShapeDtypeStruct((2 * rows, LANE), bf16)]
    u_shape = jax.ShapeDtypeStruct((rows, P7**3), f32)
    c_shape = jax.ShapeDtypeStruct((rows, P3**3), f32)

    def exchange(sends):
        face0, face1, faces_z = sends
        from_prev = shifted(faces_z, "slab", 1)
        if lax.axis_size("slab") == 2:
            from_next = from_prev
        else:
            from_next = shifted(faces_z, "slab", -1)
        return [shifted(face1, "curve", 1), shifted(face0, "curve", -1), from_prev, from_next]

    setup_out = [
        jax.ShapeDtypeStruct((3, rows, P7**3), bf16),
        jax.ShapeDtypeStruct((rows, 6 * LANE), f32),
        jax.ShapeDtypeStruct((3, rows, P3**3), f32),
        jax.ShapeDtypeStruct((rows, 6 * LANE), f32),
        jax.ShapeDtypeStruct((6, rows, rows), bf16),
        jax.ShapeDtypeStruct((len(SEND_FACES), rows, rows), bf16),
        jax.ShapeDtypeStruct((local_count, 1), f32),
        jax.ShapeDtypeStruct((rows, 1), f32),
        jax.ShapeDtypeStruct((rows, 1), f32),
        jax.ShapeDtypeStruct((rows, LANE), f32),
        jax.ShapeDtypeStruct((8, LANE), f32),
        jax.ShapeDtypeStruct((8, LANE), f32),
        jax.ShapeDtypeStruct((MOVE_CAP * field_count, rows), bf16),
        jax.ShapeDtypeStruct((MOVE_CAP * field_count, rows), bf16),
    ] + sends_shape
    setup_out = setup_out + [jax.ShapeDtypeStruct(x.shape, x.dtype) for x in (wide, mid, narrow)]
    u0 = state.reshape(rows, P7**3)
    setup_in = [u0, vt, packed, wide, mid, narrow]
    res = pl.pallas_call(
        functools.partial(setup_entry, local_count, field_count, len(setup_in), len(setup_out)),
        out_shape=setup_out,
        in_specs=[pl.BlockSpec(memory_space=pltpu.HBM) for _ in setup_in],
        out_specs=[_vmem() for _ in setup_out],
        scratch_shapes=[pltpu.VMEM(x.shape, x.dtype) for x in setup_in[:3]]
        + [pltpu.SemaphoreType.DMA((len(setup_in),))],
        compiler_params=pltpu.CompilerParams(vmem_limit_bytes=24 * 1024 * 1024),
    )(*setup_in)
    v7, m7, v3, m3, p_local, p_remote, pre, stc, sw = res[:9]
    hinfo, cnt_l, cnt_r, sel_l, sel_r = res[9:14]
    sends = res[14:17]
    wide, mid, narrow = res[17:20]
    common = [p_local, p_remote, v7, m7, pre, stc, wide, mid, narrow]
    recv = exchange(sends)
    bulk_tabs = [v7, pre, stc, wide, mid, narrow]
    (bulk7,) = run_bulk(False, local_count, [u0] + bulk_tabs, [u_shape])
    res = run_stage(
        (False, False, False, True, local_count),
        [u0] + recv + common + [bulk7],
        [u_shape] + sends_shape,
    )
    first, sends = res[0], res[1:]
    recv = exchange(sends)
    (bulk7,) = run_bulk(False, local_count, [first] + bulk_tabs, [u_shape])
    res = run_stage(
        (False, True, True, True, local_count),
        [first, u0] + recv + common + [sw, bulk7],
        [u_shape, c_shape] + sends_shape,
    )
    after, coarse, sends = res[0], res[1], res[2:]
    recv = exchange(sends)
    mixed_tail = [v3, m3, sw]
    bulk7, bulk3 = run_bulk(True, local_count, [after, coarse] + bulk_tabs + [v3], [u_shape, c_shape])
    res = run_stage(
        (True, False, False, True, local_count),
        [after, coarse] + recv + common + mixed_tail + [bulk7, bulk3],
        [u_shape, c_shape] + sends_shape,
    )
    first7, first3, sends = res[0], res[1], res[2:]
    recv = exchange(sends)
    pay_shape = jax.ShapeDtypeStruct((MOVE_CAP * field_count + 8, P7**3), f32)
    bulk7, bulk3 = run_bulk(True, local_count, [first7, first3] + bulk_tabs + [v3], [u_shape, c_shape])
    res = run_stage(
        (True, True, False, False, local_count),
        [first7, first3, after, coarse] + recv + common + mixed_tail
        + [sel_l, sel_r, cnt_l, cnt_r, bulk7, bulk3],
        [u_shape, c_shape, pay_shape, pay_shape],
    )
    final7, final3, pay_l, pay_r = res
    from_right = shifted(pay_l, "curve", -1)
    from_left = shifted(pay_r, "curve", 1)
    held = pl.pallas_call(
        functools.partial(final_kernel, field_count, HOLD7),
        out_shape=jax.ShapeDtypeStruct((HOLD7 * field_count, P7**3), f32),
        in_specs=[_vmem() for _ in range(4)],
        out_specs=_vmem(),
    )(final7, from_left, from_right, hinfo)
    state7_out = held.reshape(HOLD7, field_count, P7**3)
    state3_out = final3.reshape(local_count, field_count * P3**3)
    return (state7_out, state3_out)


def solution(mesh):
    return jax.shard_map(
        per_device,
        mesh=mesh,
        in_specs=(
            P(("slab", "curve"), None, None),
            P(None, None, ("slab", "curve")),
            P(("slab", "curve")),
            P(),
            P(("slab", "curve"), None),
            P(("slab", "curve")),
            P(("slab", "curve")),
        ),
        out_specs=(P(("slab", "curve"), None, None), P(("slab", "curve"), None)),
        check_vma=False,
    )
```

```python
import functools

import jax
import jax.numpy as jnp
import ml_dtypes
import numpy as np
from jax import lax
from jax.experimental import pallas as pl
from jax.experimental.pallas import tpu as pltpu
from jax.sharding import PartitionSpec as P

P7 = 8
P3 = 4
MOVE_CAP = 2
HOLD7 = 12
LANE = 128

TIME_STEP = 0.002
ACTIVATION = 1.5
SIDE_SIGNS = (-1.0, 1.0, -1.0, 1.0, -1.0, 1.0)
OPPOSITE = (1, 0, 3, 2, 5, 4)
SEND_FACES = (0, 1, 4, 5)
missing_id = 1 << 30

f32 = jnp.float32
bf16 = jnp.bfloat16


def shifted(value, axis, steps):
    count = lax.axis_size(axis)
    pairs = [(source, (source + steps) % count) for source in range(count)]
    return lax.ppermute(value, axis, pairs)


def lobatto_points(number):
    return -np.cos(np.pi * np.arange(number) / (number - 1))


def lagrange_weights(points):
    weights = np.ones(points.shape[0])
    for row_id in range(points.shape[0]):
        for col_id in range(points.shape[0]):
            if col_id != row_id:
                weights[row_id] = weights[row_id] / (points[row_id] - points[col_id])
    return weights


def derivative_matrix(points):
    weights = lagrange_weights(points)
    number = points.shape[0]
    matrix = np.zeros((number, number))
    for row_id in range(number):
        for col_id in range(number):
            if col_id != row_id:
                matrix[row_id, col_id] = (
                    weights[col_id] / weights[row_id] / (points[row_id] - points[col_id])
                )
        matrix[row_id, row_id] = -np.sum(matrix[row_id])
    return matrix


def interpolation_matrix(source, target):
    matrix = np.ones((target.shape[0], source.shape[0]))
    for col_id in range(source.shape[0]):
        for other_id in range(source.shape[0]):
            if other_id != col_id:
                matrix[:, col_id] = (
                    matrix[:, col_id]
                    * (target - source[other_id])
                    / (source[col_id] - source[other_id])
                )
    return matrix


def spread_three(matrix, identity):
    return (
        np.kron(matrix, np.kron(identity, identity)),
        np.kron(identity, np.kron(matrix, identity)),
        np.kron(identity, np.kron(identity, matrix)),
    )


def face_nodes(extent):
    grid = np.arange(extent**3).reshape(extent, extent, extent)
    last = extent - 1
    pieces = (grid[0], grid[last], grid[:, 0], grid[:, last], grid[:, :, 0], grid[:, :, last])
    return [piece.reshape(-1) for piece in pieces]


def to_bf16(x):
    return np.asarray(np.asarray(x, np.float32).astype(ml_dtypes.bfloat16))


def split_parts(x):
    x = np.asarray(x, np.float32)
    hi = x.astype(ml_dtypes.bfloat16)
    rest = x - hi.astype(np.float32)
    mid = rest.astype(ml_dtypes.bfloat16)
    lo = (rest - mid.astype(np.float32)).astype(ml_dtypes.bfloat16)
    return np.stack([hi, mid, lo])


def make_tables():
    fine_points = lobatto_points(P7)
    coarse_points = lobatto_points(P3)
    fine_derivs = spread_three(derivative_matrix(fine_points), np.eye(P7))
    coarse_derivs = spread_three(derivative_matrix(coarse_points), np.eye(P3))
    downward = interpolation_matrix(fine_points, coarse_points)
    upward = interpolation_matrix(coarse_points, fine_points)
    d7t = np.stack([to_bf16(m.T) for m in fine_derivs])
    d3t = np.stack([to_bf16(m).T for m in coarse_derivs])
    lift_table = to_bf16(np.kron(upward, np.kron(upward, upward)))
    projection = np.asarray(np.kron(downward, np.kron(downward, downward)), np.float32)
    mortar_up = np.asarray(np.kron(upward, upward), np.float32)
    mortar_down = np.asarray(np.kron(downward, downward), np.float32)
    nodes7 = face_nodes(P7)
    nodes3 = face_nodes(P3)
    n7 = P7**3
    n3 = P3**3
    g7 = np.zeros((n7, 6 * LANE), np.float32)
    tm = np.zeros((n3, 6 * LANE), np.float32)
    mds = np.zeros((6 * LANE, n3), np.float32)
    for side in range(6):
        for q, node in enumerate(nodes7[side]):
            g7[node, side * LANE + q] = 1.0
        for k, node in enumerate(nodes3[side]):
            tm[node, side * LANE : side * LANE + P7 * P7] = mortar_up[:, k]
            mds[side * LANE : side * LANE + P7 * P7, node] = mortar_down[k, :]
    tables = {
        "d7t": to_bf16(d7t),
        "d3t": to_bf16(d3t),
        "lift": lift_table,
        "mortar_up": mortar_up,
        "g7": to_bf16(g7),
        "tm": split_parts(tm),
        "mds": split_parts(mds),
        "pjt": split_parts(projection.T),
        "nodes7": nodes7,
        "nodes3": nodes3,
    }
    return tables


def _dot(a, b):
    return jnp.dot(a, b, preferred_element_type=f32)


def _split(x):
    hi = x.astype(bf16)
    rest = x - hi.astype(f32)
    mid = rest.astype(bf16)
    lo = (rest - mid.astype(f32)).astype(bf16)
    return hi, mid, lo


def _exact_left(x, table):
    hi, mid, lo = _split(x)
    return (_dot(hi, table) + _dot(mid, table)) + _dot(lo, table)


def _dot_t(a, b):
    return lax.dot_general(a, b, (((1,), (1,)), ((), ())), preferred_element_type=f32)


def _exact_left_t(x, table):
    hi, mid, lo = _split(x)
    return (_dot_t(hi, table) + _dot_t(mid, table)) + _dot_t(lo, table)


def _exact_right(table, x):
    hi, mid, lo = _split(x)
    return (_dot(table, hi) + _dot(table, mid)) + _dot(table, lo)


def _full_t(x, parts_ref):
    xh, xm, xl = _split(x)
    bh = parts_ref[0]
    bm = parts_ref[1]
    bl = parts_ref[2]
    return _dot_t(xh, bh) + (_dot_t(xh, bm) + _dot_t(xm, bh)) + (
        _dot_t(xh, bl) + _dot_t(xm, bm) + _dot_t(xl, bh)
    )


class View:
    def __init__(self, ref, start, rows, width, lane0):
        self.ref = ref
        self.start = start
        self.rows = rows
        self.width = width
        self.lane0 = lane0

    def __getitem__(self, k):
        if k is Ellipsis:
            k = 0
        top = self.start + k * self.rows
        return self.ref[top : top + self.rows, self.lane0 : self.lane0 + self.width]


def table_layout(rows, local):
    n7 = P7**3
    n3 = P3**3
    wide = 6 * LANE
    base = n7 + 6 * n3
    side = 4 * LANE
    return {
        "g7": (0, n7, wide, 0),
        "tm": (n7, n3, wide, 0),
        "mdst": (n7 + 3 * n3, n3, wide, 0),
        "dx": (base, n7, n7, 0),
        "lift_t": (base + n7, n3, n7, 0),
        "pj": (base + n7 + n3, n3, n7, 0),
        "byz": (base, LANE, LANE, 5 * LANE),
        "bcast": (base, rows, local, side),
        "sel": (base + rows, 3 * local, rows, side),
        "fsel": (base + rows + 3 * local, rows, local, side),
        "d3t": (base + 2 * rows + 3 * local, n3, n3, side),
    }


def table_rows():
    return P7**3 + 6 * P3**3 + P7**3 + 4 * P3**3


def table_views(tab_ref, rows, local):
    return {
        name: View(tab_ref, start, count, width, lane0)
        for name, (start, count, width, lane0) in table_layout(rows, local).items()
    }


def _full(x, parts_ref):
    xh, xm, xl = _split(x)
    bh = parts_ref[0]
    bm = parts_ref[1]
    bl = parts_ref[2]
    return _dot(xh, bh) + (_dot(xh, bm) + _dot(xm, bh)) + (
        _dot(xh, bl) + _dot(xm, bm) + _dot(xl, bh)
    )


def _rate_source(values, pre, stc, bc, sel, local):
    picked = _exact_right(sel, values)
    v0 = picked[0:local]
    v1 = picked[local : 2 * local]
    v2 = picked[2 * local : 3 * local]
    rate = pre * jnp.exp(-ACTIVATION * jnp.exp(-v0)) * v1 * v2
    return stc * _exact_right(bc, rate)


def recv_block(recv, side):
    ref = recv[side]
    if side in (4, 5):
        rows = ref.shape[0] // 2
        top = 0 if side == 4 else rows
        return ref[top : top + rows, :]
    return ref[...]


def write_sends(out_refs, send):
    rows = send.shape[0]
    out_refs[0][...] = send[:, 0:LANE]
    out_refs[1][...] = send[:, LANE : 2 * LANE]
    out_refs[2][0:rows, :] = send[:, 5 * LANE : 6 * LANE]
    out_refs[2][rows : 2 * rows, :] = send[:, 4 * LANE : 5 * LANE]


def stage_kernel(coarse, second, project, sends, local, *refs):
    refs = list(refs)

    def take():
        return refs.pop(0)

    u_ref = take()
    c_ref = take() if coarse else None
    bu_ref = take() if second else None
    bc_ref = take() if (second and coarse) else None
    recv = {s: take() for s in SEND_FACES}
    pl_ref = take()
    pr_ref = take()
    v7_ref = take()
    m7_ref = take()
    pre_ref = take()
    stc_ref = take()
    views = table_views(take(), u_ref.shape[0], local)
    bc_tab = views["bcast"]
    sel_tab = views["sel"]
    g7_ref = views["g7"]
    d3_ref = views["d3t"]
    mds_ref = views["mdst"]
    tm_ref = views["tm"]
    pj_ref = views["pj"]
    if coarse:
        v3_ref = take()
        m3_ref = take()
    if coarse or project:
        sw_ref = take()
    last = coarse and not sends
    if last:
        sel_l_ref = take()
        sel_r_ref = take()
        cnt_l_ref = take()
        cnt_r_ref = take()
    res7_ref = take()
    res3_ref = take() if coarse else None
    out_u = take()
    out_c = take() if (coarse or project) else None
    out_send = [take() for _ in range(3)] if sends else None
    if last:
        pay_l_ref = take()
        pay_r_ref = take()

    pre = pre_ref[...]
    stc = stc_ref[...]
    bcast = bc_tab[...]
    sel = sel_tab[...]
    u = u_ref[...]
    trace7 = _dot(u.astype(bf16), g7_ref[...])
    if coarse:
        c = c_ref[...]
        trace3 = _full(c, tm_ref).astype(bf16).astype(f32)
        switched = sw_ref[...] > 0.5
        own = jnp.where(switched, trace3, trace7)
    else:
        own = trace7
    own_b = own.astype(bf16)
    near_blocks = []
    for side in range(6):
        other = OPPOSITE[side]
        block = own_b[:, other * LANE : (other + 1) * LANE]
        near = _dot(pl_ref[side], block)
        if side in SEND_FACES:
            k = SEND_FACES.index(side)
            near = near + _dot(pr_ref[k], recv_block(recv, side))
        near_blocks.append(near)
    near = jnp.concatenate(near_blocks, axis=1)

    result = res7_ref[...]
    jump = (P7 * (P7 - 1) / 2.0) * (m7_ref[...] * (trace7 - near))
    rate7 = result + _exact_left_t(jump, g7_ref[...])

    if coarse:
        result3 = res3_ref[...]
        jump3 = m3_ref[...] * (trace3 - near)
        rate3 = result3 + (P3 * (P3 - 1) / 2.0) * _full_t(jump3, mds_ref)

    if second:
        new_u = 0.5 * (bu_ref[...] + u + TIME_STEP * rate7)
    else:
        new_u = u + TIME_STEP * rate7
    out_u[...] = new_u
    new_c = None
    if coarse:
        if second:
            new_c = 0.5 * (bc_ref[...] + c + TIME_STEP * rate3)
        else:
            new_c = c + TIME_STEP * rate3
        if last:
            out_c[...] = jnp.where(sw_ref[...] > 0.5, new_c, 0.0)
            moved = sel_l_ref.shape[0]
            pay_l_ref[0:moved, :] = _exact_right(sel_l_ref[...], new_u)
            pay_r_ref[0:moved, :] = _exact_right(sel_r_ref[...], new_u)
            tail = (pay_l_ref.shape[0] - moved, pay_l_ref.shape[1])
            pay_l_ref[moved:, :] = jnp.broadcast_to(cnt_l_ref[0:1, 0:1], tail)
            pay_r_ref[moved:, :] = jnp.broadcast_to(cnt_r_ref[0:1, 0:1], tail)
        else:
            out_c[...] = new_c
    if project:
        new_c = _full_t(new_u, pj_ref)
        out_c[...] = new_c
    if sends:
        send7 = _dot(new_u.astype(bf16), g7_ref[...])
        if new_c is not None:
            send3 = _full(new_c, tm_ref).astype(bf16).astype(f32)
            send = jnp.where(sw_ref[...] > 0.5, send3, send7)
        else:
            send = send7
        write_sends(out_send, send.astype(bf16))


def _vmem():
    return pl.BlockSpec(memory_space=pltpu.VMEM)


def bulk_kernel(coarse, local, *refs):
    refs = list(refs)
    u_ref = refs.pop(0)
    c_ref = refs.pop(0) if coarse else None
    v7_ref, pre_ref, stc_ref = refs.pop(0), refs.pop(0), refs.pop(0)
    views = table_views(refs.pop(0), u_ref.shape[0], local)
    v3_ref = refs.pop(0) if coarse else None
    out7 = refs.pop(0)
    out3 = refs.pop(0) if coarse else None
    pre = pre_ref[...]
    stc = stc_ref[...]
    bcast = views["bcast"][...]
    sel = views["sel"][...]
    u = u_ref[...]
    fluxes = [(v7_ref[d].astype(f32) * u).astype(bf16) for d in range(3)]
    divergence = _dot(fluxes[0], views["dx"][0])
    by = views["byz"][0]
    bz = views["byz"][1]
    chunks = []
    for k in range(u.shape[1] // LANE):
        part = slice(k * LANE, (k + 1) * LANE)
        chunks.append(_dot(fluxes[1][:, part], by) + _dot(fluxes[2][:, part], bz))
    divergence = divergence + jnp.concatenate(chunks, axis=1)
    out7[...] = _rate_source(u, pre, stc, bcast, sel, local) - divergence
    if coarse:
        c = c_ref[...]
        div3 = None
        for d in range(3):
            flux3 = (v3_ref[d] * c).astype(bf16)
            term = _dot(flux3, views["d3t"][d])
            div3 = term if div3 is None else div3 + term
        out3[...] = _rate_source(c, pre, stc, bcast, sel, local) - div3


def run_bulk(coarse, local, inputs, out_shapes):
    return pl.pallas_call(
        functools.partial(bulk_kernel, coarse, local),
        out_shape=out_shapes,
        in_specs=[_vmem() for _ in inputs],
        out_specs=[_vmem() for _ in out_shapes],
        compiler_params=pltpu.CompilerParams(vmem_limit_bytes=24 * 1024 * 1024),
    )(*inputs)


def run_stage(flags, inputs, out_shapes):
    coarse, second, project, sends, local = flags
    kernel = functools.partial(stage_kernel, coarse, second, project, sends, local)
    return pl.pallas_call(
        kernel,
        out_shape=out_shapes,
        in_specs=[_vmem() for _ in inputs],
        out_specs=[_vmem() for _ in out_shapes],
        compiler_params=pltpu.CompilerParams(vmem_limit_bytes=48 * 1024 * 1024),
    )(*inputs)


def setup_kernel(local, fields, u_ref, vt_ref, packed_ref, tab_ref, v7_out, m7_out, v3_out, m3_out, pl_out, pr_out,
                 pre_out, stc_out, sw_out, hinfo_out, cnt_l_out, cnt_r_out, sel_l_out,
                 sel_r_out, *send_refs):
    rows = local * fields
    views = table_views(tab_ref, rows, local)
    lift_ref = views["lift_t"]
    g7_ref = views["g7"]
    tm_ref = views["tm"]
    fsel_ref = views["fsel"]
    bcast = views["bcast"][...]
    lanes = lax.broadcasted_iota(jnp.int32, (local, 6 * LANE), 1) // LANE
    sign = jnp.where(lanes % 2 == 0, -1.0, 1.0)
    fvg = []
    mvg = []
    for d in range(3):
        vt = vt_ref[d]
        fv = _dot(vt, lift_ref[...]).astype(bf16)
        v7_out[d] = _dot(bcast, fv).astype(bf16)
        v3_out[d] = _dot(bcast, vt)
        fvg.append(_dot(fv, g7_ref[...]))
        mvg.append((_dot(vt, tm_ref[0]) + _dot(vt, tm_ref[1])) + _dot(vt, tm_ref[2]))

    def by_block(parts):
        return jnp.where(lanes < 2, parts[0], jnp.where(lanes < 4, parts[1], parts[2]))

    m7 = jnp.minimum(sign * by_block(fvg), 0.0)
    m7_out[...] = _dot(bcast, m7.astype(bf16))
    m3 = jnp.minimum(sign * by_block(mvg), 0.0)
    m3_out[...] = _exact_right(bcast, m3)
    eye16 = jnp.where(
        lax.broadcasted_iota(jnp.int32, (local, LANE), 0)
        == lax.broadcasted_iota(jnp.int32, (local, LANE), 1), 1.0, 0.0
    ).astype(bf16)
    p_hi, p_mid, p_lo = _split(packed_ref[...])
    packed = (_dot_t(eye16, p_hi) + _dot_t(eye16, p_mid)) + _dot_t(eye16, p_lo)
    rep = _dot(bcast, packed.astype(bf16))
    row_f = (lax.broadcasted_iota(jnp.int32, (rows, 1), 0) % fields).astype(f32)
    cols = lax.broadcasted_iota(jnp.int32, (rows, rows), 1).astype(f32)
    for side in range(6):
        code = rep[:, side : side + 1]
        far = code >= local
        target = (code - jnp.where(far, float(local), 0.0)) * fields + row_f
        hit = cols == target
        pl_out[side] = jnp.where(hit & ~far, 1.0, 0.0).astype(bf16)
        if side in SEND_FACES:
            pr_out[SEND_FACES.index(side)] = jnp.where(hit & far, 1.0, 0.0).astype(bf16)
    sw_out[...] = rep[:, 6:7]
    curve_count = lax.axis_size("curve")
    curve_pos = lax.axis_index("curve")
    left_f = ((curve_pos + curve_count - 1) % curve_count).astype(f32)
    right_f = ((curve_pos + 1) % curve_count).astype(f32)
    first_f = jnp.where(curve_pos == 0, 1.0, 0.0)
    last_f = jnp.where(curve_pos == curve_count - 1, 1.0, 0.0)
    stay_sw = packed[:, 6:7] < 0.5
    go_left = (packed[:, 9:10] == left_f) & stay_sw
    go_right = (packed[:, 9:10] == right_f) & stay_sw
    stays = stay_sw & ~go_left & ~go_right
    lane16 = lax.broadcasted_iota(jnp.int32, (local, LANE), 1)
    marks = jnp.where(
        lane16 == 0, go_left.astype(f32),
        jnp.where(lane16 == 1, go_right.astype(f32), jnp.where(lane16 == 2, stays.astype(f32), 0.0)),
    ).astype(bf16)
    er = lax.broadcasted_iota(jnp.int32, (local, local), 0)
    ec = lax.broadcasted_iota(jnp.int32, (local, local), 1)
    before = _dot(jnp.where(ec < er, 1.0, 0.0).astype(bf16), marks)
    totals = _dot(jnp.ones((local, local), bf16), marks)
    info = jnp.where(lane16 < 3, marks.astype(f32), 0.0)
    for k in range(3):
        info = jnp.where(lane16 == 3 + k, before[:, k : k + 1], info)
    info = jnp.where(lane16 == 6, totals[:, 2:3], info)
    info = jnp.where(lane16 == 7, first_f, info)
    info = jnp.where(lane16 == 8, last_f, info)
    hinfo = _dot(bcast, info.astype(bf16))
    hinfo_out[...] = hinfo
    cnt_l_out[...] = jnp.broadcast_to(totals[0:1, 0:1], cnt_l_out.shape)
    cnt_r_out[...] = jnp.broadcast_to(totals[0:1, 1:2], cnt_r_out.shape)
    rf = lax.broadcasted_iota(jnp.int32, (rows, LANE), 0) % fields
    cc = lax.broadcasted_iota(jnp.int32, (rows, LANE), 1)
    eye = jnp.where(
        lax.broadcasted_iota(jnp.int32, (MOVE_CAP * fields, LANE), 0)
        == lax.broadcasted_iota(jnp.int32, (MOVE_CAP * fields, LANE), 1), 1.0, 0.0
    ).astype(bf16)
    for mark_lane, rank_lane, out in ((0, 3, sel_l_out), (1, 4, sel_r_out)):
        hit = (
            (hinfo[:, mark_lane : mark_lane + 1] > 0.5)
            & (hinfo[:, rank_lane : rank_lane + 1] == (cc // fields).astype(f32))
            & (rf == cc % fields)
            & (cc < MOVE_CAP * fields)
        )
        out[...] = _dot_t(eye, jnp.where(hit, 1.0, 0.0).astype(bf16)).astype(bf16)
    pre_out[...] = packed[:, 7:8]
    stc_out[...] = _exact_right(fsel_ref[...], packed)[:, 8:9]
    write_sends(send_refs, _dot(u_ref[...].astype(bf16), g7_ref[...]).astype(bf16))


def final_kernel(fields, hold, home_ref, from_l_ref, from_r_ref, hinfo_ref, out_ref):
    hinfo = hinfo_ref[...]
    moved = MOVE_CAP * fields
    n_l = from_l_ref[moved : moved + 1, 0:1]
    n_r = from_r_ref[moved : moved + 1, 0:1]
    n_h = hinfo[0:1, 6:7]
    first = hinfo[0:1, 7:8] > 0.5
    final = hinfo[0:1, 8:9] > 0.5
    off_l = jnp.where(first, n_h + n_r, jnp.where(final, n_r, 0.0))
    off_h = jnp.where(first, 0.0, jnp.where(final, n_r + n_l, n_l))
    off_r = jnp.where(first, n_h, jnp.where(final, 0.0, n_l + n_h))
    width = hold * fields
    eye = jnp.where(
        lax.broadcasted_iota(jnp.int32, (width, LANE), 0)
        == lax.broadcasted_iota(jnp.int32, (width, LANE), 1), 1.0, 0.0
    ).astype(bf16)

    def gather(values, valid, pos):
        count = values.shape[0]
        rf = lax.broadcasted_iota(jnp.int32, (count, LANE), 0) % fields
        cc = lax.broadcasted_iota(jnp.int32, (count, LANE), 1)
        hit = valid & (pos == (cc // fields).astype(f32)) & (rf == cc % fields) & (cc < width)
        pick = _dot_t(eye, jnp.where(hit, 1.0, 0.0).astype(bf16)).astype(bf16)
        return _exact_right(pick, values)

    total = gather(home_ref[...], hinfo[:, 2:3] > 0.5, off_h + hinfo[:, 5:6])
    slot = (lax.broadcasted_iota(jnp.int32, (moved, 1), 0) // fields).astype(f32)
    total = total + gather(from_l_ref[0:moved, :], slot < n_l, off_l + slot)
    total = total + gather(from_r_ref[0:moved, :], slot < n_r, off_r + slot)
    out_ref[...] = total


def setup_entry(local, fields, n_in, n_out, *refs):
    sources = refs[:n_in]
    outs = refs[n_in : n_in + n_out]
    n_tab = 1
    n_own = n_in - n_tab
    buffers = refs[n_in + n_out : n_in + n_out + n_own]
    sems = refs[n_in + n_out + n_own]
    targets = list(buffers) + list(outs[n_out - n_tab :])
    copies = [
        pltpu.make_async_copy(sources[i], targets[i], sems.at[i]) for i in range(n_in)
    ]
    for copy in copies:
        copy.start()
    for copy in copies:
        copy.wait()
    setup_kernel(local, fields, *targets, *outs[: n_out - n_tab])


def per_device(state, velocity, pre_exp, stoich, neighbours, switch, new_owner):
    tab = make_tables()
    local_count = state.shape[0]
    field_count = state.shape[1]
    rows = local_count * field_count
    curve_count = lax.axis_size("curve")
    curve_pos = lax.axis_index("curve")
    device_id = lax.axis_index("slab") * curve_count + curve_pos
    first_global = device_id * local_count
    positions = jnp.arange(local_count, dtype=jnp.int32)

    near_device = neighbours // local_count
    near_local = neighbours - near_device * local_count
    remote = near_device != device_id
    codes = (near_local + local_count * remote.astype(jnp.int32)).astype(f32)
    left_pos = (curve_pos + curve_count - 1) % curve_count
    right_pos = (curve_pos + 1) % curve_count
    sto_col = jnp.pad(stoich, (0, local_count - field_count))
    packed_t = jnp.concatenate(
        [
            jnp.transpose(codes),
            jnp.stack([switch.astype(f32), pre_exp, sto_col, new_owner.astype(f32)]),
        ]
    )
    packed = jnp.pad(packed_t, ((0, local_count - 10), (0, LANE - local_count)))
    fsel_np = np.arange(rows)[:, None] % field_count == np.arange(local_count)[None, :]
    vt = jnp.transpose(velocity, (0, 2, 1))
    row_elem = np.arange(rows) // field_count
    bcast_np = row_elem[:, None] == np.arange(local_count)[None, :]
    pick_rows = (np.arange(3)[:, None] + field_count * np.arange(local_count)[None, :]).reshape(-1)
    sel_np = pick_rows[:, None] == np.arange(rows)[None, :]
    n7 = P7**3
    n3 = P3**3
    layout = table_layout(rows, local_count)
    table_np = np.zeros((table_rows(), 6 * LANE), np.float32)
    for d in (1, 2):
        block = tab["d7t"][d][:LANE, :LANE].astype(np.float32)
        assert np.array_equal(
            tab["d7t"][d].astype(np.float32), np.kron(np.eye(n7 // LANE), block)
        )
    pieces = {
        "g7": tab["g7"][None],
        "tm": tab["tm"],
        "mdst": np.transpose(tab["mds"], (0, 2, 1)),
        "dx": tab["d7t"][0:1],
        "byz": np.stack([tab["d7t"][1][:LANE, :LANE], tab["d7t"][2][:LANE, :LANE]]),
        "lift_t": tab["lift"].T[None],
        "pj": np.transpose(tab["pjt"], (0, 2, 1)),
        "bcast": bcast_np[None],
        "sel": sel_np[None],
        "fsel": fsel_np[None],
        "d3t": tab["d3t"],
    }
    filled = np.zeros(table_np.shape, bool)
    for name, (start, count, width, lane0) in layout.items():
        parts = np.asarray(pieces[name], np.float32)
        for k in range(parts.shape[0]):
            window = (slice(start + k * count, start + (k + 1) * count), slice(lane0, lane0 + width))
            assert not filled[window].any()
            filled[window] = True
            table_np[window] = parts[k]
    table = jnp.asarray(to_bf16(table_np))

    send_shape = jax.ShapeDtypeStruct((rows, LANE), bf16)
    sends_shape = [send_shape, send_shape, jax.ShapeDtypeStruct((2 * rows, LANE), bf16)]
    u_shape = jax.ShapeDtypeStruct((rows, P7**3), f32)
    c_shape = jax.ShapeDtypeStruct((rows, P3**3), f32)

    def exchange(sends):
        face0, face1, faces_z = sends
        from_prev = shifted(faces_z, "slab", 1)
        if lax.axis_size("slab") == 2:
            from_next = from_prev
        else:
            from_next = shifted(faces_z, "slab", -1)
        return [shifted(face1, "curve", 1), shifted(face0, "curve", -1), from_prev, from_next]

    setup_out = [
        jax.ShapeDtypeStruct((3, rows, P7**3), bf16),
        jax.ShapeDtypeStruct((rows, 6 * LANE), f32),
        jax.ShapeDtypeStruct((3, rows, P3**3), f32),
        jax.ShapeDtypeStruct((rows, 6 * LANE), f32),
        jax.ShapeDtypeStruct((6, rows, rows), bf16),
        jax.ShapeDtypeStruct((len(SEND_FACES), rows, rows), bf16),
        jax.ShapeDtypeStruct((local_count, 1), f32),
        jax.ShapeDtypeStruct((rows, 1), f32),
        jax.ShapeDtypeStruct((rows, 1), f32),
        jax.ShapeDtypeStruct((rows, LANE), f32),
        jax.ShapeDtypeStruct((8, LANE), f32),
        jax.ShapeDtypeStruct((8, LANE), f32),
        jax.ShapeDtypeStruct((MOVE_CAP * field_count, rows), bf16),
        jax.ShapeDtypeStruct((MOVE_CAP * field_count, rows), bf16),
    ] + sends_shape
    setup_out = setup_out + [jax.ShapeDtypeStruct(table.shape, table.dtype)]
    u0 = state.reshape(rows, P7**3)
    setup_in = [u0, vt, packed, table]
    res = pl.pallas_call(
        functools.partial(setup_entry, local_count, field_count, len(setup_in), len(setup_out)),
        out_shape=setup_out,
        in_specs=[pl.BlockSpec(memory_space=pltpu.HBM) for _ in setup_in],
        out_specs=[_vmem() for _ in setup_out],
        scratch_shapes=[pltpu.VMEM(x.shape, x.dtype) for x in setup_in[:3]]
        + [pltpu.SemaphoreType.DMA((len(setup_in),))],
        compiler_params=pltpu.CompilerParams(vmem_limit_bytes=24 * 1024 * 1024),
    )(*setup_in)
    v7, m7, v3, m3, p_local, p_remote, pre, stc, sw = res[:9]
    hinfo, cnt_l, cnt_r, sel_l, sel_r = res[9:14]
    sends = res[14:17]
    table = res[17]
    common = [p_local, p_remote, v7, m7, pre, stc, table]
    recv = exchange(sends)
    bulk_tabs = [v7, pre, stc, table]
    (bulk7,) = run_bulk(False, local_count, [u0] + bulk_tabs, [u_shape])
    res = run_stage(
        (False, False, False, True, local_count),
        [u0] + recv + common + [bulk7],
        [u_shape] + sends_shape,
    )
    first, sends = res[0], res[1:]
    recv = exchange(sends)
    (bulk7,) = run_bulk(False, local_count, [first] + bulk_tabs, [u_shape])
    res = run_stage(
        (False, True, True, True, local_count),
        [first, u0] + recv + common + [sw, bulk7],
        [u_shape, c_shape] + sends_shape,
    )
    after, coarse, sends = res[0], res[1], res[2:]
    recv = exchange(sends)
    mixed_tail = [v3, m3, sw]
    bulk7, bulk3 = run_bulk(True, local_count, [after, coarse] + bulk_tabs + [v3], [u_shape, c_shape])
    res = run_stage(
        (True, False, False, True, local_count),
        [after, coarse] + recv + common + mixed_tail + [bulk7, bulk3],
        [u_shape, c_shape] + sends_shape,
    )
    first7, first3, sends = res[0], res[1], res[2:]
    recv = exchange(sends)
    pay_shape = jax.ShapeDtypeStruct((MOVE_CAP * field_count + 8, P7**3), f32)
    bulk7, bulk3 = run_bulk(True, local_count, [first7, first3] + bulk_tabs + [v3], [u_shape, c_shape])
    res = run_stage(
        (True, True, False, False, local_count),
        [first7, first3, after, coarse] + recv + common + mixed_tail
        + [sel_l, sel_r, cnt_l, cnt_r, bulk7, bulk3],
        [u_shape, c_shape, pay_shape, pay_shape],
    )
    final7, final3, pay_l, pay_r = res
    from_right = shifted(pay_l, "curve", -1)
    from_left = shifted(pay_r, "curve", 1)
    held = pl.pallas_call(
        functools.partial(final_kernel, field_count, HOLD7),
        out_shape=jax.ShapeDtypeStruct((HOLD7 * field_count, P7**3), f32),
        in_specs=[_vmem() for _ in range(4)],
        out_specs=_vmem(),
    )(final7, from_left, from_right, hinfo)
    state7_out = held.reshape(HOLD7, field_count, P7**3)
    state3_out = final3.reshape(local_count, field_count * P3**3)
    return (state7_out, state3_out)


def solution(mesh):
    return jax.shard_map(
        per_device,
        mesh=mesh,
        in_specs=(
            P(("slab", "curve"), None, None),
            P(None, None, ("slab", "curve")),
            P(("slab", "curve")),
            P(),
            P(("slab", "curve"), None),
            P(("slab", "curve")),
            P(("slab", "curve")),
        ),
        out_specs=(P(("slab", "curve"), None, None), P(("slab", "curve"), None)),
        check_vma=False,
    )
```

```python
import functools

import jax
import jax.numpy as jnp
import ml_dtypes
import numpy as np
from jax import lax
from jax.experimental import pallas as pl
from jax.experimental.pallas import tpu as pltpu
from jax.sharding import PartitionSpec as P

P7 = 8
P3 = 4
MOVE_CAP = 2
HOLD7 = 12
LANE = 128

TIME_STEP = 0.002
ACTIVATION = 1.5
SIDE_SIGNS = (-1.0, 1.0, -1.0, 1.0, -1.0, 1.0)
OPPOSITE = (1, 0, 3, 2, 5, 4)
SEND_FACES = (0, 1, 4, 5)
missing_id = 1 << 30

f32 = jnp.float32
bf16 = jnp.bfloat16


def shifted(value, axis, steps):
    count = lax.axis_size(axis)
    pairs = [(source, (source + steps) % count) for source in range(count)]
    return lax.ppermute(value, axis, pairs)


def lobatto_points(number):
    return -np.cos(np.pi * np.arange(number) / (number - 1))


def lagrange_weights(points):
    weights = np.ones(points.shape[0])
    for row_id in range(points.shape[0]):
        for col_id in range(points.shape[0]):
            if col_id != row_id:
                weights[row_id] = weights[row_id] / (points[row_id] - points[col_id])
    return weights


def derivative_matrix(points):
    weights = lagrange_weights(points)
    number = points.shape[0]
    matrix = np.zeros((number, number))
    for row_id in range(number):
        for col_id in range(number):
            if col_id != row_id:
                matrix[row_id, col_id] = (
                    weights[col_id] / weights[row_id] / (points[row_id] - points[col_id])
                )
        matrix[row_id, row_id] = -np.sum(matrix[row_id])
    return matrix


def interpolation_matrix(source, target):
    matrix = np.ones((target.shape[0], source.shape[0]))
    for col_id in range(source.shape[0]):
        for other_id in range(source.shape[0]):
            if other_id != col_id:
                matrix[:, col_id] = (
                    matrix[:, col_id]
                    * (target - source[other_id])
                    / (source[col_id] - source[other_id])
                )
    return matrix


def spread_three(matrix, identity):
    return (
        np.kron(matrix, np.kron(identity, identity)),
        np.kron(identity, np.kron(matrix, identity)),
        np.kron(identity, np.kron(identity, matrix)),
    )


def face_nodes(extent):
    grid = np.arange(extent**3).reshape(extent, extent, extent)
    last = extent - 1
    pieces = (grid[0], grid[last], grid[:, 0], grid[:, last], grid[:, :, 0], grid[:, :, last])
    return [piece.reshape(-1) for piece in pieces]


def to_bf16(x):
    return np.asarray(np.asarray(x, np.float32).astype(ml_dtypes.bfloat16))


def split_parts(x):
    x = np.asarray(x, np.float32)
    hi = x.astype(ml_dtypes.bfloat16)
    rest = x - hi.astype(np.float32)
    mid = rest.astype(ml_dtypes.bfloat16)
    lo = (rest - mid.astype(np.float32)).astype(ml_dtypes.bfloat16)
    return np.stack([hi, mid, lo])


def make_tables():
    fine_points = lobatto_points(P7)
    coarse_points = lobatto_points(P3)
    fine_derivs = spread_three(derivative_matrix(fine_points), np.eye(P7))
    coarse_derivs = spread_three(derivative_matrix(coarse_points), np.eye(P3))
    downward = interpolation_matrix(fine_points, coarse_points)
    upward = interpolation_matrix(coarse_points, fine_points)
    d7t = np.stack([to_bf16(m.T) for m in fine_derivs])
    d3t = np.stack([to_bf16(m).T for m in coarse_derivs])
    lift_table = to_bf16(np.kron(upward, np.kron(upward, upward)))
    projection = np.asarray(np.kron(downward, np.kron(downward, downward)), np.float32)
    mortar_up = np.asarray(np.kron(upward, upward), np.float32)
    mortar_down = np.asarray(np.kron(downward, downward), np.float32)
    nodes7 = face_nodes(P7)
    nodes3 = face_nodes(P3)
    n7 = P7**3
    n3 = P3**3
    g7 = np.zeros((n7, 6 * LANE), np.float32)
    tm = np.zeros((n3, 6 * LANE), np.float32)
    mds = np.zeros((6 * LANE, n3), np.float32)
    for side in range(6):
        for q, node in enumerate(nodes7[side]):
            g7[node, side * LANE + q] = 1.0
        for k, node in enumerate(nodes3[side]):
            tm[node, side * LANE : side * LANE + P7 * P7] = mortar_up[:, k]
            mds[side * LANE : side * LANE + P7 * P7, node] = mortar_down[k, :]
    tables = {
        "d7t": to_bf16(d7t),
        "d3t": to_bf16(d3t),
        "lift": lift_table,
        "mortar_up": mortar_up,
        "g7": to_bf16(g7),
        "tm": split_parts(tm),
        "mds": split_parts(mds),
        "pjt": split_parts(projection.T),
        "nodes7": nodes7,
        "nodes3": nodes3,
    }
    return tables


def _dot(a, b):
    return jnp.dot(a, b, preferred_element_type=f32)


def _split(x):
    hi = x.astype(bf16)
    rest = x - hi.astype(f32)
    mid = rest.astype(bf16)
    lo = (rest - mid.astype(f32)).astype(bf16)
    return hi, mid, lo


def _exact_left(x, table):
    hi, mid, lo = _split(x)
    return (_dot(hi, table) + _dot(mid, table)) + _dot(lo, table)


def _dot_t(a, b):
    return lax.dot_general(a, b, (((1,), (1,)), ((), ())), preferred_element_type=f32)


def _exact_left_t(x, table):
    hi, mid, lo = _split(x)
    return (_dot_t(hi, table) + _dot_t(mid, table)) + _dot_t(lo, table)


def _exact_right(table, x):
    hi, mid, lo = _split(x)
    return (_dot(table, hi) + _dot(table, mid)) + _dot(table, lo)


def _full_t(x, parts_ref):
    xh, xm, xl = _split(x)
    bh = parts_ref[0]
    bm = parts_ref[1]
    bl = parts_ref[2]
    return _dot_t(xh, bh) + (_dot_t(xh, bm) + _dot_t(xm, bh)) + (
        _dot_t(xh, bl) + _dot_t(xm, bm) + _dot_t(xl, bh)
    )


class View:
    def __init__(self, ref, start, rows, width, lane0):
        self.ref = ref
        self.start = start
        self.rows = rows
        self.width = width
        self.lane0 = lane0

    def __getitem__(self, k):
        if k is Ellipsis:
            k = 0
        top = self.start + k * self.rows
        return self.ref[top : top + self.rows, self.lane0 : self.lane0 + self.width]


def table_layout(rows, local):
    n7 = P7**3
    n3 = P3**3
    wide = 6 * LANE
    base = n7 + 6 * n3
    side = 4 * LANE
    return {
        "g7": (0, n7, wide, 0),
        "tm": (n7, n3, wide, 0),
        "mdst": (n7 + 3 * n3, n3, wide, 0),
        "dx": (base, n7, n7, 0),
        "lift_t": (base + n7, n3, n7, 0),
        "pj": (base + n7 + n3, n3, n7, 0),
        "byz": (base, LANE, LANE, 5 * LANE),
        "bcast": (base, rows, local, side),
        "sel": (base + rows, 3 * local, rows, side),
        "fsel": (base + rows + 3 * local, rows, local, side),
        "d3t": (base + 2 * rows + 3 * local, n3, n3, side),
    }


def table_rows():
    return P7**3 + 6 * P3**3 + P7**3 + 4 * P3**3


def table_views(tab_ref, rows, local):
    return {
        name: View(tab_ref, start, count, width, lane0)
        for name, (start, count, width, lane0) in table_layout(rows, local).items()
    }


def _full(x, parts_ref):
    xh, xm, xl = _split(x)
    bh = parts_ref[0]
    bm = parts_ref[1]
    bl = parts_ref[2]
    return _dot(xh, bh) + (_dot(xh, bm) + _dot(xm, bh)) + (
        _dot(xh, bl) + _dot(xm, bm) + _dot(xl, bh)
    )


def _rate_source(values, pre, stc, bc, sel, local):
    picked = _exact_right(sel, values)
    v0 = picked[0:local]
    v1 = picked[local : 2 * local]
    v2 = picked[2 * local : 3 * local]
    rate = pre * jnp.exp(-ACTIVATION * jnp.exp(-v0)) * v1 * v2
    return stc * _exact_right(bc, rate)


def recv_block(recv, side):
    ref = recv[side]
    if side in (4, 5):
        rows = ref.shape[0] // 2
        top = 0 if side == 4 else rows
        return ref[top : top + rows, :]
    return ref[...]


def write_sends(out_refs, send):
    rows = send.shape[0]
    out_refs[0][...] = send[:, 0:LANE]
    out_refs[1][...] = send[:, LANE : 2 * LANE]
    out_refs[2][0:rows, :] = send[:, 5 * LANE : 6 * LANE]
    out_refs[2][rows : 2 * rows, :] = send[:, 4 * LANE : 5 * LANE]


def stage_kernel(coarse, second, project, sends, local, *refs):
    refs = list(refs)

    def take():
        return refs.pop(0)

    u_ref = take()
    c_ref = take() if coarse else None
    bu_ref = take() if second else None
    bc_ref = take() if (second and coarse) else None
    recv = {s: take() for s in SEND_FACES}
    pl_ref = take()
    pr_ref = take()
    v7_ref = take()
    m7_ref = take()
    pre_ref = take()
    stc_ref = take()
    views = table_views(take(), u_ref.shape[0], local)
    bc_tab = views["bcast"]
    sel_tab = views["sel"]
    g7_ref = views["g7"]
    d3_ref = views["d3t"]
    mds_ref = views["mdst"]
    tm_ref = views["tm"]
    pj_ref = views["pj"]
    if coarse:
        v3_ref = take()
        m3_ref = take()
    if coarse or project:
        sw_ref = take()
    last = coarse and not sends
    if last:
        sel_l_ref = take()
        sel_r_ref = take()
        cnt_l_ref = take()
        cnt_r_ref = take()
    res7_ref = take()
    res3_ref = take() if coarse else None
    out_u = take()
    out_c = take() if (coarse or project) else None
    out_send = [take() for _ in range(3)] if sends else None
    if last:
        pay_l_ref = take()
        pay_r_ref = take()

    pre = pre_ref[...]
    stc = stc_ref[...]
    bcast = bc_tab[...]
    sel = sel_tab[...]
    u = u_ref[...]
    trace7 = _dot(u.astype(bf16), g7_ref[...])
    if coarse:
        c = c_ref[...]
        trace3 = _full(c, tm_ref).astype(bf16).astype(f32)
        switched = sw_ref[...] > 0.5
        own = jnp.where(switched, trace3, trace7)
    else:
        own = trace7
    own_b = own.astype(bf16)
    near_blocks = []
    for side in range(6):
        other = OPPOSITE[side]
        block = own_b[:, other * LANE : (other + 1) * LANE]
        near = _dot(pl_ref[side], block)
        if side in SEND_FACES:
            k = SEND_FACES.index(side)
            near = near + _dot(pr_ref[k], recv_block(recv, side))
        near_blocks.append(near)
    near = jnp.concatenate(near_blocks, axis=1)

    result = res7_ref[...]
    jump = (P7 * (P7 - 1) / 2.0) * (m7_ref[...] * (trace7 - near))
    rate7 = result + _exact_left_t(jump, g7_ref[...])

    if coarse:
        result3 = res3_ref[...]
        jump3 = m3_ref[...] * (trace3 - near)
        rate3 = result3 + (P3 * (P3 - 1) / 2.0) * _full_t(jump3, mds_ref)

    if second:
        new_u = 0.5 * (bu_ref[...] + u + TIME_STEP * rate7)
    else:
        new_u = u + TIME_STEP * rate7
    out_u[...] = new_u
    new_c = None
    if coarse:
        if second:
            new_c = 0.5 * (bc_ref[...] + c + TIME_STEP * rate3)
        else:
            new_c = c + TIME_STEP * rate3
        if last:
            out_c[...] = jnp.where(sw_ref[...] > 0.5, new_c, 0.0)
            moved = sel_l_ref.shape[0]
            pay_l_ref[0:moved, :] = _exact_right(sel_l_ref[...], new_u)
            pay_r_ref[0:moved, :] = _exact_right(sel_r_ref[...], new_u)
            tail = (pay_l_ref.shape[0] - moved, pay_l_ref.shape[1])
            pay_l_ref[moved:, :] = jnp.broadcast_to(cnt_l_ref[0:1, 0:1], tail)
            pay_r_ref[moved:, :] = jnp.broadcast_to(cnt_r_ref[0:1, 0:1], tail)
        else:
            out_c[...] = new_c
    if project:
        new_c = _full_t(new_u, pj_ref)
        out_c[...] = new_c
    if sends:
        send7 = _dot(new_u.astype(bf16), g7_ref[...])
        if new_c is not None:
            send3 = _full(new_c, tm_ref).astype(bf16).astype(f32)
            send = jnp.where(sw_ref[...] > 0.5, send3, send7)
        else:
            send = send7
        write_sends(out_send, send.astype(bf16))


def _vmem():
    return pl.BlockSpec(memory_space=pltpu.VMEM)


def bulk_kernel(coarse, local, *refs):
    refs = list(refs)
    u_ref = refs.pop(0)
    c_ref = refs.pop(0) if coarse else None
    v7_ref, pre_ref, stc_ref = refs.pop(0), refs.pop(0), refs.pop(0)
    views = table_views(refs.pop(0), u_ref.shape[0], local)
    v3_ref = refs.pop(0) if coarse else None
    out7 = refs.pop(0)
    out3 = refs.pop(0) if coarse else None
    pre = pre_ref[...]
    stc = stc_ref[...]
    bcast = views["bcast"][...]
    sel = views["sel"][...]
    u = u_ref[...]
    fluxes = [(v7_ref[d].astype(f32) * u).astype(bf16) for d in range(3)]
    divergence = _dot(fluxes[0], views["dx"][0])
    by = views["byz"][0]
    bz = views["byz"][1]
    chunks = []
    for k in range(u.shape[1] // LANE):
        part = slice(k * LANE, (k + 1) * LANE)
        chunks.append(_dot(fluxes[1][:, part], by) + _dot(fluxes[2][:, part], bz))
    divergence = divergence + jnp.concatenate(chunks, axis=1)
    out7[...] = _rate_source(u, pre, stc, bcast, sel, local) - divergence
    if coarse:
        c = c_ref[...]
        div3 = None
        for d in range(3):
            flux3 = (v3_ref[d] * c).astype(bf16)
            term = _dot(flux3, views["d3t"][d])
            div3 = term if div3 is None else div3 + term
        out3[...] = _rate_source(c, pre, stc, bcast, sel, local) - div3


def run_bulk(coarse, local, inputs, out_shapes):
    return pl.pallas_call(
        functools.partial(bulk_kernel, coarse, local),
        out_shape=out_shapes,
        in_specs=[_vmem() for _ in inputs],
        out_specs=[_vmem() for _ in out_shapes],
        compiler_params=pltpu.CompilerParams(vmem_limit_bytes=24 * 1024 * 1024),
    )(*inputs)


def run_stage(flags, inputs, out_shapes):
    coarse, second, project, sends, local = flags
    kernel = functools.partial(stage_kernel, coarse, second, project, sends, local)
    return pl.pallas_call(
        kernel,
        out_shape=out_shapes,
        in_specs=[_vmem() for _ in inputs],
        out_specs=[_vmem() for _ in out_shapes],
        compiler_params=pltpu.CompilerParams(vmem_limit_bytes=48 * 1024 * 1024),
    )(*inputs)


def setup_kernel(local, fields, u_ref, vt_ref, packed_ref, tab_ref, v7_out, m7_out, v3_out, m3_out, pl_out, pr_out,
                 pre_out, stc_out, sw_out, hinfo_out, cnt_l_out, cnt_r_out, sel_l_out,
                 sel_r_out, *send_refs):
    rows = local * fields
    views = table_views(tab_ref, rows, local)
    lift_ref = views["lift_t"]
    g7_ref = views["g7"]
    tm_ref = views["tm"]
    fsel_ref = views["fsel"]
    bcast = views["bcast"][...]
    lanes = lax.broadcasted_iota(jnp.int32, (local, 6 * LANE), 1) // LANE
    sign = jnp.where(lanes % 2 == 0, -1.0, 1.0)
    fvg = []
    mvg = []
    for d in range(3):
        vt = vt_ref[d]
        fv = _dot(vt, lift_ref[...]).astype(bf16)
        v7_out[d] = _dot(bcast, fv).astype(bf16)
        v3_out[d] = _dot(bcast, vt)
        fvg.append(_dot(fv, g7_ref[...]))
        mvg.append((_dot(vt, tm_ref[0]) + _dot(vt, tm_ref[1])) + _dot(vt, tm_ref[2]))

    def by_block(parts):
        return jnp.where(lanes < 2, parts[0], jnp.where(lanes < 4, parts[1], parts[2]))

    m7 = jnp.minimum(sign * by_block(fvg), 0.0)
    m7_out[...] = _dot(bcast, m7.astype(bf16))
    m3 = jnp.minimum(sign * by_block(mvg), 0.0)
    m3_out[...] = _exact_right(bcast, m3)
    eye16 = jnp.where(
        lax.broadcasted_iota(jnp.int32, (local, LANE), 0)
        == lax.broadcasted_iota(jnp.int32, (local, LANE), 1), 1.0, 0.0
    ).astype(bf16)
    p_hi, p_mid, p_lo = _split(packed_ref[...])
    packed = (_dot_t(eye16, p_hi) + _dot_t(eye16, p_mid)) + _dot_t(eye16, p_lo)
    rep = _dot(bcast, packed.astype(bf16))
    row_f = (lax.broadcasted_iota(jnp.int32, (rows, 1), 0) % fields).astype(f32)
    cols = lax.broadcasted_iota(jnp.int32, (rows, rows), 1).astype(f32)
    for side in range(6):
        code = rep[:, side : side + 1]
        far = code >= local
        target = (code - jnp.where(far, float(local), 0.0)) * fields + row_f
        hit = cols == target
        pl_out[side] = jnp.where(hit & ~far, 1.0, 0.0).astype(bf16)
        if side in SEND_FACES:
            pr_out[SEND_FACES.index(side)] = jnp.where(hit & far, 1.0, 0.0).astype(bf16)
    sw_out[...] = rep[:, 6:7]
    curve_count = lax.axis_size("curve")
    curve_pos = lax.axis_index("curve")
    left_f = ((curve_pos + curve_count - 1) % curve_count).astype(f32)
    right_f = ((curve_pos + 1) % curve_count).astype(f32)
    first_f = jnp.where(curve_pos == 0, 1.0, 0.0)
    last_f = jnp.where(curve_pos == curve_count - 1, 1.0, 0.0)
    stay_sw = packed[:, 6:7] < 0.5
    go_left = (packed[:, 9:10] == left_f) & stay_sw
    go_right = (packed[:, 9:10] == right_f) & stay_sw
    stays = stay_sw & ~go_left & ~go_right
    lane16 = lax.broadcasted_iota(jnp.int32, (local, LANE), 1)
    marks = jnp.where(
        lane16 == 0, go_left.astype(f32),
        jnp.where(lane16 == 1, go_right.astype(f32), jnp.where(lane16 == 2, stays.astype(f32), 0.0)),
    ).astype(bf16)
    er = lax.broadcasted_iota(jnp.int32, (local, local), 0)
    ec = lax.broadcasted_iota(jnp.int32, (local, local), 1)
    before = _dot(jnp.where(ec < er, 1.0, 0.0).astype(bf16), marks)
    totals = _dot(jnp.ones((local, local), bf16), marks)
    info = jnp.where(lane16 < 3, marks.astype(f32), 0.0)
    for k in range(3):
        info = jnp.where(lane16 == 3 + k, before[:, k : k + 1], info)
    info = jnp.where(lane16 == 6, totals[:, 2:3], info)
    info = jnp.where(lane16 == 7, first_f, info)
    info = jnp.where(lane16 == 8, last_f, info)
    hinfo = _dot(bcast, info.astype(bf16))
    hinfo_out[...] = hinfo
    cnt_l_out[...] = jnp.broadcast_to(totals[0:1, 0:1], cnt_l_out.shape)
    cnt_r_out[...] = jnp.broadcast_to(totals[0:1, 1:2], cnt_r_out.shape)
    rf = lax.broadcasted_iota(jnp.int32, (rows, LANE), 0) % fields
    cc = lax.broadcasted_iota(jnp.int32, (rows, LANE), 1)
    eye = jnp.where(
        lax.broadcasted_iota(jnp.int32, (MOVE_CAP * fields, LANE), 0)
        == lax.broadcasted_iota(jnp.int32, (MOVE_CAP * fields, LANE), 1), 1.0, 0.0
    ).astype(bf16)
    for mark_lane, rank_lane, out in ((0, 3, sel_l_out), (1, 4, sel_r_out)):
        hit = (
            (hinfo[:, mark_lane : mark_lane + 1] > 0.5)
            & (hinfo[:, rank_lane : rank_lane + 1] == (cc // fields).astype(f32))
            & (rf == cc % fields)
            & (cc < MOVE_CAP * fields)
        )
        out[...] = _dot_t(eye, jnp.where(hit, 1.0, 0.0).astype(bf16)).astype(bf16)
    pre_out[...] = packed[:, 7:8]
    stc_out[...] = _exact_right(fsel_ref[...], packed)[:, 8:9]
    write_sends(send_refs, _dot(u_ref[...].astype(bf16), g7_ref[...]).astype(bf16))


def final_kernel(fields, hold, home_ref, from_l_ref, from_r_ref, hinfo_ref, out_ref):
    hinfo = hinfo_ref[...]
    moved = MOVE_CAP * fields
    n_l = from_l_ref[moved : moved + 1, 0:1]
    n_r = from_r_ref[moved : moved + 1, 0:1]
    n_h = hinfo[0:1, 6:7]
    first = hinfo[0:1, 7:8] > 0.5
    final = hinfo[0:1, 8:9] > 0.5
    off_l = jnp.where(first, n_h + n_r, jnp.where(final, n_r, 0.0))
    off_h = jnp.where(first, 0.0, jnp.where(final, n_r + n_l, n_l))
    off_r = jnp.where(first, n_h, jnp.where(final, 0.0, n_l + n_h))
    width = hold * fields
    eye = jnp.where(
        lax.broadcasted_iota(jnp.int32, (width, LANE), 0)
        == lax.broadcasted_iota(jnp.int32, (width, LANE), 1), 1.0, 0.0
    ).astype(bf16)

    def gather(values, valid, pos):
        count = values.shape[0]
        rf = lax.broadcasted_iota(jnp.int32, (count, LANE), 0) % fields
        cc = lax.broadcasted_iota(jnp.int32, (count, LANE), 1)
        hit = valid & (pos == (cc // fields).astype(f32)) & (rf == cc % fields) & (cc < width)
        pick = _dot_t(eye, jnp.where(hit, 1.0, 0.0).astype(bf16)).astype(bf16)
        return _exact_right(pick, values)

    total = gather(home_ref[...], hinfo[:, 2:3] > 0.5, off_h + hinfo[:, 5:6])
    slot = (lax.broadcasted_iota(jnp.int32, (moved, 1), 0) // fields).astype(f32)
    total = total + gather(from_l_ref[0:moved, :], slot < n_l, off_l + slot)
    total = total + gather(from_r_ref[0:moved, :], slot < n_r, off_r + slot)
    out_ref[...] = total


def final_entry(fields, hold, *refs):
    count = 4
    sources = refs[:count]
    out_ref = refs[count]
    buffers = refs[count + 1 : 2 * count + 1]
    sems = refs[2 * count + 1]
    copies = [pltpu.make_async_copy(sources[i], buffers[i], sems.at[i]) for i in range(count)]
    for copy in copies:
        copy.start()
    for copy in copies:
        copy.wait()
    final_kernel(fields, hold, *buffers, out_ref)


def setup_entry(local, fields, n_in, n_out, *refs):
    sources = refs[:n_in]
    outs = refs[n_in : n_in + n_out]
    n_tab = 1
    n_own = n_in - n_tab
    buffers = refs[n_in + n_out : n_in + n_out + n_own]
    sems = refs[n_in + n_out + n_own]
    targets = list(buffers) + list(outs[n_out - n_tab :])
    copies = [
        pltpu.make_async_copy(sources[i], targets[i], sems.at[i]) for i in range(n_in)
    ]
    for copy in copies:
        copy.start()
    for copy in copies:
        copy.wait()
    setup_kernel(local, fields, *targets, *outs[: n_out - n_tab])


def per_device(state, velocity, pre_exp, stoich, neighbours, switch, new_owner):
    tab = make_tables()
    local_count = state.shape[0]
    field_count = state.shape[1]
    rows = local_count * field_count
    curve_count = lax.axis_size("curve")
    curve_pos = lax.axis_index("curve")
    device_id = lax.axis_index("slab") * curve_count + curve_pos
    first_global = device_id * local_count
    positions = jnp.arange(local_count, dtype=jnp.int32)

    near_device = neighbours // local_count
    near_local = neighbours - near_device * local_count
    remote = near_device != device_id
    codes = (near_local + local_count * remote.astype(jnp.int32)).astype(f32)
    left_pos = (curve_pos + curve_count - 1) % curve_count
    right_pos = (curve_pos + 1) % curve_count
    sto_col = jnp.pad(stoich, (0, local_count - field_count))
    packed_t = jnp.concatenate(
        [
            jnp.transpose(codes),
            jnp.stack([switch.astype(f32), pre_exp, sto_col, new_owner.astype(f32)]),
        ]
    )
    packed = jnp.pad(packed_t, ((0, local_count - 10), (0, LANE - local_count)))
    fsel_np = np.arange(rows)[:, None] % field_count == np.arange(local_count)[None, :]
    vt = jnp.transpose(velocity, (0, 2, 1))
    row_elem = np.arange(rows) // field_count
    bcast_np = row_elem[:, None] == np.arange(local_count)[None, :]
    pick_rows = (np.arange(3)[:, None] + field_count * np.arange(local_count)[None, :]).reshape(-1)
    sel_np = pick_rows[:, None] == np.arange(rows)[None, :]
    n7 = P7**3
    n3 = P3**3
    layout = table_layout(rows, local_count)
    table_np = np.zeros((table_rows(), 6 * LANE), np.float32)
    for d in (1, 2):
        block = tab["d7t"][d][:LANE, :LANE].astype(np.float32)
        assert np.array_equal(
            tab["d7t"][d].astype(np.float32), np.kron(np.eye(n7 // LANE), block)
        )
    pieces = {
        "g7": tab["g7"][None],
        "tm": tab["tm"],
        "mdst": np.transpose(tab["mds"], (0, 2, 1)),
        "dx": tab["d7t"][0:1],
        "byz": np.stack([tab["d7t"][1][:LANE, :LANE], tab["d7t"][2][:LANE, :LANE]]),
        "lift_t": tab["lift"].T[None],
        "pj": np.transpose(tab["pjt"], (0, 2, 1)),
        "bcast": bcast_np[None],
        "sel": sel_np[None],
        "fsel": fsel_np[None],
        "d3t": tab["d3t"],
    }
    filled = np.zeros(table_np.shape, bool)
    for name, (start, count, width, lane0) in layout.items():
        parts = np.asarray(pieces[name], np.float32)
        for k in range(parts.shape[0]):
            window = (slice(start + k * count, start + (k + 1) * count), slice(lane0, lane0 + width))
            assert not filled[window].any()
            filled[window] = True
            table_np[window] = parts[k]
    table = jnp.asarray(to_bf16(table_np))

    send_shape = jax.ShapeDtypeStruct((rows, LANE), bf16)
    sends_shape = [send_shape, send_shape, jax.ShapeDtypeStruct((2 * rows, LANE), bf16)]
    u_shape = jax.ShapeDtypeStruct((rows, P7**3), f32)
    c_shape = jax.ShapeDtypeStruct((rows, P3**3), f32)

    def exchange(sends):
        face0, face1, faces_z = sends
        from_prev = shifted(faces_z, "slab", 1)
        if lax.axis_size("slab") == 2:
            from_next = from_prev
        else:
            from_next = shifted(faces_z, "slab", -1)
        return [shifted(face1, "curve", 1), shifted(face0, "curve", -1), from_prev, from_next]

    setup_out = [
        jax.ShapeDtypeStruct((3, rows, P7**3), bf16),
        jax.ShapeDtypeStruct((rows, 6 * LANE), f32),
        jax.ShapeDtypeStruct((3, rows, P3**3), f32),
        jax.ShapeDtypeStruct((rows, 6 * LANE), f32),
        jax.ShapeDtypeStruct((6, rows, rows), bf16),
        jax.ShapeDtypeStruct((len(SEND_FACES), rows, rows), bf16),
        jax.ShapeDtypeStruct((local_count, 1), f32),
        jax.ShapeDtypeStruct((rows, 1), f32),
        jax.ShapeDtypeStruct((rows, 1), f32),
        jax.ShapeDtypeStruct((rows, LANE), f32),
        jax.ShapeDtypeStruct((8, LANE), f32),
        jax.ShapeDtypeStruct((8, LANE), f32),
        jax.ShapeDtypeStruct((MOVE_CAP * field_count, rows), bf16),
        jax.ShapeDtypeStruct((MOVE_CAP * field_count, rows), bf16),
    ] + sends_shape
    setup_out = setup_out + [jax.ShapeDtypeStruct(table.shape, table.dtype)]
    u0 = state.reshape(rows, P7**3)
    setup_in = [u0, vt, packed, table]
    res = pl.pallas_call(
        functools.partial(setup_entry, local_count, field_count, len(setup_in), len(setup_out)),
        out_shape=setup_out,
        in_specs=[pl.BlockSpec(memory_space=pltpu.HBM) for _ in setup_in],
        out_specs=[_vmem() for _ in setup_out],
        scratch_shapes=[pltpu.VMEM(x.shape, x.dtype) for x in setup_in[:3]]
        + [pltpu.SemaphoreType.DMA((len(setup_in),))],
        compiler_params=pltpu.CompilerParams(vmem_limit_bytes=24 * 1024 * 1024),
    )(*setup_in)
    v7, m7, v3, m3, p_local, p_remote, pre, stc, sw = res[:9]
    hinfo, cnt_l, cnt_r, sel_l, sel_r = res[9:14]
    sends = res[14:17]
    table = res[17]
    common = [p_local, p_remote, v7, m7, pre, stc, table]
    recv = exchange(sends)
    bulk_tabs = [v7, pre, stc, table]
    (bulk7,) = run_bulk(False, local_count, [u0] + bulk_tabs, [u_shape])
    res = run_stage(
        (False, False, False, True, local_count),
        [u0] + recv + common + [bulk7],
        [u_shape] + sends_shape,
    )
    first, sends = res[0], res[1:]
    recv = exchange(sends)
    (bulk7,) = run_bulk(False, local_count, [first] + bulk_tabs, [u_shape])
    res = run_stage(
        (False, True, True, True, local_count),
        [first, u0] + recv + common + [sw, bulk7],
        [u_shape, c_shape] + sends_shape,
    )
    after, coarse, sends = res[0], res[1], res[2:]
    recv = exchange(sends)
    mixed_tail = [v3, m3, sw]
    bulk7, bulk3 = run_bulk(True, local_count, [after, coarse] + bulk_tabs + [v3], [u_shape, c_shape])
    res = run_stage(
        (True, False, False, True, local_count),
        [after, coarse] + recv + common + mixed_tail + [bulk7, bulk3],
        [u_shape, c_shape] + sends_shape,
    )
    first7, first3, sends = res[0], res[1], res[2:]
    recv = exchange(sends)
    pay_shape = jax.ShapeDtypeStruct((MOVE_CAP * field_count + 8, P7**3), f32)
    bulk7, bulk3 = run_bulk(True, local_count, [first7, first3] + bulk_tabs + [v3], [u_shape, c_shape])
    res = run_stage(
        (True, True, False, False, local_count),
        [first7, first3, after, coarse] + recv + common + mixed_tail
        + [sel_l, sel_r, cnt_l, cnt_r, bulk7, bulk3],
        [u_shape, c_shape, pay_shape, pay_shape],
    )
    final7, final3, pay_l, pay_r = res
    from_right = shifted(pay_l, "curve", -1)
    from_left = shifted(pay_r, "curve", 1)
    final_in = [final7, from_left, from_right, hinfo]
    held = pl.pallas_call(
        functools.partial(final_entry, field_count, HOLD7),
        out_shape=jax.ShapeDtypeStruct((HOLD7 * field_count, P7**3), f32),
        in_specs=[pl.BlockSpec(memory_space=pl.ANY) for _ in final_in],
        out_specs=_vmem(),
        scratch_shapes=[pltpu.VMEM(x.shape, x.dtype) for x in final_in]
        + [pltpu.SemaphoreType.DMA((len(final_in),))],
    )(*final_in)
    state7_out = held.reshape(HOLD7, field_count, P7**3)
    state3_out = final3.reshape(local_count, field_count * P3**3)
    return (state7_out, state3_out)


def solution(mesh):
    return jax.shard_map(
        per_device,
        mesh=mesh,
        in_specs=(
            P(("slab", "curve"), None, None),
            P(None, None, ("slab", "curve")),
            P(("slab", "curve")),
            P(),
            P(("slab", "curve"), None),
            P(("slab", "curve")),
            P(("slab", "curve")),
        ),
        out_specs=(P(("slab", "curve"), None, None), P(("slab", "curve"), None)),
        check_vma=False,
    )
```

```python
import functools

import jax
import jax.numpy as jnp
import ml_dtypes
import numpy as np
from jax import lax
from jax.experimental import pallas as pl
from jax.experimental.pallas import tpu as pltpu
from jax.sharding import PartitionSpec as P

P7 = 8
P3 = 4
MOVE_CAP = 2
HOLD7 = 12
LANE = 128

TIME_STEP = 0.002
ACTIVATION = 1.5
SIDE_SIGNS = (-1.0, 1.0, -1.0, 1.0, -1.0, 1.0)
OPPOSITE = (1, 0, 3, 2, 5, 4)
SEND_FACES = (0, 1, 4, 5)
missing_id = 1 << 30

f32 = jnp.float32
bf16 = jnp.bfloat16


def shifted(value, axis, steps):
    count = lax.axis_size(axis)
    pairs = [(source, (source + steps) % count) for source in range(count)]
    return lax.ppermute(value, axis, pairs)


def lobatto_points(number):
    return -np.cos(np.pi * np.arange(number) / (number - 1))


def lagrange_weights(points):
    weights = np.ones(points.shape[0])
    for row_id in range(points.shape[0]):
        for col_id in range(points.shape[0]):
            if col_id != row_id:
                weights[row_id] = weights[row_id] / (points[row_id] - points[col_id])
    return weights


def derivative_matrix(points):
    weights = lagrange_weights(points)
    number = points.shape[0]
    matrix = np.zeros((number, number))
    for row_id in range(number):
        for col_id in range(number):
            if col_id != row_id:
                matrix[row_id, col_id] = (
                    weights[col_id] / weights[row_id] / (points[row_id] - points[col_id])
                )
        matrix[row_id, row_id] = -np.sum(matrix[row_id])
    return matrix


def interpolation_matrix(source, target):
    matrix = np.ones((target.shape[0], source.shape[0]))
    for col_id in range(source.shape[0]):
        for other_id in range(source.shape[0]):
            if other_id != col_id:
                matrix[:, col_id] = (
                    matrix[:, col_id]
                    * (target - source[other_id])
                    / (source[col_id] - source[other_id])
                )
    return matrix


def spread_three(matrix, identity):
    return (
        np.kron(matrix, np.kron(identity, identity)),
        np.kron(identity, np.kron(matrix, identity)),
        np.kron(identity, np.kron(identity, matrix)),
    )


def face_nodes(extent):
    grid = np.arange(extent**3).reshape(extent, extent, extent)
    last = extent - 1
    pieces = (grid[0], grid[last], grid[:, 0], grid[:, last], grid[:, :, 0], grid[:, :, last])
    return [piece.reshape(-1) for piece in pieces]


def to_bf16(x):
    return np.asarray(np.asarray(x, np.float32).astype(ml_dtypes.bfloat16))


def split_parts(x):
    x = np.asarray(x, np.float32)
    hi = x.astype(ml_dtypes.bfloat16)
    rest = x - hi.astype(np.float32)
    mid = rest.astype(ml_dtypes.bfloat16)
    lo = (rest - mid.astype(np.float32)).astype(ml_dtypes.bfloat16)
    return np.stack([hi, mid, lo])


def make_tables():
    fine_points = lobatto_points(P7)
    coarse_points = lobatto_points(P3)
    fine_derivs = spread_three(derivative_matrix(fine_points), np.eye(P7))
    coarse_derivs = spread_three(derivative_matrix(coarse_points), np.eye(P3))
    downward = interpolation_matrix(fine_points, coarse_points)
    upward = interpolation_matrix(coarse_points, fine_points)
    d7t = np.stack([to_bf16(m.T) for m in fine_derivs])
    d3t = np.stack([to_bf16(m).T for m in coarse_derivs])
    lift_table = to_bf16(np.kron(upward, np.kron(upward, upward)))
    projection = np.asarray(np.kron(downward, np.kron(downward, downward)), np.float32)
    mortar_up = np.asarray(np.kron(upward, upward), np.float32)
    mortar_down = np.asarray(np.kron(downward, downward), np.float32)
    nodes7 = face_nodes(P7)
    nodes3 = face_nodes(P3)
    n7 = P7**3
    n3 = P3**3
    g7 = np.zeros((n7, 6 * LANE), np.float32)
    tm = np.zeros((n3, 6 * LANE), np.float32)
    mds = np.zeros((6 * LANE, n3), np.float32)
    for side in range(6):
        for q, node in enumerate(nodes7[side]):
            g7[node, side * LANE + q] = 1.0
        for k, node in enumerate(nodes3[side]):
            tm[node, side * LANE : side * LANE + P7 * P7] = mortar_up[:, k]
            mds[side * LANE : side * LANE + P7 * P7, node] = mortar_down[k, :]
    tables = {
        "d7t": to_bf16(d7t),
        "d3t": to_bf16(d3t),
        "lift": lift_table,
        "mortar_up": mortar_up,
        "g7": to_bf16(g7),
        "tm": split_parts(tm),
        "mds": split_parts(mds),
        "pjt": split_parts(projection.T),
        "nodes7": nodes7,
        "nodes3": nodes3,
    }
    return tables


def _dot(a, b):
    return jnp.dot(a, b, preferred_element_type=f32)


def _split(x):
    hi = x.astype(bf16)
    rest = x - hi.astype(f32)
    mid = rest.astype(bf16)
    lo = (rest - mid.astype(f32)).astype(bf16)
    return hi, mid, lo


def _exact_left(x, table):
    hi, mid, lo = _split(x)
    return (_dot(hi, table) + _dot(mid, table)) + _dot(lo, table)


def _dot_t(a, b):
    return lax.dot_general(a, b, (((1,), (1,)), ((), ())), preferred_element_type=f32)


def _exact_left_t(x, table):
    hi, mid, lo = _split(x)
    return (_dot_t(hi, table) + _dot_t(mid, table)) + _dot_t(lo, table)


def _exact_right(table, x):
    hi, mid, lo = _split(x)
    return (_dot(table, hi) + _dot(table, mid)) + _dot(table, lo)


def _full_t(x, parts_ref):
    xh, xm, xl = _split(x)
    bh = parts_ref[0]
    bm = parts_ref[1]
    bl = parts_ref[2]
    return _dot_t(xh, bh) + (_dot_t(xh, bm) + _dot_t(xm, bh)) + (
        _dot_t(xh, bl) + _dot_t(xm, bm) + _dot_t(xl, bh)
    )


class View:
    def __init__(self, ref, start, rows, width, lane0):
        self.ref = ref
        self.start = start
        self.rows = rows
        self.width = width
        self.lane0 = lane0

    def __getitem__(self, k):
        if k is Ellipsis:
            k = 0
        top = self.start + k * self.rows
        return self.ref[top : top + self.rows, self.lane0 : self.lane0 + self.width]


def table_layout(rows, local):
    n7 = P7**3
    n3 = P3**3
    wide = 6 * LANE
    base = n7 + 6 * n3
    side = 4 * LANE
    return {
        "g7": (0, n7, wide, 0),
        "tm": (n7, n3, wide, 0),
        "mdst": (n7 + 3 * n3, n3, wide, 0),
        "dx": (base, n7, n7, 0),
        "lift_t": (base + n7, n3, n7, 0),
        "pj": (base + n7 + n3, n3, n7, 0),
        "byz": (base, LANE, LANE, 5 * LANE),
        "bcast": (base, rows, local, side),
        "sel": (base + rows, 3 * local, rows, side),
        "fsel": (base + rows + 3 * local, rows, local, side),
        "d3t": (base + 2 * rows + 3 * local, n3, n3, side),
    }


def table_rows():
    return P7**3 + 6 * P3**3 + P7**3 + 4 * P3**3


def table_views(tab_ref, rows, local):
    return {
        name: View(tab_ref, start, count, width, lane0)
        for name, (start, count, width, lane0) in table_layout(rows, local).items()
    }


def _full(x, parts_ref):
    xh, xm, xl = _split(x)
    bh = parts_ref[0]
    bm = parts_ref[1]
    bl = parts_ref[2]
    return _dot(xh, bh) + (_dot(xh, bm) + _dot(xm, bh)) + (
        _dot(xh, bl) + _dot(xm, bm) + _dot(xl, bh)
    )


def _rate_source(values, pre, stc, bc, sel, local):
    picked = _exact_right(sel, values)
    v0 = picked[0:local]
    v1 = picked[local : 2 * local]
    v2 = picked[2 * local : 3 * local]
    rate = pre * jnp.exp(-ACTIVATION * jnp.exp(-v0)) * v1 * v2
    return stc * _exact_right(bc, rate)


def recv_block(recv, side):
    ref = recv[side]
    if side in (4, 5):
        rows = ref.shape[0] // 2
        top = 0 if side == 4 else rows
        return ref[top : top + rows, :]
    return ref[...]


def write_sends(out_refs, send):
    rows = send.shape[0]
    out_refs[0][...] = send[:, 0:LANE]
    out_refs[1][...] = send[:, LANE : 2 * LANE]
    out_refs[2][0:rows, :] = send[:, 5 * LANE : 6 * LANE]
    out_refs[2][rows : 2 * rows, :] = send[:, 4 * LANE : 5 * LANE]


def stage_kernel(coarse, second, project, sends, local, *refs):
    refs = list(refs)

    def take():
        return refs.pop(0)

    u_ref = take()
    c_ref = take() if coarse else None
    bu_ref = take() if second else None
    bc_ref = take() if (second and coarse) else None
    recv = {s: take() for s in SEND_FACES}
    pl_ref = take()
    pr_ref = take()
    v7_ref = take()
    m7_ref = take()
    pre_ref = take()
    stc_ref = take()
    views = table_views(take(), u_ref.shape[0], local)
    bc_tab = views["bcast"]
    sel_tab = views["sel"]
    g7_ref = views["g7"]
    d3_ref = views["d3t"]
    mds_ref = views["mdst"]
    tm_ref = views["tm"]
    pj_ref = views["pj"]
    if coarse:
        v3_ref = take()
        m3_ref = take()
    if coarse or project:
        sw_ref = take()
    last = coarse and not sends
    if last:
        sel_l_ref = take()
        sel_r_ref = take()
        cnt_l_ref = take()
        cnt_r_ref = take()
    res7_ref = take()
    res3_ref = take() if coarse else None
    out_u = take()
    out_c = take() if (coarse or project) else None
    out_send = [take() for _ in range(3)] if sends else None
    if last:
        pay_l_ref = take()
        pay_r_ref = take()

    pre = pre_ref[...]
    stc = stc_ref[...]
    bcast = bc_tab[...]
    sel = sel_tab[...]
    u = u_ref[...]
    trace7 = _dot(u.astype(bf16), g7_ref[...])
    if coarse:
        c = c_ref[...]
        trace3 = _full(c, tm_ref).astype(bf16).astype(f32)
        switched = sw_ref[...] > 0.5
        own = jnp.where(switched, trace3, trace7)
    else:
        own = trace7
    own_b = own.astype(bf16)
    near_blocks = []
    for side in range(6):
        other = OPPOSITE[side]
        block = own_b[:, other * LANE : (other + 1) * LANE]
        near = _dot(pl_ref[side], block)
        if side in SEND_FACES:
            k = SEND_FACES.index(side)
            near = near + _dot(pr_ref[k], recv_block(recv, side))
        near_blocks.append(near)
    near = jnp.concatenate(near_blocks, axis=1)

    result = res7_ref[...]
    jump = (P7 * (P7 - 1) / 2.0) * (m7_ref[...] * (trace7 - near))
    rate7 = result + _exact_left_t(jump, g7_ref[...])

    if coarse:
        result3 = res3_ref[...]
        jump3 = m3_ref[...] * (trace3 - near)
        rate3 = result3 + (P3 * (P3 - 1) / 2.0) * _full_t(jump3, mds_ref)

    if second:
        new_u = 0.5 * (bu_ref[...] + u + TIME_STEP * rate7)
    else:
        new_u = u + TIME_STEP * rate7
    out_u[...] = new_u
    new_c = None
    if coarse:
        if second:
            new_c = 0.5 * (bc_ref[...] + c + TIME_STEP * rate3)
        else:
            new_c = c + TIME_STEP * rate3
        if last:
            out_c[...] = jnp.where(sw_ref[...] > 0.5, new_c, 0.0)
            moved = sel_l_ref.shape[0]
            pay_l_ref[0:moved, :] = _exact_right(sel_l_ref[...], new_u)
            pay_r_ref[0:moved, :] = _exact_right(sel_r_ref[...], new_u)
            tail = (pay_l_ref.shape[0] - moved, pay_l_ref.shape[1])
            pay_l_ref[moved:, :] = jnp.broadcast_to(cnt_l_ref[0:1, 0:1], tail)
            pay_r_ref[moved:, :] = jnp.broadcast_to(cnt_r_ref[0:1, 0:1], tail)
        else:
            out_c[...] = new_c
    if project:
        new_c = _full_t(new_u, pj_ref)
        out_c[...] = new_c
    if sends:
        send7 = _dot(new_u.astype(bf16), g7_ref[...])
        if new_c is not None:
            send3 = _full(new_c, tm_ref).astype(bf16).astype(f32)
            send = jnp.where(sw_ref[...] > 0.5, send3, send7)
        else:
            send = send7
        write_sends(out_send, send.astype(bf16))


def _vmem():
    return pl.BlockSpec(memory_space=pltpu.VMEM)


def bulk_kernel(coarse, local, *refs):
    refs = list(refs)
    u_ref = refs.pop(0)
    c_ref = refs.pop(0) if coarse else None
    v7_ref, pre_ref, stc_ref = refs.pop(0), refs.pop(0), refs.pop(0)
    views = table_views(refs.pop(0), u_ref.shape[0], local)
    v3_ref = refs.pop(0) if coarse else None
    out7 = refs.pop(0)
    out3 = refs.pop(0) if coarse else None
    pre = pre_ref[...]
    stc = stc_ref[...]
    bcast = views["bcast"][...]
    sel = views["sel"][...]
    u = u_ref[...]
    fluxes = [(v7_ref[d].astype(f32) * u).astype(bf16) for d in range(3)]
    divergence = _dot(fluxes[0], views["dx"][0])
    by = views["byz"][0]
    bz = views["byz"][1]
    chunks = []
    for k in range(u.shape[1] // LANE):
        part = slice(k * LANE, (k + 1) * LANE)
        chunks.append(_dot(fluxes[1][:, part], by) + _dot(fluxes[2][:, part], bz))
    divergence = divergence + jnp.concatenate(chunks, axis=1)
    out7[...] = _rate_source(u, pre, stc, bcast, sel, local) - divergence
    if coarse:
        c = c_ref[...]
        div3 = None
        for d in range(3):
            flux3 = (v3_ref[d] * c).astype(bf16)
            term = _dot(flux3, views["d3t"][d])
            div3 = term if div3 is None else div3 + term
        out3[...] = _rate_source(c, pre, stc, bcast, sel, local) - div3


def run_bulk(coarse, local, inputs, out_shapes):
    return pl.pallas_call(
        functools.partial(bulk_kernel, coarse, local),
        out_shape=out_shapes,
        in_specs=[_vmem() for _ in inputs],
        out_specs=[_vmem() for _ in out_shapes],
        compiler_params=pltpu.CompilerParams(vmem_limit_bytes=24 * 1024 * 1024),
    )(*inputs)


def run_stage(flags, inputs, out_shapes):
    coarse, second, project, sends, local = flags
    kernel = functools.partial(stage_kernel, coarse, second, project, sends, local)
    return pl.pallas_call(
        kernel,
        out_shape=out_shapes,
        in_specs=[_vmem() for _ in inputs],
        out_specs=[_vmem() for _ in out_shapes],
        compiler_params=pltpu.CompilerParams(vmem_limit_bytes=48 * 1024 * 1024),
    )(*inputs)


def setup_kernel(local, fields, u_ref, vt_ref, packed_ref, tab_ref, v7_out, m7_out, v3_out, m3_out, pl_out, pr_out,
                 pre_out, stc_out, sw_out, hinfo_out, cnt_l_out, cnt_r_out, sel_l_out,
                 sel_r_out, *send_refs):
    rows = local * fields
    views = table_views(tab_ref, rows, local)
    lift_ref = views["lift_t"]
    g7_ref = views["g7"]
    tm_ref = views["tm"]
    fsel_ref = views["fsel"]
    bcast = views["bcast"][...]
    lanes = lax.broadcasted_iota(jnp.int32, (local, 6 * LANE), 1) // LANE
    sign = jnp.where(lanes % 2 == 0, -1.0, 1.0)
    fvg = []
    mvg = []
    for d in range(3):
        vt = vt_ref[d]
        fv = _dot(vt, lift_ref[...]).astype(bf16)
        v7_out[d] = _dot(bcast, fv).astype(bf16)
        v3_out[d] = _dot(bcast, vt)
        fvg.append(_dot(fv, g7_ref[...]))
        mvg.append((_dot(vt, tm_ref[0]) + _dot(vt, tm_ref[1])) + _dot(vt, tm_ref[2]))

    def by_block(parts):
        return jnp.where(lanes < 2, parts[0], jnp.where(lanes < 4, parts[1], parts[2]))

    m7 = jnp.minimum(sign * by_block(fvg), 0.0)
    m7_out[...] = _dot(bcast, m7.astype(bf16))
    m3 = jnp.minimum(sign * by_block(mvg), 0.0)
    m3_out[...] = _exact_right(bcast, m3)
    eye16 = jnp.where(
        lax.broadcasted_iota(jnp.int32, (local, LANE), 0)
        == lax.broadcasted_iota(jnp.int32, (local, LANE), 1), 1.0, 0.0
    ).astype(bf16)
    p_hi, p_mid, p_lo = _split(packed_ref[...])
    packed = (_dot_t(eye16, p_hi) + _dot_t(eye16, p_mid)) + _dot_t(eye16, p_lo)
    rep = _dot(bcast, packed.astype(bf16))
    row_f = (lax.broadcasted_iota(jnp.int32, (rows, 1), 0) % fields).astype(f32)
    cols = lax.broadcasted_iota(jnp.int32, (rows, rows), 1).astype(f32)
    for side in range(6):
        code = rep[:, side : side + 1]
        far = code >= local
        target = (code - jnp.where(far, float(local), 0.0)) * fields + row_f
        hit = cols == target
        pl_out[side] = jnp.where(hit & ~far, 1.0, 0.0).astype(bf16)
        if side in SEND_FACES:
            pr_out[SEND_FACES.index(side)] = jnp.where(hit & far, 1.0, 0.0).astype(bf16)
    sw_out[...] = rep[:, 6:7]
    curve_count = lax.axis_size("curve")
    curve_pos = lax.axis_index("curve")
    left_f = ((curve_pos + curve_count - 1) % curve_count).astype(f32)
    right_f = ((curve_pos + 1) % curve_count).astype(f32)
    first_f = jnp.where(curve_pos == 0, 1.0, 0.0)
    last_f = jnp.where(curve_pos == curve_count - 1, 1.0, 0.0)
    stay_sw = packed[:, 6:7] < 0.5
    go_left = (packed[:, 9:10] == left_f) & stay_sw
    go_right = (packed[:, 9:10] == right_f) & stay_sw
    stays = stay_sw & ~go_left & ~go_right
    lane16 = lax.broadcasted_iota(jnp.int32, (local, LANE), 1)
    marks = jnp.where(
        lane16 == 0, go_left.astype(f32),
        jnp.where(lane16 == 1, go_right.astype(f32), jnp.where(lane16 == 2, stays.astype(f32), 0.0)),
    ).astype(bf16)
    er = lax.broadcasted_iota(jnp.int32, (local, local), 0)
    ec = lax.broadcasted_iota(jnp.int32, (local, local), 1)
    before = _dot(jnp.where(ec < er, 1.0, 0.0).astype(bf16), marks)
    totals = _dot(jnp.ones((local, local), bf16), marks)
    info = jnp.where(lane16 < 3, marks.astype(f32), 0.0)
    for k in range(3):
        info = jnp.where(lane16 == 3 + k, before[:, k : k + 1], info)
    info = jnp.where(lane16 == 6, totals[:, 2:3], info)
    info = jnp.where(lane16 == 7, first_f, info)
    info = jnp.where(lane16 == 8, last_f, info)
    hinfo = _dot(bcast, info.astype(bf16))
    hinfo_out[...] = hinfo
    cnt_l_out[...] = jnp.broadcast_to(totals[0:1, 0:1], cnt_l_out.shape)
    cnt_r_out[...] = jnp.broadcast_to(totals[0:1, 1:2], cnt_r_out.shape)
    rf = lax.broadcasted_iota(jnp.int32, (rows, LANE), 0) % fields
    cc = lax.broadcasted_iota(jnp.int32, (rows, LANE), 1)
    eye = jnp.where(
        lax.broadcasted_iota(jnp.int32, (MOVE_CAP * fields, LANE), 0)
        == lax.broadcasted_iota(jnp.int32, (MOVE_CAP * fields, LANE), 1), 1.0, 0.0
    ).astype(bf16)
    for mark_lane, rank_lane, out in ((0, 3, sel_l_out), (1, 4, sel_r_out)):
        hit = (
            (hinfo[:, mark_lane : mark_lane + 1] > 0.5)
            & (hinfo[:, rank_lane : rank_lane + 1] == (cc // fields).astype(f32))
            & (rf == cc % fields)
            & (cc < MOVE_CAP * fields)
        )
        out[...] = _dot_t(eye, jnp.where(hit, 1.0, 0.0).astype(bf16)).astype(bf16)
    pre_out[...] = packed[:, 7:8]
    stc_out[...] = _exact_right(fsel_ref[...], packed)[:, 8:9]
    write_sends(send_refs, _dot(u_ref[...].astype(bf16), g7_ref[...]).astype(bf16))


def final_kernel(fields, hold, home_ref, from_l_ref, from_r_ref, hinfo_ref, out_ref):
    hinfo = hinfo_ref[...]
    moved = MOVE_CAP * fields
    n_l = from_l_ref[moved : moved + 1, 0:1]
    n_r = from_r_ref[moved : moved + 1, 0:1]
    n_h = hinfo[0:1, 6:7]
    first = hinfo[0:1, 7:8] > 0.5
    final = hinfo[0:1, 8:9] > 0.5
    off_l = jnp.where(first, n_h + n_r, jnp.where(final, n_r, 0.0))
    off_h = jnp.where(first, 0.0, jnp.where(final, n_r + n_l, n_l))
    off_r = jnp.where(first, n_h, jnp.where(final, 0.0, n_l + n_h))
    width = hold * fields
    eye = jnp.where(
        lax.broadcasted_iota(jnp.int32, (width, LANE), 0)
        == lax.broadcasted_iota(jnp.int32, (width, LANE), 1), 1.0, 0.0
    ).astype(bf16)

    def gather(values, valid, pos):
        count = values.shape[0]
        rf = lax.broadcasted_iota(jnp.int32, (count, LANE), 0) % fields
        cc = lax.broadcasted_iota(jnp.int32, (count, LANE), 1)
        hit = valid & (pos == (cc // fields).astype(f32)) & (rf == cc % fields) & (cc < width)
        pick = _dot_t(eye, jnp.where(hit, 1.0, 0.0).astype(bf16)).astype(bf16)
        return _exact_right(pick, values)

    total = gather(home_ref[...], hinfo[:, 2:3] > 0.5, off_h + hinfo[:, 5:6])
    slot = (lax.broadcasted_iota(jnp.int32, (moved, 1), 0) // fields).astype(f32)
    total = total + gather(from_l_ref[0:moved, :], slot < n_l, off_l + slot)
    total = total + gather(from_r_ref[0:moved, :], slot < n_r, off_r + slot)
    out_ref[...] = total


def final_entry(fields, hold, *refs):
    count = 4
    sources = refs[:count]
    out_ref = refs[count]
    buffers = refs[count + 1 : 2 * count + 1]
    staged = refs[2 * count + 1]
    sems = refs[2 * count + 2]
    copies = [pltpu.make_async_copy(sources[i], buffers[i], sems.at[i]) for i in range(count)]
    for copy in copies:
        copy.start()
    for copy in copies:
        copy.wait()
    final_kernel(fields, hold, *buffers, staged)
    out_copy = pltpu.make_async_copy(staged, out_ref, sems.at[count])
    out_copy.start()
    out_copy.wait()


def setup_entry(local, fields, n_in, n_out, *refs):
    sources = refs[:n_in]
    outs = refs[n_in : n_in + n_out]
    n_tab = 1
    n_own = n_in - n_tab
    buffers = refs[n_in + n_out : n_in + n_out + n_own]
    sems = refs[n_in + n_out + n_own]
    targets = list(buffers) + list(outs[n_out - n_tab :])
    copies = [
        pltpu.make_async_copy(sources[i], targets[i], sems.at[i]) for i in range(n_in)
    ]
    for copy in copies:
        copy.start()
    for copy in copies:
        copy.wait()
    setup_kernel(local, fields, *targets, *outs[: n_out - n_tab])


def per_device(state, velocity, pre_exp, stoich, neighbours, switch, new_owner):
    tab = make_tables()
    local_count = state.shape[0]
    field_count = state.shape[1]
    rows = local_count * field_count
    curve_count = lax.axis_size("curve")
    curve_pos = lax.axis_index("curve")
    device_id = lax.axis_index("slab") * curve_count + curve_pos
    first_global = device_id * local_count
    positions = jnp.arange(local_count, dtype=jnp.int32)

    near_device = neighbours // local_count
    near_local = neighbours - near_device * local_count
    remote = near_device != device_id
    codes = (near_local + local_count * remote.astype(jnp.int32)).astype(f32)
    left_pos = (curve_pos + curve_count - 1) % curve_count
    right_pos = (curve_pos + 1) % curve_count
    sto_col = jnp.pad(stoich, (0, local_count - field_count))
    packed_t = jnp.concatenate(
        [
            jnp.transpose(codes),
            jnp.stack([switch.astype(f32), pre_exp, sto_col, new_owner.astype(f32)]),
        ]
    )
    packed = jnp.pad(packed_t, ((0, local_count - 10), (0, LANE - local_count)))
    fsel_np = np.arange(rows)[:, None] % field_count == np.arange(local_count)[None, :]
    vt = jnp.transpose(velocity, (0, 2, 1))
    row_elem = np.arange(rows) // field_count
    bcast_np = row_elem[:, None] == np.arange(local_count)[None, :]
    pick_rows = (np.arange(3)[:, None] + field_count * np.arange(local_count)[None, :]).reshape(-1)
    sel_np = pick_rows[:, None] == np.arange(rows)[None, :]
    n7 = P7**3
    n3 = P3**3
    layout = table_layout(rows, local_count)
    table_np = np.zeros((table_rows(), 6 * LANE), np.float32)
    for d in (1, 2):
        block = tab["d7t"][d][:LANE, :LANE].astype(np.float32)
        assert np.array_equal(
            tab["d7t"][d].astype(np.float32), np.kron(np.eye(n7 // LANE), block)
        )
    pieces = {
        "g7": tab["g7"][None],
        "tm": tab["tm"],
        "mdst": np.transpose(tab["mds"], (0, 2, 1)),
        "dx": tab["d7t"][0:1],
        "byz": np.stack([tab["d7t"][1][:LANE, :LANE], tab["d7t"][2][:LANE, :LANE]]),
        "lift_t": tab["lift"].T[None],
        "pj": np.transpose(tab["pjt"], (0, 2, 1)),
        "bcast": bcast_np[None],
        "sel": sel_np[None],
        "fsel": fsel_np[None],
        "d3t": tab["d3t"],
    }
    filled = np.zeros(table_np.shape, bool)
    for name, (start, count, width, lane0) in layout.items():
        parts = np.asarray(pieces[name], np.float32)
        for k in range(parts.shape[0]):
            window = (slice(start + k * count, start + (k + 1) * count), slice(lane0, lane0 + width))
            assert not filled[window].any()
            filled[window] = True
            table_np[window] = parts[k]
    table = jnp.asarray(to_bf16(table_np))

    send_shape = jax.ShapeDtypeStruct((rows, LANE), bf16)
    sends_shape = [send_shape, send_shape, jax.ShapeDtypeStruct((2 * rows, LANE), bf16)]
    u_shape = jax.ShapeDtypeStruct((rows, P7**3), f32)
    c_shape = jax.ShapeDtypeStruct((rows, P3**3), f32)

    def exchange(sends):
        face0, face1, faces_z = sends
        from_prev = shifted(faces_z, "slab", 1)
        if lax.axis_size("slab") == 2:
            from_next = from_prev
        else:
            from_next = shifted(faces_z, "slab", -1)
        return [shifted(face1, "curve", 1), shifted(face0, "curve", -1), from_prev, from_next]

    setup_out = [
        jax.ShapeDtypeStruct((3, rows, P7**3), bf16),
        jax.ShapeDtypeStruct((rows, 6 * LANE), f32),
        jax.ShapeDtypeStruct((3, rows, P3**3), f32),
        jax.ShapeDtypeStruct((rows, 6 * LANE), f32),
        jax.ShapeDtypeStruct((6, rows, rows), bf16),
        jax.ShapeDtypeStruct((len(SEND_FACES), rows, rows), bf16),
        jax.ShapeDtypeStruct((local_count, 1), f32),
        jax.ShapeDtypeStruct((rows, 1), f32),
        jax.ShapeDtypeStruct((rows, 1), f32),
        jax.ShapeDtypeStruct((rows, LANE), f32),
        jax.ShapeDtypeStruct((8, LANE), f32),
        jax.ShapeDtypeStruct((8, LANE), f32),
        jax.ShapeDtypeStruct((MOVE_CAP * field_count, rows), bf16),
        jax.ShapeDtypeStruct((MOVE_CAP * field_count, rows), bf16),
    ] + sends_shape
    setup_out = setup_out + [jax.ShapeDtypeStruct(table.shape, table.dtype)]
    u0 = state.reshape(rows, P7**3)
    setup_in = [u0, vt, packed, table]
    res = pl.pallas_call(
        functools.partial(setup_entry, local_count, field_count, len(setup_in), len(setup_out)),
        out_shape=setup_out,
        in_specs=[pl.BlockSpec(memory_space=pltpu.HBM) for _ in setup_in],
        out_specs=[_vmem() for _ in setup_out],
        scratch_shapes=[pltpu.VMEM(x.shape, x.dtype) for x in setup_in[:3]]
        + [pltpu.SemaphoreType.DMA((len(setup_in),))],
        compiler_params=pltpu.CompilerParams(vmem_limit_bytes=24 * 1024 * 1024),
    )(*setup_in)
    v7, m7, v3, m3, p_local, p_remote, pre, stc, sw = res[:9]
    hinfo, cnt_l, cnt_r, sel_l, sel_r = res[9:14]
    sends = res[14:17]
    table = res[17]
    common = [p_local, p_remote, v7, m7, pre, stc, table]
    recv = exchange(sends)
    bulk_tabs = [v7, pre, stc, table]
    (bulk7,) = run_bulk(False, local_count, [u0] + bulk_tabs, [u_shape])
    res = run_stage(
        (False, False, False, True, local_count),
        [u0] + recv + common + [bulk7],
        [u_shape] + sends_shape,
    )
    first, sends = res[0], res[1:]
    recv = exchange(sends)
    (bulk7,) = run_bulk(False, local_count, [first] + bulk_tabs, [u_shape])
    res = run_stage(
        (False, True, True, True, local_count),
        [first, u0] + recv + common + [sw, bulk7],
        [u_shape, c_shape] + sends_shape,
    )
    after, coarse, sends = res[0], res[1], res[2:]
    recv = exchange(sends)
    mixed_tail = [v3, m3, sw]
    bulk7, bulk3 = run_bulk(True, local_count, [after, coarse] + bulk_tabs + [v3], [u_shape, c_shape])
    res = run_stage(
        (True, False, False, True, local_count),
        [after, coarse] + recv + common + mixed_tail + [bulk7, bulk3],
        [u_shape, c_shape] + sends_shape,
    )
    first7, first3, sends = res[0], res[1], res[2:]
    recv = exchange(sends)
    pay_shape = jax.ShapeDtypeStruct((MOVE_CAP * field_count + 8, P7**3), f32)
    bulk7, bulk3 = run_bulk(True, local_count, [first7, first3] + bulk_tabs + [v3], [u_shape, c_shape])
    res = run_stage(
        (True, True, False, False, local_count),
        [first7, first3, after, coarse] + recv + common + mixed_tail
        + [sel_l, sel_r, cnt_l, cnt_r, bulk7, bulk3],
        [u_shape, c_shape, pay_shape, pay_shape],
    )
    final7, final3, pay_l, pay_r = res
    from_right = shifted(pay_l, "curve", -1)
    from_left = shifted(pay_r, "curve", 1)
    final_in = [final7, from_left, from_right, hinfo]
    held = pl.pallas_call(
        functools.partial(final_entry, field_count, HOLD7),
        out_shape=jax.ShapeDtypeStruct((HOLD7 * field_count, P7**3), f32),
        in_specs=[pl.BlockSpec(memory_space=pl.ANY) for _ in final_in],
        out_specs=pl.BlockSpec(memory_space=pl.ANY),
        scratch_shapes=[pltpu.VMEM(x.shape, x.dtype) for x in final_in]
        + [pltpu.VMEM((HOLD7 * field_count, P7**3), f32)]
        + [pltpu.SemaphoreType.DMA((len(final_in) + 1,))],
    )(*final_in)
    state7_out = held.reshape(HOLD7, field_count, P7**3)
    state3_out = final3.reshape(local_count, field_count * P3**3)
    return (state7_out, state3_out)


def solution(mesh):
    return jax.shard_map(
        per_device,
        mesh=mesh,
        in_specs=(
            P(("slab", "curve"), None, None),
            P(None, None, ("slab", "curve")),
            P(("slab", "curve")),
            P(),
            P(("slab", "curve"), None),
            P(("slab", "curve")),
            P(("slab", "curve")),
        ),
        out_specs=(P(("slab", "curve"), None, None), P(("slab", "curve"), None)),
        check_vma=False,
    )
```

```python
import functools

import jax
import jax.numpy as jnp
import ml_dtypes
import numpy as np
from jax import lax
from jax.experimental import pallas as pl
from jax.experimental.pallas import tpu as pltpu
from jax.sharding import PartitionSpec as P

P7 = 8
P3 = 4
MOVE_CAP = 2
HOLD7 = 12
LANE = 128

TIME_STEP = 0.002
ACTIVATION = 1.5
SIDE_SIGNS = (-1.0, 1.0, -1.0, 1.0, -1.0, 1.0)
OPPOSITE = (1, 0, 3, 2, 5, 4)
SEND_FACES = (0, 1, 4, 5)
missing_id = 1 << 30

f32 = jnp.float32
bf16 = jnp.bfloat16


def shifted(value, axis, steps):
    count = lax.axis_size(axis)
    pairs = [(source, (source + steps) % count) for source in range(count)]
    return lax.ppermute(value, axis, pairs)


def lobatto_points(number):
    return -np.cos(np.pi * np.arange(number) / (number - 1))


def lagrange_weights(points):
    weights = np.ones(points.shape[0])
    for row_id in range(points.shape[0]):
        for col_id in range(points.shape[0]):
            if col_id != row_id:
                weights[row_id] = weights[row_id] / (points[row_id] - points[col_id])
    return weights


def derivative_matrix(points):
    weights = lagrange_weights(points)
    number = points.shape[0]
    matrix = np.zeros((number, number))
    for row_id in range(number):
        for col_id in range(number):
            if col_id != row_id:
                matrix[row_id, col_id] = (
                    weights[col_id] / weights[row_id] / (points[row_id] - points[col_id])
                )
        matrix[row_id, row_id] = -np.sum(matrix[row_id])
    return matrix


def interpolation_matrix(source, target):
    matrix = np.ones((target.shape[0], source.shape[0]))
    for col_id in range(source.shape[0]):
        for other_id in range(source.shape[0]):
            if other_id != col_id:
                matrix[:, col_id] = (
                    matrix[:, col_id]
                    * (target - source[other_id])
                    / (source[col_id] - source[other_id])
                )
    return matrix


def spread_three(matrix, identity):
    return (
        np.kron(matrix, np.kron(identity, identity)),
        np.kron(identity, np.kron(matrix, identity)),
        np.kron(identity, np.kron(identity, matrix)),
    )


def face_nodes(extent):
    grid = np.arange(extent**3).reshape(extent, extent, extent)
    last = extent - 1
    pieces = (grid[0], grid[last], grid[:, 0], grid[:, last], grid[:, :, 0], grid[:, :, last])
    return [piece.reshape(-1) for piece in pieces]


def to_bf16(x):
    return np.asarray(np.asarray(x, np.float32).astype(ml_dtypes.bfloat16))


def split_parts(x):
    x = np.asarray(x, np.float32)
    hi = x.astype(ml_dtypes.bfloat16)
    rest = x - hi.astype(np.float32)
    mid = rest.astype(ml_dtypes.bfloat16)
    lo = (rest - mid.astype(np.float32)).astype(ml_dtypes.bfloat16)
    return np.stack([hi, mid, lo])


def make_tables():
    fine_points = lobatto_points(P7)
    coarse_points = lobatto_points(P3)
    fine_derivs = spread_three(derivative_matrix(fine_points), np.eye(P7))
    coarse_derivs = spread_three(derivative_matrix(coarse_points), np.eye(P3))
    downward = interpolation_matrix(fine_points, coarse_points)
    upward = interpolation_matrix(coarse_points, fine_points)
    d7t = np.stack([to_bf16(m.T) for m in fine_derivs])
    d3t = np.stack([to_bf16(m).T for m in coarse_derivs])
    lift_table = to_bf16(np.kron(upward, np.kron(upward, upward)))
    projection = np.asarray(np.kron(downward, np.kron(downward, downward)), np.float32)
    mortar_up = np.asarray(np.kron(upward, upward), np.float32)
    mortar_down = np.asarray(np.kron(downward, downward), np.float32)
    nodes7 = face_nodes(P7)
    nodes3 = face_nodes(P3)
    n7 = P7**3
    n3 = P3**3
    g7 = np.zeros((n7, 6 * LANE), np.float32)
    tm = np.zeros((n3, 6 * LANE), np.float32)
    mds = np.zeros((6 * LANE, n3), np.float32)
    for side in range(6):
        for q, node in enumerate(nodes7[side]):
            g7[node, side * LANE + q] = 1.0
        for k, node in enumerate(nodes3[side]):
            tm[node, side * LANE : side * LANE + P7 * P7] = mortar_up[:, k]
            mds[side * LANE : side * LANE + P7 * P7, node] = mortar_down[k, :]
    tables = {
        "d7t": to_bf16(d7t),
        "d3t": to_bf16(d3t),
        "lift": lift_table,
        "mortar_up": mortar_up,
        "g7": to_bf16(g7),
        "tm": split_parts(tm),
        "mds": split_parts(mds),
        "pjt": split_parts(projection.T),
        "nodes7": nodes7,
        "nodes3": nodes3,
    }
    return tables


def _dot(a, b):
    return jnp.dot(a, b, preferred_element_type=f32)


def _split(x):
    hi = x.astype(bf16)
    rest = x - hi.astype(f32)
    mid = rest.astype(bf16)
    lo = (rest - mid.astype(f32)).astype(bf16)
    return hi, mid, lo


def _exact_left(x, table):
    hi, mid, lo = _split(x)
    return (_dot(hi, table) + _dot(mid, table)) + _dot(lo, table)


def _dot_t(a, b):
    return lax.dot_general(a, b, (((1,), (1,)), ((), ())), preferred_element_type=f32)


def _exact_left_t(x, table):
    hi, mid, lo = _split(x)
    return (_dot_t(hi, table) + _dot_t(mid, table)) + _dot_t(lo, table)


def _exact_right(table, x):
    hi, mid, lo = _split(x)
    return (_dot(table, hi) + _dot(table, mid)) + _dot(table, lo)


def _full_t(x, parts_ref):
    xh, xm, xl = _split(x)
    bh = parts_ref[0]
    bm = parts_ref[1]
    bl = parts_ref[2]
    return _dot_t(xh, bh) + (_dot_t(xh, bm) + _dot_t(xm, bh)) + (
        _dot_t(xh, bl) + _dot_t(xm, bm) + _dot_t(xl, bh)
    )


class View:
    def __init__(self, ref, start, rows, width, lane0):
        self.ref = ref
        self.start = start
        self.rows = rows
        self.width = width
        self.lane0 = lane0

    def __getitem__(self, k):
        if k is Ellipsis:
            k = 0
        top = self.start + k * self.rows
        return self.ref[top : top + self.rows, self.lane0 : self.lane0 + self.width]


def table_layout(rows, local):
    n7 = P7**3
    n3 = P3**3
    wide = 6 * LANE
    base = n7 + 6 * n3
    side = 4 * LANE
    return {
        "g7": (0, n7, wide, 0),
        "tm": (n7, n3, wide, 0),
        "mdst": (n7 + 3 * n3, n3, wide, 0),
        "dx": (base, n7, n7, 0),
        "lift_t": (base + n7, n3, n7, 0),
        "pj": (base + n7 + n3, n3, n7, 0),
        "byz": (base, LANE, LANE, 5 * LANE),
        "bcast": (base, rows, local, side),
        "sel": (base + rows, 3 * local, rows, side),
        "fsel": (base + rows + 3 * local, rows, local, side),
        "d3t": (base + 2 * rows + 3 * local, n3, n3, side),
    }


def table_rows():
    return P7**3 + 6 * P3**3 + P7**3 + 4 * P3**3


def table_views(tab_ref, rows, local):
    return {
        name: View(tab_ref, start, count, width, lane0)
        for name, (start, count, width, lane0) in table_layout(rows, local).items()
    }


def _full(x, parts_ref):
    xh, xm, xl = _split(x)
    bh = parts_ref[0]
    bm = parts_ref[1]
    bl = parts_ref[2]
    return _dot(xh, bh) + (_dot(xh, bm) + _dot(xm, bh)) + (
        _dot(xh, bl) + _dot(xm, bm) + _dot(xl, bh)
    )


def _rate_source(values, pre, stc, bc, sel, local):
    picked = _exact_right(sel, values)
    v0 = picked[0:local]
    v1 = picked[local : 2 * local]
    v2 = picked[2 * local : 3 * local]
    rate = pre * jnp.exp(-ACTIVATION * jnp.exp(-v0)) * v1 * v2
    return stc * _exact_right(bc, rate)


def recv_block(recv, side):
    ref = recv[side]
    if side in (4, 5):
        rows = ref.shape[0] // 2
        top = 0 if side == 4 else rows
        return ref[top : top + rows, :]
    return ref[...]


def write_sends(out_refs, send):
    rows = send.shape[0]
    out_refs[0][...] = send[:, 0:LANE]
    out_refs[1][...] = send[:, LANE : 2 * LANE]
    out_refs[2][0:rows, :] = send[:, 5 * LANE : 6 * LANE]
    out_refs[2][rows : 2 * rows, :] = send[:, 4 * LANE : 5 * LANE]


def stage_kernel(coarse, second, project, sends, local, *refs):
    refs = list(refs)

    def take():
        return refs.pop(0)

    u_ref = take()
    c_ref = take() if coarse else None
    bu_ref = take() if second else None
    bc_ref = take() if (second and coarse) else None
    recv = {s: take() for s in SEND_FACES}
    pl_ref = take()
    pr_ref = take()
    v7_ref = take()
    m7_ref = take()
    pre_ref = take()
    stc_ref = take()
    views = table_views(take(), u_ref.shape[0], local)
    bc_tab = views["bcast"]
    sel_tab = views["sel"]
    g7_ref = views["g7"]
    d3_ref = views["d3t"]
    mds_ref = views["mdst"]
    tm_ref = views["tm"]
    pj_ref = views["pj"]
    if coarse:
        v3_ref = take()
        m3_ref = take()
    if coarse or project:
        sw_ref = take()
    last = coarse and not sends
    if last:
        sel_l_ref = take()
        sel_r_ref = take()
        cnt_l_ref = take()
        cnt_r_ref = take()
    res7_ref = take()
    res3_ref = take() if coarse else None
    out_u = take()
    out_c = take() if (coarse or project) else None
    out_send = [take() for _ in range(3)] if sends else None
    if last:
        pay_l_ref = take()
        pay_r_ref = take()

    pre = pre_ref[...]
    stc = stc_ref[...]
    bcast = bc_tab[...]
    sel = sel_tab[...]
    u = u_ref[...]
    trace7 = _dot(u.astype(bf16), g7_ref[...])
    if coarse:
        c = c_ref[...]
        trace3 = _full(c, tm_ref).astype(bf16).astype(f32)
        switched = sw_ref[...] > 0.5
        own = jnp.where(switched, trace3, trace7)
    else:
        own = trace7
    own_b = own.astype(bf16)
    near_blocks = []
    for side in range(6):
        other = OPPOSITE[side]
        block = own_b[:, other * LANE : (other + 1) * LANE]
        near = _dot(pl_ref[side], block)
        if side in SEND_FACES:
            k = SEND_FACES.index(side)
            near = near + _dot(pr_ref[k], recv_block(recv, side))
        near_blocks.append(near)
    near = jnp.concatenate(near_blocks, axis=1)

    result = res7_ref[...]
    jump = (P7 * (P7 - 1) / 2.0) * (m7_ref[...] * (trace7 - near))
    rate7 = result + _exact_left_t(jump, g7_ref[...])

    if coarse:
        result3 = res3_ref[...]
        jump3 = m3_ref[...] * (trace3 - near)
        rate3 = result3 + (P3 * (P3 - 1) / 2.0) * _full_t(jump3, mds_ref)

    if second:
        new_u = 0.5 * (bu_ref[...] + u + TIME_STEP * rate7)
    else:
        new_u = u + TIME_STEP * rate7
    out_u[...] = new_u
    new_c = None
    if coarse:
        if second:
            new_c = 0.5 * (bc_ref[...] + c + TIME_STEP * rate3)
        else:
            new_c = c + TIME_STEP * rate3
        if last:
            out_c[...] = jnp.where(sw_ref[...] > 0.5, new_c, 0.0)
            moved = sel_l_ref.shape[0]
            pay_l_ref[0:moved, :] = _exact_right(sel_l_ref[...], new_u)
            pay_r_ref[0:moved, :] = _exact_right(sel_r_ref[...], new_u)
            tail = (pay_l_ref.shape[0] - moved, pay_l_ref.shape[1])
            pay_l_ref[moved:, :] = jnp.broadcast_to(cnt_l_ref[0:1, 0:1], tail)
            pay_r_ref[moved:, :] = jnp.broadcast_to(cnt_r_ref[0:1, 0:1], tail)
        else:
            out_c[...] = new_c
    if project:
        new_c = _full_t(new_u, pj_ref)
        out_c[...] = new_c
    if sends:
        send7 = _dot(new_u.astype(bf16), g7_ref[...])
        if new_c is not None:
            send3 = _full(new_c, tm_ref).astype(bf16).astype(f32)
            send = jnp.where(sw_ref[...] > 0.5, send3, send7)
        else:
            send = send7
        write_sends(out_send, send.astype(bf16))


def _vmem():
    return pl.BlockSpec(memory_space=pltpu.VMEM)


def bulk_kernel(coarse, local, *refs):
    refs = list(refs)
    u_ref = refs.pop(0)
    c_ref = refs.pop(0) if coarse else None
    v7_ref, pre_ref, stc_ref = refs.pop(0), refs.pop(0), refs.pop(0)
    views = table_views(refs.pop(0), u_ref.shape[0], local)
    v3_ref = refs.pop(0) if coarse else None
    out7 = refs.pop(0)
    out3 = refs.pop(0) if coarse else None
    pre = pre_ref[...]
    stc = stc_ref[...]
    bcast = views["bcast"][...]
    sel = views["sel"][...]
    u = u_ref[...]
    fluxes = [(v7_ref[d].astype(f32) * u).astype(bf16) for d in range(3)]
    divergence = _dot(fluxes[0], views["dx"][0])
    by = views["byz"][0]
    bz = views["byz"][1]
    chunks = []
    for k in range(u.shape[1] // LANE):
        part = slice(k * LANE, (k + 1) * LANE)
        chunks.append(_dot(fluxes[1][:, part], by) + _dot(fluxes[2][:, part], bz))
    divergence = divergence + jnp.concatenate(chunks, axis=1)
    out7[...] = _rate_source(u, pre, stc, bcast, sel, local) - divergence
    if coarse:
        c = c_ref[...]
        div3 = None
        for d in range(3):
            flux3 = (v3_ref[d] * c).astype(bf16)
            term = _dot(flux3, views["d3t"][d])
            div3 = term if div3 is None else div3 + term
        out3[...] = _rate_source(c, pre, stc, bcast, sel, local) - div3


def run_bulk(coarse, local, inputs, out_shapes):
    return pl.pallas_call(
        functools.partial(bulk_kernel, coarse, local),
        out_shape=out_shapes,
        in_specs=[_vmem() for _ in inputs],
        out_specs=[_vmem() for _ in out_shapes],
        compiler_params=pltpu.CompilerParams(vmem_limit_bytes=24 * 1024 * 1024),
    )(*inputs)


def run_stage(flags, inputs, out_shapes):
    coarse, second, project, sends, local = flags
    kernel = functools.partial(stage_kernel, coarse, second, project, sends, local)
    return pl.pallas_call(
        kernel,
        out_shape=out_shapes,
        in_specs=[_vmem() for _ in inputs],
        out_specs=[_vmem() for _ in out_shapes],
        compiler_params=pltpu.CompilerParams(vmem_limit_bytes=48 * 1024 * 1024),
    )(*inputs)


def setup_kernel(local, fields, u_ref, vt_ref, packed_ref, tab_ref, v7_out, m7_out, pl_out, pr_out,
                 pre_out, stc_out, sw_out, *send_refs):
    rows = local * fields
    views = table_views(tab_ref, rows, local)
    lift_ref = views["lift_t"]
    g7_ref = views["g7"]
    tm_ref = views["tm"]
    fsel_ref = views["fsel"]
    bcast = views["bcast"][...]
    lanes = lax.broadcasted_iota(jnp.int32, (local, 6 * LANE), 1) // LANE
    sign = jnp.where(lanes % 2 == 0, -1.0, 1.0)
    fvg = []
    mvg = []
    for d in range(3):
        vt = vt_ref[d]
        fv = _dot(vt, lift_ref[...]).astype(bf16)
        v7_out[d] = _dot(bcast, fv).astype(bf16)
        fvg.append(_dot(fv, g7_ref[...]))

    def by_block(parts):
        return jnp.where(lanes < 2, parts[0], jnp.where(lanes < 4, parts[1], parts[2]))

    m7 = jnp.minimum(sign * by_block(fvg), 0.0)
    m7_out[...] = _dot(bcast, m7.astype(bf16))
    eye16 = jnp.where(
        lax.broadcasted_iota(jnp.int32, (local, LANE), 0)
        == lax.broadcasted_iota(jnp.int32, (local, LANE), 1), 1.0, 0.0
    ).astype(bf16)
    p_hi, p_mid, p_lo = _split(packed_ref[...])
    packed = (_dot_t(eye16, p_hi) + _dot_t(eye16, p_mid)) + _dot_t(eye16, p_lo)
    rep = _dot(bcast, packed.astype(bf16))
    row_f = (lax.broadcasted_iota(jnp.int32, (rows, 1), 0) % fields).astype(f32)
    cols = lax.broadcasted_iota(jnp.int32, (rows, rows), 1).astype(f32)
    for side in range(6):
        code = rep[:, side : side + 1]
        far = code >= local
        target = (code - jnp.where(far, float(local), 0.0)) * fields + row_f
        hit = cols == target
        pl_out[side] = jnp.where(hit & ~far, 1.0, 0.0).astype(bf16)
        if side in SEND_FACES:
            pr_out[SEND_FACES.index(side)] = jnp.where(hit & far, 1.0, 0.0).astype(bf16)
    sw_out[...] = rep[:, 6:7]
    pre_out[...] = packed[:, 7:8]
    stc_out[...] = _exact_right(fsel_ref[...], packed)[:, 8:9]
    write_sends(send_refs, _dot(u_ref[...].astype(bf16), g7_ref[...]).astype(bf16))


def late_kernel(local, fields, vt_ref, packed_ref, tab_ref, v3_out, m3_out, hinfo_out,
                cnt_l_out, cnt_r_out, sel_l_out, sel_r_out):
    rows = local * fields
    views = table_views(tab_ref, rows, local)
    tm_ref = views["tm"]
    bcast = views["bcast"][...]
    lanes = lax.broadcasted_iota(jnp.int32, (local, 6 * LANE), 1) // LANE
    sign = jnp.where(lanes % 2 == 0, -1.0, 1.0)
    mvg = []
    for d in range(3):
        vt = vt_ref[d]
        v3_out[d] = _dot(bcast, vt)
        mvg.append((_dot(vt, tm_ref[0]) + _dot(vt, tm_ref[1])) + _dot(vt, tm_ref[2]))
    by_block = jnp.where(lanes < 2, mvg[0], jnp.where(lanes < 4, mvg[1], mvg[2]))
    m3_out[...] = _exact_right(bcast, jnp.minimum(sign * by_block, 0.0))
    eye16 = jnp.where(
        lax.broadcasted_iota(jnp.int32, (local, LANE), 0)
        == lax.broadcasted_iota(jnp.int32, (local, LANE), 1), 1.0, 0.0
    ).astype(bf16)
    p_hi, p_mid, p_lo = _split(packed_ref[...])
    packed = (_dot_t(eye16, p_hi) + _dot_t(eye16, p_mid)) + _dot_t(eye16, p_lo)
    curve_count = lax.axis_size("curve")
    curve_pos = lax.axis_index("curve")
    left_f = ((curve_pos + curve_count - 1) % curve_count).astype(f32)
    right_f = ((curve_pos + 1) % curve_count).astype(f32)
    first_f = jnp.where(curve_pos == 0, 1.0, 0.0)
    last_f = jnp.where(curve_pos == curve_count - 1, 1.0, 0.0)
    stay_sw = packed[:, 6:7] < 0.5
    go_left = (packed[:, 9:10] == left_f) & stay_sw
    go_right = (packed[:, 9:10] == right_f) & stay_sw
    stays = stay_sw & ~go_left & ~go_right
    lane16 = lax.broadcasted_iota(jnp.int32, (local, LANE), 1)
    marks = jnp.where(
        lane16 == 0, go_left.astype(f32),
        jnp.where(lane16 == 1, go_right.astype(f32), jnp.where(lane16 == 2, stays.astype(f32), 0.0)),
    ).astype(bf16)
    er = lax.broadcasted_iota(jnp.int32, (local, local), 0)
    ec = lax.broadcasted_iota(jnp.int32, (local, local), 1)
    before = _dot(jnp.where(ec < er, 1.0, 0.0).astype(bf16), marks)
    totals = _dot(jnp.ones((local, local), bf16), marks)
    info = jnp.where(lane16 < 3, marks.astype(f32), 0.0)
    for k in range(3):
        info = jnp.where(lane16 == 3 + k, before[:, k : k + 1], info)
    info = jnp.where(lane16 == 6, totals[:, 2:3], info)
    info = jnp.where(lane16 == 7, first_f, info)
    info = jnp.where(lane16 == 8, last_f, info)
    hinfo = _dot(bcast, info.astype(bf16))
    hinfo_out[...] = hinfo
    cnt_l_out[...] = jnp.broadcast_to(totals[0:1, 0:1], cnt_l_out.shape)
    cnt_r_out[...] = jnp.broadcast_to(totals[0:1, 1:2], cnt_r_out.shape)
    rf = lax.broadcasted_iota(jnp.int32, (rows, LANE), 0) % fields
    cc = lax.broadcasted_iota(jnp.int32, (rows, LANE), 1)
    eye = jnp.where(
        lax.broadcasted_iota(jnp.int32, (MOVE_CAP * fields, LANE), 0)
        == lax.broadcasted_iota(jnp.int32, (MOVE_CAP * fields, LANE), 1), 1.0, 0.0
    ).astype(bf16)
    for mark_lane, rank_lane, out in ((0, 3, sel_l_out), (1, 4, sel_r_out)):
        hit = (
            (hinfo[:, mark_lane : mark_lane + 1] > 0.5)
            & (hinfo[:, rank_lane : rank_lane + 1] == (cc // fields).astype(f32))
            & (rf == cc % fields)
            & (cc < MOVE_CAP * fields)
        )
        out[...] = _dot_t(eye, jnp.where(hit, 1.0, 0.0).astype(bf16)).astype(bf16)


def final_kernel(fields, hold, home_ref, from_l_ref, from_r_ref, hinfo_ref, out_ref):
    hinfo = hinfo_ref[...]
    moved = MOVE_CAP * fields
    n_l = from_l_ref[moved : moved + 1, 0:1]
    n_r = from_r_ref[moved : moved + 1, 0:1]
    n_h = hinfo[0:1, 6:7]
    first = hinfo[0:1, 7:8] > 0.5
    final = hinfo[0:1, 8:9] > 0.5
    off_l = jnp.where(first, n_h + n_r, jnp.where(final, n_r, 0.0))
    off_h = jnp.where(first, 0.0, jnp.where(final, n_r + n_l, n_l))
    off_r = jnp.where(first, n_h, jnp.where(final, 0.0, n_l + n_h))
    width = hold * fields
    eye = jnp.where(
        lax.broadcasted_iota(jnp.int32, (width, LANE), 0)
        == lax.broadcasted_iota(jnp.int32, (width, LANE), 1), 1.0, 0.0
    ).astype(bf16)

    def gather(values, valid, pos):
        count = values.shape[0]
        rf = lax.broadcasted_iota(jnp.int32, (count, LANE), 0) % fields
        cc = lax.broadcasted_iota(jnp.int32, (count, LANE), 1)
        hit = valid & (pos == (cc // fields).astype(f32)) & (rf == cc % fields) & (cc < width)
        pick = _dot_t(eye, jnp.where(hit, 1.0, 0.0).astype(bf16)).astype(bf16)
        return _exact_right(pick, values)

    total = gather(home_ref[...], hinfo[:, 2:3] > 0.5, off_h + hinfo[:, 5:6])
    slot = (lax.broadcasted_iota(jnp.int32, (moved, 1), 0) // fields).astype(f32)
    total = total + gather(from_l_ref[0:moved, :], slot < n_l, off_l + slot)
    total = total + gather(from_r_ref[0:moved, :], slot < n_r, off_r + slot)
    out_ref[...] = total


def setup_entry(local, fields, n_in, n_out, *refs):
    sources = refs[:n_in]
    outs = refs[n_in : n_in + n_out]
    n_tab = 1
    n_own = n_in - n_tab
    buffers = refs[n_in + n_out : n_in + n_out + n_own]
    sems = refs[n_in + n_out + n_own]
    targets = list(buffers) + list(outs[n_out - n_tab :])
    copies = [
        pltpu.make_async_copy(sources[i], targets[i], sems.at[i]) for i in range(n_in)
    ]
    for copy in copies:
        copy.start()
    for copy in copies:
        copy.wait()
    setup_kernel(local, fields, *targets, *outs[: n_out - n_tab])


def per_device(state, velocity, pre_exp, stoich, neighbours, switch, new_owner):
    tab = make_tables()
    local_count = state.shape[0]
    field_count = state.shape[1]
    rows = local_count * field_count
    curve_count = lax.axis_size("curve")
    curve_pos = lax.axis_index("curve")
    device_id = lax.axis_index("slab") * curve_count + curve_pos
    first_global = device_id * local_count
    positions = jnp.arange(local_count, dtype=jnp.int32)

    near_device = neighbours // local_count
    near_local = neighbours - near_device * local_count
    remote = near_device != device_id
    codes = (near_local + local_count * remote.astype(jnp.int32)).astype(f32)
    left_pos = (curve_pos + curve_count - 1) % curve_count
    right_pos = (curve_pos + 1) % curve_count
    sto_col = jnp.pad(stoich, (0, local_count - field_count))
    packed_t = jnp.concatenate(
        [
            jnp.transpose(codes),
            jnp.stack([switch.astype(f32), pre_exp, sto_col, new_owner.astype(f32)]),
        ]
    )
    packed = jnp.pad(packed_t, ((0, local_count - 10), (0, LANE - local_count)))
    fsel_np = np.arange(rows)[:, None] % field_count == np.arange(local_count)[None, :]
    vt = jnp.transpose(velocity, (0, 2, 1))
    row_elem = np.arange(rows) // field_count
    bcast_np = row_elem[:, None] == np.arange(local_count)[None, :]
    pick_rows = (np.arange(3)[:, None] + field_count * np.arange(local_count)[None, :]).reshape(-1)
    sel_np = pick_rows[:, None] == np.arange(rows)[None, :]
    n7 = P7**3
    n3 = P3**3
    layout = table_layout(rows, local_count)
    table_np = np.zeros((table_rows(), 6 * LANE), np.float32)
    for d in (1, 2):
        block = tab["d7t"][d][:LANE, :LANE].astype(np.float32)
        assert np.array_equal(
            tab["d7t"][d].astype(np.float32), np.kron(np.eye(n7 // LANE), block)
        )
    pieces = {
        "g7": tab["g7"][None],
        "tm": tab["tm"],
        "mdst": np.transpose(tab["mds"], (0, 2, 1)),
        "dx": tab["d7t"][0:1],
        "byz": np.stack([tab["d7t"][1][:LANE, :LANE], tab["d7t"][2][:LANE, :LANE]]),
        "lift_t": tab["lift"].T[None],
        "pj": np.transpose(tab["pjt"], (0, 2, 1)),
        "bcast": bcast_np[None],
        "sel": sel_np[None],
        "fsel": fsel_np[None],
        "d3t": tab["d3t"],
    }
    filled = np.zeros(table_np.shape, bool)
    for name, (start, count, width, lane0) in layout.items():
        parts = np.asarray(pieces[name], np.float32)
        for k in range(parts.shape[0]):
            window = (slice(start + k * count, start + (k + 1) * count), slice(lane0, lane0 + width))
            assert not filled[window].any()
            filled[window] = True
            table_np[window] = parts[k]
    table = jnp.asarray(to_bf16(table_np))

    send_shape = jax.ShapeDtypeStruct((rows, LANE), bf16)
    sends_shape = [send_shape, send_shape, jax.ShapeDtypeStruct((2 * rows, LANE), bf16)]
    u_shape = jax.ShapeDtypeStruct((rows, P7**3), f32)
    c_shape = jax.ShapeDtypeStruct((rows, P3**3), f32)

    def exchange(sends):
        face0, face1, faces_z = sends
        from_prev = shifted(faces_z, "slab", 1)
        if lax.axis_size("slab") == 2:
            from_next = from_prev
        else:
            from_next = shifted(faces_z, "slab", -1)
        return [shifted(face1, "curve", 1), shifted(face0, "curve", -1), from_prev, from_next]

    setup_out = [
        jax.ShapeDtypeStruct((3, rows, P7**3), bf16),
        jax.ShapeDtypeStruct((rows, 6 * LANE), f32),
        jax.ShapeDtypeStruct((6, rows, rows), bf16),
        jax.ShapeDtypeStruct((len(SEND_FACES), rows, rows), bf16),
        jax.ShapeDtypeStruct((local_count, 1), f32),
        jax.ShapeDtypeStruct((rows, 1), f32),
        jax.ShapeDtypeStruct((rows, 1), f32),
    ] + sends_shape
    late_out = [
        jax.ShapeDtypeStruct((3, rows, P3**3), f32),
        jax.ShapeDtypeStruct((rows, 6 * LANE), f32),
        jax.ShapeDtypeStruct((rows, LANE), f32),
        jax.ShapeDtypeStruct((8, LANE), f32),
        jax.ShapeDtypeStruct((8, LANE), f32),
        jax.ShapeDtypeStruct((MOVE_CAP * field_count, rows), bf16),
        jax.ShapeDtypeStruct((MOVE_CAP * field_count, rows), bf16),
    ]
    setup_out = setup_out + [jax.ShapeDtypeStruct(table.shape, table.dtype)]
    u0 = state.reshape(rows, P7**3)
    setup_in = [u0, vt, packed, table]
    res = pl.pallas_call(
        functools.partial(setup_entry, local_count, field_count, len(setup_in), len(setup_out)),
        out_shape=setup_out,
        in_specs=[pl.BlockSpec(memory_space=pltpu.HBM) for _ in setup_in],
        out_specs=[_vmem() for _ in setup_out],
        scratch_shapes=[pltpu.VMEM(x.shape, x.dtype) for x in setup_in[:3]]
        + [pltpu.SemaphoreType.DMA((len(setup_in),))],
        compiler_params=pltpu.CompilerParams(vmem_limit_bytes=24 * 1024 * 1024),
    )(*setup_in)
    v7, m7, p_local, p_remote, pre, stc, sw = res[:7]
    sends = res[7:10]
    table = res[10]
    v3, m3, hinfo, cnt_l, cnt_r, sel_l, sel_r = pl.pallas_call(
        functools.partial(late_kernel, local_count, field_count),
        out_shape=late_out,
        in_specs=[_vmem() for _ in range(3)],
        out_specs=[_vmem() for _ in late_out],
        compiler_params=pltpu.CompilerParams(vmem_limit_bytes=24 * 1024 * 1024),
    )(vt, packed, table)
    common = [p_local, p_remote, v7, m7, pre, stc, table]
    recv = exchange(sends)
    bulk_tabs = [v7, pre, stc, table]
    (bulk7,) = run_bulk(False, local_count, [u0] + bulk_tabs, [u_shape])
    res = run_stage(
        (False, False, False, True, local_count),
        [u0] + recv + common + [bulk7],
        [u_shape] + sends_shape,
    )
    first, sends = res[0], res[1:]
    recv = exchange(sends)
    (bulk7,) = run_bulk(False, local_count, [first] + bulk_tabs, [u_shape])
    res = run_stage(
        (False, True, True, True, local_count),
        [first, u0] + recv + common + [sw, bulk7],
        [u_shape, c_shape] + sends_shape,
    )
    after, coarse, sends = res[0], res[1], res[2:]
    recv = exchange(sends)
    mixed_tail = [v3, m3, sw]
    bulk7, bulk3 = run_bulk(True, local_count, [after, coarse] + bulk_tabs + [v3], [u_shape, c_shape])
    res = run_stage(
        (True, False, False, True, local_count),
        [after, coarse] + recv + common + mixed_tail + [bulk7, bulk3],
        [u_shape, c_shape] + sends_shape,
    )
    first7, first3, sends = res[0], res[1], res[2:]
    recv = exchange(sends)
    pay_shape = jax.ShapeDtypeStruct((MOVE_CAP * field_count + 8, P7**3), f32)
    bulk7, bulk3 = run_bulk(True, local_count, [first7, first3] + bulk_tabs + [v3], [u_shape, c_shape])
    res = run_stage(
        (True, True, False, False, local_count),
        [first7, first3, after, coarse] + recv + common + mixed_tail
        + [sel_l, sel_r, cnt_l, cnt_r, bulk7, bulk3],
        [u_shape, c_shape, pay_shape, pay_shape],
    )
    final7, final3, pay_l, pay_r = res
    from_right = shifted(pay_l, "curve", -1)
    from_left = shifted(pay_r, "curve", 1)
    held = pl.pallas_call(
        functools.partial(final_kernel, field_count, HOLD7),
        out_shape=jax.ShapeDtypeStruct((HOLD7 * field_count, P7**3), f32),
        in_specs=[_vmem() for _ in range(4)],
        out_specs=_vmem(),
    )(final7, from_left, from_right, hinfo)
    state7_out = held.reshape(HOLD7, field_count, P7**3)
    state3_out = final3.reshape(local_count, field_count * P3**3)
    return (state7_out, state3_out)


def solution(mesh):
    return jax.shard_map(
        per_device,
        mesh=mesh,
        in_specs=(
            P(("slab", "curve"), None, None),
            P(None, None, ("slab", "curve")),
            P(("slab", "curve")),
            P(),
            P(("slab", "curve"), None),
            P(("slab", "curve")),
            P(("slab", "curve")),
        ),
        out_specs=(P(("slab", "curve"), None, None), P(("slab", "curve"), None)),
        check_vma=False,
    )
```

```python
import functools

import jax
import jax.numpy as jnp
import ml_dtypes
import numpy as np
from jax import lax
from jax.experimental import pallas as pl
from jax.experimental.pallas import tpu as pltpu
from jax.sharding import PartitionSpec as P

P7 = 8
P3 = 4
MOVE_CAP = 2
HOLD7 = 12
LANE = 128

TIME_STEP = 0.002
ACTIVATION = 1.5
SIDE_SIGNS = (-1.0, 1.0, -1.0, 1.0, -1.0, 1.0)
OPPOSITE = (1, 0, 3, 2, 5, 4)
SEND_FACES = (0, 1, 4, 5)
missing_id = 1 << 30

f32 = jnp.float32
bf16 = jnp.bfloat16


def shifted(value, axis, steps):
    count = lax.axis_size(axis)
    pairs = [(source, (source + steps) % count) for source in range(count)]
    return lax.ppermute(value, axis, pairs)


def lobatto_points(number):
    return -np.cos(np.pi * np.arange(number) / (number - 1))


def lagrange_weights(points):
    weights = np.ones(points.shape[0])
    for row_id in range(points.shape[0]):
        for col_id in range(points.shape[0]):
            if col_id != row_id:
                weights[row_id] = weights[row_id] / (points[row_id] - points[col_id])
    return weights


def derivative_matrix(points):
    weights = lagrange_weights(points)
    number = points.shape[0]
    matrix = np.zeros((number, number))
    for row_id in range(number):
        for col_id in range(number):
            if col_id != row_id:
                matrix[row_id, col_id] = (
                    weights[col_id] / weights[row_id] / (points[row_id] - points[col_id])
                )
        matrix[row_id, row_id] = -np.sum(matrix[row_id])
    return matrix


def interpolation_matrix(source, target):
    matrix = np.ones((target.shape[0], source.shape[0]))
    for col_id in range(source.shape[0]):
        for other_id in range(source.shape[0]):
            if other_id != col_id:
                matrix[:, col_id] = (
                    matrix[:, col_id]
                    * (target - source[other_id])
                    / (source[col_id] - source[other_id])
                )
    return matrix


def spread_three(matrix, identity):
    return (
        np.kron(matrix, np.kron(identity, identity)),
        np.kron(identity, np.kron(matrix, identity)),
        np.kron(identity, np.kron(identity, matrix)),
    )


def face_nodes(extent):
    grid = np.arange(extent**3).reshape(extent, extent, extent)
    last = extent - 1
    pieces = (grid[0], grid[last], grid[:, 0], grid[:, last], grid[:, :, 0], grid[:, :, last])
    return [piece.reshape(-1) for piece in pieces]


def to_bf16(x):
    return np.asarray(np.asarray(x, np.float32).astype(ml_dtypes.bfloat16))


def split_parts(x):
    x = np.asarray(x, np.float32)
    hi = x.astype(ml_dtypes.bfloat16)
    rest = x - hi.astype(np.float32)
    mid = rest.astype(ml_dtypes.bfloat16)
    lo = (rest - mid.astype(np.float32)).astype(ml_dtypes.bfloat16)
    return np.stack([hi, mid, lo])


def make_tables():
    fine_points = lobatto_points(P7)
    coarse_points = lobatto_points(P3)
    fine_derivs = spread_three(derivative_matrix(fine_points), np.eye(P7))
    coarse_derivs = spread_three(derivative_matrix(coarse_points), np.eye(P3))
    downward = interpolation_matrix(fine_points, coarse_points)
    upward = interpolation_matrix(coarse_points, fine_points)
    d7t = np.stack([to_bf16(m.T) for m in fine_derivs])
    d3t = np.stack([to_bf16(m).T for m in coarse_derivs])
    lift_table = to_bf16(np.kron(upward, np.kron(upward, upward)))
    projection = np.asarray(np.kron(downward, np.kron(downward, downward)), np.float32)
    mortar_up = np.asarray(np.kron(upward, upward), np.float32)
    mortar_down = np.asarray(np.kron(downward, downward), np.float32)
    nodes7 = face_nodes(P7)
    nodes3 = face_nodes(P3)
    n7 = P7**3
    n3 = P3**3
    g7 = np.zeros((n7, 6 * LANE), np.float32)
    tm = np.zeros((n3, 6 * LANE), np.float32)
    mds = np.zeros((6 * LANE, n3), np.float32)
    for side in range(6):
        for q, node in enumerate(nodes7[side]):
            g7[node, side * LANE + q] = 1.0
        for k, node in enumerate(nodes3[side]):
            tm[node, side * LANE : side * LANE + P7 * P7] = mortar_up[:, k]
            mds[side * LANE : side * LANE + P7 * P7, node] = mortar_down[k, :]
    tables = {
        "d7t": to_bf16(d7t),
        "d3t": to_bf16(d3t),
        "lift": lift_table,
        "mortar_up": mortar_up,
        "g7": to_bf16(g7),
        "tm": split_parts(tm),
        "mds": split_parts(mds),
        "pjt": split_parts(projection.T),
        "nodes7": nodes7,
        "nodes3": nodes3,
    }
    return tables


def _dot(a, b):
    return jnp.dot(a, b, preferred_element_type=f32)


def _split(x):
    hi = x.astype(bf16)
    rest = x - hi.astype(f32)
    mid = rest.astype(bf16)
    lo = (rest - mid.astype(f32)).astype(bf16)
    return hi, mid, lo


def _exact_left(x, table):
    hi, mid, lo = _split(x)
    return (_dot(hi, table) + _dot(mid, table)) + _dot(lo, table)


def _dot_t(a, b):
    return lax.dot_general(a, b, (((1,), (1,)), ((), ())), preferred_element_type=f32)


def _exact_left_t(x, table):
    hi, mid, lo = _split(x)
    return (_dot_t(hi, table) + _dot_t(mid, table)) + _dot_t(lo, table)


def _exact_right(table, x):
    hi, mid, lo = _split(x)
    return (_dot(table, hi) + _dot(table, mid)) + _dot(table, lo)


def _full_t(x, parts_ref):
    xh, xm, xl = _split(x)
    bh = parts_ref[0]
    bm = parts_ref[1]
    bl = parts_ref[2]
    return _dot_t(xh, bh) + (_dot_t(xh, bm) + _dot_t(xm, bh)) + (
        _dot_t(xh, bl) + _dot_t(xm, bm) + _dot_t(xl, bh)
    )


class View:
    def __init__(self, ref, start, rows, width, lane0):
        self.ref = ref
        self.start = start
        self.rows = rows
        self.width = width
        self.lane0 = lane0

    def __getitem__(self, k):
        if k is Ellipsis:
            k = 0
        top = self.start + k * self.rows
        return self.ref[top : top + self.rows, self.lane0 : self.lane0 + self.width]


def table_layout(rows, local):
    n7 = P7**3
    n3 = P3**3
    wide = 6 * LANE
    base = n7 + 6 * n3
    side = 4 * LANE
    return {
        "g7": (0, n7, wide, 0),
        "tm": (n7, n3, wide, 0),
        "mdst": (n7 + 3 * n3, n3, wide, 0),
        "dx": (base, n7, n7, 0),
        "lift_t": (base + n7, n3, n7, 0),
        "pj": (base + n7 + n3, n3, n7, 0),
        "byz": (base, LANE, LANE, 5 * LANE),
        "bcast": (base, rows, local, side),
        "sel": (base + rows, 3 * local, rows, side),
        "fsel": (base + rows + 3 * local, rows, local, side),
        "d3t": (base + 2 * rows + 3 * local, n3, n3, side),
    }


def table_rows():
    return P7**3 + 6 * P3**3 + P7**3 + 4 * P3**3


def table_views(tab_ref, rows, local):
    return {
        name: View(tab_ref, start, count, width, lane0)
        for name, (start, count, width, lane0) in table_layout(rows, local).items()
    }


def _full(x, parts_ref):
    xh, xm, xl = _split(x)
    bh = parts_ref[0]
    bm = parts_ref[1]
    bl = parts_ref[2]
    return _dot(xh, bh) + (_dot(xh, bm) + _dot(xm, bh)) + (
        _dot(xh, bl) + _dot(xm, bm) + _dot(xl, bh)
    )


def _rate_source(values, pre, stc, bc, sel, local):
    picked = _exact_right(sel, values)
    v0 = picked[0:local]
    v1 = picked[local : 2 * local]
    v2 = picked[2 * local : 3 * local]
    rate = pre * jnp.exp(-ACTIVATION * jnp.exp(-v0)) * v1 * v2
    return stc * _exact_right(bc, rate)


def recv_block(recv, side):
    ref = recv[side]
    if side in (4, 5):
        rows = ref.shape[0] // 2
        top = 0 if side == 4 else rows
        return ref[top : top + rows, :]
    return ref[...]


def write_sends(out_refs, send):
    rows = send.shape[0]
    out_refs[0][...] = send[:, 0:LANE]
    out_refs[1][...] = send[:, LANE : 2 * LANE]
    out_refs[2][0:rows, :] = send[:, 5 * LANE : 6 * LANE]
    out_refs[2][rows : 2 * rows, :] = send[:, 4 * LANE : 5 * LANE]


def stage_kernel(coarse, second, project, sends, local, *refs):
    refs = list(refs)

    def take():
        return refs.pop(0)

    u_ref = take()
    c_ref = take() if coarse else None
    bu_ref = take() if second else None
    bc_ref = take() if (second and coarse) else None
    recv = {s: take() for s in SEND_FACES}
    pl_ref = take()
    pr_ref = take()
    v7_ref = take()
    m7_ref = take()
    pre_ref = take()
    stc_ref = take()
    views = table_views(take(), u_ref.shape[0], local)
    bc_tab = views["bcast"]
    sel_tab = views["sel"]
    g7_ref = views["g7"]
    d3_ref = views["d3t"]
    mds_ref = views["mdst"]
    tm_ref = views["tm"]
    pj_ref = views["pj"]
    if coarse:
        v3_ref = take()
        m3_ref = take()
    if coarse or project:
        sw_ref = take()
    last = coarse and not sends
    if last:
        sel_l_ref = take()
        sel_r_ref = take()
        cnt_l_ref = take()
        cnt_r_ref = take()
    res7_ref = take()
    res3_ref = take() if coarse else None
    out_u = take()
    out_c = take() if (coarse or project) else None
    out_send = [take() for _ in range(3)] if sends else None
    if last:
        pay_l_ref = take()
        pay_r_ref = take()

    pre = pre_ref[...]
    stc = stc_ref[...]
    bcast = bc_tab[...]
    sel = sel_tab[...]
    u = u_ref[...]
    trace7 = _dot(u.astype(bf16), g7_ref[...])
    if coarse:
        c = c_ref[...]
        trace3 = _full(c, tm_ref).astype(bf16).astype(f32)
        switched = sw_ref[...] > 0.5
        own = jnp.where(switched, trace3, trace7)
    else:
        own = trace7
    own_b = own.astype(bf16)
    near_blocks = []
    for side in range(6):
        other = OPPOSITE[side]
        block = own_b[:, other * LANE : (other + 1) * LANE]
        near = _dot(pl_ref[side], block)
        if side in SEND_FACES:
            k = SEND_FACES.index(side)
            near = near + _dot(pr_ref[k], recv_block(recv, side))
        near_blocks.append(near)
    near = jnp.concatenate(near_blocks, axis=1)

    result = res7_ref[...]
    jump = (P7 * (P7 - 1) / 2.0) * (m7_ref[...] * (trace7 - near))
    rate7 = result + _exact_left_t(jump, g7_ref[...])

    if coarse:
        result3 = res3_ref[...]
        jump3 = m3_ref[...] * (trace3 - near)
        rate3 = result3 + (P3 * (P3 - 1) / 2.0) * _full_t(jump3, mds_ref)

    if second:
        new_u = 0.5 * (bu_ref[...] + u + TIME_STEP * rate7)
    else:
        new_u = u + TIME_STEP * rate7
    out_u[...] = new_u
    new_c = None
    if coarse:
        if second:
            new_c = 0.5 * (bc_ref[...] + c + TIME_STEP * rate3)
        else:
            new_c = c + TIME_STEP * rate3
        if last:
            out_c[...] = jnp.where(sw_ref[...] > 0.5, new_c, 0.0)
            moved = sel_l_ref.shape[0]
            pay_l_ref[0:moved, :] = _exact_right(sel_l_ref[...], new_u)
            pay_r_ref[0:moved, :] = _exact_right(sel_r_ref[...], new_u)
            tail = (pay_l_ref.shape[0] - moved, pay_l_ref.shape[1])
            pay_l_ref[moved:, :] = jnp.broadcast_to(cnt_l_ref[0:1, 0:1], tail)
            pay_r_ref[moved:, :] = jnp.broadcast_to(cnt_r_ref[0:1, 0:1], tail)
        else:
            out_c[...] = new_c
    if project:
        new_c = _full_t(new_u, pj_ref)
        out_c[...] = new_c
    if sends:
        send7 = _dot(new_u.astype(bf16), g7_ref[...])
        if new_c is not None:
            send3 = _full(new_c, tm_ref).astype(bf16).astype(f32)
            send = jnp.where(sw_ref[...] > 0.5, send3, send7)
        else:
            send = send7
        write_sends(out_send, send.astype(bf16))


def _vmem():
    return pl.BlockSpec(memory_space=pltpu.VMEM)


def bulk_kernel(coarse, local, *refs):
    refs = list(refs)
    u_ref = refs.pop(0)
    c_ref = refs.pop(0) if coarse else None
    v7_ref, pre_ref, stc_ref = refs.pop(0), refs.pop(0), refs.pop(0)
    views = table_views(refs.pop(0), u_ref.shape[0], local)
    v3_ref = refs.pop(0) if coarse else None
    out7 = refs.pop(0)
    out3 = refs.pop(0) if coarse else None
    pre = pre_ref[...]
    stc = stc_ref[...]
    bcast = views["bcast"][...]
    sel = views["sel"][...]
    u = u_ref[...]
    fluxes = [(v7_ref[d].astype(f32) * u).astype(bf16) for d in range(3)]
    divergence = _dot(fluxes[0], views["dx"][0])
    by = views["byz"][0]
    bz = views["byz"][1]
    chunks = []
    for k in range(u.shape[1] // LANE):
        part = slice(k * LANE, (k + 1) * LANE)
        chunks.append(_dot(fluxes[1][:, part], by) + _dot(fluxes[2][:, part], bz))
    divergence = divergence + jnp.concatenate(chunks, axis=1)
    out7[...] = _rate_source(u, pre, stc, bcast, sel, local) - divergence
    if coarse:
        c = c_ref[...]
        div3 = None
        for d in range(3):
            flux3 = (v3_ref[d] * c).astype(bf16)
            term = _dot(flux3, views["d3t"][d])
            div3 = term if div3 is None else div3 + term
        out3[...] = _rate_source(c, pre, stc, bcast, sel, local) - div3


def run_bulk(coarse, local, inputs, out_shapes):
    return pl.pallas_call(
        functools.partial(bulk_kernel, coarse, local),
        out_shape=out_shapes,
        in_specs=[_vmem() for _ in inputs],
        out_specs=[_vmem() for _ in out_shapes],
        compiler_params=pltpu.CompilerParams(vmem_limit_bytes=24 * 1024 * 1024),
    )(*inputs)


def run_stage(flags, inputs, out_shapes):
    coarse, second, project, sends, local = flags
    kernel = functools.partial(stage_kernel, coarse, second, project, sends, local)
    return pl.pallas_call(
        kernel,
        out_shape=out_shapes,
        in_specs=[_vmem() for _ in inputs],
        out_specs=[_vmem() for _ in out_shapes],
        compiler_params=pltpu.CompilerParams(vmem_limit_bytes=48 * 1024 * 1024),
    )(*inputs)


def setup_kernel(local, fields, u_ref, vt_ref, packed_ref, tab_ref, v7_out, m7_out,
                 pre_out, stc_out, *send_refs):
    rows = local * fields
    views = table_views(tab_ref, rows, local)
    lift_ref = views["lift_t"]
    g7_ref = views["g7"]
    tm_ref = views["tm"]
    fsel_ref = views["fsel"]
    bcast = views["bcast"][...]
    lanes = lax.broadcasted_iota(jnp.int32, (local, 6 * LANE), 1) // LANE
    sign = jnp.where(lanes % 2 == 0, -1.0, 1.0)
    fvg = []
    mvg = []
    for d in range(3):
        vt = vt_ref[d]
        fv = _dot(vt, lift_ref[...]).astype(bf16)
        v7_out[d] = _dot(bcast, fv).astype(bf16)
        fvg.append(_dot(fv, g7_ref[...]))

    def by_block(parts):
        return jnp.where(lanes < 2, parts[0], jnp.where(lanes < 4, parts[1], parts[2]))

    m7 = jnp.minimum(sign * by_block(fvg), 0.0)
    m7_out[...] = _dot(bcast, m7.astype(bf16))
    eye16 = jnp.where(
        lax.broadcasted_iota(jnp.int32, (local, LANE), 0)
        == lax.broadcasted_iota(jnp.int32, (local, LANE), 1), 1.0, 0.0
    ).astype(bf16)
    p_hi, p_mid, p_lo = _split(packed_ref[...])
    packed = (_dot_t(eye16, p_hi) + _dot_t(eye16, p_mid)) + _dot_t(eye16, p_lo)
    pre_out[...] = packed[:, 7:8]
    stc_out[...] = _exact_right(fsel_ref[...], packed)[:, 8:9]
    write_sends(send_refs, _dot(u_ref[...].astype(bf16), g7_ref[...]).astype(bf16))


def near_kernel(local, fields, packed_ref, tab_ref, pl_out, pr_out, sw_out):
    rows = local * fields
    bcast = table_views(tab_ref, rows, local)["bcast"][...]
    eye16 = jnp.where(
        lax.broadcasted_iota(jnp.int32, (local, LANE), 0)
        == lax.broadcasted_iota(jnp.int32, (local, LANE), 1), 1.0, 0.0
    ).astype(bf16)
    packed = _dot_t(eye16, packed_ref[...].astype(bf16))
    rep = _dot(bcast, packed.astype(bf16))
    row_f = (lax.broadcasted_iota(jnp.int32, (rows, 1), 0) % fields).astype(f32)
    cols = lax.broadcasted_iota(jnp.int32, (rows, rows), 1).astype(f32)
    for side in range(6):
        code = rep[:, side : side + 1]
        far = code >= local
        target = (code - jnp.where(far, float(local), 0.0)) * fields + row_f
        hit = cols == target
        pl_out[side] = jnp.where(hit & ~far, 1.0, 0.0).astype(bf16)
        if side in SEND_FACES:
            pr_out[SEND_FACES.index(side)] = jnp.where(hit & far, 1.0, 0.0).astype(bf16)
    sw_out[...] = rep[:, 6:7]


def late_kernel(local, fields, vt_ref, packed_ref, tab_ref, v3_out, m3_out, hinfo_out,
                cnt_l_out, cnt_r_out, sel_l_out, sel_r_out):
    rows = local * fields
    views = table_views(tab_ref, rows, local)
    tm_ref = views["tm"]
    bcast = views["bcast"][...]
    lanes = lax.broadcasted_iota(jnp.int32, (local, 6 * LANE), 1) // LANE
    sign = jnp.where(lanes % 2 == 0, -1.0, 1.0)
    mvg = []
    for d in range(3):
        vt = vt_ref[d]
        v3_out[d] = _dot(bcast, vt)
        mvg.append((_dot(vt, tm_ref[0]) + _dot(vt, tm_ref[1])) + _dot(vt, tm_ref[2]))
    by_block = jnp.where(lanes < 2, mvg[0], jnp.where(lanes < 4, mvg[1], mvg[2]))
    m3_out[...] = _exact_right(bcast, jnp.minimum(sign * by_block, 0.0))
    eye16 = jnp.where(
        lax.broadcasted_iota(jnp.int32, (local, LANE), 0)
        == lax.broadcasted_iota(jnp.int32, (local, LANE), 1), 1.0, 0.0
    ).astype(bf16)
    p_hi, p_mid, p_lo = _split(packed_ref[...])
    packed = (_dot_t(eye16, p_hi) + _dot_t(eye16, p_mid)) + _dot_t(eye16, p_lo)
    curve_count = lax.axis_size("curve")
    curve_pos = lax.axis_index("curve")
    left_f = ((curve_pos + curve_count - 1) % curve_count).astype(f32)
    right_f = ((curve_pos + 1) % curve_count).astype(f32)
    first_f = jnp.where(curve_pos == 0, 1.0, 0.0)
    last_f = jnp.where(curve_pos == curve_count - 1, 1.0, 0.0)
    stay_sw = packed[:, 6:7] < 0.5
    go_left = (packed[:, 9:10] == left_f) & stay_sw
    go_right = (packed[:, 9:10] == right_f) & stay_sw
    stays = stay_sw & ~go_left & ~go_right
    lane16 = lax.broadcasted_iota(jnp.int32, (local, LANE), 1)
    marks = jnp.where(
        lane16 == 0, go_left.astype(f32),
        jnp.where(lane16 == 1, go_right.astype(f32), jnp.where(lane16 == 2, stays.astype(f32), 0.0)),
    ).astype(bf16)
    er = lax.broadcasted_iota(jnp.int32, (local, local), 0)
    ec = lax.broadcasted_iota(jnp.int32, (local, local), 1)
    before = _dot(jnp.where(ec < er, 1.0, 0.0).astype(bf16), marks)
    totals = _dot(jnp.ones((local, local), bf16), marks)
    info = jnp.where(lane16 < 3, marks.astype(f32), 0.0)
    for k in range(3):
        info = jnp.where(lane16 == 3 + k, before[:, k : k + 1], info)
    info = jnp.where(lane16 == 6, totals[:, 2:3], info)
    info = jnp.where(lane16 == 7, first_f, info)
    info = jnp.where(lane16 == 8, last_f, info)
    hinfo = _dot(bcast, info.astype(bf16))
    hinfo_out[...] = hinfo
    cnt_l_out[...] = jnp.broadcast_to(totals[0:1, 0:1], cnt_l_out.shape)
    cnt_r_out[...] = jnp.broadcast_to(totals[0:1, 1:2], cnt_r_out.shape)
    rf = lax.broadcasted_iota(jnp.int32, (rows, LANE), 0) % fields
    cc = lax.broadcasted_iota(jnp.int32, (rows, LANE), 1)
    eye = jnp.where(
        lax.broadcasted_iota(jnp.int32, (MOVE_CAP * fields, LANE), 0)
        == lax.broadcasted_iota(jnp.int32, (MOVE_CAP * fields, LANE), 1), 1.0, 0.0
    ).astype(bf16)
    for mark_lane, rank_lane, out in ((0, 3, sel_l_out), (1, 4, sel_r_out)):
        hit = (
            (hinfo[:, mark_lane : mark_lane + 1] > 0.5)
            & (hinfo[:, rank_lane : rank_lane + 1] == (cc // fields).astype(f32))
            & (rf == cc % fields)
            & (cc < MOVE_CAP * fields)
        )
        out[...] = _dot_t(eye, jnp.where(hit, 1.0, 0.0).astype(bf16)).astype(bf16)


def final_kernel(fields, hold, home_ref, from_l_ref, from_r_ref, hinfo_ref, out_ref):
    hinfo = hinfo_ref[...]
    moved = MOVE_CAP * fields
    n_l = from_l_ref[moved : moved + 1, 0:1]
    n_r = from_r_ref[moved : moved + 1, 0:1]
    n_h = hinfo[0:1, 6:7]
    first = hinfo[0:1, 7:8] > 0.5
    final = hinfo[0:1, 8:9] > 0.5
    off_l = jnp.where(first, n_h + n_r, jnp.where(final, n_r, 0.0))
    off_h = jnp.where(first, 0.0, jnp.where(final, n_r + n_l, n_l))
    off_r = jnp.where(first, n_h, jnp.where(final, 0.0, n_l + n_h))
    width = hold * fields
    eye = jnp.where(
        lax.broadcasted_iota(jnp.int32, (width, LANE), 0)
        == lax.broadcasted_iota(jnp.int32, (width, LANE), 1), 1.0, 0.0
    ).astype(bf16)

    def gather(values, valid, pos):
        count = values.shape[0]
        rf = lax.broadcasted_iota(jnp.int32, (count, LANE), 0) % fields
        cc = lax.broadcasted_iota(jnp.int32, (count, LANE), 1)
        hit = valid & (pos == (cc // fields).astype(f32)) & (rf == cc % fields) & (cc < width)
        pick = _dot_t(eye, jnp.where(hit, 1.0, 0.0).astype(bf16)).astype(bf16)
        return _exact_right(pick, values)

    total = gather(home_ref[...], hinfo[:, 2:3] > 0.5, off_h + hinfo[:, 5:6])
    slot = (lax.broadcasted_iota(jnp.int32, (moved, 1), 0) // fields).astype(f32)
    total = total + gather(from_l_ref[0:moved, :], slot < n_l, off_l + slot)
    total = total + gather(from_r_ref[0:moved, :], slot < n_r, off_r + slot)
    out_ref[...] = total


def setup_entry(local, fields, n_in, n_out, *refs):
    sources = refs[:n_in]
    outs = refs[n_in : n_in + n_out]
    n_tab = 1
    n_own = n_in - n_tab
    buffers = refs[n_in + n_out : n_in + n_out + n_own]
    sems = refs[n_in + n_out + n_own]
    targets = list(buffers) + list(outs[n_out - n_tab :])
    copies = [
        pltpu.make_async_copy(sources[i], targets[i], sems.at[i]) for i in range(n_in)
    ]
    for copy in copies:
        copy.start()
    for copy in copies:
        copy.wait()
    setup_kernel(local, fields, *targets, *outs[: n_out - n_tab])


def per_device(state, velocity, pre_exp, stoich, neighbours, switch, new_owner):
    tab = make_tables()
    local_count = state.shape[0]
    field_count = state.shape[1]
    rows = local_count * field_count
    curve_count = lax.axis_size("curve")
    curve_pos = lax.axis_index("curve")
    device_id = lax.axis_index("slab") * curve_count + curve_pos
    first_global = device_id * local_count
    positions = jnp.arange(local_count, dtype=jnp.int32)

    near_device = neighbours // local_count
    near_local = neighbours - near_device * local_count
    remote = near_device != device_id
    codes = (near_local + local_count * remote.astype(jnp.int32)).astype(f32)
    left_pos = (curve_pos + curve_count - 1) % curve_count
    right_pos = (curve_pos + 1) % curve_count
    sto_col = jnp.pad(stoich, (0, local_count - field_count))
    packed_t = jnp.concatenate(
        [
            jnp.transpose(codes),
            jnp.stack([switch.astype(f32), pre_exp, sto_col, new_owner.astype(f32)]),
        ]
    )
    packed = jnp.pad(packed_t, ((0, local_count - 10), (0, LANE - local_count)))
    fsel_np = np.arange(rows)[:, None] % field_count == np.arange(local_count)[None, :]
    vt = jnp.transpose(velocity, (0, 2, 1))
    row_elem = np.arange(rows) // field_count
    bcast_np = row_elem[:, None] == np.arange(local_count)[None, :]
    pick_rows = (np.arange(3)[:, None] + field_count * np.arange(local_count)[None, :]).reshape(-1)
    sel_np = pick_rows[:, None] == np.arange(rows)[None, :]
    n7 = P7**3
    n3 = P3**3
    layout = table_layout(rows, local_count)
    table_np = np.zeros((table_rows(), 6 * LANE), np.float32)
    for d in (1, 2):
        block = tab["d7t"][d][:LANE, :LANE].astype(np.float32)
        assert np.array_equal(
            tab["d7t"][d].astype(np.float32), np.kron(np.eye(n7 // LANE), block)
        )
    pieces = {
        "g7": tab["g7"][None],
        "tm": tab["tm"],
        "mdst": np.transpose(tab["mds"], (0, 2, 1)),
        "dx": tab["d7t"][0:1],
        "byz": np.stack([tab["d7t"][1][:LANE, :LANE], tab["d7t"][2][:LANE, :LANE]]),
        "lift_t": tab["lift"].T[None],
        "pj": np.transpose(tab["pjt"], (0, 2, 1)),
        "bcast": bcast_np[None],
        "sel": sel_np[None],
        "fsel": fsel_np[None],
        "d3t": tab["d3t"],
    }
    filled = np.zeros(table_np.shape, bool)
    for name, (start, count, width, lane0) in layout.items():
        parts = np.asarray(pieces[name], np.float32)
        for k in range(parts.shape[0]):
            window = (slice(start + k * count, start + (k + 1) * count), slice(lane0, lane0 + width))
            assert not filled[window].any()
            filled[window] = True
            table_np[window] = parts[k]
    table = jnp.asarray(to_bf16(table_np))

    send_shape = jax.ShapeDtypeStruct((rows, LANE), bf16)
    sends_shape = [send_shape, send_shape, jax.ShapeDtypeStruct((2 * rows, LANE), bf16)]
    u_shape = jax.ShapeDtypeStruct((rows, P7**3), f32)
    c_shape = jax.ShapeDtypeStruct((rows, P3**3), f32)

    def exchange(sends):
        face0, face1, faces_z = sends
        from_prev = shifted(faces_z, "slab", 1)
        if lax.axis_size("slab") == 2:
            from_next = from_prev
        else:
            from_next = shifted(faces_z, "slab", -1)
        return [shifted(face1, "curve", 1), shifted(face0, "curve", -1), from_prev, from_next]

    setup_out = [
        jax.ShapeDtypeStruct((3, rows, P7**3), bf16),
        jax.ShapeDtypeStruct((rows, 6 * LANE), f32),
        jax.ShapeDtypeStruct((local_count, 1), f32),
        jax.ShapeDtypeStruct((rows, 1), f32),
    ] + sends_shape
    near_out = [
        jax.ShapeDtypeStruct((6, rows, rows), bf16),
        jax.ShapeDtypeStruct((len(SEND_FACES), rows, rows), bf16),
        jax.ShapeDtypeStruct((rows, 1), f32),
    ]
    late_out = [
        jax.ShapeDtypeStruct((3, rows, P3**3), f32),
        jax.ShapeDtypeStruct((rows, 6 * LANE), f32),
        jax.ShapeDtypeStruct((rows, LANE), f32),
        jax.ShapeDtypeStruct((8, LANE), f32),
        jax.ShapeDtypeStruct((8, LANE), f32),
        jax.ShapeDtypeStruct((MOVE_CAP * field_count, rows), bf16),
        jax.ShapeDtypeStruct((MOVE_CAP * field_count, rows), bf16),
    ]
    setup_out = setup_out + [jax.ShapeDtypeStruct(table.shape, table.dtype)]
    u0 = state.reshape(rows, P7**3)
    setup_in = [u0, vt, packed, table]
    res = pl.pallas_call(
        functools.partial(setup_entry, local_count, field_count, len(setup_in), len(setup_out)),
        out_shape=setup_out,
        in_specs=[pl.BlockSpec(memory_space=pltpu.HBM) for _ in setup_in],
        out_specs=[_vmem() for _ in setup_out],
        scratch_shapes=[pltpu.VMEM(x.shape, x.dtype) for x in setup_in[:3]]
        + [pltpu.SemaphoreType.DMA((len(setup_in),))],
        compiler_params=pltpu.CompilerParams(vmem_limit_bytes=24 * 1024 * 1024),
    )(*setup_in)
    v7, m7, pre, stc = res[:4]
    sends = res[4:7]
    table = res[7]
    p_local, p_remote, sw = pl.pallas_call(
        functools.partial(near_kernel, local_count, field_count),
        out_shape=near_out,
        in_specs=[_vmem() for _ in range(2)],
        out_specs=[_vmem() for _ in near_out],
        compiler_params=pltpu.CompilerParams(vmem_limit_bytes=24 * 1024 * 1024),
    )(packed, table)
    v3, m3, hinfo, cnt_l, cnt_r, sel_l, sel_r = pl.pallas_call(
        functools.partial(late_kernel, local_count, field_count),
        out_shape=late_out,
        in_specs=[_vmem() for _ in range(3)],
        out_specs=[_vmem() for _ in late_out],
        compiler_params=pltpu.CompilerParams(vmem_limit_bytes=24 * 1024 * 1024),
    )(vt, packed, table)
    common = [p_local, p_remote, v7, m7, pre, stc, table]
    recv = exchange(sends)
    bulk_tabs = [v7, pre, stc, table]
    (bulk7,) = run_bulk(False, local_count, [u0] + bulk_tabs, [u_shape])
    res = run_stage(
        (False, False, False, True, local_count),
        [u0] + recv + common + [bulk7],
        [u_shape] + sends_shape,
    )
    first, sends = res[0], res[1:]
    recv = exchange(sends)
    (bulk7,) = run_bulk(False, local_count, [first] + bulk_tabs, [u_shape])
    res = run_stage(
        (False, True, True, True, local_count),
        [first, u0] + recv + common + [sw, bulk7],
        [u_shape, c_shape] + sends_shape,
    )
    after, coarse, sends = res[0], res[1], res[2:]
    recv = exchange(sends)
    mixed_tail = [v3, m3, sw]
    bulk7, bulk3 = run_bulk(True, local_count, [after, coarse] + bulk_tabs + [v3], [u_shape, c_shape])
    res = run_stage(
        (True, False, False, True, local_count),
        [after, coarse] + recv + common + mixed_tail + [bulk7, bulk3],
        [u_shape, c_shape] + sends_shape,
    )
    first7, first3, sends = res[0], res[1], res[2:]
    recv = exchange(sends)
    pay_shape = jax.ShapeDtypeStruct((MOVE_CAP * field_count + 8, P7**3), f32)
    bulk7, bulk3 = run_bulk(True, local_count, [first7, first3] + bulk_tabs + [v3], [u_shape, c_shape])
    res = run_stage(
        (True, True, False, False, local_count),
        [first7, first3, after, coarse] + recv + common + mixed_tail
        + [sel_l, sel_r, cnt_l, cnt_r, bulk7, bulk3],
        [u_shape, c_shape, pay_shape, pay_shape],
    )
    final7, final3, pay_l, pay_r = res
    from_right = shifted(pay_l, "curve", -1)
    from_left = shifted(pay_r, "curve", 1)
    held = pl.pallas_call(
        functools.partial(final_kernel, field_count, HOLD7),
        out_shape=jax.ShapeDtypeStruct((HOLD7 * field_count, P7**3), f32),
        in_specs=[_vmem() for _ in range(4)],
        out_specs=_vmem(),
    )(final7, from_left, from_right, hinfo)
    state7_out = held.reshape(HOLD7, field_count, P7**3)
    state3_out = final3.reshape(local_count, field_count * P3**3)
    return (state7_out, state3_out)


def solution(mesh):
    return jax.shard_map(
        per_device,
        mesh=mesh,
        in_specs=(
            P(("slab", "curve"), None, None),
            P(None, None, ("slab", "curve")),
            P(("slab", "curve")),
            P(),
            P(("slab", "curve"), None),
            P(("slab", "curve")),
            P(("slab", "curve")),
        ),
        out_specs=(P(("slab", "curve"), None, None), P(("slab", "curve"), None)),
        check_vma=False,
    )
```

```python
import functools

import jax
import jax.numpy as jnp
import ml_dtypes
import numpy as np
from jax import lax
from jax.experimental import pallas as pl
from jax.experimental.pallas import tpu as pltpu
from jax.sharding import PartitionSpec as P

P7 = 8
P3 = 4
MOVE_CAP = 2
HOLD7 = 12
LANE = 128

TIME_STEP = 0.002
ACTIVATION = 1.5
SIDE_SIGNS = (-1.0, 1.0, -1.0, 1.0, -1.0, 1.0)
OPPOSITE = (1, 0, 3, 2, 5, 4)
SEND_FACES = (0, 1, 4, 5)
missing_id = 1 << 30

f32 = jnp.float32
bf16 = jnp.bfloat16


def shifted(value, axis, steps):
    count = lax.axis_size(axis)
    pairs = [(source, (source + steps) % count) for source in range(count)]
    return lax.ppermute(value, axis, pairs)


def lobatto_points(number):
    return -np.cos(np.pi * np.arange(number) / (number - 1))


def lagrange_weights(points):
    weights = np.ones(points.shape[0])
    for row_id in range(points.shape[0]):
        for col_id in range(points.shape[0]):
            if col_id != row_id:
                weights[row_id] = weights[row_id] / (points[row_id] - points[col_id])
    return weights


def derivative_matrix(points):
    weights = lagrange_weights(points)
    number = points.shape[0]
    matrix = np.zeros((number, number))
    for row_id in range(number):
        for col_id in range(number):
            if col_id != row_id:
                matrix[row_id, col_id] = (
                    weights[col_id] / weights[row_id] / (points[row_id] - points[col_id])
                )
        matrix[row_id, row_id] = -np.sum(matrix[row_id])
    return matrix


def interpolation_matrix(source, target):
    matrix = np.ones((target.shape[0], source.shape[0]))
    for col_id in range(source.shape[0]):
        for other_id in range(source.shape[0]):
            if other_id != col_id:
                matrix[:, col_id] = (
                    matrix[:, col_id]
                    * (target - source[other_id])
                    / (source[col_id] - source[other_id])
                )
    return matrix


def spread_three(matrix, identity):
    return (
        np.kron(matrix, np.kron(identity, identity)),
        np.kron(identity, np.kron(matrix, identity)),
        np.kron(identity, np.kron(identity, matrix)),
    )


def face_nodes(extent):
    grid = np.arange(extent**3).reshape(extent, extent, extent)
    last = extent - 1
    pieces = (grid[0], grid[last], grid[:, 0], grid[:, last], grid[:, :, 0], grid[:, :, last])
    return [piece.reshape(-1) for piece in pieces]


def to_bf16(x):
    return np.asarray(np.asarray(x, np.float32).astype(ml_dtypes.bfloat16))


def split_parts(x):
    x = np.asarray(x, np.float32)
    hi = x.astype(ml_dtypes.bfloat16)
    rest = x - hi.astype(np.float32)
    mid = rest.astype(ml_dtypes.bfloat16)
    lo = (rest - mid.astype(np.float32)).astype(ml_dtypes.bfloat16)
    return np.stack([hi, mid, lo])


def make_tables():
    fine_points = lobatto_points(P7)
    coarse_points = lobatto_points(P3)
    fine_derivs = spread_three(derivative_matrix(fine_points), np.eye(P7))
    coarse_derivs = spread_three(derivative_matrix(coarse_points), np.eye(P3))
    downward = interpolation_matrix(fine_points, coarse_points)
    upward = interpolation_matrix(coarse_points, fine_points)
    d7t = np.stack([to_bf16(m.T) for m in fine_derivs])
    d3t = np.stack([to_bf16(m).T for m in coarse_derivs])
    lift_table = to_bf16(np.kron(upward, np.kron(upward, upward)))
    projection = np.asarray(np.kron(downward, np.kron(downward, downward)), np.float32)
    mortar_up = np.asarray(np.kron(upward, upward), np.float32)
    mortar_down = np.asarray(np.kron(downward, downward), np.float32)
    nodes7 = face_nodes(P7)
    nodes3 = face_nodes(P3)
    n7 = P7**3
    n3 = P3**3
    g7 = np.zeros((n7, 6 * LANE), np.float32)
    tm = np.zeros((n3, 6 * LANE), np.float32)
    mds = np.zeros((6 * LANE, n3), np.float32)
    for side in range(6):
        for q, node in enumerate(nodes7[side]):
            g7[node, side * LANE + q] = 1.0
        for k, node in enumerate(nodes3[side]):
            tm[node, side * LANE : side * LANE + P7 * P7] = mortar_up[:, k]
            mds[side * LANE : side * LANE + P7 * P7, node] = mortar_down[k, :]
    tables = {
        "d7t": to_bf16(d7t),
        "d3t": to_bf16(d3t),
        "lift": lift_table,
        "mortar_up": mortar_up,
        "g7": to_bf16(g7),
        "tm": split_parts(tm),
        "mds": split_parts(mds),
        "pjt": split_parts(projection.T),
        "nodes7": nodes7,
        "nodes3": nodes3,
    }
    return tables


def _dot(a, b):
    return jnp.dot(a, b, preferred_element_type=f32)


def _split(x):
    hi = x.astype(bf16)
    rest = x - hi.astype(f32)
    mid = rest.astype(bf16)
    lo = (rest - mid.astype(f32)).astype(bf16)
    return hi, mid, lo


def _exact_left(x, table):
    hi, mid, lo = _split(x)
    return (_dot(hi, table) + _dot(mid, table)) + _dot(lo, table)


def _dot_t(a, b):
    return lax.dot_general(a, b, (((1,), (1,)), ((), ())), preferred_element_type=f32)


def _exact_left_t(x, table):
    hi, mid, lo = _split(x)
    return (_dot_t(hi, table) + _dot_t(mid, table)) + _dot_t(lo, table)


def _exact_right(table, x):
    hi, mid, lo = _split(x)
    return (_dot(table, hi) + _dot(table, mid)) + _dot(table, lo)


def _full_t(x, parts_ref):
    xh, xm, xl = _split(x)
    bh = parts_ref[0]
    bm = parts_ref[1]
    bl = parts_ref[2]
    return _dot_t(xh, bh) + (_dot_t(xh, bm) + _dot_t(xm, bh)) + (
        _dot_t(xh, bl) + _dot_t(xm, bm) + _dot_t(xl, bh)
    )


class View:
    def __init__(self, ref, start, rows, width, lane0):
        self.ref = ref
        self.start = start
        self.rows = rows
        self.width = width
        self.lane0 = lane0

    def __getitem__(self, k):
        if k is Ellipsis:
            k = 0
        top = self.start + k * self.rows
        return self.ref[top : top + self.rows, self.lane0 : self.lane0 + self.width]


def table_layout(rows, local):
    n7 = P7**3
    n3 = P3**3
    wide = 6 * LANE
    base = n7 + 6 * n3
    side = 4 * LANE
    return {
        "g7": (0, n7, wide, 0),
        "tm": (n7, n3, wide, 0),
        "mdst": (n7 + 3 * n3, n3, wide, 0),
        "dx": (base, n7, n7, 0),
        "lift_t": (base + n7, n3, n7, 0),
        "pj": (base + n7 + n3, n3, n7, 0),
        "byz": (base, LANE, LANE, 5 * LANE),
        "bcast": (base, rows, local, side),
        "sel": (base + rows, 3 * local, rows, side),
        "fsel": (base + rows + 3 * local, rows, local, side),
        "d3t": (base + 2 * rows + 3 * local, n3, n3, side),
    }


def table_rows():
    return P7**3 + 6 * P3**3 + P7**3 + 4 * P3**3


def table_views(tab_ref, rows, local):
    return {
        name: View(tab_ref, start, count, width, lane0)
        for name, (start, count, width, lane0) in table_layout(rows, local).items()
    }


def _full(x, parts_ref):
    xh, xm, xl = _split(x)
    bh = parts_ref[0]
    bm = parts_ref[1]
    bl = parts_ref[2]
    return _dot(xh, bh) + (_dot(xh, bm) + _dot(xm, bh)) + (
        _dot(xh, bl) + _dot(xm, bm) + _dot(xl, bh)
    )


def _rate_source(values, pre, stc, bc, sel, local):
    picked = _exact_right(sel, values)
    v0 = picked[0:local]
    v1 = picked[local : 2 * local]
    v2 = picked[2 * local : 3 * local]
    rate = pre * jnp.exp(-ACTIVATION * jnp.exp(-v0)) * v1 * v2
    return stc * _exact_right(bc, rate)


def recv_block(recv, side):
    ref = recv[side]
    if side in (4, 5):
        rows = ref.shape[0] // 2
        top = 0 if side == 4 else rows
        return ref[top : top + rows, :]
    return ref[...]


def write_sends(out_refs, send):
    rows = send.shape[0]
    out_refs[0][...] = send[:, 0:LANE]
    out_refs[1][...] = send[:, LANE : 2 * LANE]
    out_refs[2][0:rows, :] = send[:, 5 * LANE : 6 * LANE]
    out_refs[2][rows : 2 * rows, :] = send[:, 4 * LANE : 5 * LANE]


def stage_kernel(coarse, second, project, sends, local, *refs):
    refs = list(refs)

    def take():
        return refs.pop(0)

    u_ref = take()
    c_ref = take() if coarse else None
    bu_ref = take() if second else None
    bc_ref = take() if (second and coarse) else None
    recv = {s: take() for s in SEND_FACES}
    pl_ref = take()
    pr_ref = take()
    v7_ref = take()
    m7_ref = take()
    pre_ref = take()
    stc_ref = take()
    views = table_views(take(), u_ref.shape[0], local)
    bc_tab = views["bcast"]
    sel_tab = views["sel"]
    g7_ref = views["g7"]
    d3_ref = views["d3t"]
    mds_ref = views["mdst"]
    tm_ref = views["tm"]
    pj_ref = views["pj"]
    if coarse:
        v3_ref = take()
        m3_ref = take()
    if coarse or project:
        sw_ref = take()
    last = coarse and not sends
    if last:
        sel_l_ref = take()
        sel_r_ref = take()
        cnt_l_ref = take()
        cnt_r_ref = take()
    res7_ref = take()
    res3_ref = take() if coarse else None
    out_u = take()
    out_c = take() if (coarse or project) else None
    out_send = [take() for _ in range(3)] if sends else None
    if last:
        pay_l_ref = take()
        pay_r_ref = take()

    pre = pre_ref[...]
    stc = stc_ref[...]
    bcast = bc_tab[...]
    sel = sel_tab[...]
    u = u_ref[...]
    trace7 = _dot(u.astype(bf16), g7_ref[...])
    if coarse:
        c = c_ref[...]
        trace3 = _full(c, tm_ref).astype(bf16).astype(f32)
        switched = sw_ref[...] > 0.5
        own = jnp.where(switched, trace3, trace7)
    else:
        own = trace7
    own_b = own.astype(bf16)
    near_blocks = []
    for side in range(6):
        other = OPPOSITE[side]
        block = own_b[:, other * LANE : (other + 1) * LANE]
        near = _dot(pl_ref[side], block)
        if side in SEND_FACES:
            k = SEND_FACES.index(side)
            near = near + _dot(pr_ref[k], recv_block(recv, side))
        near_blocks.append(near)
    near = jnp.concatenate(near_blocks, axis=1)

    result = res7_ref[...]
    jump = (P7 * (P7 - 1) / 2.0) * (m7_ref[...] * (trace7 - near))
    rate7 = result + _exact_left_t(jump, g7_ref[...])

    if coarse:
        result3 = res3_ref[...]
        jump3 = m3_ref[...] * (trace3 - near)
        rate3 = result3 + (P3 * (P3 - 1) / 2.0) * _full_t(jump3, mds_ref)

    if second:
        new_u = 0.5 * (bu_ref[...] + u + TIME_STEP * rate7)
    else:
        new_u = u + TIME_STEP * rate7
    out_u[...] = new_u
    new_c = None
    if coarse:
        if second:
            new_c = 0.5 * (bc_ref[...] + c + TIME_STEP * rate3)
        else:
            new_c = c + TIME_STEP * rate3
        if last:
            out_c[...] = jnp.where(sw_ref[...] > 0.5, new_c, 0.0)
            moved = sel_l_ref.shape[0]
            pay_l_ref[0:moved, :] = _exact_right(sel_l_ref[...], new_u)
            pay_r_ref[0:moved, :] = _exact_right(sel_r_ref[...], new_u)
            tail = (pay_l_ref.shape[0] - moved, pay_l_ref.shape[1])
            pay_l_ref[moved:, :] = jnp.broadcast_to(cnt_l_ref[0:1, 0:1], tail)
            pay_r_ref[moved:, :] = jnp.broadcast_to(cnt_r_ref[0:1, 0:1], tail)
        else:
            out_c[...] = new_c
    if project:
        new_c = _full_t(new_u, pj_ref)
        out_c[...] = new_c
    if sends:
        send7 = _dot(new_u.astype(bf16), g7_ref[...])
        if new_c is not None:
            send3 = _full(new_c, tm_ref).astype(bf16).astype(f32)
            send = jnp.where(sw_ref[...] > 0.5, send3, send7)
        else:
            send = send7
        write_sends(out_send, send.astype(bf16))


def _vmem():
    return pl.BlockSpec(memory_space=pltpu.VMEM)


def bulk_kernel(coarse, local, *refs):
    refs = list(refs)
    u_ref = refs.pop(0)
    c_ref = refs.pop(0) if coarse else None
    v7_ref, pre_ref, stc_ref = refs.pop(0), refs.pop(0), refs.pop(0)
    views = table_views(refs.pop(0), u_ref.shape[0], local)
    v3_ref = refs.pop(0) if coarse else None
    out7 = refs.pop(0)
    out3 = refs.pop(0) if coarse else None
    pre = pre_ref[...]
    stc = stc_ref[...]
    bcast = views["bcast"][...]
    sel = views["sel"][...]
    u = u_ref[...]
    fluxes = [(v7_ref[d].astype(f32) * u).astype(bf16) for d in range(3)]
    divergence = _dot(fluxes[0], views["dx"][0])
    by = views["byz"][0]
    bz = views["byz"][1]
    chunks = []
    for k in range(u.shape[1] // LANE):
        part = slice(k * LANE, (k + 1) * LANE)
        chunks.append(_dot(fluxes[1][:, part], by) + _dot(fluxes[2][:, part], bz))
    divergence = divergence + jnp.concatenate(chunks, axis=1)
    out7[...] = _rate_source(u, pre, stc, bcast, sel, local) - divergence
    if coarse:
        c = c_ref[...]
        div3 = None
        for d in range(3):
            flux3 = (v3_ref[d] * c).astype(bf16)
            term = _dot(flux3, views["d3t"][d])
            div3 = term if div3 is None else div3 + term
        out3[...] = _rate_source(c, pre, stc, bcast, sel, local) - div3


def run_bulk(coarse, local, inputs, out_shapes):
    return pl.pallas_call(
        functools.partial(bulk_kernel, coarse, local),
        out_shape=out_shapes,
        in_specs=[_vmem() for _ in inputs],
        out_specs=[_vmem() for _ in out_shapes],
        compiler_params=pltpu.CompilerParams(vmem_limit_bytes=24 * 1024 * 1024),
    )(*inputs)


def run_stage(flags, inputs, out_shapes):
    coarse, second, project, sends, local = flags
    kernel = functools.partial(stage_kernel, coarse, second, project, sends, local)
    return pl.pallas_call(
        kernel,
        out_shape=out_shapes,
        in_specs=[_vmem() for _ in inputs],
        out_specs=[_vmem() for _ in out_shapes],
        compiler_params=pltpu.CompilerParams(vmem_limit_bytes=48 * 1024 * 1024),
    )(*inputs)


def setup_kernel(local, fields, u_ref, vt_ref, packed_ref, tab_ref, v7_out, m7_out,
                 pre_out, stc_out, *send_refs):
    rows = local * fields
    views = table_views(tab_ref, rows, local)
    lift_ref = views["lift_t"]
    g7_ref = views["g7"]
    tm_ref = views["tm"]
    fsel_ref = views["fsel"]
    bcast = views["bcast"][...]
    lanes = lax.broadcasted_iota(jnp.int32, (local, 6 * LANE), 1) // LANE
    sign = jnp.where(lanes % 2 == 0, -1.0, 1.0)
    fvg = []
    mvg = []
    for d in range(3):
        vt = vt_ref[d]
        fv = _dot(vt, lift_ref[...]).astype(bf16)
        v7_out[d] = _dot(bcast, fv).astype(bf16)
        fvg.append(_dot(fv, g7_ref[...]))

    def by_block(parts):
        return jnp.where(lanes < 2, parts[0], jnp.where(lanes < 4, parts[1], parts[2]))

    m7 = jnp.minimum(sign * by_block(fvg), 0.0)
    m7_out[...] = _dot(bcast, m7.astype(bf16))
    eye16 = jnp.where(
        lax.broadcasted_iota(jnp.int32, (local, LANE), 0)
        == lax.broadcasted_iota(jnp.int32, (local, LANE), 1), 1.0, 0.0
    ).astype(bf16)
    p_hi, p_mid, p_lo = _split(packed_ref[...])
    packed = (_dot_t(eye16, p_hi) + _dot_t(eye16, p_mid)) + _dot_t(eye16, p_lo)
    pre_out[...] = packed[:, 7:8]
    stc_out[...] = _exact_right(fsel_ref[...], packed)[:, 8:9]
    write_sends(send_refs, _dot(u_ref[...].astype(bf16), g7_ref[...]).astype(bf16))


def near_kernel(local, fields, packed_ref, tab_ref, pl_out, pr_out, sw_out):
    rows = local * fields
    bcast = table_views(tab_ref, rows, local)["bcast"][...]
    eye16 = jnp.where(
        lax.broadcasted_iota(jnp.int32, (local, LANE), 0)
        == lax.broadcasted_iota(jnp.int32, (local, LANE), 1), 1.0, 0.0
    ).astype(bf16)
    packed = _dot_t(eye16, packed_ref[...].astype(bf16))
    rep = _dot(bcast, packed.astype(bf16))
    row_f = (lax.broadcasted_iota(jnp.int32, (rows, 1), 0) % fields).astype(f32)
    cols = lax.broadcasted_iota(jnp.int32, (rows, rows), 1).astype(f32)
    for side in range(6):
        code = rep[:, side : side + 1]
        far = code >= local
        target = (code - jnp.where(far, float(local), 0.0)) * fields + row_f
        hit = cols == target
        pl_out[side] = jnp.where(hit & ~far, 1.0, 0.0).astype(bf16)
        if side in SEND_FACES:
            pr_out[SEND_FACES.index(side)] = jnp.where(hit & far, 1.0, 0.0).astype(bf16)
    sw_out[...] = rep[:, 6:7]


def late_kernel(local, fields, vt_ref, tab_ref, v3_out, m3_out):
    rows = local * fields
    views = table_views(tab_ref, rows, local)
    tm_ref = views["tm"]
    bcast = views["bcast"][...]
    lanes = lax.broadcasted_iota(jnp.int32, (local, 6 * LANE), 1) // LANE
    sign = jnp.where(lanes % 2 == 0, -1.0, 1.0)
    mvg = []
    for d in range(3):
        vt = vt_ref[d]
        v3_out[d] = _dot(bcast, vt)
        mvg.append((_dot(vt, tm_ref[0]) + _dot(vt, tm_ref[1])) + _dot(vt, tm_ref[2]))
    by_block = jnp.where(lanes < 2, mvg[0], jnp.where(lanes < 4, mvg[1], mvg[2]))
    m3_out[...] = _exact_right(bcast, jnp.minimum(sign * by_block, 0.0))


def move_kernel(local, fields, packed_ref, tab_ref, hinfo_out, cnt_l_out, cnt_r_out, sel_l_out,
                sel_r_out):
    rows = local * fields
    bcast = table_views(tab_ref, rows, local)["bcast"][...]
    eye16 = jnp.where(
        lax.broadcasted_iota(jnp.int32, (local, LANE), 0)
        == lax.broadcasted_iota(jnp.int32, (local, LANE), 1), 1.0, 0.0
    ).astype(bf16)
    p_hi, p_mid, p_lo = _split(packed_ref[...])
    packed = (_dot_t(eye16, p_hi) + _dot_t(eye16, p_mid)) + _dot_t(eye16, p_lo)
    curve_count = lax.axis_size("curve")
    curve_pos = lax.axis_index("curve")
    left_f = ((curve_pos + curve_count - 1) % curve_count).astype(f32)
    right_f = ((curve_pos + 1) % curve_count).astype(f32)
    first_f = jnp.where(curve_pos == 0, 1.0, 0.0)
    last_f = jnp.where(curve_pos == curve_count - 1, 1.0, 0.0)
    stay_sw = packed[:, 6:7] < 0.5
    go_left = (packed[:, 9:10] == left_f) & stay_sw
    go_right = (packed[:, 9:10] == right_f) & stay_sw
    stays = stay_sw & ~go_left & ~go_right
    lane16 = lax.broadcasted_iota(jnp.int32, (local, LANE), 1)
    marks = jnp.where(
        lane16 == 0, go_left.astype(f32),
        jnp.where(lane16 == 1, go_right.astype(f32), jnp.where(lane16 == 2, stays.astype(f32), 0.0)),
    ).astype(bf16)
    er = lax.broadcasted_iota(jnp.int32, (local, local), 0)
    ec = lax.broadcasted_iota(jnp.int32, (local, local), 1)
    before = _dot(jnp.where(ec < er, 1.0, 0.0).astype(bf16), marks)
    totals = _dot(jnp.ones((local, local), bf16), marks)
    info = jnp.where(lane16 < 3, marks.astype(f32), 0.0)
    for k in range(3):
        info = jnp.where(lane16 == 3 + k, before[:, k : k + 1], info)
    info = jnp.where(lane16 == 6, totals[:, 2:3], info)
    info = jnp.where(lane16 == 7, first_f, info)
    info = jnp.where(lane16 == 8, last_f, info)
    hinfo = _dot(bcast, info.astype(bf16))
    hinfo_out[...] = hinfo
    cnt_l_out[...] = jnp.broadcast_to(totals[0:1, 0:1], cnt_l_out.shape)
    cnt_r_out[...] = jnp.broadcast_to(totals[0:1, 1:2], cnt_r_out.shape)
    rf = lax.broadcasted_iota(jnp.int32, (rows, LANE), 0) % fields
    cc = lax.broadcasted_iota(jnp.int32, (rows, LANE), 1)
    eye = jnp.where(
        lax.broadcasted_iota(jnp.int32, (MOVE_CAP * fields, LANE), 0)
        == lax.broadcasted_iota(jnp.int32, (MOVE_CAP * fields, LANE), 1), 1.0, 0.0
    ).astype(bf16)
    for mark_lane, rank_lane, out in ((0, 3, sel_l_out), (1, 4, sel_r_out)):
        hit = (
            (hinfo[:, mark_lane : mark_lane + 1] > 0.5)
            & (hinfo[:, rank_lane : rank_lane + 1] == (cc // fields).astype(f32))
            & (rf == cc % fields)
            & (cc < MOVE_CAP * fields)
        )
        out[...] = _dot_t(eye, jnp.where(hit, 1.0, 0.0).astype(bf16)).astype(bf16)


def final_kernel(fields, hold, home_ref, from_l_ref, from_r_ref, hinfo_ref, out_ref):
    hinfo = hinfo_ref[...]
    moved = MOVE_CAP * fields
    n_l = from_l_ref[moved : moved + 1, 0:1]
    n_r = from_r_ref[moved : moved + 1, 0:1]
    n_h = hinfo[0:1, 6:7]
    first = hinfo[0:1, 7:8] > 0.5
    final = hinfo[0:1, 8:9] > 0.5
    off_l = jnp.where(first, n_h + n_r, jnp.where(final, n_r, 0.0))
    off_h = jnp.where(first, 0.0, jnp.where(final, n_r + n_l, n_l))
    off_r = jnp.where(first, n_h, jnp.where(final, 0.0, n_l + n_h))
    width = hold * fields
    eye = jnp.where(
        lax.broadcasted_iota(jnp.int32, (width, LANE), 0)
        == lax.broadcasted_iota(jnp.int32, (width, LANE), 1), 1.0, 0.0
    ).astype(bf16)

    def gather(values, valid, pos):
        count = values.shape[0]
        rf = lax.broadcasted_iota(jnp.int32, (count, LANE), 0) % fields
        cc = lax.broadcasted_iota(jnp.int32, (count, LANE), 1)
        hit = valid & (pos == (cc // fields).astype(f32)) & (rf == cc % fields) & (cc < width)
        pick = _dot_t(eye, jnp.where(hit, 1.0, 0.0).astype(bf16)).astype(bf16)
        return _exact_right(pick, values)

    total = gather(home_ref[...], hinfo[:, 2:3] > 0.5, off_h + hinfo[:, 5:6])
    slot = (lax.broadcasted_iota(jnp.int32, (moved, 1), 0) // fields).astype(f32)
    total = total + gather(from_l_ref[0:moved, :], slot < n_l, off_l + slot)
    total = total + gather(from_r_ref[0:moved, :], slot < n_r, off_r + slot)
    out_ref[...] = total


def setup_entry(local, fields, n_in, n_out, *refs):
    sources = refs[:n_in]
    outs = refs[n_in : n_in + n_out]
    n_tab = 1
    n_own = n_in - n_tab
    buffers = refs[n_in + n_out : n_in + n_out + n_own]
    sems = refs[n_in + n_out + n_own]
    targets = list(buffers) + list(outs[n_out - n_tab :])
    copies = [
        pltpu.make_async_copy(sources[i], targets[i], sems.at[i]) for i in range(n_in)
    ]
    for copy in copies:
        copy.start()
    for copy in copies:
        copy.wait()
    setup_kernel(local, fields, *targets, *outs[: n_out - n_tab])


def per_device(state, velocity, pre_exp, stoich, neighbours, switch, new_owner):
    tab = make_tables()
    local_count = state.shape[0]
    field_count = state.shape[1]
    rows = local_count * field_count
    curve_count = lax.axis_size("curve")
    curve_pos = lax.axis_index("curve")
    device_id = lax.axis_index("slab") * curve_count + curve_pos
    first_global = device_id * local_count
    positions = jnp.arange(local_count, dtype=jnp.int32)

    near_device = neighbours // local_count
    near_local = neighbours - near_device * local_count
    remote = near_device != device_id
    codes = (near_local + local_count * remote.astype(jnp.int32)).astype(f32)
    left_pos = (curve_pos + curve_count - 1) % curve_count
    right_pos = (curve_pos + 1) % curve_count
    sto_col = jnp.pad(stoich, (0, local_count - field_count))
    packed_t = jnp.concatenate(
        [
            jnp.transpose(codes),
            jnp.stack([switch.astype(f32), pre_exp, sto_col, new_owner.astype(f32)]),
        ]
    )
    packed = jnp.pad(packed_t, ((0, local_count - 10), (0, LANE - local_count)))
    fsel_np = np.arange(rows)[:, None] % field_count == np.arange(local_count)[None, :]
    vt = jnp.transpose(velocity, (0, 2, 1))
    row_elem = np.arange(rows) // field_count
    bcast_np = row_elem[:, None] == np.arange(local_count)[None, :]
    pick_rows = (np.arange(3)[:, None] + field_count * np.arange(local_count)[None, :]).reshape(-1)
    sel_np = pick_rows[:, None] == np.arange(rows)[None, :]
    n7 = P7**3
    n3 = P3**3
    layout = table_layout(rows, local_count)
    table_np = np.zeros((table_rows(), 6 * LANE), np.float32)
    for d in (1, 2):
        block = tab["d7t"][d][:LANE, :LANE].astype(np.float32)
        assert np.array_equal(
            tab["d7t"][d].astype(np.float32), np.kron(np.eye(n7 // LANE), block)
        )
    pieces = {
        "g7": tab["g7"][None],
        "tm": tab["tm"],
        "mdst": np.transpose(tab["mds"], (0, 2, 1)),
        "dx": tab["d7t"][0:1],
        "byz": np.stack([tab["d7t"][1][:LANE, :LANE], tab["d7t"][2][:LANE, :LANE]]),
        "lift_t": tab["lift"].T[None],
        "pj": np.transpose(tab["pjt"], (0, 2, 1)),
        "bcast": bcast_np[None],
        "sel": sel_np[None],
        "fsel": fsel_np[None],
        "d3t": tab["d3t"],
    }
    filled = np.zeros(table_np.shape, bool)
    for name, (start, count, width, lane0) in layout.items():
        parts = np.asarray(pieces[name], np.float32)
        for k in range(parts.shape[0]):
            window = (slice(start + k * count, start + (k + 1) * count), slice(lane0, lane0 + width))
            assert not filled[window].any()
            filled[window] = True
            table_np[window] = parts[k]
    table = jnp.asarray(to_bf16(table_np))

    send_shape = jax.ShapeDtypeStruct((rows, LANE), bf16)
    sends_shape = [send_shape, send_shape, jax.ShapeDtypeStruct((2 * rows, LANE), bf16)]
    u_shape = jax.ShapeDtypeStruct((rows, P7**3), f32)
    c_shape = jax.ShapeDtypeStruct((rows, P3**3), f32)

    def exchange(sends):
        face0, face1, faces_z = sends
        from_prev = shifted(faces_z, "slab", 1)
        if lax.axis_size("slab") == 2:
            from_next = from_prev
        else:
            from_next = shifted(faces_z, "slab", -1)
        return [shifted(face1, "curve", 1), shifted(face0, "curve", -1), from_prev, from_next]

    setup_out = [
        jax.ShapeDtypeStruct((3, rows, P7**3), bf16),
        jax.ShapeDtypeStruct((rows, 6 * LANE), f32),
        jax.ShapeDtypeStruct((local_count, 1), f32),
        jax.ShapeDtypeStruct((rows, 1), f32),
    ] + sends_shape
    near_out = [
        jax.ShapeDtypeStruct((6, rows, rows), bf16),
        jax.ShapeDtypeStruct((len(SEND_FACES), rows, rows), bf16),
        jax.ShapeDtypeStruct((rows, 1), f32),
    ]
    late_out = [
        jax.ShapeDtypeStruct((3, rows, P3**3), f32),
        jax.ShapeDtypeStruct((rows, 6 * LANE), f32),
    ]
    move_out = [
        jax.ShapeDtypeStruct((rows, LANE), f32),
        jax.ShapeDtypeStruct((8, LANE), f32),
        jax.ShapeDtypeStruct((8, LANE), f32),
        jax.ShapeDtypeStruct((MOVE_CAP * field_count, rows), bf16),
        jax.ShapeDtypeStruct((MOVE_CAP * field_count, rows), bf16),
    ]
    setup_out = setup_out + [jax.ShapeDtypeStruct(table.shape, table.dtype)]
    u0 = state.reshape(rows, P7**3)
    setup_in = [u0, vt, packed, table]
    res = pl.pallas_call(
        functools.partial(setup_entry, local_count, field_count, len(setup_in), len(setup_out)),
        out_shape=setup_out,
        in_specs=[pl.BlockSpec(memory_space=pltpu.HBM) for _ in setup_in],
        out_specs=[_vmem() for _ in setup_out],
        scratch_shapes=[pltpu.VMEM(x.shape, x.dtype) for x in setup_in[:3]]
        + [pltpu.SemaphoreType.DMA((len(setup_in),))],
        compiler_params=pltpu.CompilerParams(vmem_limit_bytes=24 * 1024 * 1024),
    )(*setup_in)
    v7, m7, pre, stc = res[:4]
    sends = res[4:7]
    table = res[7]
    p_local, p_remote, sw = pl.pallas_call(
        functools.partial(near_kernel, local_count, field_count),
        out_shape=near_out,
        in_specs=[_vmem() for _ in range(2)],
        out_specs=[_vmem() for _ in near_out],
        compiler_params=pltpu.CompilerParams(vmem_limit_bytes=24 * 1024 * 1024),
    )(packed, table)
    v3, m3 = pl.pallas_call(
        functools.partial(late_kernel, local_count, field_count),
        out_shape=late_out,
        in_specs=[_vmem() for _ in range(2)],
        out_specs=[_vmem() for _ in late_out],
        compiler_params=pltpu.CompilerParams(vmem_limit_bytes=24 * 1024 * 1024),
    )(vt, table)
    hinfo, cnt_l, cnt_r, sel_l, sel_r = pl.pallas_call(
        functools.partial(move_kernel, local_count, field_count),
        out_shape=move_out,
        in_specs=[_vmem() for _ in range(2)],
        out_specs=[_vmem() for _ in move_out],
        compiler_params=pltpu.CompilerParams(vmem_limit_bytes=24 * 1024 * 1024),
    )(packed, table)
    common = [p_local, p_remote, v7, m7, pre, stc, table]
    recv = exchange(sends)
    bulk_tabs = [v7, pre, stc, table]
    (bulk7,) = run_bulk(False, local_count, [u0] + bulk_tabs, [u_shape])
    res = run_stage(
        (False, False, False, True, local_count),
        [u0] + recv + common + [bulk7],
        [u_shape] + sends_shape,
    )
    first, sends = res[0], res[1:]
    recv = exchange(sends)
    (bulk7,) = run_bulk(False, local_count, [first] + bulk_tabs, [u_shape])
    res = run_stage(
        (False, True, True, True, local_count),
        [first, u0] + recv + common + [sw, bulk7],
        [u_shape, c_shape] + sends_shape,
    )
    after, coarse, sends = res[0], res[1], res[2:]
    recv = exchange(sends)
    mixed_tail = [v3, m3, sw]
    bulk7, bulk3 = run_bulk(True, local_count, [after, coarse] + bulk_tabs + [v3], [u_shape, c_shape])
    res = run_stage(
        (True, False, False, True, local_count),
        [after, coarse] + recv + common + mixed_tail + [bulk7, bulk3],
        [u_shape, c_shape] + sends_shape,
    )
    first7, first3, sends = res[0], res[1], res[2:]
    recv = exchange(sends)
    pay_shape = jax.ShapeDtypeStruct((MOVE_CAP * field_count + 8, P7**3), f32)
    bulk7, bulk3 = run_bulk(True, local_count, [first7, first3] + bulk_tabs + [v3], [u_shape, c_shape])
    res = run_stage(
        (True, True, False, False, local_count),
        [first7, first3, after, coarse] + recv + common + mixed_tail
        + [sel_l, sel_r, cnt_l, cnt_r, bulk7, bulk3],
        [u_shape, c_shape, pay_shape, pay_shape],
    )
    final7, final3, pay_l, pay_r = res
    from_right = shifted(pay_l, "curve", -1)
    from_left = shifted(pay_r, "curve", 1)
    held = pl.pallas_call(
        functools.partial(final_kernel, field_count, HOLD7),
        out_shape=jax.ShapeDtypeStruct((HOLD7 * field_count, P7**3), f32),
        in_specs=[_vmem() for _ in range(4)],
        out_specs=_vmem(),
    )(final7, from_left, from_right, hinfo)
    state7_out = held.reshape(HOLD7, field_count, P7**3)
    state3_out = final3.reshape(local_count, field_count * P3**3)
    return (state7_out, state3_out)


def solution(mesh):
    return jax.shard_map(
        per_device,
        mesh=mesh,
        in_specs=(
            P(("slab", "curve"), None, None),
            P(None, None, ("slab", "curve")),
            P(("slab", "curve")),
            P(),
            P(("slab", "curve"), None),
            P(("slab", "curve")),
            P(("slab", "curve")),
        ),
        out_specs=(P(("slab", "curve"), None, None), P(("slab", "curve"), None)),
        check_vma=False,
    )
```

```python
import functools

import jax
import jax.numpy as jnp
import ml_dtypes
import numpy as np
from jax import lax
from jax.experimental import pallas as pl
from jax.experimental.pallas import tpu as pltpu
from jax.sharding import PartitionSpec as P

P7 = 8
P3 = 4
MOVE_CAP = 2
HOLD7 = 12
LANE = 128

TIME_STEP = 0.002
ACTIVATION = 1.5
SIDE_SIGNS = (-1.0, 1.0, -1.0, 1.0, -1.0, 1.0)
OPPOSITE = (1, 0, 3, 2, 5, 4)
SEND_FACES = (0, 1, 4, 5)
missing_id = 1 << 30

f32 = jnp.float32
bf16 = jnp.bfloat16


def shifted(value, axis, steps):
    count = lax.axis_size(axis)
    pairs = [(source, (source + steps) % count) for source in range(count)]
    return lax.ppermute(value, axis, pairs)


def lobatto_points(number):
    return -np.cos(np.pi * np.arange(number) / (number - 1))


def lagrange_weights(points):
    weights = np.ones(points.shape[0])
    for row_id in range(points.shape[0]):
        for col_id in range(points.shape[0]):
            if col_id != row_id:
                weights[row_id] = weights[row_id] / (points[row_id] - points[col_id])
    return weights


def derivative_matrix(points):
    weights = lagrange_weights(points)
    number = points.shape[0]
    matrix = np.zeros((number, number))
    for row_id in range(number):
        for col_id in range(number):
            if col_id != row_id:
                matrix[row_id, col_id] = (
                    weights[col_id] / weights[row_id] / (points[row_id] - points[col_id])
                )
        matrix[row_id, row_id] = -np.sum(matrix[row_id])
    return matrix


def interpolation_matrix(source, target):
    matrix = np.ones((target.shape[0], source.shape[0]))
    for col_id in range(source.shape[0]):
        for other_id in range(source.shape[0]):
            if other_id != col_id:
                matrix[:, col_id] = (
                    matrix[:, col_id]
                    * (target - source[other_id])
                    / (source[col_id] - source[other_id])
                )
    return matrix


def spread_three(matrix, identity):
    return (
        np.kron(matrix, np.kron(identity, identity)),
        np.kron(identity, np.kron(matrix, identity)),
        np.kron(identity, np.kron(identity, matrix)),
    )


def face_nodes(extent):
    grid = np.arange(extent**3).reshape(extent, extent, extent)
    last = extent - 1
    pieces = (grid[0], grid[last], grid[:, 0], grid[:, last], grid[:, :, 0], grid[:, :, last])
    return [piece.reshape(-1) for piece in pieces]


def to_bf16(x):
    return np.asarray(np.asarray(x, np.float32).astype(ml_dtypes.bfloat16))


def split_parts(x):
    x = np.asarray(x, np.float32)
    hi = x.astype(ml_dtypes.bfloat16)
    rest = x - hi.astype(np.float32)
    mid = rest.astype(ml_dtypes.bfloat16)
    lo = (rest - mid.astype(np.float32)).astype(ml_dtypes.bfloat16)
    return np.stack([hi, mid, lo])


def make_tables():
    fine_points = lobatto_points(P7)
    coarse_points = lobatto_points(P3)
    fine_derivs = spread_three(derivative_matrix(fine_points), np.eye(P7))
    coarse_derivs = spread_three(derivative_matrix(coarse_points), np.eye(P3))
    downward = interpolation_matrix(fine_points, coarse_points)
    upward = interpolation_matrix(coarse_points, fine_points)
    d7t = np.stack([to_bf16(m.T) for m in fine_derivs])
    d3t = np.stack([to_bf16(m).T for m in coarse_derivs])
    lift_table = to_bf16(np.kron(upward, np.kron(upward, upward)))
    projection = np.asarray(np.kron(downward, np.kron(downward, downward)), np.float32)
    mortar_up = np.asarray(np.kron(upward, upward), np.float32)
    mortar_down = np.asarray(np.kron(downward, downward), np.float32)
    nodes7 = face_nodes(P7)
    nodes3 = face_nodes(P3)
    n7 = P7**3
    n3 = P3**3
    g7 = np.zeros((n7, 6 * LANE), np.float32)
    tm = np.zeros((n3, 6 * LANE), np.float32)
    mds = np.zeros((6 * LANE, n3), np.float32)
    for side in range(6):
        for q, node in enumerate(nodes7[side]):
            g7[node, side * LANE + q] = 1.0
        for k, node in enumerate(nodes3[side]):
            tm[node, side * LANE : side * LANE + P7 * P7] = mortar_up[:, k]
            mds[side * LANE : side * LANE + P7 * P7, node] = mortar_down[k, :]
    tables = {
        "d7t": to_bf16(d7t),
        "d3t": to_bf16(d3t),
        "lift": lift_table,
        "mortar_up": mortar_up,
        "g7": to_bf16(g7),
        "tm": split_parts(tm),
        "mds": split_parts(mds),
        "pjt": split_parts(projection.T),
        "nodes7": nodes7,
        "nodes3": nodes3,
    }
    return tables


def _dot(a, b):
    return jnp.dot(a, b, preferred_element_type=f32)


def _split(x):
    hi = x.astype(bf16)
    rest = x - hi.astype(f32)
    mid = rest.astype(bf16)
    lo = (rest - mid.astype(f32)).astype(bf16)
    return hi, mid, lo


def _exact_left(x, table):
    hi, mid, lo = _split(x)
    return (_dot(hi, table) + _dot(mid, table)) + _dot(lo, table)


def _dot_t(a, b):
    return lax.dot_general(a, b, (((1,), (1,)), ((), ())), preferred_element_type=f32)


def _exact_left_t(x, table):
    hi, mid, lo = _split(x)
    return (_dot_t(hi, table) + _dot_t(mid, table)) + _dot_t(lo, table)


def _exact_right(table, x):
    hi, mid, lo = _split(x)
    return (_dot(table, hi) + _dot(table, mid)) + _dot(table, lo)


def _full_t(x, parts_ref):
    xh, xm, xl = _split(x)
    bh = parts_ref[0]
    bm = parts_ref[1]
    bl = parts_ref[2]
    return _dot_t(xh, bh) + (_dot_t(xh, bm) + _dot_t(xm, bh)) + (
        _dot_t(xh, bl) + _dot_t(xm, bm) + _dot_t(xl, bh)
    )


class View:
    def __init__(self, ref, start, rows, width, lane0):
        self.ref = ref
        self.start = start
        self.rows = rows
        self.width = width
        self.lane0 = lane0

    def __getitem__(self, k):
        if k is Ellipsis:
            k = 0
        top = self.start + k * self.rows
        return self.ref[top : top + self.rows, self.lane0 : self.lane0 + self.width]


def table_layout(rows, local):
    n7 = P7**3
    n3 = P3**3
    wide = 6 * LANE
    base = n7 + 6 * n3
    side = 4 * LANE
    return {
        "g7": (0, n7, wide, 0),
        "tm": (n7, n3, wide, 0),
        "mdst": (n7 + 3 * n3, n3, wide, 0),
        "dx": (base, n7, n7, 0),
        "lift_t": (base + n7, n3, n7, 0),
        "pj": (base + n7 + n3, n3, n7, 0),
        "byz": (base, LANE, LANE, 5 * LANE),
        "bcast": (base, rows, local, side),
        "sel": (base + rows, 3 * local, rows, side),
        "fsel": (base + rows + 3 * local, rows, local, side),
        "d3t": (base + 2 * rows + 3 * local, n3, n3, side),
    }


def table_rows():
    return P7**3 + 6 * P3**3 + P7**3 + 4 * P3**3


def table_views(tab_ref, rows, local):
    return {
        name: View(tab_ref, start, count, width, lane0)
        for name, (start, count, width, lane0) in table_layout(rows, local).items()
    }


def _full(x, parts_ref):
    xh, xm, xl = _split(x)
    bh = parts_ref[0]
    bm = parts_ref[1]
    bl = parts_ref[2]
    return _dot(xh, bh) + (_dot(xh, bm) + _dot(xm, bh)) + (
        _dot(xh, bl) + _dot(xm, bm) + _dot(xl, bh)
    )


def _rate_source(values, pre, stc, bc, sel, local):
    picked = _exact_right(sel, values)
    v0 = picked[0:local]
    v1 = picked[local : 2 * local]
    v2 = picked[2 * local : 3 * local]
    rate = pre * jnp.exp(-ACTIVATION * jnp.exp(-v0)) * v1 * v2
    return stc * _exact_right(bc, rate)


def recv_block(recv, side):
    ref = recv[side]
    if side in (4, 5):
        rows = ref.shape[0] // 2
        top = 0 if side == 4 else rows
        return ref[top : top + rows, :]
    return ref[...]


def write_sends(out_refs, send):
    rows = send.shape[0]
    out_refs[0][...] = send[:, 0:LANE]
    out_refs[1][...] = send[:, LANE : 2 * LANE]
    out_refs[2][0:rows, :] = send[:, 5 * LANE : 6 * LANE]
    out_refs[2][rows : 2 * rows, :] = send[:, 4 * LANE : 5 * LANE]


def stage_kernel(coarse, second, project, sends, local, *refs):
    refs = list(refs)

    def take():
        return refs.pop(0)

    u_ref = take()
    c_ref = take() if coarse else None
    bu_ref = take() if second else None
    bc_ref = take() if (second and coarse) else None
    recv = {s: take() for s in SEND_FACES}
    pl_ref = take()
    pr_ref = take()
    v7_ref = take()
    m7_ref = take()
    pre_ref = take()
    stc_ref = take()
    views = table_views(take(), u_ref.shape[0], local)
    bc_tab = views["bcast"]
    sel_tab = views["sel"]
    g7_ref = views["g7"]
    d3_ref = views["d3t"]
    mds_ref = views["mdst"]
    tm_ref = views["tm"]
    pj_ref = views["pj"]
    if coarse:
        v3_ref = take()
        m3_ref = take()
    if coarse or project:
        sw_ref = take()
    last = coarse and not sends
    if last:
        sel_l_ref = take()
        sel_r_ref = take()
        cnt_l_ref = take()
        cnt_r_ref = take()
    res7_ref = take()
    res3_ref = take() if coarse else None
    if project:
        take()
    out_u = take()
    out_c = take() if (coarse or project) else None
    out_send = [take() for _ in range(3)] if sends else None
    if last:
        pay_l_ref = take()
        pay_r_ref = take()

    pre = pre_ref[...]
    stc = stc_ref[...]
    bcast = bc_tab[...]
    sel = sel_tab[...]
    u = u_ref[...]
    trace7 = _dot(u.astype(bf16), g7_ref[...])
    if coarse:
        c = c_ref[...]
        trace3 = _full(c, tm_ref).astype(bf16).astype(f32)
        switched = sw_ref[...] > 0.5
        own = jnp.where(switched, trace3, trace7)
    else:
        own = trace7
    own_b = own.astype(bf16)
    near_blocks = []
    for side in range(6):
        other = OPPOSITE[side]
        block = own_b[:, other * LANE : (other + 1) * LANE]
        near = _dot(pl_ref[side], block)
        if side in SEND_FACES:
            k = SEND_FACES.index(side)
            near = near + _dot(pr_ref[k], recv_block(recv, side))
        near_blocks.append(near)
    near = jnp.concatenate(near_blocks, axis=1)

    result = res7_ref[...]
    jump = (P7 * (P7 - 1) / 2.0) * (m7_ref[...] * (trace7 - near))
    rate7 = result + _exact_left_t(jump, g7_ref[...])

    if coarse:
        result3 = res3_ref[...]
        jump3 = m3_ref[...] * (trace3 - near)
        rate3 = result3 + (P3 * (P3 - 1) / 2.0) * _full_t(jump3, mds_ref)

    if second:
        new_u = 0.5 * (bu_ref[...] + u + TIME_STEP * rate7)
    else:
        new_u = u + TIME_STEP * rate7
    out_u[...] = new_u
    new_c = None
    if coarse:
        if second:
            new_c = 0.5 * (bc_ref[...] + c + TIME_STEP * rate3)
        else:
            new_c = c + TIME_STEP * rate3
        if last:
            out_c[...] = jnp.where(sw_ref[...] > 0.5, new_c, 0.0)
            moved = sel_l_ref.shape[0]
            pay_l_ref[0:moved, :] = _exact_right(sel_l_ref[...], new_u)
            pay_r_ref[0:moved, :] = _exact_right(sel_r_ref[...], new_u)
            tail = (pay_l_ref.shape[0] - moved, pay_l_ref.shape[1])
            pay_l_ref[moved:, :] = jnp.broadcast_to(cnt_l_ref[0:1, 0:1], tail)
            pay_r_ref[moved:, :] = jnp.broadcast_to(cnt_r_ref[0:1, 0:1], tail)
        else:
            out_c[...] = new_c
    if project:
        new_c = _full_t(new_u, pj_ref)
        out_c[...] = new_c
    if sends:
        send7 = _dot(new_u.astype(bf16), g7_ref[...])
        if new_c is not None:
            send3 = _full(new_c, tm_ref).astype(bf16).astype(f32)
            send = jnp.where(sw_ref[...] > 0.5, send3, send7)
        else:
            send = send7
        write_sends(out_send, send.astype(bf16))


def _vmem():
    return pl.BlockSpec(memory_space=pltpu.VMEM)


def bulk_kernel(coarse, local, *refs):
    refs = list(refs)
    u_ref = refs.pop(0)
    c_ref = refs.pop(0) if coarse else None
    v7_ref, pre_ref, stc_ref = refs.pop(0), refs.pop(0), refs.pop(0)
    views = table_views(refs.pop(0), u_ref.shape[0], local)
    v3_ref = refs.pop(0) if coarse else None
    out7 = refs.pop(0)
    out3 = refs.pop(0) if coarse else None
    pre = pre_ref[...]
    stc = stc_ref[...]
    bcast = views["bcast"][...]
    sel = views["sel"][...]
    u = u_ref[...]
    fluxes = [(v7_ref[d].astype(f32) * u).astype(bf16) for d in range(3)]
    divergence = _dot(fluxes[0], views["dx"][0])
    by = views["byz"][0]
    bz = views["byz"][1]
    chunks = []
    for k in range(u.shape[1] // LANE):
        part = slice(k * LANE, (k + 1) * LANE)
        chunks.append(_dot(fluxes[1][:, part], by) + _dot(fluxes[2][:, part], bz))
    divergence = divergence + jnp.concatenate(chunks, axis=1)
    out7[...] = _rate_source(u, pre, stc, bcast, sel, local) - divergence
    if coarse:
        c = c_ref[...]
        div3 = None
        for d in range(3):
            flux3 = (v3_ref[d] * c).astype(bf16)
            term = _dot(flux3, views["d3t"][d])
            div3 = term if div3 is None else div3 + term
        out3[...] = _rate_source(c, pre, stc, bcast, sel, local) - div3


def run_bulk(coarse, local, inputs, out_shapes):
    return pl.pallas_call(
        functools.partial(bulk_kernel, coarse, local),
        out_shape=out_shapes,
        in_specs=[_vmem() for _ in inputs],
        out_specs=[_vmem() for _ in out_shapes],
        compiler_params=pltpu.CompilerParams(vmem_limit_bytes=24 * 1024 * 1024),
    )(*inputs)


def run_stage(flags, inputs, out_shapes):
    coarse, second, project, sends, local = flags
    kernel = functools.partial(stage_kernel, coarse, second, project, sends, local)
    return pl.pallas_call(
        kernel,
        out_shape=out_shapes,
        in_specs=[_vmem() for _ in inputs],
        out_specs=[_vmem() for _ in out_shapes],
        compiler_params=pltpu.CompilerParams(vmem_limit_bytes=48 * 1024 * 1024),
    )(*inputs)


def setup_kernel(local, fields, u_ref, vt_ref, packed_ref, tab_ref, v7_out, m7_out,
                 pre_out, stc_out, *send_refs):
    rows = local * fields
    views = table_views(tab_ref, rows, local)
    lift_ref = views["lift_t"]
    g7_ref = views["g7"]
    tm_ref = views["tm"]
    fsel_ref = views["fsel"]
    bcast = views["bcast"][...]
    lanes = lax.broadcasted_iota(jnp.int32, (local, 6 * LANE), 1) // LANE
    sign = jnp.where(lanes % 2 == 0, -1.0, 1.0)
    fvg = []
    mvg = []
    for d in range(3):
        vt = vt_ref[d]
        fv = _dot(vt, lift_ref[...]).astype(bf16)
        v7_out[d] = _dot(bcast, fv).astype(bf16)
        fvg.append(_dot(fv, g7_ref[...]))

    def by_block(parts):
        return jnp.where(lanes < 2, parts[0], jnp.where(lanes < 4, parts[1], parts[2]))

    m7 = jnp.minimum(sign * by_block(fvg), 0.0)
    m7_out[...] = _dot(bcast, m7.astype(bf16))
    eye16 = jnp.where(
        lax.broadcasted_iota(jnp.int32, (local, LANE), 0)
        == lax.broadcasted_iota(jnp.int32, (local, LANE), 1), 1.0, 0.0
    ).astype(bf16)
    p_hi, p_mid, p_lo = _split(packed_ref[...])
    packed = (_dot_t(eye16, p_hi) + _dot_t(eye16, p_mid)) + _dot_t(eye16, p_lo)
    pre_out[...] = packed[:, 7:8]
    stc_out[...] = _exact_right(fsel_ref[...], packed)[:, 8:9]
    write_sends(send_refs, _dot(u_ref[...].astype(bf16), g7_ref[...]).astype(bf16))


def near_kernel(local, fields, packed_ref, tab_ref, pl_out, pr_out, sw_out):
    rows = local * fields
    bcast = table_views(tab_ref, rows, local)["bcast"][...]
    eye16 = jnp.where(
        lax.broadcasted_iota(jnp.int32, (local, LANE), 0)
        == lax.broadcasted_iota(jnp.int32, (local, LANE), 1), 1.0, 0.0
    ).astype(bf16)
    packed = _dot_t(eye16, packed_ref[...].astype(bf16))
    rep = _dot(bcast, packed.astype(bf16))
    row_f = (lax.broadcasted_iota(jnp.int32, (rows, 1), 0) % fields).astype(f32)
    cols = lax.broadcasted_iota(jnp.int32, (rows, rows), 1).astype(f32)
    for side in range(6):
        code = rep[:, side : side + 1]
        far = code >= local
        target = (code - jnp.where(far, float(local), 0.0)) * fields + row_f
        hit = cols == target
        pl_out[side] = jnp.where(hit & ~far, 1.0, 0.0).astype(bf16)
        if side in SEND_FACES:
            pr_out[SEND_FACES.index(side)] = jnp.where(hit & far, 1.0, 0.0).astype(bf16)
    sw_out[...] = rep[:, 6:7]


def late_kernel(local, fields, vt_ref, tab_ref, after_ref, v3_out, m3_out):
    rows = local * fields
    views = table_views(tab_ref, rows, local)
    tm_ref = views["tm"]
    bcast = views["bcast"][...]
    lanes = lax.broadcasted_iota(jnp.int32, (local, 6 * LANE), 1) // LANE
    sign = jnp.where(lanes % 2 == 0, -1.0, 1.0)
    mvg = []
    for d in range(3):
        vt = vt_ref[d]
        v3_out[d] = _dot(bcast, vt)
        mvg.append((_dot(vt, tm_ref[0]) + _dot(vt, tm_ref[1])) + _dot(vt, tm_ref[2]))
    by_block = jnp.where(lanes < 2, mvg[0], jnp.where(lanes < 4, mvg[1], mvg[2]))
    m3_out[...] = _exact_right(bcast, jnp.minimum(sign * by_block, 0.0))


def move_kernel(local, fields, packed_ref, tab_ref, hinfo_out, cnt_l_out, cnt_r_out, sel_l_out,
                sel_r_out):
    rows = local * fields
    bcast = table_views(tab_ref, rows, local)["bcast"][...]
    eye16 = jnp.where(
        lax.broadcasted_iota(jnp.int32, (local, LANE), 0)
        == lax.broadcasted_iota(jnp.int32, (local, LANE), 1), 1.0, 0.0
    ).astype(bf16)
    p_hi, p_mid, p_lo = _split(packed_ref[...])
    packed = (_dot_t(eye16, p_hi) + _dot_t(eye16, p_mid)) + _dot_t(eye16, p_lo)
    curve_count = lax.axis_size("curve")
    curve_pos = lax.axis_index("curve")
    left_f = ((curve_pos + curve_count - 1) % curve_count).astype(f32)
    right_f = ((curve_pos + 1) % curve_count).astype(f32)
    first_f = jnp.where(curve_pos == 0, 1.0, 0.0)
    last_f = jnp.where(curve_pos == curve_count - 1, 1.0, 0.0)
    stay_sw = packed[:, 6:7] < 0.5
    go_left = (packed[:, 9:10] == left_f) & stay_sw
    go_right = (packed[:, 9:10] == right_f) & stay_sw
    stays = stay_sw & ~go_left & ~go_right
    lane16 = lax.broadcasted_iota(jnp.int32, (local, LANE), 1)
    marks = jnp.where(
        lane16 == 0, go_left.astype(f32),
        jnp.where(lane16 == 1, go_right.astype(f32), jnp.where(lane16 == 2, stays.astype(f32), 0.0)),
    ).astype(bf16)
    er = lax.broadcasted_iota(jnp.int32, (local, local), 0)
    ec = lax.broadcasted_iota(jnp.int32, (local, local), 1)
    before = _dot(jnp.where(ec < er, 1.0, 0.0).astype(bf16), marks)
    totals = _dot(jnp.ones((local, local), bf16), marks)
    info = jnp.where(lane16 < 3, marks.astype(f32), 0.0)
    for k in range(3):
        info = jnp.where(lane16 == 3 + k, before[:, k : k + 1], info)
    info = jnp.where(lane16 == 6, totals[:, 2:3], info)
    info = jnp.where(lane16 == 7, first_f, info)
    info = jnp.where(lane16 == 8, last_f, info)
    hinfo = _dot(bcast, info.astype(bf16))
    hinfo_out[...] = hinfo
    cnt_l_out[...] = jnp.broadcast_to(totals[0:1, 0:1], cnt_l_out.shape)
    cnt_r_out[...] = jnp.broadcast_to(totals[0:1, 1:2], cnt_r_out.shape)
    rf = lax.broadcasted_iota(jnp.int32, (rows, LANE), 0) % fields
    cc = lax.broadcasted_iota(jnp.int32, (rows, LANE), 1)
    eye = jnp.where(
        lax.broadcasted_iota(jnp.int32, (MOVE_CAP * fields, LANE), 0)
        == lax.broadcasted_iota(jnp.int32, (MOVE_CAP * fields, LANE), 1), 1.0, 0.0
    ).astype(bf16)
    for mark_lane, rank_lane, out in ((0, 3, sel_l_out), (1, 4, sel_r_out)):
        hit = (
            (hinfo[:, mark_lane : mark_lane + 1] > 0.5)
            & (hinfo[:, rank_lane : rank_lane + 1] == (cc // fields).astype(f32))
            & (rf == cc % fields)
            & (cc < MOVE_CAP * fields)
        )
        out[...] = _dot_t(eye, jnp.where(hit, 1.0, 0.0).astype(bf16)).astype(bf16)


def final_kernel(fields, hold, home_ref, from_l_ref, from_r_ref, hinfo_ref, out_ref):
    hinfo = hinfo_ref[...]
    moved = MOVE_CAP * fields
    n_l = from_l_ref[moved : moved + 1, 0:1]
    n_r = from_r_ref[moved : moved + 1, 0:1]
    n_h = hinfo[0:1, 6:7]
    first = hinfo[0:1, 7:8] > 0.5
    final = hinfo[0:1, 8:9] > 0.5
    off_l = jnp.where(first, n_h + n_r, jnp.where(final, n_r, 0.0))
    off_h = jnp.where(first, 0.0, jnp.where(final, n_r + n_l, n_l))
    off_r = jnp.where(first, n_h, jnp.where(final, 0.0, n_l + n_h))
    width = hold * fields
    eye = jnp.where(
        lax.broadcasted_iota(jnp.int32, (width, LANE), 0)
        == lax.broadcasted_iota(jnp.int32, (width, LANE), 1), 1.0, 0.0
    ).astype(bf16)

    def gather(values, valid, pos):
        count = values.shape[0]
        rf = lax.broadcasted_iota(jnp.int32, (count, LANE), 0) % fields
        cc = lax.broadcasted_iota(jnp.int32, (count, LANE), 1)
        hit = valid & (pos == (cc // fields).astype(f32)) & (rf == cc % fields) & (cc < width)
        pick = _dot_t(eye, jnp.where(hit, 1.0, 0.0).astype(bf16)).astype(bf16)
        return _exact_right(pick, values)

    total = gather(home_ref[...], hinfo[:, 2:3] > 0.5, off_h + hinfo[:, 5:6])
    slot = (lax.broadcasted_iota(jnp.int32, (moved, 1), 0) // fields).astype(f32)
    total = total + gather(from_l_ref[0:moved, :], slot < n_l, off_l + slot)
    total = total + gather(from_r_ref[0:moved, :], slot < n_r, off_r + slot)
    out_ref[...] = total


def setup_entry(local, fields, n_in, n_out, *refs):
    sources = refs[:n_in]
    outs = refs[n_in : n_in + n_out]
    n_tab = 1
    n_own = n_in - n_tab
    buffers = refs[n_in + n_out : n_in + n_out + n_own]
    sems = refs[n_in + n_out + n_own]
    targets = list(buffers) + list(outs[n_out - n_tab :])
    copies = [
        pltpu.make_async_copy(sources[i], targets[i], sems.at[i]) for i in range(n_in)
    ]
    for copy in copies:
        copy.start()
    for copy in copies:
        copy.wait()
    setup_kernel(local, fields, *targets, *outs[: n_out - n_tab])


def per_device(state, velocity, pre_exp, stoich, neighbours, switch, new_owner):
    tab = make_tables()
    local_count = state.shape[0]
    field_count = state.shape[1]
    rows = local_count * field_count
    curve_count = lax.axis_size("curve")
    curve_pos = lax.axis_index("curve")
    device_id = lax.axis_index("slab") * curve_count + curve_pos
    first_global = device_id * local_count
    positions = jnp.arange(local_count, dtype=jnp.int32)

    near_device = neighbours // local_count
    near_local = neighbours - near_device * local_count
    remote = near_device != device_id
    codes = (near_local + local_count * remote.astype(jnp.int32)).astype(f32)
    left_pos = (curve_pos + curve_count - 1) % curve_count
    right_pos = (curve_pos + 1) % curve_count
    sto_col = jnp.pad(stoich, (0, local_count - field_count))
    packed_t = jnp.concatenate(
        [
            jnp.transpose(codes),
            jnp.stack([switch.astype(f32), pre_exp, sto_col, new_owner.astype(f32)]),
        ]
    )
    packed = jnp.pad(packed_t, ((0, local_count - 10), (0, LANE - local_count)))
    fsel_np = np.arange(rows)[:, None] % field_count == np.arange(local_count)[None, :]
    vt = jnp.transpose(velocity, (0, 2, 1))
    row_elem = np.arange(rows) // field_count
    bcast_np = row_elem[:, None] == np.arange(local_count)[None, :]
    pick_rows = (np.arange(3)[:, None] + field_count * np.arange(local_count)[None, :]).reshape(-1)
    sel_np = pick_rows[:, None] == np.arange(rows)[None, :]
    n7 = P7**3
    n3 = P3**3
    layout = table_layout(rows, local_count)
    table_np = np.zeros((table_rows(), 6 * LANE), np.float32)
    for d in (1, 2):
        block = tab["d7t"][d][:LANE, :LANE].astype(np.float32)
        assert np.array_equal(
            tab["d7t"][d].astype(np.float32), np.kron(np.eye(n7 // LANE), block)
        )
    pieces = {
        "g7": tab["g7"][None],
        "tm": tab["tm"],
        "mdst": np.transpose(tab["mds"], (0, 2, 1)),
        "dx": tab["d7t"][0:1],
        "byz": np.stack([tab["d7t"][1][:LANE, :LANE], tab["d7t"][2][:LANE, :LANE]]),
        "lift_t": tab["lift"].T[None],
        "pj": np.transpose(tab["pjt"], (0, 2, 1)),
        "bcast": bcast_np[None],
        "sel": sel_np[None],
        "fsel": fsel_np[None],
        "d3t": tab["d3t"],
    }
    filled = np.zeros(table_np.shape, bool)
    for name, (start, count, width, lane0) in layout.items():
        parts = np.asarray(pieces[name], np.float32)
        for k in range(parts.shape[0]):
            window = (slice(start + k * count, start + (k + 1) * count), slice(lane0, lane0 + width))
            assert not filled[window].any()
            filled[window] = True
            table_np[window] = parts[k]
    table = jnp.asarray(to_bf16(table_np))

    send_shape = jax.ShapeDtypeStruct((rows, LANE), bf16)
    sends_shape = [send_shape, send_shape, jax.ShapeDtypeStruct((2 * rows, LANE), bf16)]
    u_shape = jax.ShapeDtypeStruct((rows, P7**3), f32)
    c_shape = jax.ShapeDtypeStruct((rows, P3**3), f32)

    def exchange(sends):
        face0, face1, faces_z = sends
        from_prev = shifted(faces_z, "slab", 1)
        if lax.axis_size("slab") == 2:
            from_next = from_prev
        else:
            from_next = shifted(faces_z, "slab", -1)
        return [shifted(face1, "curve", 1), shifted(face0, "curve", -1), from_prev, from_next]

    setup_out = [
        jax.ShapeDtypeStruct((3, rows, P7**3), bf16),
        jax.ShapeDtypeStruct((rows, 6 * LANE), f32),
        jax.ShapeDtypeStruct((local_count, 1), f32),
        jax.ShapeDtypeStruct((rows, 1), f32),
    ] + sends_shape
    near_out = [
        jax.ShapeDtypeStruct((6, rows, rows), bf16),
        jax.ShapeDtypeStruct((len(SEND_FACES), rows, rows), bf16),
        jax.ShapeDtypeStruct((rows, 1), f32),
    ]
    late_out = [
        jax.ShapeDtypeStruct((3, rows, P3**3), f32),
        jax.ShapeDtypeStruct((rows, 6 * LANE), f32),
    ]
    move_out = [
        jax.ShapeDtypeStruct((rows, LANE), f32),
        jax.ShapeDtypeStruct((8, LANE), f32),
        jax.ShapeDtypeStruct((8, LANE), f32),
        jax.ShapeDtypeStruct((MOVE_CAP * field_count, rows), bf16),
        jax.ShapeDtypeStruct((MOVE_CAP * field_count, rows), bf16),
    ]
    setup_out = setup_out + [jax.ShapeDtypeStruct(table.shape, table.dtype)]
    u0 = state.reshape(rows, P7**3)
    setup_in = [u0, vt, packed, table]
    res = pl.pallas_call(
        functools.partial(setup_entry, local_count, field_count, len(setup_in), len(setup_out)),
        out_shape=setup_out,
        in_specs=[pl.BlockSpec(memory_space=pltpu.HBM) for _ in setup_in],
        out_specs=[_vmem() for _ in setup_out],
        scratch_shapes=[pltpu.VMEM(x.shape, x.dtype) for x in setup_in[:3]]
        + [pltpu.SemaphoreType.DMA((len(setup_in),))],
        compiler_params=pltpu.CompilerParams(vmem_limit_bytes=24 * 1024 * 1024),
    )(*setup_in)
    v7, m7, pre, stc = res[:4]
    sends = res[4:7]
    table = res[7]
    p_local, p_remote, sw = pl.pallas_call(
        functools.partial(near_kernel, local_count, field_count),
        out_shape=near_out,
        in_specs=[_vmem() for _ in range(2)],
        out_specs=[_vmem() for _ in near_out],
        compiler_params=pltpu.CompilerParams(vmem_limit_bytes=24 * 1024 * 1024),
    )(packed, table)
    hinfo, cnt_l, cnt_r, sel_l, sel_r = pl.pallas_call(
        functools.partial(move_kernel, local_count, field_count),
        out_shape=move_out,
        in_specs=[_vmem() for _ in range(2)],
        out_specs=[_vmem() for _ in move_out],
        compiler_params=pltpu.CompilerParams(vmem_limit_bytes=24 * 1024 * 1024),
    )(packed, table)
    common = [p_local, p_remote, v7, m7, pre, stc, table]
    recv = exchange(sends)
    bulk_tabs = [v7, pre, stc, table]
    (bulk7,) = run_bulk(False, local_count, [u0] + bulk_tabs, [u_shape])
    res = run_stage(
        (False, False, False, True, local_count),
        [u0] + recv + common + [bulk7],
        [u_shape] + sends_shape,
    )
    first, sends = res[0], res[1:]
    v3, m3 = pl.pallas_call(
        functools.partial(late_kernel, local_count, field_count),
        out_shape=late_out,
        in_specs=[_vmem() for _ in range(3)],
        out_specs=[_vmem() for _ in late_out],
        compiler_params=pltpu.CompilerParams(vmem_limit_bytes=24 * 1024 * 1024),
    )(vt, table, first)
    recv = exchange(sends)
    (bulk7,) = run_bulk(False, local_count, [first] + bulk_tabs, [u_shape])
    res = run_stage(
        (False, True, True, True, local_count),
        [first, u0] + recv + common + [sw, bulk7, v3],
        [u_shape, c_shape] + sends_shape,
    )
    after, coarse, sends = res[0], res[1], res[2:]
    recv = exchange(sends)
    mixed_tail = [v3, m3, sw]
    bulk7, bulk3 = run_bulk(True, local_count, [after, coarse] + bulk_tabs + [v3], [u_shape, c_shape])
    res = run_stage(
        (True, False, False, True, local_count),
        [after, coarse] + recv + common + mixed_tail + [bulk7, bulk3],
        [u_shape, c_shape] + sends_shape,
    )
    first7, first3, sends = res[0], res[1], res[2:]
    recv = exchange(sends)
    pay_shape = jax.ShapeDtypeStruct((MOVE_CAP * field_count + 8, P7**3), f32)
    bulk7, bulk3 = run_bulk(True, local_count, [first7, first3] + bulk_tabs + [v3], [u_shape, c_shape])
    res = run_stage(
        (True, True, False, False, local_count),
        [first7, first3, after, coarse] + recv + common + mixed_tail
        + [sel_l, sel_r, cnt_l, cnt_r, bulk7, bulk3],
        [u_shape, c_shape, pay_shape, pay_shape],
    )
    final7, final3, pay_l, pay_r = res
    from_right = shifted(pay_l, "curve", -1)
    from_left = shifted(pay_r, "curve", 1)
    held = pl.pallas_call(
        functools.partial(final_kernel, field_count, HOLD7),
        out_shape=jax.ShapeDtypeStruct((HOLD7 * field_count, P7**3), f32),
        in_specs=[_vmem() for _ in range(4)],
        out_specs=_vmem(),
    )(final7, from_left, from_right, hinfo)
    state7_out = held.reshape(HOLD7, field_count, P7**3)
    state3_out = final3.reshape(local_count, field_count * P3**3)
    return (state7_out, state3_out)


def solution(mesh):
    return jax.shard_map(
        per_device,
        mesh=mesh,
        in_specs=(
            P(("slab", "curve"), None, None),
            P(None, None, ("slab", "curve")),
            P(("slab", "curve")),
            P(),
            P(("slab", "curve"), None),
            P(("slab", "curve")),
            P(("slab", "curve")),
        ),
        out_specs=(P(("slab", "curve"), None, None), P(("slab", "curve"), None)),
        check_vma=False,
    )
```
